32 devices in a mesh: real: 2 (over y), slab: 4 (over z), pencil: 2 (over x), sub: 2 (over core).
Axes of the slice: x: 2, y: 2, z: 4, core: 2. Of those that a mesh axis runs over, the one named last changes fastest.
Arguments:
- permeability: float32 [128, 64, 256], P(('real', 'slab'), ('pencil', 'sub')), parts along dimension 0, may hold values from 0.1 to 10
- source: float32 [128, 64, 256], P(('real', 'slab'), ('pencil', 'sub')), parts along dimension 0, may hold values from -24 to 24
- pressure: float32 [128, 64, 256], P(('real', 'slab'), ('pencil', 'sub')), parts along dimension 0, may hold values from -24 to 24
- aggregate: int32 [128], P('real'), parts along dimension 0, may hold values from 0 to 31, as said below
Outputs:
- pressure_out: float32 [128, 64, 256], P(('real', 'slab'), ('pencil', 'sub')), parts along dimension 0
The draws below stay inside these ranges and needn't reach their ends.
There are 2 independent parts, one for each index of `real`. The reference program is written for one: setup_inputs(seed, part) draws one part's arguments, and reference() takes and returns one part's arrays. A program takes and returns all parts, laid end to end along the dimension named above; each array names one. Nothing has to cross between parts.
Inputs may be any that keep to these rules, and one draw needn't show every extreme that they name: `aggregate`: never falls along its dimension; each value covers 1 to 4 consecutive positions, some value exactly 4; positions k * 16 - 1 and k * 16 always hold the same value.
All inputs are finite; a program needn't handle non-finite values.
Results may differ from the reference program's by a relative error of at most 0.000068.
Values sent between devices are 32-bit elements; how exact they have to be, the bound alone decides.
No kernel may reach another device: no remote copies, remote signals or barrier semaphores. Data moves between devices by JAX's collectives and lax.ppermute only.
A program may use at most 64 MiB of HBM per device.

```python
import math
import jax
import jax.numpy as jnp

NZ = 256
NU = 2
NCS = 4
NX = 64
NY = 64
NXC = 32


def draw_aggregate(key, part):
    patterns = jnp.array([[2, 2, 2, 2], [1, 1, 2, 4], [4, 1, 1, 2], [1, 4, 1, 2], [3, 1, 1, 3], [1, 3, 2, 2], [2, 1, 1, 4]], dtype=jnp.int32)
    block_count = NX // 8 - 1
    picks = jax.random.randint(jax.random.fold_in(key, 11), (block_count,), 0, 7)
    picks = jnp.concatenate([jnp.ones((1,), jnp.int32), picks[1:]])
    block_lens = patterns[picks].reshape(-1)
    lengths = jnp.concatenate([jnp.ones((1,), jnp.int32), block_lens, jnp.array([2, 2, 3], dtype=jnp.int32)])
    ends = jnp.cumsum(lengths).astype(jnp.int32)
    positions = jnp.arange(NX, dtype=jnp.int32)
    return jnp.sum((ends[None, :] <= positions[:, None]).astype(jnp.int32), axis=1).astype(jnp.int32)


def block_scale(own_key, shape, split, smallest, top_value):
    factor_of, own = 1.0, jax.random.fold_in(own_key, 6)
    for dim, parts in split:
        steps = jnp.exp(jax.random.uniform(jax.random.fold_in(own, dim), (parts,), jnp.float32, smallest / len(split), top_value / len(split)))
        factor_of = factor_of * jnp.repeat(steps, shape[dim] // parts).reshape([-1 if axis == dim else 1 for axis in range(len(shape))])
    return factor_of


def normal_values(key, shape, scale, reach, shards=(), kind=jnp.bfloat16):
    values = jax.random.normal(key, shape, jnp.float32) * scale
    if len(shards) > 0:
        values = block_scale(key, shape, shards, -0.22, 0.18) * values
    return jnp.clip(values, min=-reach, max=reach).astype(kind)


def setup_inputs(seed: int = 0, part: int = 0) -> dict:
    keys = jax.random.split(jax.random.key(seed), 5)
    part_keys = jax.random.split(jax.random.fold_in(keys[4], part), 5)
    return {
        "permeability": jnp.clip(jnp.exp(math.log(10.0) - 4.6051702 * jax.random.uniform(part_keys[0], (NX, NY, NZ), jnp.float32) ** block_scale(part_keys[0], (NX, NY, NZ), ((0, 4), (1, 4)), -0.2, 0.2)), 0.1, 10.0),
        "source": normal_values(part_keys[1], (NX, NY, NZ), 4.0, 24.0, ((0, 4), (1, 4)), jnp.float32),
        "pressure": normal_values(part_keys[2], (NX, NY, NZ), 4.0, 24.0, ((0, 4), (1, 4)), jnp.float32),
        "aggregate": draw_aggregate(jax.random.fold_in(jax.random.fold_in(keys[4], part), 71), part),
    }


OMEGA = 0.8


def harmonic(lower_k, upper_k):
    return 2.0 * lower_k * upper_k / (lower_k + upper_k)


def geometry(permeability):
    count_x, count_y, count_z = permeability.shape
    kind = permeability.dtype
    face_x = harmonic(permeability[:-1], permeability[1:])
    face_y = harmonic(permeability[:, :-1], permeability[:, 1:])
    face_z = harmonic(permeability[:, :, :-1], permeability[:, :, 1:])
    zero_x = jnp.zeros_like(permeability[:1])
    zero_y = jnp.zeros_like(permeability[:, :1])
    zero_z = jnp.zeros_like(permeability[:, :, :1])
    face_west = jnp.concatenate([zero_x, face_x], axis=0)
    face_east = jnp.concatenate([face_x, zero_x], axis=0)
    face_south = jnp.concatenate([zero_y, face_y], axis=1)
    face_north = jnp.concatenate([face_y, zero_y], axis=1)
    face_below = jnp.concatenate([zero_z, face_z], axis=2)
    face_above = jnp.concatenate([face_z, zero_z], axis=2)
    index_x = jnp.arange(count_x)
    index_y = jnp.arange(count_y)
    index_z = jnp.arange(count_z)
    ends_x = (index_x == 0).astype(kind) + (index_x == count_x - 1).astype(kind)
    ends_y = (index_y == 0).astype(kind) + (index_y == count_y - 1).astype(kind)
    ends_z = (index_z == 0).astype(kind) + (index_z == count_z - 1).astype(kind)
    edges = ends_x[:, None, None] + ends_y[None, :, None] + ends_z[None, None, :]
    boundary = 2.0 * permeability * edges
    diagonal = face_west + face_east + face_south + face_north + face_below + face_above + boundary
    return face_west, face_east, face_south, face_north, face_below, face_above, boundary, diagonal


def apply_fine(field_in, faces_all):
    face_west, face_east, face_south, face_north, face_below, face_above, boundary, diagonal = faces_all
    padded = jnp.pad(field_in, 1)
    center = padded[1:-1, 1:-1, 1:-1]
    beside_all = face_west * padded[:-2, 1:-1, 1:-1] + face_east * padded[2:, 1:-1, 1:-1]
    beside_all = beside_all + face_south * padded[1:-1, :-2, 1:-1] + face_north * padded[1:-1, 2:, 1:-1]
    beside_all = beside_all + face_below * padded[1:-1, 1:-1, :-2] + face_above * padded[1:-1, 1:-1, 2:]
    return diagonal * center - beside_all


def reference(permeability, source, pressure, aggregate):
    faces_all = geometry(permeability)
    face_east = faces_all[1]
    face_north = faces_all[3]
    face_above = faces_all[5]
    boundary = faces_all[6]
    diagonal = faces_all[7]
    count_x, count_y, count_z = permeability.shape
    half_y = count_y // 2
    half_z = count_z // 2
    for sweep_index in range(NU):
        pressure = pressure + OMEGA * (source - apply_fine(pressure, faces_all)) / diagonal
    residual = source - apply_fine(pressure, faces_all)

    def pair_sum(block):
        return block.reshape(count_x, half_y, 2, half_z, 2).sum(axis=(2, 4))

    def by_plane(block):
        return jax.ops.segment_sum(block, aggregate, num_segments=NXC)

    crossing = jnp.concatenate([aggregate[:-1] != aggregate[1:], jnp.zeros((1,), dtype=bool)]).astype(permeability.dtype)
    coarse_rhs = by_plane(pair_sum(residual))
    coarse_east = by_plane(pair_sum(face_east * crossing[:, None, None]))
    coarse_north = by_plane(face_north[:, 1::2].reshape(count_x, half_y, half_z, 2).sum(axis=3))
    coarse_above = by_plane(face_above[:, :, 1::2].reshape(count_x, half_y, 2, half_z).sum(axis=2))
    coarse_bound = by_plane(pair_sum(boundary))
    coarse_west = jnp.concatenate([jnp.zeros_like(coarse_east[:1]), coarse_east[:-1]], axis=0)
    coarse_south = jnp.concatenate([jnp.zeros_like(coarse_north[:, :1]), coarse_north[:, :-1]], axis=1)
    coarse_below = jnp.concatenate([jnp.zeros_like(coarse_above[:, :, :1]), coarse_above[:, :, :-1]], axis=2)
    coarse_diag = coarse_east + coarse_west + coarse_north + coarse_south + coarse_above + coarse_below + coarse_bound
    correction = jnp.zeros_like(coarse_rhs)
    for sweep_index in range(NCS):
        padded = jnp.pad(correction, 1)
        center = padded[1:-1, 1:-1, 1:-1]
        beside_all = coarse_east * padded[2:, 1:-1, 1:-1] + coarse_west * padded[:-2, 1:-1, 1:-1]
        beside_all = beside_all + coarse_north * padded[1:-1, 2:, 1:-1] + coarse_south * padded[1:-1, :-2, 1:-1]
        beside_all = beside_all + coarse_above * padded[1:-1, 1:-1, 2:] + coarse_below * padded[1:-1, 1:-1, :-2]
        correction = center + OMEGA * (coarse_rhs - (coarse_diag * center - beside_all)) / coarse_diag
    spread = jnp.take(correction, aggregate, axis=0)
    spread = jnp.repeat(jnp.repeat(spread, 2, axis=1), 2, axis=2)
    pressure = pressure + spread
    for sweep_index in range(NU):
        pressure = pressure + OMEGA * (source - apply_fine(pressure, faces_all)) / diagonal
    return pressure
```

```python
import jax
import jax.numpy as jnp
from jax import lax
from jax.sharding import PartitionSpec as P

NU = 2
NCS = 4


OMEGA = 0.8


def padded(array, sides, width):
    for axis, dim in sides:
        count, length = (lax.axis_size(axis), array.shape[dim])
        up = [(i, (i + 1) % count) for i in range(count - 1)]
        down = [(j, i) for i, j in up]
        last = lax.slice_in_dim(array, length - width, length, axis=dim)
        leading = lax.slice_in_dim(array, 0, width, axis=dim)
        before = lax.ppermute(last, axis, up)
        after = lax.ppermute(leading, axis, down)
        array = jnp.concatenate([before, array, after], axis=dim)
    return array


def passed_along(array, axis, by):
    count = lax.axis_size(axis)
    pairs = [(i, i + by) for i in range(count) if 0 <= i + by < count]
    return lax.ppermute(array, axis, pairs)


def harmonic(lower_k, upper_k, inside):
    denom_sum = jnp.where(inside, lower_k + upper_k, 1.0)
    return jnp.where(inside, 2.0 * lower_k * upper_k / denom_sum, 0.0)


def geometry(perm_ext, glob_x, glob_y, inside_x, inside_y, total_x, total_y):
    count_z = perm_ext.shape[2]
    both_x = (inside_x[:-1] & inside_x[1:])[:, None, None] & inside_y[None, :, None]
    both_y = (inside_y[:-1] & inside_y[1:])[None, :, None] & inside_x[:, None, None]
    plane_in = inside_x[:, None, None] & inside_y[None, :, None]
    face_x = harmonic(perm_ext[:-1], perm_ext[1:], both_x)
    face_y = harmonic(perm_ext[:, :-1], perm_ext[:, 1:], both_y)
    face_z = harmonic(perm_ext[:, :, :-1], perm_ext[:, :, 1:], plane_in)
    cell_perm = perm_ext[1:-1, 1:-1]
    face_west = face_x[:-1, 1:-1]
    face_east = face_x[1:, 1:-1]
    face_south = face_y[1:-1, :-1]
    face_north = face_y[1:-1, 1:]
    zero_plane = jnp.zeros_like(cell_perm[:, :, :1])
    face_below = jnp.concatenate([zero_plane, face_z[1:-1, 1:-1]], axis=2)
    face_above = jnp.concatenate([face_z[1:-1, 1:-1], zero_plane], axis=2)
    cell_x = glob_x[1:-1]
    cell_y = glob_y[1:-1]
    index_z = jnp.arange(count_z)
    ends_x = (cell_x == 0).astype(jnp.float32) + (cell_x == total_x - 1).astype(jnp.float32)
    ends_y = (cell_y == 0).astype(jnp.float32) + (cell_y == total_y - 1).astype(jnp.float32)
    ends_z = (index_z == 0).astype(jnp.float32) + (index_z == count_z - 1).astype(jnp.float32)
    edges = ends_x[:, None, None] + ends_y[None, :, None] + ends_z[None, None, :]
    boundary = 2.0 * cell_perm * edges
    diagonal = face_west + face_east + face_south + face_north + face_below + face_above + boundary
    cell_in = plane_in[1:-1, 1:-1]
    safe_diag = jnp.where(cell_in, diagonal, 1.0)
    return (
        face_west,
        face_east,
        face_south,
        face_north,
        face_below,
        face_above,
        boundary,
        safe_diag,
    )


def apply_fine(ext_field, faces_now):
    face_west, face_east, face_south, face_north, face_below, face_above, boundary, safe_diag = (
        faces_now
    )
    center = ext_field[1:-1, 1:-1]
    zero_plane = jnp.zeros_like(center[:, :, :1])
    below_vals = jnp.concatenate([zero_plane, center[:, :, :-1]], axis=2)
    above_vals = jnp.concatenate([center[:, :, 1:], zero_plane], axis=2)
    beside_all = face_west * ext_field[:-2, 1:-1] + face_east * ext_field[2:, 1:-1]
    beside_all = beside_all + face_south * ext_field[1:-1, :-2] + face_north * ext_field[1:-1, 2:]
    beside_all = beside_all + face_below * below_vals + face_above * above_vals
    return (center, safe_diag * center - beside_all)


def crop(array, rim):
    if rim == 0:
        return array
    return array[rim : array.shape[0] - rim, rim : array.shape[1] - rim]


def sweeps(field_ext, source_ext, faces_ext, count, width):
    def rim_of(array):
        return (array.shape[0] - width) // 2

    for sweep_index in range(count):
        out_rim = rim_of(field_ext) - 1
        faces_now = tuple(crop(member, rim_of(member) - out_rim) for member in faces_ext)
        center, product = apply_fine(field_ext, faces_now)
        source_now = crop(source_ext, rim_of(source_ext) - out_rim)
        field_ext = center + OMEGA * (source_now - product) / faces_now[7]
    return field_ext


def body(permeability, source, pressure, aggregate):
    width_x, width_y, depth_cells = permeability.shape
    slab_index = lax.axis_index("slab")
    slab_count = lax.axis_size("slab")
    row_index = lax.axis_index(("pencil", "sub"))
    row_count = lax.axis_size(("pencil", "sub"))
    total_x = width_x * slab_count
    total_y = width_y * row_count
    sides = (("slab", 0), (("pencil", "sub"), 1))
    stacked_sides = (("slab", 1), (("pencil", "sub"), 2))
    fine_rim = NU + 1
    ext_all = padded(jnp.stack([permeability, source, pressure]), stacked_sides, fine_rim)
    perm_ext = ext_all[0]
    source_ext = crop(ext_all[1], 1)
    glob_x = slab_index * width_x - fine_rim + jnp.arange(width_x + 2 * fine_rim)
    glob_y = row_index * width_y - fine_rim + jnp.arange(width_y + 2 * fine_rim)
    inside_x = (glob_x >= 0) & (glob_x < total_x)
    inside_y = (glob_y >= 0) & (glob_y < total_y)
    faces_ext = geometry(perm_ext, glob_x, glob_y, inside_x, inside_y, total_x, total_y)
    smooth_ext = sweeps(ext_all[2], source_ext, faces_ext, NU, width_x)
    faces_zero = tuple(crop(member, fine_rim - 1) for member in faces_ext)
    pressure = crop(smooth_ext, 1)
    center, product = apply_fine(smooth_ext, faces_zero)
    residual = source - product
    half_y = width_y // 2
    half_z = depth_cells // 2

    def pair_sum(block_in):
        return block_in.reshape(width_x, half_y, 2, half_z, 2).sum(axis=(2, 4))

    padded_ids = jnp.concatenate([aggregate[:1], aggregate, aggregate[-1:]])
    ext_ids = lax.dynamic_slice_in_dim(padded_ids, slab_index * width_x, width_x + 2)
    local_ids = ext_ids[1:-1]
    straddles = (slab_index > 0) & (ext_ids[0] == local_ids[0])
    first_id = local_ids[0] + straddles.astype(jnp.int32)
    count_live = local_ids[-1] - first_id + 1
    slot_ids = local_ids - first_id
    crossing = (local_ids != ext_ids[2:]).astype(jnp.float32)
    face_east = faces_zero[1]
    face_north = faces_zero[3]
    face_above = faces_zero[5]
    boundary = faces_zero[6]
    east_part = pair_sum(face_east * crossing[:, None, None])
    north_part = face_north[:, 1::2].reshape(width_x, half_y, half_z, 2).sum(axis=3)
    above_part = face_above[:, :, 1::2].reshape(width_x, half_y, 2, half_z).sum(axis=2)
    stacked = jnp.stack([pair_sum(residual), east_part, north_part, above_part, pair_sum(boundary)])
    slot_range = jnp.arange(width_x)
    owner_map = (slot_ids[:, None] == slot_range[None, :]).astype(jnp.float32)
    spill_map = (slot_ids == -1).astype(jnp.float32)
    coarse = jnp.einsum("qxjk,xs->qsjk", stacked, owner_map, precision=lax.Precision.HIGHEST)
    edge_sums = jnp.einsum("qxjk,x->qjk", stacked, spill_map, precision=lax.Precision.HIGHEST)
    arriving = passed_along(edge_sums, "slab", -1)
    last_slot = (slot_range == count_live - 1).astype(jnp.float32)
    coarse = coarse + arriving[:, None] * last_slot[None, :, None, None]

    def coarse_extend(coarse_block, rim_width):
        tail_planes = lax.dynamic_slice_in_dim(
            coarse_block, count_live - rim_width, rim_width, axis=1
        )
        sent_block = jnp.concatenate([coarse_block, tail_planes], axis=1)
        wide_block = padded(sent_block, (("slab", 1), (("pencil", "sub"), 2)), rim_width)
        ahead_planes = wide_block[:, width_x + 2 * rim_width :]
        base_block = wide_block[:, : width_x + 2 * rim_width]
        return lax.dynamic_update_slice_in_dim(
            base_block, ahead_planes, rim_width + count_live, axis=1
        )

    coarse_rim = NCS
    coef_ext = coarse_extend(coarse, coarse_rim)
    coarse_corr = jnp.zeros((width_x + 2 * NCS, half_y + 2 * NCS, half_z), jnp.float32)
    for sweep_index in range(NCS):
        out_rim = NCS - 1 - sweep_index
        start_at = coarse_rim - out_rim
        size_x = width_x + 2 * out_rim
        size_y = half_y + 2 * out_rim

        def region(offset_x, offset_y):
            return coef_ext[
                :,
                start_at + offset_x : start_at + offset_x + size_x,
                start_at + offset_y : start_at + offset_y + size_y,
            ]

        here_coef = region(0, 0)
        coarse_rhs = here_coef[0]
        coarse_east = here_coef[1]
        coarse_north = here_coef[2]
        coarse_above = here_coef[3]
        coarse_bound = here_coef[4]
        coarse_west = region(-1, 0)[1]
        coarse_south = region(0, -1)[2]
        zero_plane = jnp.zeros_like(coarse_above[:, :, :1])
        coarse_below = jnp.concatenate([zero_plane, coarse_above[:, :, :-1]], axis=2)
        diag_coarse = (
            coarse_east
            + coarse_west
            + coarse_north
            + coarse_south
            + coarse_above
            + coarse_below
            + coarse_bound
        )
        safe_coarse = jnp.where(diag_coarse > 0, diag_coarse, 1.0)
        coarse_center = coarse_corr[1:-1, 1:-1]
        above_vals = jnp.concatenate([coarse_center[:, :, 1:], zero_plane], axis=2)
        below_vals = jnp.concatenate([zero_plane, coarse_center[:, :, :-1]], axis=2)
        beside_all = coarse_east * coarse_corr[2:, 1:-1] + coarse_west * coarse_corr[:-2, 1:-1]
        beside_all = (
            beside_all
            + coarse_north * coarse_corr[1:-1, 2:]
            + coarse_south * coarse_corr[1:-1, :-2]
        )
        beside_all = beside_all + coarse_above * above_vals + coarse_below * below_vals
        coarse_corr = (
            coarse_center
            + OMEGA * (coarse_rhs - (diag_coarse * coarse_center - beside_all)) / safe_coarse
        )
    last_corr = lax.dynamic_index_in_dim(coarse_corr, count_live - 1, axis=0, keepdims=False)
    corr_wide = jnp.concatenate([passed_along(last_corr, "slab", 1)[None], coarse_corr], axis=0)
    pick_map = ((slot_ids + 1)[:, None] == jnp.arange(width_x + 1)[None, :]).astype(jnp.float32)
    correction = jnp.einsum("xs,sjk->xjk", pick_map, corr_wide, precision=lax.Precision.HIGHEST)
    correction = jnp.repeat(jnp.repeat(correction, 2, axis=1), 2, axis=2)
    pressure = pressure + correction
    post_ext = padded(pressure, sides, NU)
    return sweeps(post_ext, source_ext, faces_ext, NU, width_x)


def solution(mesh):
    in_specs = (
        P(("real", "slab"), ("pencil", "sub"), None),
        P(("real", "slab"), ("pencil", "sub"), None),
        P(("real", "slab"), ("pencil", "sub"), None),
        P("real"),
    )
    out_specs = P(("real", "slab"), ("pencil", "sub"), None)
    return jax.shard_map(body, mesh=mesh, in_specs=in_specs, out_specs=out_specs, check_vma=False)
```

```python
import jax
import jax.numpy as jnp
from jax import lax
from jax.sharding import PartitionSpec as P

NU = 2
NCS = 4


OMEGA = 0.8


def padded(array, sides, width):
    for axis, dim in sides:
        count, length = (lax.axis_size(axis), array.shape[dim])
        up = [(i, (i + 1) % count) for i in range(count - 1)]
        down = [(j, i) for i, j in up]
        last = lax.slice_in_dim(array, length - width, length, axis=dim)
        leading = lax.slice_in_dim(array, 0, width, axis=dim)
        before = lax.ppermute(last, axis, up)
        after = lax.ppermute(leading, axis, down)
        array = jnp.concatenate([before, array, after], axis=dim)
    return array


def passed_along(array, axis, by):
    count = lax.axis_size(axis)
    pairs = [(i, i + by) for i in range(count) if 0 <= i + by < count]
    return lax.ppermute(array, axis, pairs)


def harmonic(lower_k, upper_k, inside):
    denom_sum = jnp.where(inside, lower_k + upper_k, 1.0)
    return jnp.where(inside, 2.0 * lower_k * upper_k / denom_sum, 0.0)


def geometry(perm_ext, glob_x, glob_y, inside_x, inside_y, total_x, total_y):
    count_z = perm_ext.shape[2]
    both_x = (inside_x[:-1] & inside_x[1:])[:, None, None] & inside_y[None, :, None]
    both_y = (inside_y[:-1] & inside_y[1:])[None, :, None] & inside_x[:, None, None]
    plane_in = inside_x[:, None, None] & inside_y[None, :, None]
    face_x = harmonic(perm_ext[:-1], perm_ext[1:], both_x)
    face_y = harmonic(perm_ext[:, :-1], perm_ext[:, 1:], both_y)
    face_z = harmonic(perm_ext[:, :, :-1], perm_ext[:, :, 1:], plane_in)
    cell_perm = perm_ext[1:-1, 1:-1]
    face_west = face_x[:-1, 1:-1]
    face_east = face_x[1:, 1:-1]
    face_south = face_y[1:-1, :-1]
    face_north = face_y[1:-1, 1:]
    zero_plane = jnp.zeros_like(cell_perm[:, :, :1])
    face_below = jnp.concatenate([zero_plane, face_z[1:-1, 1:-1]], axis=2)
    face_above = jnp.concatenate([face_z[1:-1, 1:-1], zero_plane], axis=2)
    cell_x = glob_x[1:-1]
    cell_y = glob_y[1:-1]
    index_z = jnp.arange(count_z)
    ends_x = (cell_x == 0).astype(jnp.float32) + (cell_x == total_x - 1).astype(jnp.float32)
    ends_y = (cell_y == 0).astype(jnp.float32) + (cell_y == total_y - 1).astype(jnp.float32)
    ends_z = (index_z == 0).astype(jnp.float32) + (index_z == count_z - 1).astype(jnp.float32)
    edges = ends_x[:, None, None] + ends_y[None, :, None] + ends_z[None, None, :]
    boundary = 2.0 * cell_perm * edges
    diagonal = face_west + face_east + face_south + face_north + face_below + face_above + boundary
    cell_in = plane_in[1:-1, 1:-1]
    safe_diag = jnp.where(cell_in, diagonal, 1.0)
    return (
        face_west,
        face_east,
        face_south,
        face_north,
        face_below,
        face_above,
        boundary,
        safe_diag,
    )


def apply_fine(ext_field, faces_now):
    face_west, face_east, face_south, face_north, face_below, face_above, boundary, safe_diag = (
        faces_now
    )
    center = ext_field[1:-1, 1:-1]
    zero_plane = jnp.zeros_like(center[:, :, :1])
    below_vals = jnp.concatenate([zero_plane, center[:, :, :-1]], axis=2)
    above_vals = jnp.concatenate([center[:, :, 1:], zero_plane], axis=2)
    beside_all = face_west * ext_field[:-2, 1:-1] + face_east * ext_field[2:, 1:-1]
    beside_all = beside_all + face_south * ext_field[1:-1, :-2] + face_north * ext_field[1:-1, 2:]
    beside_all = beside_all + face_below * below_vals + face_above * above_vals
    return (center, safe_diag * center - beside_all)


def crop(array, rim):
    if rim == 0:
        return array
    return array[rim : array.shape[0] - rim, rim : array.shape[1] - rim]


def sweeps(field_ext, source_ext, faces_ext, count, width):
    def rim_of(array):
        return (array.shape[0] - width) // 2

    for sweep_index in range(count):
        out_rim = rim_of(field_ext) - 1
        faces_now = tuple(crop(member, rim_of(member) - out_rim) for member in faces_ext)
        center, product = apply_fine(field_ext, faces_now)
        source_now = crop(source_ext, rim_of(source_ext) - out_rim)
        field_ext = center + OMEGA * (source_now - product) / faces_now[7]
    return field_ext


def body(permeability, source, pressure, aggregate):
    width_x, width_y, depth_cells = permeability.shape
    slab_index = lax.axis_index("slab")
    slab_count = lax.axis_size("slab")
    row_index = lax.axis_index(("pencil", "sub"))
    row_count = lax.axis_size(("pencil", "sub"))
    total_x = width_x * slab_count
    total_y = width_y * row_count
    sides = (("slab", 0), (("pencil", "sub"), 1))
    stacked_sides = (("slab", 1), (("pencil", "sub"), 2))
    fine_rim = NU + 1
    ext_all = padded(jnp.stack([permeability, source, pressure]), stacked_sides, fine_rim)
    perm_ext = ext_all[0]
    source_ext = crop(ext_all[1], 1)
    glob_x = slab_index * width_x - fine_rim + jnp.arange(width_x + 2 * fine_rim)
    glob_y = row_index * width_y - fine_rim + jnp.arange(width_y + 2 * fine_rim)
    inside_x = (glob_x >= 0) & (glob_x < total_x)
    inside_y = (glob_y >= 0) & (glob_y < total_y)
    faces_ext = geometry(perm_ext, glob_x, glob_y, inside_x, inside_y, total_x, total_y)
    smooth_ext = sweeps(ext_all[2], source_ext, faces_ext, NU, width_x)
    faces_zero = tuple(crop(member, fine_rim - 1) for member in faces_ext)
    pressure = crop(smooth_ext, 1)
    center, product = apply_fine(smooth_ext, faces_zero)
    residual = source - product
    half_y = width_y // 2
    half_z = depth_cells // 2

    padded_ids = jnp.concatenate([aggregate[:1], aggregate, aggregate[-1:]])
    ext_ids = lax.dynamic_slice_in_dim(padded_ids, slab_index * width_x, width_x + 2)
    local_ids = ext_ids[1:-1]
    straddles = (slab_index > 0) & (ext_ids[0] == local_ids[0])
    first_id = local_ids[0] + straddles.astype(jnp.int32)
    count_live = local_ids[-1] - first_id + 1
    slot_ids = local_ids - first_id
    crossing = (local_ids != ext_ids[2:]).astype(jnp.float32)
    face_east = faces_zero[1]
    face_north = faces_zero[3]
    face_above = faces_zero[5]
    boundary = faces_zero[6]
    index_z = jnp.arange(depth_cells)[:, None]
    coarse_z = jnp.arange(half_z)[None, :]
    pair_z = (index_z // 2 == coarse_z).astype(jnp.float32)
    odd_z = (index_z == 2 * coarse_z + 1).astype(jnp.float32)
    cells = width_x * width_y

    def z_sum(block_in, pick_z):
        flat = block_in.reshape(cells, depth_cells)
        return jnp.dot(flat, pick_z, precision=lax.Precision.HIGHEST)

    z_parts = jnp.stack(
        [
            z_sum(residual, pair_z),
            z_sum(face_east * crossing[:, None, None], pair_z),
            z_sum(face_north, pair_z),
            z_sum(face_above, odd_z),
            z_sum(boundary, pair_z),
        ]
    )
    slot_wide = jnp.arange(width_x + 1)
    owner_wide = ((slot_ids + 1)[:, None] == slot_wide[None, :]).astype(jnp.float32)
    index_y = jnp.arange(width_y)[:, None]
    coarse_y = jnp.arange(half_y)[None, :]
    pair_y = (index_y // 2 == coarse_y).astype(jnp.float32)
    odd_y = (index_y == 2 * coarse_y + 1).astype(jnp.float32)

    def xy_map(pick_y):
        joint = owner_wide[:, None, :, None] * pick_y[None, :, None, :]
        return joint.reshape(cells, (width_x + 1) * half_y)

    spread_map = xy_map(pair_y)
    north_map = xy_map(odd_y)
    maps = jnp.stack([spread_map, spread_map, north_map, spread_map, spread_map])
    slot_sums = jnp.einsum("qnm,qnl->qml", maps, z_parts, precision=lax.Precision.HIGHEST)
    slot_sums = slot_sums.reshape(5, width_x + 1, half_y, half_z)
    coarse = slot_sums[:, 1:]
    edge_sums = slot_sums[:, 0]
    arriving = passed_along(edge_sums, "slab", -1)
    slot_range = jnp.arange(width_x)
    last_slot = (slot_range == count_live - 1).astype(jnp.float32)
    coarse = coarse + arriving[:, None] * last_slot[None, :, None, None]

    def coarse_extend(coarse_block, rim_width):
        tail_planes = lax.dynamic_slice_in_dim(
            coarse_block, count_live - rim_width, rim_width, axis=1
        )
        sent_block = jnp.concatenate([coarse_block, tail_planes], axis=1)
        wide_block = padded(sent_block, (("slab", 1), (("pencil", "sub"), 2)), rim_width)
        ahead_planes = wide_block[:, width_x + 2 * rim_width :]
        base_block = wide_block[:, : width_x + 2 * rim_width]
        return lax.dynamic_update_slice_in_dim(
            base_block, ahead_planes, rim_width + count_live, axis=1
        )

    coarse_rim = NCS
    coef_ext = coarse_extend(coarse, coarse_rim)
    coarse_corr = jnp.zeros((width_x + 2 * NCS, half_y + 2 * NCS, half_z), jnp.float32)
    for sweep_index in range(NCS):
        out_rim = NCS - 1 - sweep_index
        start_at = coarse_rim - out_rim
        size_x = width_x + 2 * out_rim
        size_y = half_y + 2 * out_rim

        def region(offset_x, offset_y):
            return coef_ext[
                :,
                start_at + offset_x : start_at + offset_x + size_x,
                start_at + offset_y : start_at + offset_y + size_y,
            ]

        here_coef = region(0, 0)
        coarse_rhs = here_coef[0]
        coarse_east = here_coef[1]
        coarse_north = here_coef[2]
        coarse_above = here_coef[3]
        coarse_bound = here_coef[4]
        coarse_west = region(-1, 0)[1]
        coarse_south = region(0, -1)[2]
        zero_plane = jnp.zeros_like(coarse_above[:, :, :1])
        coarse_below = jnp.concatenate([zero_plane, coarse_above[:, :, :-1]], axis=2)
        diag_coarse = (
            coarse_east
            + coarse_west
            + coarse_north
            + coarse_south
            + coarse_above
            + coarse_below
            + coarse_bound
        )
        safe_coarse = jnp.where(diag_coarse > 0, diag_coarse, 1.0)
        coarse_center = coarse_corr[1:-1, 1:-1]
        above_vals = jnp.concatenate([coarse_center[:, :, 1:], zero_plane], axis=2)
        below_vals = jnp.concatenate([zero_plane, coarse_center[:, :, :-1]], axis=2)
        beside_all = coarse_east * coarse_corr[2:, 1:-1] + coarse_west * coarse_corr[:-2, 1:-1]
        beside_all = (
            beside_all
            + coarse_north * coarse_corr[1:-1, 2:]
            + coarse_south * coarse_corr[1:-1, :-2]
        )
        beside_all = beside_all + coarse_above * above_vals + coarse_below * below_vals
        coarse_corr = (
            coarse_center
            + OMEGA * (coarse_rhs - (diag_coarse * coarse_center - beside_all)) / safe_coarse
        )
    last_corr = lax.dynamic_index_in_dim(coarse_corr, count_live - 1, axis=0, keepdims=False)
    corr_wide = jnp.concatenate([passed_along(last_corr, "slab", 1)[None], coarse_corr], axis=0)
    corr_z = jnp.dot(
        corr_wide.reshape((width_x + 1) * half_y, half_z), pair_z.T, precision=lax.Precision.HIGHEST
    )
    correction = jnp.dot(spread_map, corr_z, precision=lax.Precision.HIGHEST)
    correction = correction.reshape(width_x, width_y, depth_cells)
    pressure = pressure + correction
    post_ext = padded(pressure, sides, NU)
    return sweeps(post_ext, source_ext, faces_ext, NU, width_x)


def solution(mesh):
    in_specs = (
        P(("real", "slab"), ("pencil", "sub"), None),
        P(("real", "slab"), ("pencil", "sub"), None),
        P(("real", "slab"), ("pencil", "sub"), None),
        P("real"),
    )
    out_specs = P(("real", "slab"), ("pencil", "sub"), None)
    return jax.shard_map(body, mesh=mesh, in_specs=in_specs, out_specs=out_specs, check_vma=False)
```

```python
import jax
import jax.numpy as jnp
from jax import lax
from jax.sharding import PartitionSpec as P

NU = 2
NCS = 4


OMEGA = 0.8


def padded(array, sides, width):
    for axis, dim in sides:
        count, length = (lax.axis_size(axis), array.shape[dim])
        up = [(i, (i + 1) % count) for i in range(count - 1)]
        down = [(j, i) for i, j in up]
        last = lax.slice_in_dim(array, length - width, length, axis=dim)
        leading = lax.slice_in_dim(array, 0, width, axis=dim)
        before = lax.ppermute(last, axis, up)
        after = lax.ppermute(leading, axis, down)
        array = jnp.concatenate([before, array, after], axis=dim)
    return array


def passed_along(array, axis, by):
    count = lax.axis_size(axis)
    pairs = [(i, i + by) for i in range(count) if 0 <= i + by < count]
    return lax.ppermute(array, axis, pairs)


def harmonic(lower_k, upper_k, inside):
    denom_sum = jnp.where(inside, lower_k + upper_k, 1.0)
    return jnp.where(inside, 2.0 * lower_k * upper_k / denom_sum, 0.0)


def geometry(perm_ext, glob_x, glob_y, inside_x, inside_y, total_x, total_y):
    count_z = perm_ext.shape[2]
    both_x = (inside_x[:-1] & inside_x[1:])[:, None, None] & inside_y[None, :, None]
    both_y = (inside_y[:-1] & inside_y[1:])[None, :, None] & inside_x[:, None, None]
    plane_in = inside_x[:, None, None] & inside_y[None, :, None]
    face_x = harmonic(perm_ext[:-1], perm_ext[1:], both_x)
    face_y = harmonic(perm_ext[:, :-1], perm_ext[:, 1:], both_y)
    face_z = harmonic(perm_ext[:, :, :-1], perm_ext[:, :, 1:], plane_in)
    cell_perm = perm_ext[1:-1, 1:-1]
    face_west = face_x[:-1, 1:-1]
    face_east = face_x[1:, 1:-1]
    face_south = face_y[1:-1, :-1]
    face_north = face_y[1:-1, 1:]
    zero_plane = jnp.zeros_like(cell_perm[:, :, :1])
    face_below = jnp.concatenate([zero_plane, face_z[1:-1, 1:-1]], axis=2)
    face_above = jnp.concatenate([face_z[1:-1, 1:-1], zero_plane], axis=2)
    cell_x = glob_x[1:-1]
    cell_y = glob_y[1:-1]
    index_z = jnp.arange(count_z)
    ends_x = (cell_x == 0).astype(jnp.float32) + (cell_x == total_x - 1).astype(jnp.float32)
    ends_y = (cell_y == 0).astype(jnp.float32) + (cell_y == total_y - 1).astype(jnp.float32)
    ends_z = (index_z == 0).astype(jnp.float32) + (index_z == count_z - 1).astype(jnp.float32)
    edges = ends_x[:, None, None] + ends_y[None, :, None] + ends_z[None, None, :]
    boundary = 2.0 * cell_perm * edges
    diagonal = face_west + face_east + face_south + face_north + face_below + face_above + boundary
    cell_in = plane_in[1:-1, 1:-1]
    safe_diag = jnp.where(cell_in, diagonal, 1.0)
    return (
        face_west,
        face_east,
        face_south,
        face_north,
        face_below,
        face_above,
        boundary,
        safe_diag,
    )


def apply_fine(ext_field, faces_now):
    face_west, face_east, face_south, face_north, face_below, face_above, boundary, safe_diag = (
        faces_now
    )
    center = ext_field[1:-1, 1:-1]
    zero_plane = jnp.zeros_like(center[:, :, :1])
    below_vals = jnp.concatenate([zero_plane, center[:, :, :-1]], axis=2)
    above_vals = jnp.concatenate([center[:, :, 1:], zero_plane], axis=2)
    beside_all = face_west * ext_field[:-2, 1:-1] + face_east * ext_field[2:, 1:-1]
    beside_all = beside_all + face_south * ext_field[1:-1, :-2] + face_north * ext_field[1:-1, 2:]
    beside_all = beside_all + face_below * below_vals + face_above * above_vals
    return (center, safe_diag * center - beside_all)


def crop(array, rim):
    if rim == 0:
        return array
    return array[rim : array.shape[0] - rim, rim : array.shape[1] - rim]


def sweeps(field_ext, source_ext, faces_ext, count, width):
    def rim_of(array):
        return (array.shape[0] - width) // 2

    for sweep_index in range(count):
        out_rim = rim_of(field_ext) - 1
        faces_now = tuple(crop(member, rim_of(member) - out_rim) for member in faces_ext)
        center, product = apply_fine(field_ext, faces_now)
        source_now = crop(source_ext, rim_of(source_ext) - out_rim)
        field_ext = center + OMEGA * (source_now - product) / faces_now[7]
    return field_ext


def body(permeability, source, pressure, aggregate):
    width_x, width_y, depth_cells = permeability.shape
    slab_index = lax.axis_index("slab")
    slab_count = lax.axis_size("slab")
    row_index = lax.axis_index(("pencil", "sub"))
    row_count = lax.axis_size(("pencil", "sub"))
    total_x = width_x * slab_count
    total_y = width_y * row_count
    sides = (("slab", 0), (("pencil", "sub"), 1))
    stacked_sides = (("slab", 1), (("pencil", "sub"), 2))
    fine_rim = NU + 1
    ext_all = padded(jnp.stack([permeability, source, pressure]), stacked_sides, fine_rim)
    perm_ext = ext_all[0]
    source_ext = crop(ext_all[1], 1)
    glob_x = slab_index * width_x - fine_rim + jnp.arange(width_x + 2 * fine_rim)
    glob_y = row_index * width_y - fine_rim + jnp.arange(width_y + 2 * fine_rim)
    inside_x = (glob_x >= 0) & (glob_x < total_x)
    inside_y = (glob_y >= 0) & (glob_y < total_y)
    faces_ext = geometry(perm_ext, glob_x, glob_y, inside_x, inside_y, total_x, total_y)
    smooth_ext = sweeps(ext_all[2], source_ext, faces_ext, NU, width_x)
    faces_zero = tuple(crop(member, fine_rim - 1) for member in faces_ext)
    pressure = crop(smooth_ext, 1)
    center, product = apply_fine(smooth_ext, faces_zero)
    residual = source - product
    half_y = width_y // 2
    half_z = depth_cells // 2

    padded_ids = jnp.concatenate([aggregate[:1], aggregate, aggregate[-1:]])
    ext_ids = lax.dynamic_slice_in_dim(padded_ids, slab_index * width_x, width_x + 2)
    local_ids = ext_ids[1:-1]
    straddles = (slab_index > 0) & (ext_ids[0] == local_ids[0])
    first_id = local_ids[0] + straddles.astype(jnp.int32)
    count_live = local_ids[-1] - first_id + 1
    slot_ids = local_ids - first_id
    crossing = (local_ids != ext_ids[2:]).astype(jnp.float32)
    face_east = faces_zero[1]
    face_north = faces_zero[3]
    face_above = faces_zero[5]
    boundary = faces_zero[6]
    index_z = jnp.arange(depth_cells)[:, None]
    coarse_z = jnp.arange(half_z)[None, :]
    pair_z = (index_z // 2 == coarse_z).astype(jnp.float32)
    odd_z = (index_z == 2 * coarse_z + 1).astype(jnp.float32)
    cells = width_x * width_y

    def z_sum(block_in, pick_z):
        flat = block_in.reshape(cells, depth_cells)
        return jnp.dot(flat, pick_z, precision=lax.Precision.HIGHEST)

    z_parts = jnp.stack(
        [
            z_sum(residual, pair_z),
            z_sum(face_east * crossing[:, None, None], pair_z),
            z_sum(face_north, pair_z),
            z_sum(face_above, odd_z),
            z_sum(boundary, pair_z),
        ]
    )
    slot_wide = jnp.arange(width_x + 1)
    owner_wide = ((slot_ids + 1)[:, None] == slot_wide[None, :]).astype(jnp.float32)
    index_y = jnp.arange(width_y)[:, None]
    coarse_y = jnp.arange(half_y)[None, :]
    pair_y = (index_y // 2 == coarse_y).astype(jnp.float32)
    odd_y = (index_y == 2 * coarse_y + 1).astype(jnp.float32)

    def xy_map(pick_y):
        joint = owner_wide[:, None, :, None] * pick_y[None, :, None, :]
        return joint.reshape(cells, (width_x + 1) * half_y)

    spread_map = xy_map(pair_y)
    north_map = xy_map(odd_y)
    maps = jnp.stack([spread_map, spread_map, north_map, spread_map, spread_map])
    slot_sums = jnp.einsum("qnm,qnl->qml", maps, z_parts, precision=lax.Precision.HIGHEST)
    slot_sums = slot_sums.reshape(5, width_x + 1, half_y, half_z)
    coarse = slot_sums[:, 1:]
    edge_sums = slot_sums[:, 0]
    slot_range = jnp.arange(width_x)
    last_slot = (slot_range == count_live - 1).astype(jnp.float32)
    tail_planes = lax.dynamic_slice_in_dim(coarse, count_live - NCS, NCS, axis=1)
    head_planes = jnp.concatenate([coarse[:, :NCS], edge_sums[:, None]], axis=1)
    from_prev = passed_along(tail_planes, "slab", 1)
    from_next = passed_along(head_planes, "slab", -1)
    coarse = coarse + from_next[:, NCS][:, None] * last_slot[None, :, None, None]
    prev_last = (jnp.arange(NCS) == NCS - 1).astype(jnp.float32)
    from_prev = from_prev + edge_sums[:, None] * prev_last[None, :, None, None]
    x_ext = jnp.concatenate([from_prev, coarse, jnp.zeros_like(tail_planes)], axis=1)
    x_ext = lax.dynamic_update_slice_in_dim(x_ext, from_next[:, :NCS], NCS + count_live, axis=1)
    coarse_rim = NCS
    coef_ext = padded(x_ext, ((("pencil", "sub"), 2),), coarse_rim)
    coarse_corr = jnp.zeros((width_x + 2 * NCS, half_y + 2 * NCS, half_z), jnp.float32)
    for sweep_index in range(NCS):
        out_rim = NCS - 1 - sweep_index
        start_at = coarse_rim - out_rim
        size_x = width_x + 2 * out_rim
        size_y = half_y + 2 * out_rim

        def region(offset_x, offset_y):
            return coef_ext[
                :,
                start_at + offset_x : start_at + offset_x + size_x,
                start_at + offset_y : start_at + offset_y + size_y,
            ]

        here_coef = region(0, 0)
        coarse_rhs = here_coef[0]
        coarse_east = here_coef[1]
        coarse_north = here_coef[2]
        coarse_above = here_coef[3]
        coarse_bound = here_coef[4]
        coarse_west = region(-1, 0)[1]
        coarse_south = region(0, -1)[2]
        zero_plane = jnp.zeros_like(coarse_above[:, :, :1])
        coarse_below = jnp.concatenate([zero_plane, coarse_above[:, :, :-1]], axis=2)
        diag_coarse = (
            coarse_east
            + coarse_west
            + coarse_north
            + coarse_south
            + coarse_above
            + coarse_below
            + coarse_bound
        )
        safe_coarse = jnp.where(diag_coarse > 0, diag_coarse, 1.0)
        coarse_center = coarse_corr[1:-1, 1:-1]
        above_vals = jnp.concatenate([coarse_center[:, :, 1:], zero_plane], axis=2)
        below_vals = jnp.concatenate([zero_plane, coarse_center[:, :, :-1]], axis=2)
        beside_all = coarse_east * coarse_corr[2:, 1:-1] + coarse_west * coarse_corr[:-2, 1:-1]
        beside_all = (
            beside_all
            + coarse_north * coarse_corr[1:-1, 2:]
            + coarse_south * coarse_corr[1:-1, :-2]
        )
        beside_all = beside_all + coarse_above * above_vals + coarse_below * below_vals
        coarse_corr = (
            coarse_center
            + OMEGA * (coarse_rhs - (diag_coarse * coarse_center - beside_all)) / safe_coarse
        )
    last_corr = lax.dynamic_index_in_dim(coarse_corr, count_live - 1, axis=0, keepdims=False)
    corr_wide = jnp.concatenate([jnp.zeros_like(last_corr)[None], coarse_corr], axis=0)
    corr_z = jnp.dot(
        corr_wide.reshape((width_x + 1) * half_y, half_z), pair_z.T, precision=lax.Precision.HIGHEST
    )
    correction = jnp.dot(spread_map, corr_z, precision=lax.Precision.HIGHEST)
    base = pressure + correction.reshape(width_x, width_y, depth_cells)
    last_z = jnp.dot(last_corr, pair_z.T, precision=lax.Precision.HIGHEST)
    last_fine = jnp.dot(pair_y, last_z, precision=lax.Precision.HIGHEST)
    up_block = jnp.concatenate([base[width_x - NU :], last_fine[None]], axis=0)
    below_prev = passed_along(up_block, "slab", 1)
    above_next = passed_along(base[:NU], "slab", -1)
    from_owner = (slot_ids == -1).astype(jnp.float32)
    own = base + from_owner[:, None, None] * below_prev[NU][None]
    tail_ids = jnp.concatenate([aggregate, jnp.full((NU,), -1, aggregate.dtype)])
    next_ids = lax.dynamic_slice_in_dim(tail_ids, (slab_index + 1) * width_x, NU)
    to_owner = (next_ids == local_ids[-1]).astype(jnp.float32)
    high_halo = above_next + to_owner[:, None, None] * last_fine[None]
    post_x = jnp.concatenate([below_prev[:NU], own, high_halo], axis=0)
    post_ext = padded(post_x, ((("pencil", "sub"), 1),), NU)
    return sweeps(post_ext, source_ext, faces_ext, NU, width_x)


def solution(mesh):
    in_specs = (
        P(("real", "slab"), ("pencil", "sub"), None),
        P(("real", "slab"), ("pencil", "sub"), None),
        P(("real", "slab"), ("pencil", "sub"), None),
        P("real"),
    )
    out_specs = P(("real", "slab"), ("pencil", "sub"), None)
    return jax.shard_map(body, mesh=mesh, in_specs=in_specs, out_specs=out_specs, check_vma=False)
```

```python
import jax
import jax.numpy as jnp
from jax import lax
from jax.sharding import PartitionSpec as P

NU = 2
NCS = 4


OMEGA = 0.8


def padded(array, sides, width):
    for axis, dim in sides:
        count, length = (lax.axis_size(axis), array.shape[dim])
        up = [(i, (i + 1) % count) for i in range(count - 1)]
        down = [(j, i) for i, j in up]
        last = lax.slice_in_dim(array, length - width, length, axis=dim)
        leading = lax.slice_in_dim(array, 0, width, axis=dim)
        before = lax.ppermute(last, axis, up)
        after = lax.ppermute(leading, axis, down)
        array = jnp.concatenate([before, array, after], axis=dim)
    return array


def passed_along(array, axis, by):
    count = lax.axis_size(axis)
    pairs = [(i, i + by) for i in range(count) if 0 <= i + by < count]
    return lax.ppermute(array, axis, pairs)


def harmonic(lower_k, upper_k, inside):
    denom_sum = jnp.where(inside, lower_k + upper_k, 1.0)
    return jnp.where(inside, 2.0 * lower_k * upper_k / denom_sum, 0.0)


def geometry(perm_ext, glob_x, glob_y, inside_x, inside_y, total_x, total_y):
    count_z = perm_ext.shape[2]
    both_x = (inside_x[:-1] & inside_x[1:])[:, None, None] & inside_y[None, :, None]
    both_y = (inside_y[:-1] & inside_y[1:])[None, :, None] & inside_x[:, None, None]
    plane_in = inside_x[:, None, None] & inside_y[None, :, None]
    face_x = harmonic(perm_ext[:-1], perm_ext[1:], both_x)
    face_y = harmonic(perm_ext[:, :-1], perm_ext[:, 1:], both_y)
    face_z = harmonic(perm_ext[:, :, :-1], perm_ext[:, :, 1:], plane_in)
    cell_perm = perm_ext[1:-1, 1:-1]
    face_west = face_x[:-1, 1:-1]
    face_east = face_x[1:, 1:-1]
    face_south = face_y[1:-1, :-1]
    face_north = face_y[1:-1, 1:]
    zero_plane = jnp.zeros_like(cell_perm[:, :, :1])
    face_below = jnp.concatenate([zero_plane, face_z[1:-1, 1:-1]], axis=2)
    face_above = jnp.concatenate([face_z[1:-1, 1:-1], zero_plane], axis=2)
    cell_x = glob_x[1:-1]
    cell_y = glob_y[1:-1]
    index_z = jnp.arange(count_z)
    ends_x = (cell_x == 0).astype(jnp.float32) + (cell_x == total_x - 1).astype(jnp.float32)
    ends_y = (cell_y == 0).astype(jnp.float32) + (cell_y == total_y - 1).astype(jnp.float32)
    ends_z = (index_z == 0).astype(jnp.float32) + (index_z == count_z - 1).astype(jnp.float32)
    edges = ends_x[:, None, None] + ends_y[None, :, None] + ends_z[None, None, :]
    boundary = 2.0 * cell_perm * edges
    diagonal = face_west + face_east + face_south + face_north + face_below + face_above + boundary
    cell_in = plane_in[1:-1, 1:-1]
    safe_diag = jnp.where(cell_in, diagonal, 1.0)
    return (
        face_west,
        face_east,
        face_south,
        face_north,
        face_below,
        face_above,
        boundary,
        safe_diag,
    )


def apply_fine(ext_field, faces_now):
    face_west, face_east, face_south, face_north, face_below, face_above, boundary, safe_diag = (
        faces_now
    )
    center = ext_field[1:-1, 1:-1]
    zero_plane = jnp.zeros_like(center[:, :, :1])
    below_vals = jnp.concatenate([zero_plane, center[:, :, :-1]], axis=2)
    above_vals = jnp.concatenate([center[:, :, 1:], zero_plane], axis=2)
    beside_all = face_west * ext_field[:-2, 1:-1] + face_east * ext_field[2:, 1:-1]
    beside_all = beside_all + face_south * ext_field[1:-1, :-2] + face_north * ext_field[1:-1, 2:]
    beside_all = beside_all + face_below * below_vals + face_above * above_vals
    return (center, safe_diag * center - beside_all)


def crop(array, rim):
    if rim == 0:
        return array
    return array[rim : array.shape[0] - rim, rim : array.shape[1] - rim]


def sweeps(field_ext, source_ext, faces_ext, count, width):
    def rim_of(array):
        return (array.shape[0] - width) // 2

    for sweep_index in range(count):
        out_rim = rim_of(field_ext) - 1
        faces_now = tuple(crop(member, rim_of(member) - out_rim) for member in faces_ext)
        center, product = apply_fine(field_ext, faces_now)
        source_now = crop(source_ext, rim_of(source_ext) - out_rim)
        field_ext = center + OMEGA * (source_now - product) / faces_now[7]
    return field_ext


def body(permeability, source, pressure, aggregate):
    width_x, width_y, depth_cells = permeability.shape
    slab_index = lax.axis_index("slab")
    slab_count = lax.axis_size("slab")
    row_index = lax.axis_index(("pencil", "sub"))
    row_count = lax.axis_size(("pencil", "sub"))
    total_x = width_x * slab_count
    total_y = width_y * row_count
    sides = (("slab", 0), (("pencil", "sub"), 1))
    stacked_sides = (("slab", 1), (("pencil", "sub"), 2))
    fine_rim = NU + 1
    ext_all = padded(jnp.stack([permeability, source, pressure]), stacked_sides, fine_rim)
    perm_ext = ext_all[0]
    source_ext = crop(ext_all[1], 1)
    glob_x = slab_index * width_x - fine_rim + jnp.arange(width_x + 2 * fine_rim)
    glob_y = row_index * width_y - fine_rim + jnp.arange(width_y + 2 * fine_rim)
    inside_x = (glob_x >= 0) & (glob_x < total_x)
    inside_y = (glob_y >= 0) & (glob_y < total_y)
    faces_ext = geometry(perm_ext, glob_x, glob_y, inside_x, inside_y, total_x, total_y)
    smooth_ext = sweeps(ext_all[2], source_ext, faces_ext, NU, width_x)
    faces_zero = tuple(crop(member, fine_rim - 1) for member in faces_ext)
    pressure = crop(smooth_ext, 1)
    center, product = apply_fine(smooth_ext, faces_zero)
    residual = source - product
    half_y = width_y // 2
    half_z = depth_cells // 2

    padded_ids = jnp.concatenate([aggregate[:1], aggregate, aggregate[-1:]])
    ext_ids = lax.dynamic_slice_in_dim(padded_ids, slab_index * width_x, width_x + 2)
    local_ids = ext_ids[1:-1]
    straddles = (slab_index > 0) & (ext_ids[0] == local_ids[0])
    first_id = local_ids[0] + straddles.astype(jnp.int32)
    count_live = local_ids[-1] - first_id + 1
    slot_ids = local_ids - first_id
    crossing = (local_ids != ext_ids[2:]).astype(jnp.float32)
    face_east = faces_zero[1]
    face_north = faces_zero[3]
    face_above = faces_zero[5]
    boundary = faces_zero[6]
    index_z = jnp.arange(depth_cells)[:, None]
    coarse_z = jnp.arange(half_z)[None, :]
    pair_z = (index_z // 2 == coarse_z).astype(jnp.float32)
    odd_z = (index_z == 2 * coarse_z + 1).astype(jnp.float32)
    cells = width_x * width_y

    def z_sum(block_in, pick_z):
        flat = block_in.reshape(cells, depth_cells)
        return jnp.dot(flat, pick_z, precision=lax.Precision.HIGHEST)

    z_parts = jnp.stack(
        [
            z_sum(residual, pair_z),
            z_sum(face_east * crossing[:, None, None], pair_z),
            z_sum(face_north, pair_z),
            z_sum(face_above, odd_z),
            z_sum(boundary, pair_z),
        ]
    )
    slot_wide = jnp.arange(width_x + 1)
    owner_wide = ((slot_ids + 1)[:, None] == slot_wide[None, :]).astype(jnp.float32)
    index_y = jnp.arange(width_y)[:, None]
    coarse_y = jnp.arange(half_y)[None, :]
    pair_y = (index_y // 2 == coarse_y).astype(jnp.float32)
    odd_y = (index_y == 2 * coarse_y + 1).astype(jnp.float32)

    def xy_map(pick_y):
        joint = owner_wide[:, None, :, None] * pick_y[None, :, None, :]
        return joint.reshape(cells, (width_x + 1) * half_y)

    spread_map = xy_map(pair_y)
    north_map = xy_map(odd_y)
    maps = jnp.stack([spread_map, spread_map, north_map, spread_map, spread_map])
    slot_sums = jnp.einsum("qnm,qnl->qml", maps, z_parts, precision=lax.Precision.HIGHEST)
    slot_sums = slot_sums.reshape(5, width_x + 1, half_y, half_z)
    coarse = slot_sums[:, 1:]
    edge_sums = slot_sums[:, 0]
    slot_range = jnp.arange(width_x)
    last_slot = (slot_range == count_live - 1).astype(jnp.float32)
    tail_planes = lax.dynamic_slice_in_dim(coarse, count_live - NCS, NCS, axis=1)
    head_planes = jnp.concatenate([coarse[:, :NCS], edge_sums[:, None]], axis=1)
    tail_planes, head_planes = lax.optimization_barrier((tail_planes, head_planes))
    from_prev = passed_along(tail_planes, "slab", 1)
    from_next = passed_along(head_planes, "slab", -1)
    coarse = coarse + from_next[:, NCS][:, None] * last_slot[None, :, None, None]
    prev_last = (jnp.arange(NCS) == NCS - 1).astype(jnp.float32)
    from_prev = from_prev + edge_sums[:, None] * prev_last[None, :, None, None]
    x_ext = jnp.concatenate([from_prev, coarse, jnp.zeros_like(tail_planes)], axis=1)
    x_ext = lax.dynamic_update_slice_in_dim(x_ext, from_next[:, :NCS], NCS + count_live, axis=1)
    coarse_rim = NCS
    coef_ext = padded(x_ext, ((("pencil", "sub"), 2),), coarse_rim)
    coarse_corr = jnp.zeros((width_x + 2 * NCS, half_y + 2 * NCS, half_z), jnp.float32)
    for sweep_index in range(NCS):
        out_rim = NCS - 1 - sweep_index
        start_at = coarse_rim - out_rim
        size_x = width_x + 2 * out_rim
        size_y = half_y + 2 * out_rim

        def region(offset_x, offset_y):
            return coef_ext[
                :,
                start_at + offset_x : start_at + offset_x + size_x,
                start_at + offset_y : start_at + offset_y + size_y,
            ]

        here_coef = region(0, 0)
        coarse_rhs = here_coef[0]
        coarse_east = here_coef[1]
        coarse_north = here_coef[2]
        coarse_above = here_coef[3]
        coarse_bound = here_coef[4]
        coarse_west = region(-1, 0)[1]
        coarse_south = region(0, -1)[2]
        zero_plane = jnp.zeros_like(coarse_above[:, :, :1])
        coarse_below = jnp.concatenate([zero_plane, coarse_above[:, :, :-1]], axis=2)
        diag_coarse = (
            coarse_east
            + coarse_west
            + coarse_north
            + coarse_south
            + coarse_above
            + coarse_below
            + coarse_bound
        )
        safe_coarse = jnp.where(diag_coarse > 0, diag_coarse, 1.0)
        coarse_center = coarse_corr[1:-1, 1:-1]
        above_vals = jnp.concatenate([coarse_center[:, :, 1:], zero_plane], axis=2)
        below_vals = jnp.concatenate([zero_plane, coarse_center[:, :, :-1]], axis=2)
        beside_all = coarse_east * coarse_corr[2:, 1:-1] + coarse_west * coarse_corr[:-2, 1:-1]
        beside_all = (
            beside_all
            + coarse_north * coarse_corr[1:-1, 2:]
            + coarse_south * coarse_corr[1:-1, :-2]
        )
        beside_all = beside_all + coarse_above * above_vals + coarse_below * below_vals
        coarse_corr = (
            coarse_center
            + OMEGA * (coarse_rhs - (diag_coarse * coarse_center - beside_all)) / safe_coarse
        )
    last_corr = lax.dynamic_index_in_dim(coarse_corr, count_live - 1, axis=0, keepdims=False)
    corr_wide = jnp.concatenate([jnp.zeros_like(last_corr)[None], coarse_corr], axis=0)
    corr_z = jnp.dot(
        corr_wide.reshape((width_x + 1) * half_y, half_z), pair_z.T, precision=lax.Precision.HIGHEST
    )
    correction = jnp.dot(spread_map, corr_z, precision=lax.Precision.HIGHEST)
    base = pressure + correction.reshape(width_x, width_y, depth_cells)
    last_z = jnp.dot(last_corr, pair_z.T, precision=lax.Precision.HIGHEST)
    last_fine = jnp.dot(pair_y, last_z, precision=lax.Precision.HIGHEST)
    up_block = jnp.concatenate([base[width_x - NU :], last_fine[None]], axis=0)
    below_prev = passed_along(up_block, "slab", 1)
    above_next = passed_along(base[:NU], "slab", -1)
    from_owner = (slot_ids == -1).astype(jnp.float32)
    own = base + from_owner[:, None, None] * below_prev[NU][None]
    tail_ids = jnp.concatenate([aggregate, jnp.full((NU,), -1, aggregate.dtype)])
    next_ids = lax.dynamic_slice_in_dim(tail_ids, (slab_index + 1) * width_x, NU)
    to_owner = (next_ids == local_ids[-1]).astype(jnp.float32)
    high_halo = above_next + to_owner[:, None, None] * last_fine[None]
    post_x = jnp.concatenate([below_prev[:NU], own, high_halo], axis=0)
    post_ext = padded(post_x, ((("pencil", "sub"), 1),), NU)
    return sweeps(post_ext, source_ext, faces_ext, NU, width_x)


def solution(mesh):
    in_specs = (
        P(("real", "slab"), ("pencil", "sub"), None),
        P(("real", "slab"), ("pencil", "sub"), None),
        P(("real", "slab"), ("pencil", "sub"), None),
        P("real"),
    )
    out_specs = P(("real", "slab"), ("pencil", "sub"), None)
    return jax.shard_map(body, mesh=mesh, in_specs=in_specs, out_specs=out_specs, check_vma=False)
```

```python
import jax
import jax.numpy as jnp
from jax import lax
from jax.sharding import PartitionSpec as P

NU = 2
NCS = 4


OMEGA = 0.8


def padded(array, sides, width):
    for axis, dim in sides:
        count, length = (lax.axis_size(axis), array.shape[dim])
        up = [(i, (i + 1) % count) for i in range(count - 1)]
        down = [(j, i) for i, j in up]
        last = lax.slice_in_dim(array, length - width, length, axis=dim)
        leading = lax.slice_in_dim(array, 0, width, axis=dim)
        before = lax.ppermute(last, axis, up)
        after = lax.ppermute(leading, axis, down)
        array = jnp.concatenate([before, array, after], axis=dim)
    return array


def halo_round(array, dim_x, dim_y, width):
    count_x = lax.axis_size("slab")
    count_y = lax.axis_size(("pencil", "sub"))
    size_x, size_y = array.shape[dim_x], array.shape[dim_y]

    def part(lo_x, hi_x, lo_y, hi_y):
        block = lax.slice_in_dim(array, lo_x, hi_x, axis=dim_x)
        return lax.slice_in_dim(block, lo_y, hi_y, axis=dim_y)

    def moved(block, step_x, step_y):
        pairs = [
            (i * count_y + j, (i + step_x) * count_y + j + step_y)
            for i in range(count_x)
            for j in range(count_y)
            if 0 <= i + step_x < count_x and 0 <= j + step_y < count_y
        ]
        return lax.ppermute(block, ("slab", "pencil", "sub"), pairs)

    spans_x = {-1: (0, width), 0: (0, size_x), 1: (size_x - width, size_x)}
    spans_y = {-1: (0, width), 0: (0, size_y), 1: (size_y - width, size_y)}
    rows = []
    for from_x in (-1, 0, 1):
        row = []
        for from_y in (-1, 0, 1):
            if from_x == 0 and from_y == 0:
                row.append(array)
                continue
            lo_x, hi_x = spans_x[-from_x]
            lo_y, hi_y = spans_y[-from_y]
            row.append(moved(part(lo_x, hi_x, lo_y, hi_y), -from_x, -from_y))
        rows.append(jnp.concatenate(row, axis=dim_y))
    return jnp.concatenate(rows, axis=dim_x)


def passed_along(array, axis, by):
    count = lax.axis_size(axis)
    pairs = [(i, i + by) for i in range(count) if 0 <= i + by < count]
    return lax.ppermute(array, axis, pairs)


def harmonic(lower_k, upper_k, inside):
    denom_sum = jnp.where(inside, lower_k + upper_k, 1.0)
    return jnp.where(inside, 2.0 * lower_k * upper_k / denom_sum, 0.0)


def geometry(perm_ext, glob_x, glob_y, inside_x, inside_y, total_x, total_y):
    count_z = perm_ext.shape[2]
    both_x = (inside_x[:-1] & inside_x[1:])[:, None, None] & inside_y[None, :, None]
    both_y = (inside_y[:-1] & inside_y[1:])[None, :, None] & inside_x[:, None, None]
    plane_in = inside_x[:, None, None] & inside_y[None, :, None]
    face_x = harmonic(perm_ext[:-1], perm_ext[1:], both_x)
    face_y = harmonic(perm_ext[:, :-1], perm_ext[:, 1:], both_y)
    face_z = harmonic(perm_ext[:, :, :-1], perm_ext[:, :, 1:], plane_in)
    cell_perm = perm_ext[1:-1, 1:-1]
    face_west = face_x[:-1, 1:-1]
    face_east = face_x[1:, 1:-1]
    face_south = face_y[1:-1, :-1]
    face_north = face_y[1:-1, 1:]
    zero_plane = jnp.zeros_like(cell_perm[:, :, :1])
    face_below = jnp.concatenate([zero_plane, face_z[1:-1, 1:-1]], axis=2)
    face_above = jnp.concatenate([face_z[1:-1, 1:-1], zero_plane], axis=2)
    cell_x = glob_x[1:-1]
    cell_y = glob_y[1:-1]
    index_z = jnp.arange(count_z)
    ends_x = (cell_x == 0).astype(jnp.float32) + (cell_x == total_x - 1).astype(jnp.float32)
    ends_y = (cell_y == 0).astype(jnp.float32) + (cell_y == total_y - 1).astype(jnp.float32)
    ends_z = (index_z == 0).astype(jnp.float32) + (index_z == count_z - 1).astype(jnp.float32)
    edges = ends_x[:, None, None] + ends_y[None, :, None] + ends_z[None, None, :]
    boundary = 2.0 * cell_perm * edges
    diagonal = face_west + face_east + face_south + face_north + face_below + face_above + boundary
    cell_in = plane_in[1:-1, 1:-1]
    safe_diag = jnp.where(cell_in, diagonal, 1.0)
    return (
        face_west,
        face_east,
        face_south,
        face_north,
        face_below,
        face_above,
        boundary,
        safe_diag,
    )


def apply_fine(ext_field, faces_now):
    face_west, face_east, face_south, face_north, face_below, face_above, boundary, safe_diag = (
        faces_now
    )
    center = ext_field[1:-1, 1:-1]
    zero_plane = jnp.zeros_like(center[:, :, :1])
    below_vals = jnp.concatenate([zero_plane, center[:, :, :-1]], axis=2)
    above_vals = jnp.concatenate([center[:, :, 1:], zero_plane], axis=2)
    beside_all = face_west * ext_field[:-2, 1:-1] + face_east * ext_field[2:, 1:-1]
    beside_all = beside_all + face_south * ext_field[1:-1, :-2] + face_north * ext_field[1:-1, 2:]
    beside_all = beside_all + face_below * below_vals + face_above * above_vals
    return (center, safe_diag * center - beside_all)


def crop(array, rim):
    if rim == 0:
        return array
    return array[rim : array.shape[0] - rim, rim : array.shape[1] - rim]


def sweeps(field_ext, source_ext, faces_ext, count, width):
    def rim_of(array):
        return (array.shape[0] - width) // 2

    for sweep_index in range(count):
        out_rim = rim_of(field_ext) - 1
        faces_now = tuple(crop(member, rim_of(member) - out_rim) for member in faces_ext)
        center, product = apply_fine(field_ext, faces_now)
        source_now = crop(source_ext, rim_of(source_ext) - out_rim)
        field_ext = center + OMEGA * (source_now - product) / faces_now[7]
    return field_ext


def body(permeability, source, pressure, aggregate):
    width_x, width_y, depth_cells = permeability.shape
    slab_index = lax.axis_index("slab")
    slab_count = lax.axis_size("slab")
    row_index = lax.axis_index(("pencil", "sub"))
    row_count = lax.axis_size(("pencil", "sub"))
    total_x = width_x * slab_count
    total_y = width_y * row_count
    sides = (("slab", 0), (("pencil", "sub"), 1))
    stacked_sides = (("slab", 1), (("pencil", "sub"), 2))
    fine_rim = NU + 1
    ext_all = halo_round(jnp.stack([permeability, source, pressure]), 1, 2, fine_rim)
    perm_ext = ext_all[0]
    source_ext = crop(ext_all[1], 1)
    glob_x = slab_index * width_x - fine_rim + jnp.arange(width_x + 2 * fine_rim)
    glob_y = row_index * width_y - fine_rim + jnp.arange(width_y + 2 * fine_rim)
    inside_x = (glob_x >= 0) & (glob_x < total_x)
    inside_y = (glob_y >= 0) & (glob_y < total_y)
    faces_ext = geometry(perm_ext, glob_x, glob_y, inside_x, inside_y, total_x, total_y)
    smooth_ext = sweeps(ext_all[2], source_ext, faces_ext, NU, width_x)
    faces_zero = tuple(crop(member, fine_rim - 1) for member in faces_ext)
    pressure = crop(smooth_ext, 1)
    center, product = apply_fine(smooth_ext, faces_zero)
    residual = source - product
    half_y = width_y // 2
    half_z = depth_cells // 2

    padded_ids = jnp.concatenate([aggregate[:1], aggregate, aggregate[-1:]])
    ext_ids = lax.dynamic_slice_in_dim(padded_ids, slab_index * width_x, width_x + 2)
    local_ids = ext_ids[1:-1]
    straddles = (slab_index > 0) & (ext_ids[0] == local_ids[0])
    first_id = local_ids[0] + straddles.astype(jnp.int32)
    count_live = local_ids[-1] - first_id + 1
    slot_ids = local_ids - first_id
    crossing = (local_ids != ext_ids[2:]).astype(jnp.float32)
    face_east = faces_zero[1]
    face_north = faces_zero[3]
    face_above = faces_zero[5]
    boundary = faces_zero[6]
    index_z = jnp.arange(depth_cells)[:, None]
    coarse_z = jnp.arange(half_z)[None, :]
    pair_z = (index_z // 2 == coarse_z).astype(jnp.float32)
    odd_z = (index_z == 2 * coarse_z + 1).astype(jnp.float32)
    cells = width_x * width_y

    def z_sum(block_in, pick_z):
        flat = block_in.reshape(cells, depth_cells)
        return jnp.dot(flat, pick_z, precision=lax.Precision.HIGHEST)

    z_parts = jnp.stack(
        [
            z_sum(residual, pair_z),
            z_sum(face_east * crossing[:, None, None], pair_z),
            z_sum(face_north, pair_z),
            z_sum(face_above, odd_z),
            z_sum(boundary, pair_z),
        ]
    )
    slot_wide = jnp.arange(width_x + 1)
    owner_wide = ((slot_ids + 1)[:, None] == slot_wide[None, :]).astype(jnp.float32)
    index_y = jnp.arange(width_y)[:, None]
    coarse_y = jnp.arange(half_y)[None, :]
    pair_y = (index_y // 2 == coarse_y).astype(jnp.float32)
    odd_y = (index_y == 2 * coarse_y + 1).astype(jnp.float32)

    def xy_map(pick_y):
        joint = owner_wide[:, None, :, None] * pick_y[None, :, None, :]
        return joint.reshape(cells, (width_x + 1) * half_y)

    spread_map = xy_map(pair_y)
    north_map = xy_map(odd_y)
    maps = jnp.stack([spread_map, spread_map, north_map, spread_map, spread_map])
    slot_sums = jnp.einsum("qnm,qnl->qml", maps, z_parts, precision=lax.Precision.HIGHEST)
    slot_sums = slot_sums.reshape(5, width_x + 1, half_y, half_z)
    coarse = slot_sums[:, 1:]
    edge_sums = slot_sums[:, 0]
    slot_range = jnp.arange(width_x)
    last_slot = (slot_range == count_live - 1).astype(jnp.float32)
    tail_planes = lax.dynamic_slice_in_dim(coarse, count_live - NCS, NCS, axis=1)
    head_planes = jnp.concatenate([coarse[:, :NCS], edge_sums[:, None]], axis=1)
    tail_planes, head_planes = lax.optimization_barrier((tail_planes, head_planes))
    from_prev = passed_along(tail_planes, "slab", 1)
    from_next = passed_along(head_planes, "slab", -1)
    coarse = coarse + from_next[:, NCS][:, None] * last_slot[None, :, None, None]
    prev_last = (jnp.arange(NCS) == NCS - 1).astype(jnp.float32)
    from_prev = from_prev + edge_sums[:, None] * prev_last[None, :, None, None]
    x_ext = jnp.concatenate([from_prev, coarse, jnp.zeros_like(tail_planes)], axis=1)
    x_ext = lax.dynamic_update_slice_in_dim(x_ext, from_next[:, :NCS], NCS + count_live, axis=1)
    coarse_rim = NCS
    coef_ext = padded(x_ext, ((("pencil", "sub"), 2),), coarse_rim)
    coarse_corr = jnp.zeros((width_x + 2 * NCS, half_y + 2 * NCS, half_z), jnp.float32)
    for sweep_index in range(NCS):
        out_rim = NCS - 1 - sweep_index
        start_at = coarse_rim - out_rim
        size_x = width_x + 2 * out_rim
        size_y = half_y + 2 * out_rim

        def region(offset_x, offset_y):
            return coef_ext[
                :,
                start_at + offset_x : start_at + offset_x + size_x,
                start_at + offset_y : start_at + offset_y + size_y,
            ]

        here_coef = region(0, 0)
        coarse_rhs = here_coef[0]
        coarse_east = here_coef[1]
        coarse_north = here_coef[2]
        coarse_above = here_coef[3]
        coarse_bound = here_coef[4]
        coarse_west = region(-1, 0)[1]
        coarse_south = region(0, -1)[2]
        zero_plane = jnp.zeros_like(coarse_above[:, :, :1])
        coarse_below = jnp.concatenate([zero_plane, coarse_above[:, :, :-1]], axis=2)
        diag_coarse = (
            coarse_east
            + coarse_west
            + coarse_north
            + coarse_south
            + coarse_above
            + coarse_below
            + coarse_bound
        )
        safe_coarse = jnp.where(diag_coarse > 0, diag_coarse, 1.0)
        coarse_center = coarse_corr[1:-1, 1:-1]
        above_vals = jnp.concatenate([coarse_center[:, :, 1:], zero_plane], axis=2)
        below_vals = jnp.concatenate([zero_plane, coarse_center[:, :, :-1]], axis=2)
        beside_all = coarse_east * coarse_corr[2:, 1:-1] + coarse_west * coarse_corr[:-2, 1:-1]
        beside_all = (
            beside_all
            + coarse_north * coarse_corr[1:-1, 2:]
            + coarse_south * coarse_corr[1:-1, :-2]
        )
        beside_all = beside_all + coarse_above * above_vals + coarse_below * below_vals
        coarse_corr = (
            coarse_center
            + OMEGA * (coarse_rhs - (diag_coarse * coarse_center - beside_all)) / safe_coarse
        )
    last_corr = lax.dynamic_index_in_dim(coarse_corr, count_live - 1, axis=0, keepdims=False)
    corr_wide = jnp.concatenate([jnp.zeros_like(last_corr)[None], coarse_corr], axis=0)
    corr_z = jnp.dot(
        corr_wide.reshape((width_x + 1) * half_y, half_z), pair_z.T, precision=lax.Precision.HIGHEST
    )
    correction = jnp.dot(spread_map, corr_z, precision=lax.Precision.HIGHEST)
    base = pressure + correction.reshape(width_x, width_y, depth_cells)
    last_z = jnp.dot(last_corr, pair_z.T, precision=lax.Precision.HIGHEST)
    last_fine = jnp.dot(pair_y, last_z, precision=lax.Precision.HIGHEST)
    up_block = jnp.concatenate([base[width_x - NU :], last_fine[None]], axis=0)
    below_prev = passed_along(up_block, "slab", 1)
    above_next = passed_along(base[:NU], "slab", -1)
    from_owner = (slot_ids == -1).astype(jnp.float32)
    own = base + from_owner[:, None, None] * below_prev[NU][None]
    tail_ids = jnp.concatenate([aggregate, jnp.full((NU,), -1, aggregate.dtype)])
    next_ids = lax.dynamic_slice_in_dim(tail_ids, (slab_index + 1) * width_x, NU)
    to_owner = (next_ids == local_ids[-1]).astype(jnp.float32)
    high_halo = above_next + to_owner[:, None, None] * last_fine[None]
    post_x = jnp.concatenate([below_prev[:NU], own, high_halo], axis=0)
    post_ext = padded(post_x, ((("pencil", "sub"), 1),), NU)
    return sweeps(post_ext, source_ext, faces_ext, NU, width_x)


def solution(mesh):
    in_specs = (
        P(("real", "slab"), ("pencil", "sub"), None),
        P(("real", "slab"), ("pencil", "sub"), None),
        P(("real", "slab"), ("pencil", "sub"), None),
        P("real"),
    )
    out_specs = P(("real", "slab"), ("pencil", "sub"), None)
    return jax.shard_map(body, mesh=mesh, in_specs=in_specs, out_specs=out_specs, check_vma=False)
```

```python
import jax
import jax.numpy as jnp
from jax import lax
from jax.sharding import PartitionSpec as P

NU = 2
NCS = 4


OMEGA = 0.8


def padded(array, sides, width):
    for axis, dim in sides:
        count, length = (lax.axis_size(axis), array.shape[dim])
        up = [(i, (i + 1) % count) for i in range(count - 1)]
        down = [(j, i) for i, j in up]
        last = lax.slice_in_dim(array, length - width, length, axis=dim)
        leading = lax.slice_in_dim(array, 0, width, axis=dim)
        before = lax.ppermute(last, axis, up)
        after = lax.ppermute(leading, axis, down)
        array = jnp.concatenate([before, array, after], axis=dim)
    return array


def passed_along(array, axis, by):
    count = lax.axis_size(axis)
    pairs = [(i, i + by) for i in range(count) if 0 <= i + by < count]
    return lax.ppermute(array, axis, pairs)


def harmonic(lower_k, upper_k, inside):
    denom_sum = jnp.where(inside, lower_k + upper_k, 1.0)
    return jnp.where(inside, 2.0 * lower_k * upper_k / denom_sum, 0.0)


def geometry(perm_ext, glob_x, glob_y, inside_x, inside_y, total_x, total_y):
    count_z = perm_ext.shape[2]
    both_x = (inside_x[:-1] & inside_x[1:])[:, None, None] & inside_y[None, :, None]
    both_y = (inside_y[:-1] & inside_y[1:])[None, :, None] & inside_x[:, None, None]
    plane_in = inside_x[:, None, None] & inside_y[None, :, None]
    face_x = harmonic(perm_ext[:-1], perm_ext[1:], both_x)
    face_y = harmonic(perm_ext[:, :-1], perm_ext[:, 1:], both_y)
    face_z = harmonic(perm_ext[:, :, :-1], perm_ext[:, :, 1:], plane_in)
    cell_perm = perm_ext[1:-1, 1:-1]
    face_west = face_x[:-1, 1:-1]
    face_east = face_x[1:, 1:-1]
    face_south = face_y[1:-1, :-1]
    face_north = face_y[1:-1, 1:]
    zero_plane = jnp.zeros_like(cell_perm[:, :, :1])
    face_below = jnp.concatenate([zero_plane, face_z[1:-1, 1:-1]], axis=2)
    face_above = jnp.concatenate([face_z[1:-1, 1:-1], zero_plane], axis=2)
    cell_x = glob_x[1:-1]
    cell_y = glob_y[1:-1]
    index_z = jnp.arange(count_z)
    ends_x = (cell_x == 0).astype(jnp.float32) + (cell_x == total_x - 1).astype(jnp.float32)
    ends_y = (cell_y == 0).astype(jnp.float32) + (cell_y == total_y - 1).astype(jnp.float32)
    ends_z = (index_z == 0).astype(jnp.float32) + (index_z == count_z - 1).astype(jnp.float32)
    edges = ends_x[:, None, None] + ends_y[None, :, None] + ends_z[None, None, :]
    boundary = 2.0 * cell_perm * edges
    diagonal = face_west + face_east + face_south + face_north + face_below + face_above + boundary
    cell_in = plane_in[1:-1, 1:-1]
    safe_diag = jnp.where(cell_in, diagonal, 1.0)
    return (
        face_west,
        face_east,
        face_south,
        face_north,
        face_below,
        face_above,
        boundary,
        safe_diag,
    )


def apply_fine(ext_field, faces_now):
    face_west, face_east, face_south, face_north, face_below, face_above, boundary, safe_diag = (
        faces_now
    )
    center = ext_field[1:-1, 1:-1]
    zero_plane = jnp.zeros_like(center[:, :, :1])
    below_vals = jnp.concatenate([zero_plane, center[:, :, :-1]], axis=2)
    above_vals = jnp.concatenate([center[:, :, 1:], zero_plane], axis=2)
    beside_all = face_west * ext_field[:-2, 1:-1] + face_east * ext_field[2:, 1:-1]
    beside_all = beside_all + face_south * ext_field[1:-1, :-2] + face_north * ext_field[1:-1, 2:]
    beside_all = beside_all + face_below * below_vals + face_above * above_vals
    return (center, safe_diag * center - beside_all)


def crop(array, rim):
    if rim == 0:
        return array
    return array[rim : array.shape[0] - rim, rim : array.shape[1] - rim]


def sweeps(field_ext, source_ext, faces_ext, count, width):
    def rim_of(array):
        return (array.shape[0] - width) // 2

    for sweep_index in range(count):
        out_rim = rim_of(field_ext) - 1
        faces_now = tuple(crop(member, rim_of(member) - out_rim) for member in faces_ext)
        center, product = apply_fine(field_ext, faces_now)
        source_now = crop(source_ext, rim_of(source_ext) - out_rim)
        field_ext = center + OMEGA * (source_now - product) / faces_now[7]
    return field_ext


def body(permeability, source, pressure, aggregate):
    width_x, width_y, depth_cells = permeability.shape
    slab_index = lax.axis_index("slab")
    slab_count = lax.axis_size("slab")
    row_index = lax.axis_index(("pencil", "sub"))
    row_count = lax.axis_size(("pencil", "sub"))
    total_x = width_x * slab_count
    total_y = width_y * row_count
    sides = (("slab", 0), (("pencil", "sub"), 1))
    stacked_sides = (("slab", 1), (("pencil", "sub"), 2))
    fine_rim = NU + 1
    ext_all = padded(jnp.stack([permeability, source, pressure]), stacked_sides, fine_rim)
    perm_ext = ext_all[0]
    source_ext = crop(ext_all[1], 1)
    glob_x = slab_index * width_x - fine_rim + jnp.arange(width_x + 2 * fine_rim)
    glob_y = row_index * width_y - fine_rim + jnp.arange(width_y + 2 * fine_rim)
    inside_x = (glob_x >= 0) & (glob_x < total_x)
    inside_y = (glob_y >= 0) & (glob_y < total_y)
    faces_ext = geometry(perm_ext, glob_x, glob_y, inside_x, inside_y, total_x, total_y)
    smooth_ext = sweeps(ext_all[2], source_ext, faces_ext, NU, width_x)
    faces_zero = tuple(crop(member, fine_rim - 1) for member in faces_ext)
    pressure = crop(smooth_ext, 1)
    center, product = apply_fine(smooth_ext, faces_zero)
    residual = source - product
    half_y = width_y // 2
    half_z = depth_cells // 2

    plane_count = aggregate.shape[0]
    ext_pos = slab_index * width_x - 1 + jnp.arange(width_x + 1 + NU)
    pick_ids = ext_pos[:, None] == jnp.arange(plane_count)[None, :]
    ext_ids = jnp.sum(jnp.where(pick_ids, aggregate.astype(jnp.float32)[None, :], 0.0), axis=1)
    local_ids = ext_ids[1 : width_x + 1]
    straddles = (slab_index > 0) & (ext_ids[0] == local_ids[0])
    first_id = local_ids[0] + straddles.astype(jnp.float32)
    count_live = local_ids[-1] - first_id + 1
    slot_ids = local_ids - first_id
    has_next = ext_pos[2 : width_x + 2] < plane_count
    crossing = ((local_ids != ext_ids[2 : width_x + 2]) & has_next).astype(jnp.float32)
    face_east = faces_zero[1]
    face_north = faces_zero[3]
    face_above = faces_zero[5]
    boundary = faces_zero[6]
    index_z = jnp.arange(depth_cells)[:, None]
    coarse_z = jnp.arange(half_z)[None, :]
    pair_z = (index_z // 2 == coarse_z).astype(jnp.float32)
    odd_z = (index_z == 2 * coarse_z + 1).astype(jnp.float32)
    cells = width_x * width_y

    def z_sum(block_in, pick_z):
        flat = block_in.reshape(cells, depth_cells)
        return jnp.dot(flat, pick_z, precision=lax.Precision.HIGHEST)

    z_parts = jnp.stack(
        [
            z_sum(residual, pair_z),
            z_sum(face_east * crossing[:, None, None], pair_z),
            z_sum(face_north, pair_z),
            z_sum(face_above, odd_z),
            z_sum(boundary, pair_z),
        ]
    )
    slot_wide = jnp.arange(width_x + 1)
    owner_wide = ((slot_ids + 1)[:, None] == slot_wide[None, :]).astype(jnp.float32)
    index_y = jnp.arange(width_y)[:, None]
    coarse_y = jnp.arange(half_y)[None, :]
    pair_y = (index_y // 2 == coarse_y).astype(jnp.float32)
    odd_y = (index_y == 2 * coarse_y + 1).astype(jnp.float32)

    def xy_map(pick_y):
        joint = owner_wide[:, None, :, None] * pick_y[None, :, None, :]
        return joint.reshape(cells, (width_x + 1) * half_y)

    spread_map = xy_map(pair_y)
    north_map = xy_map(odd_y)
    maps = jnp.stack([spread_map, spread_map, north_map, spread_map, spread_map])
    slot_sums = jnp.einsum("qnm,qnl->qml", maps, z_parts, precision=lax.Precision.HIGHEST)
    slot_sums = slot_sums.reshape(5, width_x + 1, half_y, half_z)
    coarse = slot_sums[:, 1:]
    edge_sums = slot_sums[:, 0]
    slot_range = jnp.arange(width_x)
    last_slot = (slot_range == count_live - 1).astype(jnp.float32)
    tail_pick = (slot_range[None, :] == count_live - NCS + jnp.arange(NCS)[:, None]).astype(jnp.float32)
    tail_planes = jnp.einsum("ks,qsjl->qkjl", tail_pick, coarse, precision=lax.Precision.HIGHEST)
    head_planes = jnp.concatenate([coarse[:, :NCS], edge_sums[:, None]], axis=1)
    tail_planes, head_planes = lax.optimization_barrier((tail_planes, head_planes))
    from_prev = passed_along(tail_planes, "slab", 1)
    from_next = passed_along(head_planes, "slab", -1)
    coarse = coarse + from_next[:, NCS][:, None] * last_slot[None, :, None, None]
    prev_last = (jnp.arange(NCS) == NCS - 1).astype(jnp.float32)
    from_prev = from_prev + edge_sums[:, None] * prev_last[None, :, None, None]
    x_ext = jnp.concatenate([from_prev, coarse, jnp.zeros_like(tail_planes)], axis=1)
    wide_range = jnp.arange(width_x + 2 * NCS)[:, None]
    place = (wide_range == NCS + count_live + jnp.arange(NCS)[None, :]).astype(jnp.float32)
    x_ext = x_ext + jnp.einsum("tk,qkjl->qtjl", place, from_next[:, :NCS], precision=lax.Precision.HIGHEST)
    coarse_rim = NCS
    coef_ext = padded(x_ext, ((("pencil", "sub"), 2),), coarse_rim)
    coarse_corr = jnp.zeros((width_x + 2 * NCS, half_y + 2 * NCS, half_z), jnp.float32)
    for sweep_index in range(NCS):
        out_rim = NCS - 1 - sweep_index
        start_at = coarse_rim - out_rim
        size_x = width_x + 2 * out_rim
        size_y = half_y + 2 * out_rim

        def region(offset_x, offset_y):
            return coef_ext[
                :,
                start_at + offset_x : start_at + offset_x + size_x,
                start_at + offset_y : start_at + offset_y + size_y,
            ]

        here_coef = region(0, 0)
        coarse_rhs = here_coef[0]
        coarse_east = here_coef[1]
        coarse_north = here_coef[2]
        coarse_above = here_coef[3]
        coarse_bound = here_coef[4]
        coarse_west = region(-1, 0)[1]
        coarse_south = region(0, -1)[2]
        zero_plane = jnp.zeros_like(coarse_above[:, :, :1])
        coarse_below = jnp.concatenate([zero_plane, coarse_above[:, :, :-1]], axis=2)
        diag_coarse = (
            coarse_east
            + coarse_west
            + coarse_north
            + coarse_south
            + coarse_above
            + coarse_below
            + coarse_bound
        )
        safe_coarse = jnp.where(diag_coarse > 0, diag_coarse, 1.0)
        coarse_center = coarse_corr[1:-1, 1:-1]
        above_vals = jnp.concatenate([coarse_center[:, :, 1:], zero_plane], axis=2)
        below_vals = jnp.concatenate([zero_plane, coarse_center[:, :, :-1]], axis=2)
        beside_all = coarse_east * coarse_corr[2:, 1:-1] + coarse_west * coarse_corr[:-2, 1:-1]
        beside_all = (
            beside_all
            + coarse_north * coarse_corr[1:-1, 2:]
            + coarse_south * coarse_corr[1:-1, :-2]
        )
        beside_all = beside_all + coarse_above * above_vals + coarse_below * below_vals
        coarse_corr = (
            coarse_center
            + OMEGA * (coarse_rhs - (diag_coarse * coarse_center - beside_all)) / safe_coarse
        )
    last_corr = jnp.sum(last_slot[:, None, None] * coarse_corr, axis=0)
    corr_wide = jnp.concatenate([jnp.zeros_like(last_corr)[None], coarse_corr], axis=0)
    corr_z = jnp.dot(
        corr_wide.reshape((width_x + 1) * half_y, half_z), pair_z.T, precision=lax.Precision.HIGHEST
    )
    correction = jnp.dot(spread_map, corr_z, precision=lax.Precision.HIGHEST)
    base = pressure + correction.reshape(width_x, width_y, depth_cells)
    last_z = jnp.dot(last_corr, pair_z.T, precision=lax.Precision.HIGHEST)
    last_fine = jnp.dot(pair_y, last_z, precision=lax.Precision.HIGHEST)
    up_block = jnp.concatenate([base[width_x - NU :], last_fine[None]], axis=0)
    below_prev = passed_along(up_block, "slab", 1)
    above_next = passed_along(base[:NU], "slab", -1)
    from_owner = (slot_ids == -1).astype(jnp.float32)
    own = base + from_owner[:, None, None] * below_prev[NU][None]
    next_ids = ext_ids[width_x + 1 :]
    next_in = ext_pos[width_x + 1 :] < plane_count
    to_owner = ((next_ids == local_ids[-1]) & next_in).astype(jnp.float32)
    high_halo = above_next + to_owner[:, None, None] * last_fine[None]
    post_x = jnp.concatenate([below_prev[:NU], own, high_halo], axis=0)
    post_ext = padded(post_x, ((("pencil", "sub"), 1),), NU)
    return sweeps(post_ext, source_ext, faces_ext, NU, width_x)


def solution(mesh):
    in_specs = (
        P(("real", "slab"), ("pencil", "sub"), None),
        P(("real", "slab"), ("pencil", "sub"), None),
        P(("real", "slab"), ("pencil", "sub"), None),
        P("real"),
    )
    out_specs = P(("real", "slab"), ("pencil", "sub"), None)
    return jax.shard_map(body, mesh=mesh, in_specs=in_specs, out_specs=out_specs, check_vma=False)
```

```python
import numpy as np
import jax
import jax.numpy as jnp
from jax import lax
from jax.sharding import PartitionSpec as P

NU = 2
NCS = 4


OMEGA = 0.8


def padded(array, sides, width):
    for axis, dim in sides:
        count, length = (lax.axis_size(axis), array.shape[dim])
        up = [(i, (i + 1) % count) for i in range(count - 1)]
        down = [(j, i) for i, j in up]
        last = lax.slice_in_dim(array, length - width, length, axis=dim)
        leading = lax.slice_in_dim(array, 0, width, axis=dim)
        before = lax.ppermute(last, axis, up)
        after = lax.ppermute(leading, axis, down)
        array = jnp.concatenate([before, array, after], axis=dim)
    return array


def passed_along(array, axis, by):
    count = lax.axis_size(axis)
    pairs = [(i, i + by) for i in range(count) if 0 <= i + by < count]
    return lax.ppermute(array, axis, pairs)


def harmonic(lower_k, upper_k, inside):
    denom_sum = jnp.where(inside, lower_k + upper_k, 1.0)
    return jnp.where(inside, 2.0 * lower_k * upper_k / denom_sum, 0.0)


def geometry(perm_ext, glob_x, glob_y, inside_x, inside_y, total_x, total_y):
    count_z = perm_ext.shape[2]
    both_x = (inside_x[:-1] & inside_x[1:])[:, None, None] & inside_y[None, :, None]
    both_y = (inside_y[:-1] & inside_y[1:])[None, :, None] & inside_x[:, None, None]
    plane_in = inside_x[:, None, None] & inside_y[None, :, None]
    face_x = harmonic(perm_ext[:-1], perm_ext[1:], both_x)
    face_y = harmonic(perm_ext[:, :-1], perm_ext[:, 1:], both_y)
    face_z = harmonic(perm_ext[:, :, :-1], perm_ext[:, :, 1:], plane_in)
    cell_perm = perm_ext[1:-1, 1:-1]
    face_west = face_x[:-1, 1:-1]
    face_east = face_x[1:, 1:-1]
    face_south = face_y[1:-1, :-1]
    face_north = face_y[1:-1, 1:]
    zero_plane = jnp.zeros_like(cell_perm[:, :, :1])
    face_below = jnp.concatenate([zero_plane, face_z[1:-1, 1:-1]], axis=2)
    face_above = jnp.concatenate([face_z[1:-1, 1:-1], zero_plane], axis=2)
    cell_x = glob_x[1:-1]
    cell_y = glob_y[1:-1]
    index_z = jnp.arange(count_z)
    ends_x = (cell_x == 0).astype(jnp.float32) + (cell_x == total_x - 1).astype(jnp.float32)
    ends_y = (cell_y == 0).astype(jnp.float32) + (cell_y == total_y - 1).astype(jnp.float32)
    ends_z = (index_z == 0).astype(jnp.float32) + (index_z == count_z - 1).astype(jnp.float32)
    edges = ends_x[:, None, None] + ends_y[None, :, None] + ends_z[None, None, :]
    boundary = 2.0 * cell_perm * edges
    diagonal = face_west + face_east + face_south + face_north + face_below + face_above + boundary
    cell_in = plane_in[1:-1, 1:-1]
    safe_diag = jnp.where(cell_in, diagonal, 1.0)
    return (
        face_west,
        face_east,
        face_south,
        face_north,
        face_below,
        face_above,
        boundary,
        safe_diag,
    )


def apply_fine(ext_field, faces_now):
    face_west, face_east, face_south, face_north, face_below, face_above, boundary, safe_diag = (
        faces_now
    )
    center = ext_field[1:-1, 1:-1]
    zero_plane = jnp.zeros_like(center[:, :, :1])
    below_vals = jnp.concatenate([zero_plane, center[:, :, :-1]], axis=2)
    above_vals = jnp.concatenate([center[:, :, 1:], zero_plane], axis=2)
    beside_all = face_west * ext_field[:-2, 1:-1] + face_east * ext_field[2:, 1:-1]
    beside_all = beside_all + face_south * ext_field[1:-1, :-2] + face_north * ext_field[1:-1, 2:]
    beside_all = beside_all + face_below * below_vals + face_above * above_vals
    return (center, safe_diag * center - beside_all)


def crop(array, rim):
    if rim == 0:
        return array
    return array[rim : array.shape[0] - rim, rim : array.shape[1] - rim]


def sweeps(field_ext, source_ext, faces_ext, count, width):
    def rim_of(array):
        return (array.shape[0] - width) // 2

    for sweep_index in range(count):
        out_rim = rim_of(field_ext) - 1
        faces_now = tuple(crop(member, rim_of(member) - out_rim) for member in faces_ext)
        center, product = apply_fine(field_ext, faces_now)
        source_now = crop(source_ext, rim_of(source_ext) - out_rim)
        field_ext = center + OMEGA * (source_now - product) / faces_now[7]
    return field_ext


def body(permeability, source, pressure, aggregate):
    width_x, width_y, depth_cells = permeability.shape
    slab_index = lax.axis_index("slab")
    slab_count = lax.axis_size("slab")
    row_index = lax.axis_index(("pencil", "sub"))
    row_count = lax.axis_size(("pencil", "sub"))
    total_x = width_x * slab_count
    total_y = width_y * row_count
    sides = (("slab", 0), (("pencil", "sub"), 1))
    stacked_sides = (("slab", 1), (("pencil", "sub"), 2))
    fine_rim = NU + 1
    ext_all = padded(jnp.stack([permeability, source, pressure]), stacked_sides, fine_rim)
    perm_ext = ext_all[0]
    source_ext = crop(ext_all[1], 1)
    glob_x = slab_index * width_x - fine_rim + jnp.arange(width_x + 2 * fine_rim)
    glob_y = row_index * width_y - fine_rim + jnp.arange(width_y + 2 * fine_rim)
    inside_x = (glob_x >= 0) & (glob_x < total_x)
    inside_y = (glob_y >= 0) & (glob_y < total_y)
    faces_ext = geometry(perm_ext, glob_x, glob_y, inside_x, inside_y, total_x, total_y)
    smooth_ext = sweeps(ext_all[2], source_ext, faces_ext, NU, width_x)
    faces_zero = tuple(crop(member, fine_rim - 1) for member in faces_ext)
    pressure = crop(smooth_ext, 1)
    center, product = apply_fine(smooth_ext, faces_zero)
    residual = source - product
    half_y = width_y // 2
    half_z = depth_cells // 2

    plane_count = aggregate.shape[0]
    ext_pos = slab_index * width_x - 1 + jnp.arange(width_x + 1 + NU)
    pick_ids = ext_pos[:, None] == jnp.arange(plane_count)[None, :]
    ext_ids = jnp.sum(jnp.where(pick_ids, aggregate.astype(jnp.float32)[None, :], 0.0), axis=1)
    local_ids = ext_ids[1 : width_x + 1]
    straddles = (slab_index > 0) & (ext_ids[0] == local_ids[0])
    first_id = local_ids[0] + straddles.astype(jnp.float32)
    count_live = local_ids[-1] - first_id + 1
    slot_ids = local_ids - first_id
    has_next = ext_pos[2 : width_x + 2] < plane_count
    crossing = ((local_ids != ext_ids[2 : width_x + 2]) & has_next).astype(jnp.float32)
    face_east = faces_zero[1]
    face_north = faces_zero[3]
    face_above = faces_zero[5]
    boundary = faces_zero[6]
    index_z = np.arange(depth_cells)[:, None]
    coarse_z = np.arange(half_z)[None, :]
    pair_z = jnp.asarray((index_z // 2 == coarse_z).astype(np.float32))
    odd_z = jnp.asarray((index_z == 2 * coarse_z + 1).astype(np.float32))
    cells = width_x * width_y

    def z_sum(block_in, pick_z):
        flat = block_in.reshape(cells, depth_cells)
        return jnp.dot(flat, pick_z, precision=lax.Precision.HIGHEST)

    z_parts = jnp.stack(
        [
            z_sum(residual, pair_z),
            z_sum(face_east * crossing[:, None, None], pair_z),
            z_sum(face_north, pair_z),
            z_sum(face_above, odd_z),
            z_sum(boundary, pair_z),
        ]
    )
    index_y = np.arange(width_y)[:, None]
    coarse_y = np.arange(half_y)[None, :]
    pair_y = jnp.asarray((index_y // 2 == coarse_y).astype(np.float32))
    row_y = np.tile(np.arange(width_y), width_x)
    col_slot = np.repeat(np.arange(width_x + 1), half_y)
    col_y = np.tile(np.arange(half_y), width_x + 1)
    row_slot = jnp.repeat(slot_ids + 1, width_y)
    same_slot = row_slot[:, None] == jnp.asarray(col_slot.astype(np.float32))[None, :]
    pair_rows = row_y[:, None] // 2 == col_y[None, :]
    odd_rows = row_y[:, None] == 2 * col_y[None, :] + 1
    spread_map = (same_slot & pair_rows).astype(jnp.float32)
    gather_map = (same_slot.T & pair_rows.T).astype(jnp.float32)
    north_gather = (same_slot.T & odd_rows.T).astype(jnp.float32)
    paired = jnp.dot(
        gather_map,
        jnp.concatenate([z_parts[0], z_parts[1], z_parts[3], z_parts[4]], axis=1),
        precision=lax.Precision.HIGHEST,
    ).reshape((width_x + 1) * half_y, 4, half_z)
    north_sums = jnp.dot(north_gather, z_parts[2], precision=lax.Precision.HIGHEST)
    slot_sums = jnp.stack([paired[:, 0], paired[:, 1], north_sums, paired[:, 2], paired[:, 3]])
    slot_sums = slot_sums.reshape(5, width_x + 1, half_y, half_z)
    coarse = slot_sums[:, 1:]
    edge_sums = slot_sums[:, 0]
    slot_range = jnp.arange(width_x)
    last_slot = (slot_range == count_live - 1).astype(jnp.float32)
    tail_pick = (slot_range[None, :] == count_live - NCS + jnp.arange(NCS)[:, None]).astype(jnp.float32)
    tail_planes = jnp.einsum("ks,qsjl->qkjl", tail_pick, coarse, precision=lax.Precision.HIGHEST)
    head_planes = jnp.concatenate([coarse[:, :NCS], edge_sums[:, None]], axis=1)
    tail_planes, head_planes = lax.optimization_barrier((tail_planes, head_planes))
    from_prev = passed_along(tail_planes, "slab", 1)
    from_next = passed_along(head_planes, "slab", -1)
    coarse = coarse + from_next[:, NCS][:, None] * last_slot[None, :, None, None]
    prev_last = (jnp.arange(NCS) == NCS - 1).astype(jnp.float32)
    from_prev = from_prev + edge_sums[:, None] * prev_last[None, :, None, None]
    x_ext = jnp.concatenate([from_prev, coarse, jnp.zeros_like(tail_planes)], axis=1)
    wide_range = jnp.arange(width_x + 2 * NCS)[:, None]
    place = (wide_range == NCS + count_live + jnp.arange(NCS)[None, :]).astype(jnp.float32)
    x_ext = x_ext + jnp.einsum("tk,qkjl->qtjl", place, from_next[:, :NCS], precision=lax.Precision.HIGHEST)
    coarse_rim = NCS
    coef_ext = padded(x_ext, ((("pencil", "sub"), 2),), coarse_rim)
    coarse_corr = jnp.zeros((width_x + 2 * NCS, half_y + 2 * NCS, half_z), jnp.float32)
    for sweep_index in range(NCS):
        out_rim = NCS - 1 - sweep_index
        start_at = coarse_rim - out_rim
        size_x = width_x + 2 * out_rim
        size_y = half_y + 2 * out_rim

        def region(offset_x, offset_y):
            return coef_ext[
                :,
                start_at + offset_x : start_at + offset_x + size_x,
                start_at + offset_y : start_at + offset_y + size_y,
            ]

        here_coef = region(0, 0)
        coarse_rhs = here_coef[0]
        coarse_east = here_coef[1]
        coarse_north = here_coef[2]
        coarse_above = here_coef[3]
        coarse_bound = here_coef[4]
        coarse_west = region(-1, 0)[1]
        coarse_south = region(0, -1)[2]
        zero_plane = jnp.zeros_like(coarse_above[:, :, :1])
        coarse_below = jnp.concatenate([zero_plane, coarse_above[:, :, :-1]], axis=2)
        diag_coarse = (
            coarse_east
            + coarse_west
            + coarse_north
            + coarse_south
            + coarse_above
            + coarse_below
            + coarse_bound
        )
        safe_coarse = jnp.where(diag_coarse > 0, diag_coarse, 1.0)
        coarse_center = coarse_corr[1:-1, 1:-1]
        above_vals = jnp.concatenate([coarse_center[:, :, 1:], zero_plane], axis=2)
        below_vals = jnp.concatenate([zero_plane, coarse_center[:, :, :-1]], axis=2)
        beside_all = coarse_east * coarse_corr[2:, 1:-1] + coarse_west * coarse_corr[:-2, 1:-1]
        beside_all = (
            beside_all
            + coarse_north * coarse_corr[1:-1, 2:]
            + coarse_south * coarse_corr[1:-1, :-2]
        )
        beside_all = beside_all + coarse_above * above_vals + coarse_below * below_vals
        coarse_corr = (
            coarse_center
            + OMEGA * (coarse_rhs - (diag_coarse * coarse_center - beside_all)) / safe_coarse
        )
    last_corr = jnp.sum(last_slot[:, None, None] * coarse_corr, axis=0)
    corr_wide = jnp.concatenate([jnp.zeros_like(last_corr)[None], coarse_corr], axis=0)
    corr_z = jnp.dot(
        corr_wide.reshape((width_x + 1) * half_y, half_z), pair_z.T, precision=lax.Precision.HIGHEST
    )
    correction = jnp.dot(spread_map, corr_z, precision=lax.Precision.HIGHEST)
    base = pressure + correction.reshape(width_x, width_y, depth_cells)
    last_z = jnp.dot(last_corr, pair_z.T, precision=lax.Precision.HIGHEST)
    last_fine = jnp.dot(pair_y, last_z, precision=lax.Precision.HIGHEST)
    up_block = jnp.concatenate([base[width_x - NU :], last_fine[None]], axis=0)
    below_prev = passed_along(up_block, "slab", 1)
    above_next = passed_along(base[:NU], "slab", -1)
    from_owner = (slot_ids == -1).astype(jnp.float32)
    own = base + from_owner[:, None, None] * below_prev[NU][None]
    next_ids = ext_ids[width_x + 1 :]
    next_in = ext_pos[width_x + 1 :] < plane_count
    to_owner = ((next_ids == local_ids[-1]) & next_in).astype(jnp.float32)
    high_halo = above_next + to_owner[:, None, None] * last_fine[None]
    post_x = jnp.concatenate([below_prev[:NU], own, high_halo], axis=0)
    post_ext = padded(post_x, ((("pencil", "sub"), 1),), NU)
    return sweeps(post_ext, source_ext, faces_ext, NU, width_x)


def solution(mesh):
    in_specs = (
        P(("real", "slab"), ("pencil", "sub"), None),
        P(("real", "slab"), ("pencil", "sub"), None),
        P(("real", "slab"), ("pencil", "sub"), None),
        P("real"),
    )
    out_specs = P(("real", "slab"), ("pencil", "sub"), None)
    return jax.shard_map(body, mesh=mesh, in_specs=in_specs, out_specs=out_specs, check_vma=False)
```

```python
import numpy as np
import jax
import jax.numpy as jnp
from jax import lax
from jax.sharding import PartitionSpec as P

NU = 2
NCS = 4


OMEGA = 0.8


def padded(array, sides, width):
    for axis, dim in sides:
        count, length = (lax.axis_size(axis), array.shape[dim])
        up = [(i, (i + 1) % count) for i in range(count - 1)]
        down = [(j, i) for i, j in up]
        last = lax.slice_in_dim(array, length - width, length, axis=dim)
        leading = lax.slice_in_dim(array, 0, width, axis=dim)
        before = lax.ppermute(last, axis, up)
        after = lax.ppermute(leading, axis, down)
        array = jnp.concatenate([before, array, after], axis=dim)
    return array


def passed_along(array, axis, by):
    count = lax.axis_size(axis)
    pairs = [(i, i + by) for i in range(count) if 0 <= i + by < count]
    return lax.ppermute(array, axis, pairs)


def harmonic(lower_k, upper_k, inside):
    denom_sum = jnp.where(inside, lower_k + upper_k, 1.0)
    return jnp.where(inside, 2.0 * lower_k * upper_k / denom_sum, 0.0)


def geometry(perm_ext, glob_x, glob_y, inside_x, inside_y, total_x, total_y):
    count_z = perm_ext.shape[2]
    both_x = (inside_x[:-1] & inside_x[1:])[:, None, None] & inside_y[None, :, None]
    both_y = (inside_y[:-1] & inside_y[1:])[None, :, None] & inside_x[:, None, None]
    plane_in = inside_x[:, None, None] & inside_y[None, :, None]
    face_x = harmonic(perm_ext[:-1], perm_ext[1:], both_x)
    face_y = harmonic(perm_ext[:, :-1], perm_ext[:, 1:], both_y)
    face_z = harmonic(perm_ext[:, :, :-1], perm_ext[:, :, 1:], plane_in)
    cell_perm = perm_ext[1:-1, 1:-1]
    face_west = face_x[:-1, 1:-1]
    face_east = face_x[1:, 1:-1]
    face_south = face_y[1:-1, :-1]
    face_north = face_y[1:-1, 1:]
    zero_plane = jnp.zeros_like(cell_perm[:, :, :1])
    face_below = jnp.concatenate([zero_plane, face_z[1:-1, 1:-1]], axis=2)
    face_above = jnp.concatenate([face_z[1:-1, 1:-1], zero_plane], axis=2)
    cell_x = glob_x[1:-1]
    cell_y = glob_y[1:-1]
    index_z = jnp.arange(count_z)
    ends_x = (cell_x == 0).astype(jnp.float32) + (cell_x == total_x - 1).astype(jnp.float32)
    ends_y = (cell_y == 0).astype(jnp.float32) + (cell_y == total_y - 1).astype(jnp.float32)
    ends_z = (index_z == 0).astype(jnp.float32) + (index_z == count_z - 1).astype(jnp.float32)
    edges = ends_x[:, None, None] + ends_y[None, :, None] + ends_z[None, None, :]
    boundary = 2.0 * cell_perm * edges
    diagonal = face_west + face_east + face_south + face_north + face_below + face_above + boundary
    cell_in = plane_in[1:-1, 1:-1]
    safe_diag = jnp.where(cell_in, diagonal, 1.0)
    return (
        face_west,
        face_east,
        face_south,
        face_north,
        face_below,
        face_above,
        boundary,
        safe_diag,
    )


def apply_fine(ext_field, faces_now):
    face_west, face_east, face_south, face_north, face_below, face_above, boundary, safe_diag = (
        faces_now
    )
    center = ext_field[1:-1, 1:-1]
    zero_plane = jnp.zeros_like(center[:, :, :1])
    below_vals = jnp.concatenate([zero_plane, center[:, :, :-1]], axis=2)
    above_vals = jnp.concatenate([center[:, :, 1:], zero_plane], axis=2)
    beside_all = face_west * ext_field[:-2, 1:-1] + face_east * ext_field[2:, 1:-1]
    beside_all = beside_all + face_south * ext_field[1:-1, :-2] + face_north * ext_field[1:-1, 2:]
    beside_all = beside_all + face_below * below_vals + face_above * above_vals
    return (center, safe_diag * center - beside_all)


def crop(array, rim):
    if rim == 0:
        return array
    return array[rim : array.shape[0] - rim, rim : array.shape[1] - rim]


def sweeps(field_ext, source_ext, faces_ext, count, width):
    def rim_of(array):
        return (array.shape[0] - width) // 2

    for sweep_index in range(count):
        out_rim = rim_of(field_ext) - 1
        faces_now = tuple(crop(member, rim_of(member) - out_rim) for member in faces_ext)
        center, product = apply_fine(field_ext, faces_now)
        source_now = crop(source_ext, rim_of(source_ext) - out_rim)
        field_ext = center + OMEGA * (source_now - product) / faces_now[7]
    return field_ext


def body(permeability, source, pressure, aggregate):
    width_x, width_y, depth_cells = permeability.shape
    slab_index = lax.axis_index("slab")
    slab_count = lax.axis_size("slab")
    row_index = lax.axis_index(("pencil", "sub"))
    row_count = lax.axis_size(("pencil", "sub"))
    total_x = width_x * slab_count
    total_y = width_y * row_count
    sides = (("slab", 0), (("pencil", "sub"), 1))
    stacked_sides = (("slab", 1), (("pencil", "sub"), 2))
    fine_rim = NU + 1
    ext_all = padded(jnp.stack([permeability, source, pressure]), stacked_sides, fine_rim)
    perm_ext = ext_all[0]
    source_ext = crop(ext_all[1], 1)
    glob_x = slab_index * width_x - fine_rim + jnp.arange(width_x + 2 * fine_rim)
    glob_y = row_index * width_y - fine_rim + jnp.arange(width_y + 2 * fine_rim)
    inside_x = (glob_x >= 0) & (glob_x < total_x)
    inside_y = (glob_y >= 0) & (glob_y < total_y)
    faces_ext = geometry(perm_ext, glob_x, glob_y, inside_x, inside_y, total_x, total_y)
    smooth_ext = sweeps(ext_all[2], source_ext, faces_ext, NU, width_x)
    faces_zero = tuple(crop(member, fine_rim - 1) for member in faces_ext)
    pressure = crop(smooth_ext, 1)
    center, product = apply_fine(smooth_ext, faces_zero)
    residual = source - product
    half_y = width_y // 2
    half_z = depth_cells // 2

    plane_count = aggregate.shape[0]
    ext_pos = slab_index * width_x - 1 + jnp.arange(width_x + 1 + NU)
    pick_ids = ext_pos[:, None] == jnp.arange(plane_count)[None, :]
    ext_ids = jnp.sum(jnp.where(pick_ids, aggregate.astype(jnp.float32)[None, :], 0.0), axis=1)
    local_ids = ext_ids[1 : width_x + 1]
    straddles = (slab_index > 0) & (ext_ids[0] == local_ids[0])
    first_id = local_ids[0] + straddles.astype(jnp.float32)
    count_live = local_ids[-1] - first_id + 1
    slot_ids = local_ids - first_id
    has_next = ext_pos[2 : width_x + 2] < plane_count
    crossing = ((local_ids != ext_ids[2 : width_x + 2]) & has_next).astype(jnp.float32)
    face_east = faces_zero[1]
    face_north = faces_zero[3]
    face_above = faces_zero[5]
    boundary = faces_zero[6]
    index_z = np.arange(depth_cells)[:, None]
    coarse_z = np.arange(half_z)[None, :]
    pair_z = jnp.asarray((index_z // 2 == coarse_z).astype(np.float32))
    odd_z = jnp.asarray((index_z == 2 * coarse_z + 1).astype(np.float32))
    cells = width_x * width_y

    def z_sum(block_in, pick_z):
        flat = block_in.reshape(cells, depth_cells)
        return jnp.dot(flat, pick_z, precision=lax.Precision.HIGHEST)

    z_parts = jnp.stack(
        [
            z_sum(residual, pair_z),
            z_sum(face_east * crossing[:, None, None], pair_z),
            z_sum(face_north, pair_z),
            z_sum(face_above, odd_z),
            z_sum(boundary, pair_z),
        ]
    )
    index_y = np.arange(width_y)[:, None]
    coarse_y = np.arange(half_y)[None, :]
    pair_y = jnp.asarray((index_y // 2 == coarse_y).astype(np.float32))
    row_y = np.tile(np.arange(width_y), width_x)
    col_slot = np.repeat(np.arange(width_x + 1), half_y)
    col_y = np.tile(np.arange(half_y), width_x + 1)
    row_slot = jnp.repeat(slot_ids + 1, width_y)
    same_slot = row_slot[:, None] == jnp.asarray(col_slot.astype(np.float32))[None, :]
    pair_rows = row_y[:, None] // 2 == col_y[None, :]
    odd_rows = row_y[:, None] == 2 * col_y[None, :] + 1
    spread_map = (same_slot & pair_rows).astype(jnp.float32)
    gather_map = (same_slot.T & pair_rows.T).astype(jnp.float32)
    north_gather = (same_slot.T & odd_rows.T).astype(jnp.float32)
    paired = jnp.dot(
        gather_map,
        jnp.concatenate([z_parts[0], z_parts[1], z_parts[3], z_parts[4]], axis=1),
        precision=lax.Precision.HIGHEST,
    )
    north_sums = jnp.dot(north_gather, z_parts[2], precision=lax.Precision.HIGHEST)

    def column(index):
        return paired[:, index * half_z : (index + 1) * half_z]

    slot_sums = jnp.stack([column(0), column(1), north_sums, column(2), column(3)])
    slot_sums = slot_sums.reshape(5, width_x + 1, half_y, half_z)
    coarse = slot_sums[:, 1:]
    edge_sums = slot_sums[:, 0]
    slot_range = jnp.arange(width_x)
    last_slot = (slot_range == count_live - 1).astype(jnp.float32)
    tail_pick = (slot_range[None, :] == count_live - NCS + jnp.arange(NCS)[:, None]).astype(jnp.float32)
    tail_planes = jnp.einsum("ks,qsjl->qkjl", tail_pick, coarse, precision=lax.Precision.HIGHEST)
    head_planes = jnp.concatenate([coarse[:, :NCS], edge_sums[:, None]], axis=1)
    tail_planes, head_planes = lax.optimization_barrier((tail_planes, head_planes))
    from_prev = passed_along(tail_planes, "slab", 1)
    from_next = passed_along(head_planes, "slab", -1)
    coarse = coarse + from_next[:, NCS][:, None] * last_slot[None, :, None, None]
    prev_last = (jnp.arange(NCS) == NCS - 1).astype(jnp.float32)
    from_prev = from_prev + edge_sums[:, None] * prev_last[None, :, None, None]
    x_ext = jnp.concatenate([from_prev, coarse, jnp.zeros_like(tail_planes)], axis=1)
    wide_range = jnp.arange(width_x + 2 * NCS)[:, None]
    place = (wide_range == NCS + count_live + jnp.arange(NCS)[None, :]).astype(jnp.float32)
    x_ext = x_ext + jnp.einsum("tk,qkjl->qtjl", place, from_next[:, :NCS], precision=lax.Precision.HIGHEST)
    coarse_rim = NCS
    coef_ext = padded(x_ext, ((("pencil", "sub"), 2),), coarse_rim)
    coarse_corr = jnp.zeros((width_x + 2 * NCS, half_y + 2 * NCS, half_z), jnp.float32)
    for sweep_index in range(NCS):
        out_rim = NCS - 1 - sweep_index
        start_at = coarse_rim - out_rim
        size_x = width_x + 2 * out_rim
        size_y = half_y + 2 * out_rim

        def region(offset_x, offset_y):
            return coef_ext[
                :,
                start_at + offset_x : start_at + offset_x + size_x,
                start_at + offset_y : start_at + offset_y + size_y,
            ]

        here_coef = region(0, 0)
        coarse_rhs = here_coef[0]
        coarse_east = here_coef[1]
        coarse_north = here_coef[2]
        coarse_above = here_coef[3]
        coarse_bound = here_coef[4]
        coarse_west = region(-1, 0)[1]
        coarse_south = region(0, -1)[2]
        zero_plane = jnp.zeros_like(coarse_above[:, :, :1])
        coarse_below = jnp.concatenate([zero_plane, coarse_above[:, :, :-1]], axis=2)
        diag_coarse = (
            coarse_east
            + coarse_west
            + coarse_north
            + coarse_south
            + coarse_above
            + coarse_below
            + coarse_bound
        )
        safe_coarse = jnp.where(diag_coarse > 0, diag_coarse, 1.0)
        coarse_center = coarse_corr[1:-1, 1:-1]
        above_vals = jnp.concatenate([coarse_center[:, :, 1:], zero_plane], axis=2)
        below_vals = jnp.concatenate([zero_plane, coarse_center[:, :, :-1]], axis=2)
        beside_all = coarse_east * coarse_corr[2:, 1:-1] + coarse_west * coarse_corr[:-2, 1:-1]
        beside_all = (
            beside_all
            + coarse_north * coarse_corr[1:-1, 2:]
            + coarse_south * coarse_corr[1:-1, :-2]
        )
        beside_all = beside_all + coarse_above * above_vals + coarse_below * below_vals
        coarse_corr = (
            coarse_center
            + OMEGA * (coarse_rhs - (diag_coarse * coarse_center - beside_all)) / safe_coarse
        )
    last_corr = jnp.sum(last_slot[:, None, None] * coarse_corr, axis=0)
    corr_wide = jnp.concatenate([jnp.zeros_like(last_corr)[None], coarse_corr], axis=0)
    corr_z = jnp.dot(
        corr_wide.reshape((width_x + 1) * half_y, half_z), pair_z.T, precision=lax.Precision.HIGHEST
    )
    correction = jnp.dot(spread_map, corr_z, precision=lax.Precision.HIGHEST)
    base = pressure + correction.reshape(width_x, width_y, depth_cells)
    last_z = jnp.dot(last_corr, pair_z.T, precision=lax.Precision.HIGHEST)
    last_fine = jnp.dot(pair_y, last_z, precision=lax.Precision.HIGHEST)
    up_block = jnp.concatenate([base[width_x - NU :], last_fine[None]], axis=0)
    below_prev = passed_along(up_block, "slab", 1)
    above_next = passed_along(base[:NU], "slab", -1)
    from_owner = (slot_ids == -1).astype(jnp.float32)
    own = base + from_owner[:, None, None] * below_prev[NU][None]
    next_ids = ext_ids[width_x + 1 :]
    next_in = ext_pos[width_x + 1 :] < plane_count
    to_owner = ((next_ids == local_ids[-1]) & next_in).astype(jnp.float32)
    high_halo = above_next + to_owner[:, None, None] * last_fine[None]
    post_x = jnp.concatenate([below_prev[:NU], own, high_halo], axis=0)
    post_ext = padded(post_x, ((("pencil", "sub"), 1),), NU)
    return sweeps(post_ext, source_ext, faces_ext, NU, width_x)


def solution(mesh):
    in_specs = (
        P(("real", "slab"), ("pencil", "sub"), None),
        P(("real", "slab"), ("pencil", "sub"), None),
        P(("real", "slab"), ("pencil", "sub"), None),
        P("real"),
    )
    out_specs = P(("real", "slab"), ("pencil", "sub"), None)
    return jax.shard_map(body, mesh=mesh, in_specs=in_specs, out_specs=out_specs, check_vma=False)
```

```python
import numpy as np
import jax
import jax.numpy as jnp
from jax import lax
from jax.sharding import PartitionSpec as P

NU = 2
NCS = 4


OMEGA = 0.8


def padded(array, sides, width):
    for axis, dim in sides:
        count, length = (lax.axis_size(axis), array.shape[dim])
        up = [(i, (i + 1) % count) for i in range(count - 1)]
        down = [(j, i) for i, j in up]
        last = lax.slice_in_dim(array, length - width, length, axis=dim)
        leading = lax.slice_in_dim(array, 0, width, axis=dim)
        before = lax.ppermute(last, axis, up)
        after = lax.ppermute(leading, axis, down)
        array = jnp.concatenate([before, array, after], axis=dim)
    return array


def passed_along(array, axis, by):
    count = lax.axis_size(axis)
    pairs = [(i, i + by) for i in range(count) if 0 <= i + by < count]
    return lax.ppermute(array, axis, pairs)


def harmonic(lower_k, upper_k, inside):
    denom_sum = jnp.where(inside, lower_k + upper_k, 1.0)
    return jnp.where(inside, 2.0 * lower_k * upper_k / denom_sum, 0.0)


def geometry(perm_ext, glob_x, glob_y, inside_x, inside_y, total_x, total_y):
    count_z = perm_ext.shape[2]
    both_x = (inside_x[:-1] & inside_x[1:])[:, None, None] & inside_y[None, :, None]
    both_y = (inside_y[:-1] & inside_y[1:])[None, :, None] & inside_x[:, None, None]
    plane_in = inside_x[:, None, None] & inside_y[None, :, None]
    face_x = harmonic(perm_ext[:-1], perm_ext[1:], both_x)
    face_y = harmonic(perm_ext[:, :-1], perm_ext[:, 1:], both_y)
    face_z = harmonic(perm_ext[:, :, :-1], perm_ext[:, :, 1:], plane_in)
    cell_perm = perm_ext[1:-1, 1:-1]
    face_west = face_x[:-1, 1:-1]
    face_east = face_x[1:, 1:-1]
    face_south = face_y[1:-1, :-1]
    face_north = face_y[1:-1, 1:]
    zero_plane = jnp.zeros_like(cell_perm[:, :, :1])
    face_below = jnp.concatenate([zero_plane, face_z[1:-1, 1:-1]], axis=2)
    face_above = jnp.concatenate([face_z[1:-1, 1:-1], zero_plane], axis=2)
    cell_x = glob_x[1:-1]
    cell_y = glob_y[1:-1]
    index_z = jnp.arange(count_z)
    ends_x = (cell_x == 0).astype(jnp.float32) + (cell_x == total_x - 1).astype(jnp.float32)
    ends_y = (cell_y == 0).astype(jnp.float32) + (cell_y == total_y - 1).astype(jnp.float32)
    ends_z = (index_z == 0).astype(jnp.float32) + (index_z == count_z - 1).astype(jnp.float32)
    edges = ends_x[:, None, None] + ends_y[None, :, None] + ends_z[None, None, :]
    boundary = 2.0 * cell_perm * edges
    diagonal = face_west + face_east + face_south + face_north + face_below + face_above + boundary
    cell_in = plane_in[1:-1, 1:-1]
    safe_diag = jnp.where(cell_in, diagonal, 1.0)
    return (
        face_west,
        face_east,
        face_south,
        face_north,
        face_below,
        face_above,
        boundary,
        safe_diag,
    )


def apply_fine(ext_field, faces_now):
    face_west, face_east, face_south, face_north, face_below, face_above, boundary, safe_diag = (
        faces_now
    )
    center = ext_field[1:-1, 1:-1]
    zero_plane = jnp.zeros_like(center[:, :, :1])
    below_vals = jnp.concatenate([zero_plane, center[:, :, :-1]], axis=2)
    above_vals = jnp.concatenate([center[:, :, 1:], zero_plane], axis=2)
    beside_all = face_west * ext_field[:-2, 1:-1] + face_east * ext_field[2:, 1:-1]
    beside_all = beside_all + face_south * ext_field[1:-1, :-2] + face_north * ext_field[1:-1, 2:]
    beside_all = beside_all + face_below * below_vals + face_above * above_vals
    return (center, safe_diag * center - beside_all)


def crop(array, rim):
    if rim == 0:
        return array
    return array[rim : array.shape[0] - rim, rim : array.shape[1] - rim]


def sweeps(field_ext, source_ext, faces_ext, count, width):
    def rim_of(array):
        return (array.shape[0] - width) // 2

    for sweep_index in range(count):
        out_rim = rim_of(field_ext) - 1
        faces_now = tuple(crop(member, rim_of(member) - out_rim) for member in faces_ext)
        center, product = apply_fine(field_ext, faces_now)
        source_now = crop(source_ext, rim_of(source_ext) - out_rim)
        field_ext = center + OMEGA * (source_now - product) / faces_now[7]
    return field_ext


def shifted(array, axis, step):
    zero = jnp.zeros_like(lax.slice_in_dim(array, 0, 1, axis=axis))
    size = array.shape[axis]
    if step > 0:
        return jnp.concatenate([lax.slice_in_dim(array, 1, size, axis=axis), zero], axis=axis)
    return jnp.concatenate([zero, lax.slice_in_dim(array, 0, size - 1, axis=axis)], axis=axis)


def body(permeability, source, pressure, aggregate):
    width_x, width_y, depth_cells = permeability.shape
    slab_index = lax.axis_index("slab")
    slab_count = lax.axis_size("slab")
    row_index = lax.axis_index(("pencil", "sub"))
    row_count = lax.axis_size(("pencil", "sub"))
    total_x = width_x * slab_count
    total_y = width_y * row_count
    stacked_sides = (("slab", 1), (("pencil", "sub"), 2))
    fine_rim = 2 * NU
    ext_all = padded(jnp.stack([permeability, source, pressure]), stacked_sides, fine_rim)
    perm_ext = ext_all[0]
    source_ext = crop(ext_all[1], 1)
    glob_x = slab_index * width_x - fine_rim + jnp.arange(width_x + 2 * fine_rim)
    glob_y = row_index * width_y - fine_rim + jnp.arange(width_y + 2 * fine_rim)
    inside_x = (glob_x >= 0) & (glob_x < total_x)
    inside_y = (glob_y >= 0) & (glob_y < total_y)
    faces_ext = geometry(perm_ext, glob_x, glob_y, inside_x, inside_y, total_x, total_y)
    smooth_ext = sweeps(ext_all[2], source_ext, faces_ext, NU, width_x)
    faces_zero = tuple(crop(member, fine_rim - 1) for member in faces_ext)
    center, product = apply_fine(crop(smooth_ext, NU - 1), faces_zero)
    residual = source - product
    half_y = width_y // 2
    half_z = depth_cells // 2

    plane_count = aggregate.shape[0]
    agg_f = aggregate.astype(jnp.float32)
    plane_range = jnp.arange(plane_count)

    def ids_at(positions):
        pick = positions[:, None] == plane_range[None, :]
        return jnp.sum(jnp.where(pick, agg_f[None, :], 0.0), axis=1)

    ext_pos = slab_index * width_x - NU + jnp.arange(width_x + 2 * NU)
    ext_ids = ids_at(ext_pos)
    local_ids = ext_ids[NU : NU + width_x]
    straddles = (slab_index > 0) & (ext_ids[NU - 1] == local_ids[0])
    first_id = local_ids[0] + straddles.astype(jnp.float32)
    count_live = local_ids[-1] - first_id + 1
    slot_ids = local_ids - first_id
    has_next = ext_pos[NU + 1 : NU + 1 + width_x] < plane_count
    crossing = ((local_ids != ext_ids[NU + 1 : NU + 1 + width_x]) & has_next).astype(jnp.float32)
    side_pos = jnp.stack(
        [
            (slab_index - 1) * width_x - 1,
            (slab_index - 1) * width_x,
            slab_index * width_x - 1,
            (slab_index + 1) * width_x + width_x - 1,
        ]
    )
    side_ids = ids_at(side_pos)
    prev_first = side_ids[1] + ((slab_index > 1) & (side_ids[0] == side_ids[1])).astype(jnp.float32)
    count_prev = side_ids[2] - prev_first + 1
    count_next = side_ids[3] - (local_ids[-1] + 1) + 1

    face_east = faces_zero[1]
    face_north = faces_zero[3]
    face_above = faces_zero[5]
    boundary = faces_zero[6]
    index_z = np.arange(depth_cells)[:, None]
    coarse_z = np.arange(half_z)[None, :]
    pair_z = jnp.asarray((index_z // 2 == coarse_z).astype(np.float32))
    odd_z = jnp.asarray((index_z == 2 * coarse_z + 1).astype(np.float32))
    cells = width_x * width_y

    def z_sum(block_in, pick_z):
        flat = block_in.reshape(cells, depth_cells)
        return jnp.dot(flat, pick_z, precision=lax.Precision.HIGHEST)

    z_parts = jnp.stack(
        [
            z_sum(residual, pair_z),
            z_sum(face_east * crossing[:, None, None], pair_z),
            z_sum(face_north, pair_z),
            z_sum(face_above, odd_z),
            z_sum(boundary, pair_z),
        ]
    )
    row_y = np.tile(np.arange(width_y), width_x)
    col_slot = np.repeat(np.arange(width_x + 1), half_y)
    col_y = np.tile(np.arange(half_y), width_x + 1)
    row_slot = jnp.repeat(slot_ids + 1, width_y)
    same_slot = row_slot[:, None] == jnp.asarray(col_slot.astype(np.float32))[None, :]
    pair_rows = row_y[:, None] // 2 == col_y[None, :]
    odd_rows = row_y[:, None] == 2 * col_y[None, :] + 1
    gather_map = (same_slot.T & pair_rows.T).astype(jnp.float32)
    north_gather = (same_slot.T & odd_rows.T).astype(jnp.float32)
    paired = jnp.dot(
        gather_map,
        jnp.concatenate([z_parts[0], z_parts[1], z_parts[3], z_parts[4]], axis=1),
        precision=lax.Precision.HIGHEST,
    )
    north_sums = jnp.dot(north_gather, z_parts[2], precision=lax.Precision.HIGHEST)

    def column(index):
        return paired[:, index * half_z : (index + 1) * half_z]

    slot_sums = jnp.stack([column(0), column(1), north_sums, column(2), column(3)])
    slot_sums = slot_sums.reshape(5, width_x + 1, half_y, half_z)
    coarse = slot_sums[:, 1:]
    edge_sums = slot_sums[:, 0]
    slot_range = jnp.arange(width_x)

    def pick_slots(first_slot, count):
        chosen = slot_range[None, :] == first_slot + jnp.arange(count)[:, None]
        return jnp.einsum(
            "ks,qsjl->qkjl", chosen.astype(jnp.float32), coarse, precision=lax.Precision.HIGHEST
        )

    low_rim = NCS + NU
    up_one = jnp.concatenate([pick_slots(count_live - low_rim, low_rim), edge_sums[:, None]], axis=1)
    up_two = pick_slots(count_live - NU, NU)
    down_one = jnp.concatenate([coarse[:, :NCS], edge_sums[:, None]], axis=1)
    down_two = edge_sums
    up_one, up_two, down_one, down_two = lax.optimization_barrier((up_one, up_two, down_one, down_two))
    from_prev = passed_along(up_one, "slab", 1)
    from_prev_two = passed_along(up_two, "slab", 2)
    from_next = passed_along(down_one, "slab", -1)
    from_next_two = passed_along(down_two, "slab", -2)
    last_slot = (slot_range == count_live - 1).astype(jnp.float32)
    coarse = coarse + from_next[:, NCS][:, None] * last_slot[None, :, None, None]
    prev_last = (jnp.arange(NU) == NU - 1).astype(jnp.float32)
    before_prev = from_prev_two + from_prev[:, low_rim][:, None] * prev_last[None, :, None, None]
    rim_range = jnp.arange(low_rim)[:, None]
    from_before = (jnp.arange(NU)[None, :] == rim_range - (low_rim - NU) + count_prev) & (
        rim_range < low_rim - count_prev
    )
    low_part = from_prev[:, :low_rim] + jnp.einsum(
        "kj,qjyl->qkyl", from_before.astype(jnp.float32), before_prev, precision=lax.Precision.HIGHEST
    )
    own_fix = (jnp.arange(low_rim) == low_rim - 1).astype(jnp.float32)
    low_part = low_part + edge_sums[:, None] * own_fix[None, :, None, None]
    next_last = (jnp.arange(NCS) == count_next - 1).astype(jnp.float32)
    high_part = from_next[:, :NCS] + from_next_two[:, None] * next_last[None, :, None, None]
    x_ext = jnp.concatenate([low_part, coarse, jnp.zeros_like(high_part)], axis=1)
    wide_range = jnp.arange(low_rim + width_x + NCS)[:, None]
    place = (wide_range == low_rim + count_live + jnp.arange(NCS)[None, :]).astype(jnp.float32)
    x_ext = x_ext + jnp.einsum("tk,qkjl->qtjl", place, high_part, precision=lax.Precision.HIGHEST)
    y_rim = NCS + 1
    coef_ext = padded(x_ext, ((("pencil", "sub"), 2),), y_rim)
    coarse_rhs = coef_ext[0]
    coarse_east = coef_ext[1]
    coarse_north = coef_ext[2]
    coarse_above = coef_ext[3]
    coarse_bound = coef_ext[4]
    coarse_west = shifted(coarse_east, 0, -1)
    coarse_south = shifted(coarse_north, 1, -1)
    coarse_below = shifted(coarse_above, 2, -1)
    diag_coarse = (
        coarse_east
        + coarse_west
        + coarse_north
        + coarse_south
        + coarse_above
        + coarse_below
        + coarse_bound
    )
    safe_coarse = jnp.where(diag_coarse > 0, diag_coarse, 1.0)
    coarse_corr = jnp.zeros_like(coarse_rhs)
    for sweep_index in range(NCS):
        beside_all = coarse_east * shifted(coarse_corr, 0, 1) + coarse_west * shifted(coarse_corr, 0, -1)
        beside_all = (
            beside_all
            + coarse_north * shifted(coarse_corr, 1, 1)
            + coarse_south * shifted(coarse_corr, 1, -1)
        )
        beside_all = (
            beside_all
            + coarse_above * shifted(coarse_corr, 2, 1)
            + coarse_below * shifted(coarse_corr, 2, -1)
        )
        coarse_corr = (
            coarse_corr
            + OMEGA * (coarse_rhs - (diag_coarse * coarse_corr - beside_all)) / safe_coarse
        )
    span = width_x + 2 * NU
    coarse_rows = coarse_corr.shape[1]
    coarse_planes = coarse_corr.shape[0]
    corr_z = jnp.dot(
        coarse_corr.reshape(coarse_planes * coarse_rows, half_z), pair_z.T, precision=lax.Precision.HIGHEST
    )
    fine_rows = np.tile(np.arange(span) - NU, span)
    col_plane = np.repeat(np.arange(coarse_planes), coarse_rows)
    col_row = np.tile(np.arange(coarse_rows), coarse_planes)
    row_match = (fine_rows[:, None] // 2 + y_rim) == col_row[None, :]
    plane_slot = jnp.repeat(ext_ids - first_id + low_rim, span)
    spread_map = (plane_slot[:, None] == jnp.asarray(col_plane.astype(np.float32))[None, :]) & row_match
    correction = jnp.dot(spread_map.astype(jnp.float32), corr_z, precision=lax.Precision.HIGHEST)
    post_ext = smooth_ext + correction.reshape(span, span, depth_cells)
    return sweeps(post_ext, source_ext, faces_ext, NU, width_x)


def solution(mesh):
    in_specs = (
        P(("real", "slab"), ("pencil", "sub"), None),
        P(("real", "slab"), ("pencil", "sub"), None),
        P(("real", "slab"), ("pencil", "sub"), None),
        P("real"),
    )
    out_specs = P(("real", "slab"), ("pencil", "sub"), None)
    return jax.shard_map(body, mesh=mesh, in_specs=in_specs, out_specs=out_specs, check_vma=False)
```

```python
import numpy as np
import jax
import jax.numpy as jnp
from jax import lax
from jax.sharding import PartitionSpec as P

NU = 2
NCS = 4


OMEGA = 0.8


def padded(array, sides, width):
    for axis, dim in sides:
        count, length = (lax.axis_size(axis), array.shape[dim])
        up = [(i, (i + 1) % count) for i in range(count - 1)]
        down = [(j, i) for i, j in up]
        last = lax.slice_in_dim(array, length - width, length, axis=dim)
        leading = lax.slice_in_dim(array, 0, width, axis=dim)
        before = lax.ppermute(last, axis, up)
        after = lax.ppermute(leading, axis, down)
        array = jnp.concatenate([before, array, after], axis=dim)
    return array


def passed_along(array, axis, by):
    count = lax.axis_size(axis)
    pairs = [(i, i + by) for i in range(count) if 0 <= i + by < count]
    return lax.ppermute(array, axis, pairs)


def harmonic(lower_k, upper_k, inside):
    denom_sum = jnp.where(inside, lower_k + upper_k, 1.0)
    return jnp.where(inside, 2.0 * lower_k * upper_k / denom_sum, 0.0)


def geometry(perm_ext, glob_x, glob_y, inside_x, inside_y, total_x, total_y):
    count_z = perm_ext.shape[2]
    both_x = (inside_x[:-1] & inside_x[1:])[:, None, None] & inside_y[None, :, None]
    both_y = (inside_y[:-1] & inside_y[1:])[None, :, None] & inside_x[:, None, None]
    plane_in = inside_x[:, None, None] & inside_y[None, :, None]
    face_x = harmonic(perm_ext[:-1], perm_ext[1:], both_x)
    face_y = harmonic(perm_ext[:, :-1], perm_ext[:, 1:], both_y)
    face_z = harmonic(perm_ext[:, :, :-1], perm_ext[:, :, 1:], plane_in)
    cell_perm = perm_ext[1:-1, 1:-1]
    face_west = face_x[:-1, 1:-1]
    face_east = face_x[1:, 1:-1]
    face_south = face_y[1:-1, :-1]
    face_north = face_y[1:-1, 1:]
    zero_plane = jnp.zeros_like(cell_perm[:, :, :1])
    face_below = jnp.concatenate([zero_plane, face_z[1:-1, 1:-1]], axis=2)
    face_above = jnp.concatenate([face_z[1:-1, 1:-1], zero_plane], axis=2)
    cell_x = glob_x[1:-1]
    cell_y = glob_y[1:-1]
    index_z = jnp.arange(count_z)
    ends_x = (cell_x == 0).astype(jnp.float32) + (cell_x == total_x - 1).astype(jnp.float32)
    ends_y = (cell_y == 0).astype(jnp.float32) + (cell_y == total_y - 1).astype(jnp.float32)
    ends_z = (index_z == 0).astype(jnp.float32) + (index_z == count_z - 1).astype(jnp.float32)
    edges = ends_x[:, None, None] + ends_y[None, :, None] + ends_z[None, None, :]
    boundary = 2.0 * cell_perm * edges
    diagonal = face_west + face_east + face_south + face_north + face_below + face_above + boundary
    cell_in = plane_in[1:-1, 1:-1]
    safe_diag = jnp.where(cell_in, diagonal, 1.0)
    return (
        face_west,
        face_east,
        face_south,
        face_north,
        face_below,
        face_above,
        boundary,
        safe_diag,
    )


def apply_fine(ext_field, faces_now):
    face_west, face_east, face_south, face_north, face_below, face_above, boundary, safe_diag = (
        faces_now
    )
    center = ext_field[1:-1, 1:-1]
    zero_plane = jnp.zeros_like(center[:, :, :1])
    below_vals = jnp.concatenate([zero_plane, center[:, :, :-1]], axis=2)
    above_vals = jnp.concatenate([center[:, :, 1:], zero_plane], axis=2)
    beside_all = face_west * ext_field[:-2, 1:-1] + face_east * ext_field[2:, 1:-1]
    beside_all = beside_all + face_south * ext_field[1:-1, :-2] + face_north * ext_field[1:-1, 2:]
    beside_all = beside_all + face_below * below_vals + face_above * above_vals
    return (center, safe_diag * center - beside_all)


def crop(array, rim):
    if rim == 0:
        return array
    return array[rim : array.shape[0] - rim, rim : array.shape[1] - rim]


def sweeps(field_ext, source_ext, faces_ext, count, width):
    def rim_of(array):
        return (array.shape[0] - width) // 2

    for sweep_index in range(count):
        out_rim = rim_of(field_ext) - 1
        faces_now = tuple(crop(member, rim_of(member) - out_rim) for member in faces_ext)
        center, product = apply_fine(field_ext, faces_now)
        source_now = crop(source_ext, rim_of(source_ext) - out_rim)
        field_ext = center + OMEGA * (source_now - product) / faces_now[7]
    return field_ext


def body(permeability, source, pressure, aggregate):
    width_x, width_y, depth_cells = permeability.shape
    slab_index = lax.axis_index("slab")
    slab_count = lax.axis_size("slab")
    row_index = lax.axis_index(("pencil", "sub"))
    row_count = lax.axis_size(("pencil", "sub"))
    total_x = width_x * slab_count
    total_y = width_y * row_count
    sides = (("slab", 0), (("pencil", "sub"), 1))
    stacked_sides = (("slab", 1), (("pencil", "sub"), 2))
    fine_rim = NU + 1
    ext_x = padded(jnp.stack([permeability, source, pressure]), (("slab", 1),), fine_rim)
    ext_x, aggregate = lax.optimization_barrier((ext_x, aggregate))
    ext_all = padded(ext_x, ((("pencil", "sub"), 2),), fine_rim)
    perm_ext = ext_all[0]
    source_ext = crop(ext_all[1], 1)
    glob_x = slab_index * width_x - fine_rim + jnp.arange(width_x + 2 * fine_rim)
    glob_y = row_index * width_y - fine_rim + jnp.arange(width_y + 2 * fine_rim)
    inside_x = (glob_x >= 0) & (glob_x < total_x)
    inside_y = (glob_y >= 0) & (glob_y < total_y)
    faces_ext = geometry(perm_ext, glob_x, glob_y, inside_x, inside_y, total_x, total_y)
    smooth_ext = sweeps(ext_all[2], source_ext, faces_ext, NU, width_x)
    faces_zero = tuple(crop(member, fine_rim - 1) for member in faces_ext)
    pressure = crop(smooth_ext, 1)
    center, product = apply_fine(smooth_ext, faces_zero)
    residual = source - product
    half_y = width_y // 2
    half_z = depth_cells // 2

    plane_count = aggregate.shape[0]
    ext_pos = slab_index * width_x - 1 + jnp.arange(width_x + 1 + NU)
    pick_ids = ext_pos[:, None] == jnp.arange(plane_count)[None, :]
    ext_ids = jnp.sum(jnp.where(pick_ids, aggregate.astype(jnp.float32)[None, :], 0.0), axis=1)
    local_ids = ext_ids[1 : width_x + 1]
    straddles = (slab_index > 0) & (ext_ids[0] == local_ids[0])
    first_id = local_ids[0] + straddles.astype(jnp.float32)
    count_live = local_ids[-1] - first_id + 1
    slot_ids = local_ids - first_id
    has_next = ext_pos[2 : width_x + 2] < plane_count
    crossing = ((local_ids != ext_ids[2 : width_x + 2]) & has_next).astype(jnp.float32)
    face_east = faces_zero[1]
    face_north = faces_zero[3]
    face_above = faces_zero[5]
    boundary = faces_zero[6]
    index_z = np.arange(depth_cells)[:, None]
    coarse_z = np.arange(half_z)[None, :]
    pair_z = jnp.asarray((index_z // 2 == coarse_z).astype(np.float32))
    odd_z = jnp.asarray((index_z == 2 * coarse_z + 1).astype(np.float32))
    cells = width_x * width_y

    def z_sum(block_in, pick_z):
        flat = block_in.reshape(cells, depth_cells)
        return jnp.dot(flat, pick_z, precision=lax.Precision.HIGHEST)

    z_parts = jnp.stack(
        [
            z_sum(residual, pair_z),
            z_sum(face_east * crossing[:, None, None], pair_z),
            z_sum(face_north, pair_z),
            z_sum(face_above, odd_z),
            z_sum(boundary, pair_z),
        ]
    )
    index_y = np.arange(width_y)[:, None]
    coarse_y = np.arange(half_y)[None, :]
    pair_y = jnp.asarray((index_y // 2 == coarse_y).astype(np.float32))
    row_y = np.tile(np.arange(width_y), width_x)
    col_slot = np.repeat(np.arange(width_x + 1), half_y)
    col_y = np.tile(np.arange(half_y), width_x + 1)
    row_slot = jnp.repeat(slot_ids + 1, width_y)
    same_slot = row_slot[:, None] == jnp.asarray(col_slot.astype(np.float32))[None, :]
    pair_rows = row_y[:, None] // 2 == col_y[None, :]
    odd_rows = row_y[:, None] == 2 * col_y[None, :] + 1
    spread_map = (same_slot & pair_rows).astype(jnp.float32)
    gather_map = (same_slot.T & pair_rows.T).astype(jnp.float32)
    north_gather = (same_slot.T & odd_rows.T).astype(jnp.float32)
    paired = jnp.dot(
        gather_map,
        jnp.concatenate([z_parts[0], z_parts[1], z_parts[3], z_parts[4]], axis=1),
        precision=lax.Precision.HIGHEST,
    )
    north_sums = jnp.dot(north_gather, z_parts[2], precision=lax.Precision.HIGHEST)

    def column(index):
        return paired[:, index * half_z : (index + 1) * half_z]

    slot_sums = jnp.stack([column(0), column(1), north_sums, column(2), column(3)])
    slot_sums = slot_sums.reshape(5, width_x + 1, half_y, half_z)
    coarse = slot_sums[:, 1:]
    edge_sums = slot_sums[:, 0]
    slot_range = jnp.arange(width_x)
    last_slot = (slot_range == count_live - 1).astype(jnp.float32)
    tail_pick = (slot_range[None, :] == count_live - NCS + jnp.arange(NCS)[:, None]).astype(jnp.float32)
    tail_planes = jnp.einsum("ks,qsjl->qkjl", tail_pick, coarse, precision=lax.Precision.HIGHEST)
    head_planes = jnp.concatenate([coarse[:, :NCS], edge_sums[:, None]], axis=1)
    tail_planes, head_planes = lax.optimization_barrier((tail_planes, head_planes))
    from_prev = passed_along(tail_planes, "slab", 1)
    from_next = passed_along(head_planes, "slab", -1)
    coarse = coarse + from_next[:, NCS][:, None] * last_slot[None, :, None, None]
    prev_last = (jnp.arange(NCS) == NCS - 1).astype(jnp.float32)
    from_prev = from_prev + edge_sums[:, None] * prev_last[None, :, None, None]
    x_ext = jnp.concatenate([from_prev, coarse, jnp.zeros_like(tail_planes)], axis=1)
    wide_range = jnp.arange(width_x + 2 * NCS)[:, None]
    place = (wide_range == NCS + count_live + jnp.arange(NCS)[None, :]).astype(jnp.float32)
    x_ext = x_ext + jnp.einsum("tk,qkjl->qtjl", place, from_next[:, :NCS], precision=lax.Precision.HIGHEST)
    coarse_rim = NCS
    coef_ext = padded(x_ext, ((("pencil", "sub"), 2),), coarse_rim)
    coarse_corr = jnp.zeros((width_x + 2 * NCS, half_y + 2 * NCS, half_z), jnp.float32)
    for sweep_index in range(NCS):
        out_rim = NCS - 1 - sweep_index
        start_at = coarse_rim - out_rim
        size_x = width_x + 2 * out_rim
        size_y = half_y + 2 * out_rim

        def region(offset_x, offset_y):
            return coef_ext[
                :,
                start_at + offset_x : start_at + offset_x + size_x,
                start_at + offset_y : start_at + offset_y + size_y,
            ]

        here_coef = region(0, 0)
        coarse_rhs = here_coef[0]
        coarse_east = here_coef[1]
        coarse_north = here_coef[2]
        coarse_above = here_coef[3]
        coarse_bound = here_coef[4]
        coarse_west = region(-1, 0)[1]
        coarse_south = region(0, -1)[2]
        zero_plane = jnp.zeros_like(coarse_above[:, :, :1])
        coarse_below = jnp.concatenate([zero_plane, coarse_above[:, :, :-1]], axis=2)
        diag_coarse = (
            coarse_east
            + coarse_west
            + coarse_north
            + coarse_south
            + coarse_above
            + coarse_below
            + coarse_bound
        )
        safe_coarse = jnp.where(diag_coarse > 0, diag_coarse, 1.0)
        coarse_center = coarse_corr[1:-1, 1:-1]
        above_vals = jnp.concatenate([coarse_center[:, :, 1:], zero_plane], axis=2)
        below_vals = jnp.concatenate([zero_plane, coarse_center[:, :, :-1]], axis=2)
        beside_all = coarse_east * coarse_corr[2:, 1:-1] + coarse_west * coarse_corr[:-2, 1:-1]
        beside_all = (
            beside_all
            + coarse_north * coarse_corr[1:-1, 2:]
            + coarse_south * coarse_corr[1:-1, :-2]
        )
        beside_all = beside_all + coarse_above * above_vals + coarse_below * below_vals
        coarse_corr = (
            coarse_center
            + OMEGA * (coarse_rhs - (diag_coarse * coarse_center - beside_all)) / safe_coarse
        )
    last_corr = jnp.sum(last_slot[:, None, None] * coarse_corr, axis=0)
    corr_wide = jnp.concatenate([jnp.zeros_like(last_corr)[None], coarse_corr], axis=0)
    corr_z = jnp.dot(
        corr_wide.reshape((width_x + 1) * half_y, half_z), pair_z.T, precision=lax.Precision.HIGHEST
    )
    correction = jnp.dot(spread_map, corr_z, precision=lax.Precision.HIGHEST)
    base = pressure + correction.reshape(width_x, width_y, depth_cells)
    last_z = jnp.dot(last_corr, pair_z.T, precision=lax.Precision.HIGHEST)
    last_fine = jnp.dot(pair_y, last_z, precision=lax.Precision.HIGHEST)
    up_block = jnp.concatenate([base[width_x - NU :], last_fine[None]], axis=0)
    below_prev = passed_along(up_block, "slab", 1)
    above_next = passed_along(base[:NU], "slab", -1)
    from_owner = (slot_ids == -1).astype(jnp.float32)
    own = base + from_owner[:, None, None] * below_prev[NU][None]
    next_ids = ext_ids[width_x + 1 :]
    next_in = ext_pos[width_x + 1 :] < plane_count
    to_owner = ((next_ids == local_ids[-1]) & next_in).astype(jnp.float32)
    high_halo = above_next + to_owner[:, None, None] * last_fine[None]
    post_x = jnp.concatenate([below_prev[:NU], own, high_halo], axis=0)
    post_ext = padded(post_x, ((("pencil", "sub"), 1),), NU)
    return sweeps(post_ext, source_ext, faces_ext, NU, width_x)


def solution(mesh):
    in_specs = (
        P(("real", "slab"), ("pencil", "sub"), None),
        P(("real", "slab"), ("pencil", "sub"), None),
        P(("real", "slab"), ("pencil", "sub"), None),
        P("real"),
    )
    out_specs = P(("real", "slab"), ("pencil", "sub"), None)
    return jax.shard_map(body, mesh=mesh, in_specs=in_specs, out_specs=out_specs, check_vma=False)
```

```python
import numpy as np
import jax
import jax.numpy as jnp
from jax import lax
from jax.sharding import PartitionSpec as P

NU = 2
NCS = 4


OMEGA = 0.8


def padded(array, sides, width):
    for axis, dim in sides:
        count, length = (lax.axis_size(axis), array.shape[dim])
        up = [(i, (i + 1) % count) for i in range(count - 1)]
        down = [(j, i) for i, j in up]
        last = lax.slice_in_dim(array, length - width, length, axis=dim)
        leading = lax.slice_in_dim(array, 0, width, axis=dim)
        before = lax.ppermute(last, axis, up)
        after = lax.ppermute(leading, axis, down)
        array = jnp.concatenate([before, array, after], axis=dim)
    return array


def passed_along(array, axis, by):
    count = lax.axis_size(axis)
    pairs = [(i, i + by) for i in range(count) if 0 <= i + by < count]
    return lax.ppermute(array, axis, pairs)


def harmonic(lower_k, upper_k, inside):
    denom_sum = jnp.where(inside, lower_k + upper_k, 1.0)
    return jnp.where(inside, 2.0 * lower_k * upper_k / denom_sum, 0.0)


def geometry(perm_ext, glob_x, glob_y, inside_x, inside_y, total_x, total_y):
    count_z = perm_ext.shape[2]
    both_x = (inside_x[:-1] & inside_x[1:])[:, None, None] & inside_y[None, :, None]
    both_y = (inside_y[:-1] & inside_y[1:])[None, :, None] & inside_x[:, None, None]
    plane_in = inside_x[:, None, None] & inside_y[None, :, None]
    face_x = harmonic(perm_ext[:-1], perm_ext[1:], both_x)
    face_y = harmonic(perm_ext[:, :-1], perm_ext[:, 1:], both_y)
    face_z = harmonic(perm_ext[:, :, :-1], perm_ext[:, :, 1:], plane_in)
    cell_perm = perm_ext[1:-1, 1:-1]
    face_west = face_x[:-1, 1:-1]
    face_east = face_x[1:, 1:-1]
    face_south = face_y[1:-1, :-1]
    face_north = face_y[1:-1, 1:]
    zero_plane = jnp.zeros_like(cell_perm[:, :, :1])
    face_below = jnp.concatenate([zero_plane, face_z[1:-1, 1:-1]], axis=2)
    face_above = jnp.concatenate([face_z[1:-1, 1:-1], zero_plane], axis=2)
    cell_x = glob_x[1:-1]
    cell_y = glob_y[1:-1]
    index_z = jnp.arange(count_z)
    ends_x = (cell_x == 0).astype(jnp.float32) + (cell_x == total_x - 1).astype(jnp.float32)
    ends_y = (cell_y == 0).astype(jnp.float32) + (cell_y == total_y - 1).astype(jnp.float32)
    ends_z = (index_z == 0).astype(jnp.float32) + (index_z == count_z - 1).astype(jnp.float32)
    edges = ends_x[:, None, None] + ends_y[None, :, None] + ends_z[None, None, :]
    boundary = 2.0 * cell_perm * edges
    diagonal = face_west + face_east + face_south + face_north + face_below + face_above + boundary
    cell_in = plane_in[1:-1, 1:-1]
    safe_diag = jnp.where(cell_in, diagonal, 1.0)
    return (
        face_west,
        face_east,
        face_south,
        face_north,
        face_below,
        face_above,
        boundary,
        safe_diag,
    )


def apply_fine(ext_field, faces_now):
    face_west, face_east, face_south, face_north, face_below, face_above, boundary, safe_diag = (
        faces_now
    )
    center = ext_field[1:-1, 1:-1]
    zero_plane = jnp.zeros_like(center[:, :, :1])
    below_vals = jnp.concatenate([zero_plane, center[:, :, :-1]], axis=2)
    above_vals = jnp.concatenate([center[:, :, 1:], zero_plane], axis=2)
    beside_all = face_west * ext_field[:-2, 1:-1] + face_east * ext_field[2:, 1:-1]
    beside_all = beside_all + face_south * ext_field[1:-1, :-2] + face_north * ext_field[1:-1, 2:]
    beside_all = beside_all + face_below * below_vals + face_above * above_vals
    return (center, safe_diag * center - beside_all)


def crop(array, rim):
    if rim == 0:
        return array
    return array[rim : array.shape[0] - rim, rim : array.shape[1] - rim]


def sweeps(field_ext, source_ext, faces_ext, count, width):
    def rim_of(array):
        return (array.shape[0] - width) // 2

    for sweep_index in range(count):
        out_rim = rim_of(field_ext) - 1
        faces_now = tuple(crop(member, rim_of(member) - out_rim) for member in faces_ext)
        center, product = apply_fine(field_ext, faces_now)
        source_now = crop(source_ext, rim_of(source_ext) - out_rim)
        field_ext = center + OMEGA * (source_now - product) / faces_now[7]
    return field_ext


def body(permeability, source, pressure, aggregate):
    width_x, width_y, depth_cells = permeability.shape
    slab_index = lax.axis_index("slab")
    slab_count = lax.axis_size("slab")
    row_index = lax.axis_index(("pencil", "sub"))
    row_count = lax.axis_size(("pencil", "sub"))
    total_x = width_x * slab_count
    total_y = width_y * row_count
    sides = (("slab", 0), (("pencil", "sub"), 1))
    stacked_sides = (("slab", 1), (("pencil", "sub"), 2))
    fine_rim = 2 * NU
    ext_x = padded(jnp.stack([permeability, source, pressure]), (("slab", 1),), fine_rim)
    ext_x, aggregate = lax.optimization_barrier((ext_x, aggregate))
    ext_all = padded(ext_x, ((("pencil", "sub"), 2),), fine_rim)
    perm_ext = ext_all[0]
    source_ext = crop(ext_all[1], 1)
    glob_x = slab_index * width_x - fine_rim + jnp.arange(width_x + 2 * fine_rim)
    glob_y = row_index * width_y - fine_rim + jnp.arange(width_y + 2 * fine_rim)
    inside_x = (glob_x >= 0) & (glob_x < total_x)
    inside_y = (glob_y >= 0) & (glob_y < total_y)
    faces_ext = geometry(perm_ext, glob_x, glob_y, inside_x, inside_y, total_x, total_y)
    smooth_ext = sweeps(ext_all[2], source_ext, faces_ext, NU, width_x)
    faces_zero = tuple(crop(member, fine_rim - 1) for member in faces_ext)
    smooth_rows = smooth_ext[NU : NU + width_x]
    center, product = apply_fine(crop(smooth_ext, NU - 1), faces_zero)
    residual = source - product
    half_y = width_y // 2
    half_z = depth_cells // 2

    plane_count = aggregate.shape[0]
    ext_pos = slab_index * width_x - 1 + jnp.arange(width_x + 1 + NU)
    pick_ids = ext_pos[:, None] == jnp.arange(plane_count)[None, :]
    ext_ids = jnp.sum(jnp.where(pick_ids, aggregate.astype(jnp.float32)[None, :], 0.0), axis=1)
    local_ids = ext_ids[1 : width_x + 1]
    straddles = (slab_index > 0) & (ext_ids[0] == local_ids[0])
    first_id = local_ids[0] + straddles.astype(jnp.float32)
    count_live = local_ids[-1] - first_id + 1
    slot_ids = local_ids - first_id
    has_next = ext_pos[2 : width_x + 2] < plane_count
    crossing = ((local_ids != ext_ids[2 : width_x + 2]) & has_next).astype(jnp.float32)
    face_east = faces_zero[1]
    face_north = faces_zero[3]
    face_above = faces_zero[5]
    boundary = faces_zero[6]
    index_z = np.arange(depth_cells)[:, None]
    coarse_z = np.arange(half_z)[None, :]
    pair_z = jnp.asarray((index_z // 2 == coarse_z).astype(np.float32))
    odd_z = jnp.asarray((index_z == 2 * coarse_z + 1).astype(np.float32))
    cells = width_x * width_y

    def z_sum(block_in, pick_z):
        flat = block_in.reshape(cells, depth_cells)
        return jnp.dot(flat, pick_z, precision=lax.Precision.HIGHEST)

    z_parts = jnp.stack(
        [
            z_sum(residual, pair_z),
            z_sum(face_east * crossing[:, None, None], pair_z),
            z_sum(face_north, pair_z),
            z_sum(face_above, odd_z),
            z_sum(boundary, pair_z),
        ]
    )
    index_y = np.arange(width_y)[:, None]
    coarse_y = np.arange(half_y)[None, :]
    pair_y = jnp.asarray((index_y // 2 == coarse_y).astype(np.float32))
    row_y = np.tile(np.arange(width_y), width_x)
    col_slot = np.repeat(np.arange(width_x + 1), half_y)
    col_y = np.tile(np.arange(half_y), width_x + 1)
    row_slot = jnp.repeat(slot_ids + 1, width_y)
    same_slot = row_slot[:, None] == jnp.asarray(col_slot.astype(np.float32))[None, :]
    pair_rows = row_y[:, None] // 2 == col_y[None, :]
    odd_rows = row_y[:, None] == 2 * col_y[None, :] + 1
    spread_map = (same_slot & pair_rows).astype(jnp.float32)
    gather_map = (same_slot.T & pair_rows.T).astype(jnp.float32)
    north_gather = (same_slot.T & odd_rows.T).astype(jnp.float32)
    paired = jnp.dot(
        gather_map,
        jnp.concatenate([z_parts[0], z_parts[1], z_parts[3], z_parts[4]], axis=1),
        precision=lax.Precision.HIGHEST,
    )
    north_sums = jnp.dot(north_gather, z_parts[2], precision=lax.Precision.HIGHEST)

    def column(index):
        return paired[:, index * half_z : (index + 1) * half_z]

    slot_sums = jnp.stack([column(0), column(1), north_sums, column(2), column(3)])
    slot_sums = slot_sums.reshape(5, width_x + 1, half_y, half_z)
    coarse = slot_sums[:, 1:]
    edge_sums = slot_sums[:, 0]
    slot_range = jnp.arange(width_x)
    last_slot = (slot_range == count_live - 1).astype(jnp.float32)
    tail_pick = (slot_range[None, :] == count_live - NCS + jnp.arange(NCS)[:, None]).astype(jnp.float32)
    tail_planes = jnp.einsum("ks,qsjl->qkjl", tail_pick, coarse, precision=lax.Precision.HIGHEST)
    head_planes = jnp.concatenate([coarse[:, :NCS], edge_sums[:, None]], axis=1)
    tail_planes, head_planes = lax.optimization_barrier((tail_planes, head_planes))
    from_prev = passed_along(tail_planes, "slab", 1)
    from_next = passed_along(head_planes, "slab", -1)
    coarse = coarse + from_next[:, NCS][:, None] * last_slot[None, :, None, None]
    prev_last = (jnp.arange(NCS) == NCS - 1).astype(jnp.float32)
    from_prev = from_prev + edge_sums[:, None] * prev_last[None, :, None, None]
    x_ext = jnp.concatenate([from_prev, coarse, jnp.zeros_like(tail_planes)], axis=1)
    wide_range = jnp.arange(width_x + 2 * NCS)[:, None]
    place = (wide_range == NCS + count_live + jnp.arange(NCS)[None, :]).astype(jnp.float32)
    x_ext = x_ext + jnp.einsum("tk,qkjl->qtjl", place, from_next[:, :NCS], precision=lax.Precision.HIGHEST)
    coarse_rim = NCS
    rim_y = NCS + 1
    coef_ext = padded(x_ext, ((("pencil", "sub"), 2),), rim_y)
    coarse_corr = jnp.zeros((width_x + 2 * NCS, half_y + 2 * rim_y, half_z), jnp.float32)
    for sweep_index in range(NCS):
        out_rim = NCS - 1 - sweep_index
        start_at = coarse_rim - out_rim
        start_y = start_at
        size_x = width_x + 2 * out_rim
        size_y = half_y + 2 * (out_rim + 1)

        def region(offset_x, offset_y):
            return coef_ext[
                :,
                start_at + offset_x : start_at + offset_x + size_x,
                start_y + offset_y : start_y + offset_y + size_y,
            ]

        here_coef = region(0, 0)
        coarse_rhs = here_coef[0]
        coarse_east = here_coef[1]
        coarse_north = here_coef[2]
        coarse_above = here_coef[3]
        coarse_bound = here_coef[4]
        coarse_west = region(-1, 0)[1]
        coarse_south = region(0, -1)[2]
        zero_plane = jnp.zeros_like(coarse_above[:, :, :1])
        coarse_below = jnp.concatenate([zero_plane, coarse_above[:, :, :-1]], axis=2)
        diag_coarse = (
            coarse_east
            + coarse_west
            + coarse_north
            + coarse_south
            + coarse_above
            + coarse_below
            + coarse_bound
        )
        safe_coarse = jnp.where(diag_coarse > 0, diag_coarse, 1.0)
        coarse_center = coarse_corr[1:-1, 1:-1]
        above_vals = jnp.concatenate([coarse_center[:, :, 1:], zero_plane], axis=2)
        below_vals = jnp.concatenate([zero_plane, coarse_center[:, :, :-1]], axis=2)
        beside_all = coarse_east * coarse_corr[2:, 1:-1] + coarse_west * coarse_corr[:-2, 1:-1]
        beside_all = (
            beside_all
            + coarse_north * coarse_corr[1:-1, 2:]
            + coarse_south * coarse_corr[1:-1, :-2]
        )
        beside_all = beside_all + coarse_above * above_vals + coarse_below * below_vals
        coarse_corr = (
            coarse_center
            + OMEGA * (coarse_rhs - (diag_coarse * coarse_center - beside_all)) / safe_coarse
        )
    last_corr = jnp.sum(last_slot[:, None, None] * coarse_corr, axis=0)
    corr_wide = jnp.concatenate([jnp.zeros_like(last_corr)[None], coarse_corr], axis=0)
    corr_core = corr_wide[:, 1 : 1 + half_y]
    corr_z = jnp.dot(
        corr_core.reshape((width_x + 1) * half_y, half_z), pair_z.T, precision=lax.Precision.HIGHEST
    )
    correction = jnp.dot(spread_map, corr_z, precision=lax.Precision.HIGHEST)
    correction = correction.reshape(width_x, width_y, depth_cells)
    owner_rows = (slot_ids[:, None] + 1 == jnp.arange(width_x + 1)[None, :]).astype(jnp.float32)

    def rim_rows(coarse_row):
        row_z = jnp.dot(corr_wide[:, coarse_row], pair_z.T, precision=lax.Precision.HIGHEST)
        row_fine = jnp.dot(owner_rows, row_z, precision=lax.Precision.HIGHEST)
        return jnp.broadcast_to(row_fine[:, None], (width_x, NU, depth_cells))

    correction = jnp.concatenate([rim_rows(0), correction, rim_rows(half_y + 1)], axis=1)
    base = smooth_rows + correction
    last_z = jnp.dot(last_corr, pair_z.T, precision=lax.Precision.HIGHEST)
    fine_y = np.arange(width_y + 2 * NU) - NU
    rows_ext = jnp.asarray((fine_y[:, None] // 2 + 1 == np.arange(half_y + 2)[None, :]).astype(np.float32))
    last_fine = jnp.dot(rows_ext, last_z, precision=lax.Precision.HIGHEST)
    up_block = jnp.concatenate([base[width_x - NU :], last_fine[None]], axis=0)
    below_prev = passed_along(up_block, "slab", 1)
    above_next = passed_along(base[:NU], "slab", -1)
    from_owner = (slot_ids == -1).astype(jnp.float32)
    own = base + from_owner[:, None, None] * below_prev[NU][None]
    next_ids = ext_ids[width_x + 1 :]
    next_in = ext_pos[width_x + 1 :] < plane_count
    to_owner = ((next_ids == local_ids[-1]) & next_in).astype(jnp.float32)
    high_halo = above_next + to_owner[:, None, None] * last_fine[None]
    post_ext = jnp.concatenate([below_prev[:NU], own, high_halo], axis=0)
    return sweeps(post_ext, source_ext, faces_ext, NU, width_x)


def solution(mesh):
    in_specs = (
        P(("real", "slab"), ("pencil", "sub"), None),
        P(("real", "slab"), ("pencil", "sub"), None),
        P(("real", "slab"), ("pencil", "sub"), None),
        P("real"),
    )
    out_specs = P(("real", "slab"), ("pencil", "sub"), None)
    return jax.shard_map(body, mesh=mesh, in_specs=in_specs, out_specs=out_specs, check_vma=False)
```

```python
import numpy as np
import jax
import jax.numpy as jnp
from jax import lax
from jax.sharding import PartitionSpec as P

NU = 2
NCS = 4


OMEGA = 0.8


def padded(array, sides, width):
    for axis, dim in sides:
        count, length = (lax.axis_size(axis), array.shape[dim])
        up = [(i, (i + 1) % count) for i in range(count - 1)]
        down = [(j, i) for i, j in up]
        last = lax.slice_in_dim(array, length - width, length, axis=dim)
        leading = lax.slice_in_dim(array, 0, width, axis=dim)
        before = lax.ppermute(last, axis, up)
        after = lax.ppermute(leading, axis, down)
        array = jnp.concatenate([before, array, after], axis=dim)
    return array


def passed_along(array, axis, by):
    count = lax.axis_size(axis)
    pairs = [(i, i + by) for i in range(count) if 0 <= i + by < count]
    return lax.ppermute(array, axis, pairs)


def harmonic(lower_k, upper_k, inside):
    denom_sum = jnp.where(inside, lower_k + upper_k, 1.0)
    return jnp.where(inside, 2.0 * lower_k * upper_k / denom_sum, 0.0)


def geometry(perm_ext, glob_x, glob_y, inside_x, inside_y, total_x, total_y):
    count_z = perm_ext.shape[2]
    both_x = (inside_x[:-1] & inside_x[1:])[:, None, None] & inside_y[None, :, None]
    both_y = (inside_y[:-1] & inside_y[1:])[None, :, None] & inside_x[:, None, None]
    plane_in = inside_x[:, None, None] & inside_y[None, :, None]
    face_x = harmonic(perm_ext[:-1], perm_ext[1:], both_x)
    face_y = harmonic(perm_ext[:, :-1], perm_ext[:, 1:], both_y)
    face_z = harmonic(perm_ext[:, :, :-1], perm_ext[:, :, 1:], plane_in)
    cell_perm = perm_ext[1:-1, 1:-1]
    face_west = face_x[:-1, 1:-1]
    face_east = face_x[1:, 1:-1]
    face_south = face_y[1:-1, :-1]
    face_north = face_y[1:-1, 1:]
    zero_plane = jnp.zeros_like(cell_perm[:, :, :1])
    face_below = jnp.concatenate([zero_plane, face_z[1:-1, 1:-1]], axis=2)
    face_above = jnp.concatenate([face_z[1:-1, 1:-1], zero_plane], axis=2)
    cell_x = glob_x[1:-1]
    cell_y = glob_y[1:-1]
    index_z = jnp.arange(count_z)
    ends_x = (cell_x == 0).astype(jnp.float32) + (cell_x == total_x - 1).astype(jnp.float32)
    ends_y = (cell_y == 0).astype(jnp.float32) + (cell_y == total_y - 1).astype(jnp.float32)
    ends_z = (index_z == 0).astype(jnp.float32) + (index_z == count_z - 1).astype(jnp.float32)
    edges = ends_x[:, None, None] + ends_y[None, :, None] + ends_z[None, None, :]
    boundary = 2.0 * cell_perm * edges
    diagonal = face_west + face_east + face_south + face_north + face_below + face_above + boundary
    cell_in = plane_in[1:-1, 1:-1]
    safe_diag = jnp.where(cell_in, diagonal, 1.0)
    return (
        face_west,
        face_east,
        face_south,
        face_north,
        face_below,
        face_above,
        boundary,
        safe_diag,
    )


def apply_fine(ext_field, faces_now):
    face_west, face_east, face_south, face_north, face_below, face_above, boundary, safe_diag = (
        faces_now
    )
    center = ext_field[1:-1, 1:-1]
    zero_plane = jnp.zeros_like(center[:, :, :1])
    below_vals = jnp.concatenate([zero_plane, center[:, :, :-1]], axis=2)
    above_vals = jnp.concatenate([center[:, :, 1:], zero_plane], axis=2)
    beside_all = face_west * ext_field[:-2, 1:-1] + face_east * ext_field[2:, 1:-1]
    beside_all = beside_all + face_south * ext_field[1:-1, :-2] + face_north * ext_field[1:-1, 2:]
    beside_all = beside_all + face_below * below_vals + face_above * above_vals
    return (center, safe_diag * center - beside_all)


def crop(array, rim):
    if rim == 0:
        return array
    return array[rim : array.shape[0] - rim, rim : array.shape[1] - rim]


def sweeps(field_ext, source_ext, faces_ext, count, width):
    def rim_of(array):
        return (array.shape[0] - width) // 2

    for sweep_index in range(count):
        out_rim = rim_of(field_ext) - 1
        faces_now = tuple(crop(member, rim_of(member) - out_rim) for member in faces_ext)
        center, product = apply_fine(field_ext, faces_now)
        source_now = crop(source_ext, rim_of(source_ext) - out_rim)
        field_ext = center + OMEGA * (source_now - product) / faces_now[7]
    return field_ext


def body(permeability, source, pressure, aggregate):
    width_x, width_y, depth_cells = permeability.shape
    slab_index = lax.axis_index("slab")
    slab_count = lax.axis_size("slab")
    row_index = lax.axis_index(("pencil", "sub"))
    row_count = lax.axis_size(("pencil", "sub"))
    total_x = width_x * slab_count
    total_y = width_y * row_count
    sides = (("slab", 0), (("pencil", "sub"), 1))
    stacked_sides = (("slab", 1), (("pencil", "sub"), 2))
    fine_rim = 2 * NU
    ext_x = padded(jnp.stack([permeability, source, pressure]), (("slab", 1),), fine_rim)
    ext_x, aggregate = lax.optimization_barrier((ext_x, aggregate))
    ext_all = padded(ext_x, ((("pencil", "sub"), 2),), fine_rim)
    perm_ext = ext_all[0]
    source_ext = crop(ext_all[1], 1)
    glob_x = slab_index * width_x - fine_rim + jnp.arange(width_x + 2 * fine_rim)
    glob_y = row_index * width_y - fine_rim + jnp.arange(width_y + 2 * fine_rim)
    inside_x = (glob_x >= 0) & (glob_x < total_x)
    inside_y = (glob_y >= 0) & (glob_y < total_y)
    faces_ext = geometry(perm_ext, glob_x, glob_y, inside_x, inside_y, total_x, total_y)
    smooth_ext = sweeps(ext_all[2], source_ext, faces_ext, NU, width_x)
    faces_zero = tuple(crop(member, fine_rim - 1) for member in faces_ext)
    smooth_rows = smooth_ext[NU : NU + width_x]
    center, product = apply_fine(crop(smooth_ext, NU - 1), faces_zero)
    residual = source - product
    half_y = width_y // 2
    half_z = depth_cells // 2

    plane_count = aggregate.shape[0]
    ext_pos = slab_index * width_x - 1 + jnp.arange(width_x + 1 + NU)
    pick_ids = ext_pos[:, None] == jnp.arange(plane_count)[None, :]
    ext_ids = jnp.sum(jnp.where(pick_ids, aggregate.astype(jnp.float32)[None, :], 0.0), axis=1)
    local_ids = ext_ids[1 : width_x + 1]
    straddles = (slab_index > 0) & (ext_ids[0] == local_ids[0])
    first_id = local_ids[0] + straddles.astype(jnp.float32)
    count_live = local_ids[-1] - first_id + 1
    slot_ids = local_ids - first_id
    has_next = ext_pos[2 : width_x + 2] < plane_count
    crossing = ((local_ids != ext_ids[2 : width_x + 2]) & has_next).astype(jnp.float32)
    face_east = faces_zero[1]
    face_north = faces_zero[3]
    face_above = faces_zero[5]
    boundary = faces_zero[6]
    index_z = np.arange(depth_cells)[:, None]
    coarse_z = np.arange(half_z)[None, :]
    pair_z = jnp.asarray((index_z // 2 == coarse_z).astype(np.float32))
    odd_z = jnp.asarray((index_z == 2 * coarse_z + 1).astype(np.float32))
    cells = width_x * width_y

    def z_sum(block_in, pick_z):
        flat = block_in.reshape(cells, depth_cells)
        return jnp.dot(flat, pick_z, precision=lax.Precision.HIGHEST)

    z_rows = jnp.concatenate(
        [
            block_in.reshape(cells, depth_cells)
            for block_in in (residual, face_east * crossing[:, None, None], face_north, face_above, boundary)
        ],
        axis=0,
    )
    z_all = jnp.dot(z_rows, jnp.concatenate([pair_z, odd_z], axis=1), precision=lax.Precision.HIGHEST)

    def z_part(index, odd):
        return z_all[index * cells : (index + 1) * cells, odd * half_z : (odd + 1) * half_z]

    z_parts = [z_part(0, 0), z_part(1, 0), z_part(2, 0), z_part(3, 1), z_part(4, 0)]
    index_y = np.arange(width_y)[:, None]
    coarse_y = np.arange(half_y)[None, :]
    pair_y = jnp.asarray((index_y // 2 == coarse_y).astype(np.float32))
    row_y = np.tile(np.arange(width_y), width_x)
    col_slot = np.repeat(np.arange(width_x + 1), half_y)
    col_y = np.tile(np.arange(half_y), width_x + 1)
    row_slot = jnp.repeat(slot_ids + 1, width_y)
    same_slot = row_slot[:, None] == jnp.asarray(col_slot.astype(np.float32))[None, :]
    pair_rows = row_y[:, None] // 2 == col_y[None, :]
    odd_rows = row_y[:, None] == 2 * col_y[None, :] + 1
    spread_map = (same_slot & pair_rows).astype(jnp.float32)
    gather_map = (same_slot.T & pair_rows.T).astype(jnp.float32)
    north_gather = (same_slot.T & odd_rows.T).astype(jnp.float32)
    paired = jnp.dot(
        gather_map,
        jnp.concatenate([z_parts[0], z_parts[1], z_parts[3], z_parts[4]], axis=1),
        precision=lax.Precision.HIGHEST,
    )
    north_sums = jnp.dot(north_gather, z_parts[2], precision=lax.Precision.HIGHEST)

    def column(index):
        return paired[:, index * half_z : (index + 1) * half_z]

    slot_sums = jnp.stack([column(0), column(1), north_sums, column(2), column(3)])
    slot_sums = slot_sums.reshape(5, width_x + 1, half_y, half_z)
    coarse = slot_sums[:, 1:]
    edge_sums = slot_sums[:, 0]
    slot_range = jnp.arange(width_x)
    last_slot = (slot_range == count_live - 1).astype(jnp.float32)
    tail_pick = (slot_range[None, :] == count_live - NCS + jnp.arange(NCS)[:, None]).astype(jnp.float32)
    tail_planes = jnp.einsum("ks,qsjl->qkjl", tail_pick, coarse, precision=lax.Precision.HIGHEST)
    head_planes = jnp.concatenate([coarse[:, :NCS], edge_sums[:, None]], axis=1)
    tail_planes, head_planes = lax.optimization_barrier((tail_planes, head_planes))
    from_prev = passed_along(tail_planes, "slab", 1)
    from_next = passed_along(head_planes, "slab", -1)
    coarse = coarse + from_next[:, NCS][:, None] * last_slot[None, :, None, None]
    prev_last = (jnp.arange(NCS) == NCS - 1).astype(jnp.float32)
    from_prev = from_prev + edge_sums[:, None] * prev_last[None, :, None, None]
    x_ext = jnp.concatenate([from_prev, coarse, jnp.zeros_like(tail_planes)], axis=1)
    wide_range = jnp.arange(width_x + 2 * NCS)[:, None]
    place = (wide_range == NCS + count_live + jnp.arange(NCS)[None, :]).astype(jnp.float32)
    x_ext = x_ext + jnp.einsum("tk,qkjl->qtjl", place, from_next[:, :NCS], precision=lax.Precision.HIGHEST)
    coarse_rim = NCS
    rim_y = NCS + 1
    coef_ext = padded(x_ext, ((("pencil", "sub"), 2),), rim_y)
    coarse_corr = jnp.zeros((width_x + 2 * NCS, half_y + 2 * rim_y, half_z), jnp.float32)
    for sweep_index in range(NCS):
        out_rim = NCS - 1 - sweep_index
        start_at = coarse_rim - out_rim
        start_y = start_at
        size_x = width_x + 2 * out_rim
        size_y = half_y + 2 * (out_rim + 1)

        def region(offset_x, offset_y):
            return coef_ext[
                :,
                start_at + offset_x : start_at + offset_x + size_x,
                start_y + offset_y : start_y + offset_y + size_y,
            ]

        here_coef = region(0, 0)
        coarse_rhs = here_coef[0]
        coarse_east = here_coef[1]
        coarse_north = here_coef[2]
        coarse_above = here_coef[3]
        coarse_bound = here_coef[4]
        coarse_west = region(-1, 0)[1]
        coarse_south = region(0, -1)[2]
        zero_plane = jnp.zeros_like(coarse_above[:, :, :1])
        coarse_below = jnp.concatenate([zero_plane, coarse_above[:, :, :-1]], axis=2)
        diag_coarse = (
            coarse_east
            + coarse_west
            + coarse_north
            + coarse_south
            + coarse_above
            + coarse_below
            + coarse_bound
        )
        safe_coarse = jnp.where(diag_coarse > 0, diag_coarse, 1.0)
        coarse_center = coarse_corr[1:-1, 1:-1]
        above_vals = jnp.concatenate([coarse_center[:, :, 1:], zero_plane], axis=2)
        below_vals = jnp.concatenate([zero_plane, coarse_center[:, :, :-1]], axis=2)
        beside_all = coarse_east * coarse_corr[2:, 1:-1] + coarse_west * coarse_corr[:-2, 1:-1]
        beside_all = (
            beside_all
            + coarse_north * coarse_corr[1:-1, 2:]
            + coarse_south * coarse_corr[1:-1, :-2]
        )
        beside_all = beside_all + coarse_above * above_vals + coarse_below * below_vals
        coarse_corr = (
            coarse_center
            + OMEGA * (coarse_rhs - (diag_coarse * coarse_center - beside_all)) / safe_coarse
        )
    last_corr = jnp.sum(last_slot[:, None, None] * coarse_corr, axis=0)
    corr_wide = jnp.concatenate([jnp.zeros_like(last_corr)[None], coarse_corr], axis=0)
    corr_core = corr_wide[:, 1 : 1 + half_y]
    corr_z = jnp.dot(
        corr_core.reshape((width_x + 1) * half_y, half_z), pair_z.T, precision=lax.Precision.HIGHEST
    )
    correction = jnp.dot(spread_map, corr_z, precision=lax.Precision.HIGHEST)
    correction = correction.reshape(width_x, width_y, depth_cells)
    owner_rows = (slot_ids[:, None] + 1 == jnp.arange(width_x + 1)[None, :]).astype(jnp.float32)

    def rim_rows(coarse_row):
        row_z = jnp.dot(corr_wide[:, coarse_row], pair_z.T, precision=lax.Precision.HIGHEST)
        row_fine = jnp.dot(owner_rows, row_z, precision=lax.Precision.HIGHEST)
        return jnp.broadcast_to(row_fine[:, None], (width_x, NU, depth_cells))

    correction = jnp.concatenate([rim_rows(0), correction, rim_rows(half_y + 1)], axis=1)
    base = smooth_rows + correction
    last_z = jnp.dot(last_corr, pair_z.T, precision=lax.Precision.HIGHEST)
    fine_y = np.arange(width_y + 2 * NU) - NU
    rows_ext = jnp.asarray((fine_y[:, None] // 2 + 1 == np.arange(half_y + 2)[None, :]).astype(np.float32))
    last_fine = jnp.dot(rows_ext, last_z, precision=lax.Precision.HIGHEST)
    up_block = jnp.concatenate([base[width_x - NU :], last_fine[None]], axis=0)
    below_prev = passed_along(up_block, "slab", 1)
    above_next = passed_along(base[:NU], "slab", -1)
    from_owner = (slot_ids == -1).astype(jnp.float32)
    own = base + from_owner[:, None, None] * below_prev[NU][None]
    next_ids = ext_ids[width_x + 1 :]
    next_in = ext_pos[width_x + 1 :] < plane_count
    to_owner = ((next_ids == local_ids[-1]) & next_in).astype(jnp.float32)
    high_halo = above_next + to_owner[:, None, None] * last_fine[None]
    post_ext = jnp.concatenate([below_prev[:NU], own, high_halo], axis=0)
    return sweeps(post_ext, source_ext, faces_ext, NU, width_x)


def solution(mesh):
    in_specs = (
        P(("real", "slab"), ("pencil", "sub"), None),
        P(("real", "slab"), ("pencil", "sub"), None),
        P(("real", "slab"), ("pencil", "sub"), None),
        P("real"),
    )
    out_specs = P(("real", "slab"), ("pencil", "sub"), None)
    return jax.shard_map(body, mesh=mesh, in_specs=in_specs, out_specs=out_specs, check_vma=False)
```

```python
import numpy as np
import jax
import jax.numpy as jnp
from jax import lax
from jax.sharding import PartitionSpec as P

NU = 2
NCS = 4


OMEGA = 0.8


def padded(array, sides, width):
    for axis, dim in sides:
        count, length = (lax.axis_size(axis), array.shape[dim])
        up = [(i, (i + 1) % count) for i in range(count - 1)]
        down = [(j, i) for i, j in up]
        last = lax.slice_in_dim(array, length - width, length, axis=dim)
        leading = lax.slice_in_dim(array, 0, width, axis=dim)
        before = lax.ppermute(last, axis, up)
        after = lax.ppermute(leading, axis, down)
        array = jnp.concatenate([before, array, after], axis=dim)
    return array


def passed_along(array, axis, by):
    count = lax.axis_size(axis)
    pairs = [(i, i + by) for i in range(count) if 0 <= i + by < count]
    return lax.ppermute(array, axis, pairs)


def harmonic(lower_k, upper_k, inside):
    denom_sum = jnp.where(inside, lower_k + upper_k, 1.0)
    return jnp.where(inside, 2.0 * lower_k * upper_k / denom_sum, 0.0)


def geometry(perm_ext, glob_x, glob_y, inside_x, inside_y, total_x, total_y):
    count_z = perm_ext.shape[2]
    both_x = (inside_x[:-1] & inside_x[1:])[:, None, None] & inside_y[None, :, None]
    both_y = (inside_y[:-1] & inside_y[1:])[None, :, None] & inside_x[:, None, None]
    plane_in = inside_x[:, None, None] & inside_y[None, :, None]
    face_x = harmonic(perm_ext[:-1], perm_ext[1:], both_x)
    face_y = harmonic(perm_ext[:, :-1], perm_ext[:, 1:], both_y)
    face_z = harmonic(perm_ext[:, :, :-1], perm_ext[:, :, 1:], plane_in)
    cell_perm = perm_ext[1:-1, 1:-1]
    face_west = face_x[:-1, 1:-1]
    face_east = face_x[1:, 1:-1]
    face_south = face_y[1:-1, :-1]
    face_north = face_y[1:-1, 1:]
    zero_plane = jnp.zeros_like(cell_perm[:, :, :1])
    face_below = jnp.concatenate([zero_plane, face_z[1:-1, 1:-1]], axis=2)
    face_above = jnp.concatenate([face_z[1:-1, 1:-1], zero_plane], axis=2)
    cell_x = glob_x[1:-1]
    cell_y = glob_y[1:-1]
    index_z = jnp.arange(count_z)
    ends_x = (cell_x == 0).astype(jnp.float32) + (cell_x == total_x - 1).astype(jnp.float32)
    ends_y = (cell_y == 0).astype(jnp.float32) + (cell_y == total_y - 1).astype(jnp.float32)
    ends_z = (index_z == 0).astype(jnp.float32) + (index_z == count_z - 1).astype(jnp.float32)
    edges = ends_x[:, None, None] + ends_y[None, :, None] + ends_z[None, None, :]
    boundary = 2.0 * cell_perm * edges
    diagonal = face_west + face_east + face_south + face_north + face_below + face_above + boundary
    cell_in = plane_in[1:-1, 1:-1]
    safe_diag = jnp.where(cell_in, diagonal, 1.0)
    return (
        face_west,
        face_east,
        face_south,
        face_north,
        face_below,
        face_above,
        boundary,
        safe_diag,
    )


def apply_fine(ext_field, faces_now):
    face_west, face_east, face_south, face_north, face_below, face_above, boundary, safe_diag = (
        faces_now
    )
    center = ext_field[1:-1, 1:-1]
    zero_plane = jnp.zeros_like(center[:, :, :1])
    below_vals = jnp.concatenate([zero_plane, center[:, :, :-1]], axis=2)
    above_vals = jnp.concatenate([center[:, :, 1:], zero_plane], axis=2)
    beside_all = face_west * ext_field[:-2, 1:-1] + face_east * ext_field[2:, 1:-1]
    beside_all = beside_all + face_south * ext_field[1:-1, :-2] + face_north * ext_field[1:-1, 2:]
    beside_all = beside_all + face_below * below_vals + face_above * above_vals
    return (center, safe_diag * center - beside_all)


def crop(array, rim):
    if rim == 0:
        return array
    return array[rim : array.shape[0] - rim, rim : array.shape[1] - rim]


def sweeps(field_ext, source_ext, faces_ext, count, width):
    def rim_of(array):
        return (array.shape[0] - width) // 2

    for sweep_index in range(count):
        out_rim = rim_of(field_ext) - 1
        faces_now = tuple(crop(member, rim_of(member) - out_rim) for member in faces_ext)
        center, product = apply_fine(field_ext, faces_now)
        source_now = crop(source_ext, rim_of(source_ext) - out_rim)
        field_ext = center + OMEGA * (source_now - product) / faces_now[7]
    return field_ext


def body(permeability, source, pressure, aggregate):
    width_x, width_y, depth_cells = permeability.shape
    slab_index = lax.axis_index("slab")
    slab_count = lax.axis_size("slab")
    row_index = lax.axis_index(("pencil", "sub"))
    row_count = lax.axis_size(("pencil", "sub"))
    total_x = width_x * slab_count
    total_y = width_y * row_count
    sides = (("slab", 0), (("pencil", "sub"), 1))
    stacked_sides = (("slab", 1), (("pencil", "sub"), 2))
    fine_rim = 2 * NU
    ext_y = padded(jnp.stack([permeability, source, pressure]), ((("pencil", "sub"), 2),), fine_rim)
    ext_y, aggregate = lax.optimization_barrier((ext_y, aggregate))
    ext_all = padded(ext_y, (("slab", 1),), fine_rim)
    perm_ext = ext_all[0]
    source_ext = crop(ext_all[1], 1)
    glob_x = slab_index * width_x - fine_rim + jnp.arange(width_x + 2 * fine_rim)
    glob_y = row_index * width_y - fine_rim + jnp.arange(width_y + 2 * fine_rim)
    inside_x = (glob_x >= 0) & (glob_x < total_x)
    inside_y = (glob_y >= 0) & (glob_y < total_y)
    faces_ext = geometry(perm_ext, glob_x, glob_y, inside_x, inside_y, total_x, total_y)
    smooth_ext = sweeps(ext_all[2], source_ext, faces_ext, NU, width_x)
    faces_zero = tuple(crop(member, fine_rim - 1) for member in faces_ext)
    smooth_rows = smooth_ext[NU : NU + width_x]
    center, product = apply_fine(crop(smooth_ext, NU - 1), faces_zero)
    residual = source - product
    half_y = width_y // 2
    half_z = depth_cells // 2

    plane_count = aggregate.shape[0]
    ext_pos = slab_index * width_x - 1 + jnp.arange(width_x + 1 + NU)
    pick_ids = ext_pos[:, None] == jnp.arange(plane_count)[None, :]
    ext_ids = jnp.sum(jnp.where(pick_ids, aggregate.astype(jnp.float32)[None, :], 0.0), axis=1)
    local_ids = ext_ids[1 : width_x + 1]
    straddles = (slab_index > 0) & (ext_ids[0] == local_ids[0])
    first_id = local_ids[0] + straddles.astype(jnp.float32)
    count_live = local_ids[-1] - first_id + 1
    slot_ids = local_ids - first_id
    has_next = ext_pos[2 : width_x + 2] < plane_count
    crossing = ((local_ids != ext_ids[2 : width_x + 2]) & has_next).astype(jnp.float32)
    face_east = faces_zero[1]
    face_north = faces_zero[3]
    face_above = faces_zero[5]
    boundary = faces_zero[6]
    index_z = np.arange(depth_cells)[:, None]
    coarse_z = np.arange(half_z)[None, :]
    pair_z = jnp.asarray((index_z // 2 == coarse_z).astype(np.float32))
    odd_z = jnp.asarray((index_z == 2 * coarse_z + 1).astype(np.float32))
    cells = width_x * width_y

    def z_sum(block_in, pick_z):
        flat = block_in.reshape(cells, depth_cells)
        return jnp.dot(flat, pick_z, precision=lax.Precision.HIGHEST)

    z_parts = jnp.stack(
        [
            z_sum(residual, pair_z),
            z_sum(face_east * crossing[:, None, None], pair_z),
            z_sum(face_north, pair_z),
            z_sum(face_above, odd_z),
            z_sum(boundary, pair_z),
        ]
    )
    index_y = np.arange(width_y)[:, None]
    coarse_y = np.arange(half_y)[None, :]
    pair_y = jnp.asarray((index_y // 2 == coarse_y).astype(np.float32))
    row_y = np.tile(np.arange(width_y), width_x)
    col_slot = np.repeat(np.arange(width_x + 1), half_y)
    col_y = np.tile(np.arange(half_y), width_x + 1)
    row_slot = jnp.repeat(slot_ids + 1, width_y)
    same_slot = row_slot[:, None] == jnp.asarray(col_slot.astype(np.float32))[None, :]
    pair_rows = row_y[:, None] // 2 == col_y[None, :]
    odd_rows = row_y[:, None] == 2 * col_y[None, :] + 1
    spread_map = (same_slot & pair_rows).astype(jnp.float32)
    gather_map = (same_slot.T & pair_rows.T).astype(jnp.float32)
    north_gather = (same_slot.T & odd_rows.T).astype(jnp.float32)
    paired = jnp.dot(
        gather_map,
        jnp.concatenate([z_parts[0], z_parts[1], z_parts[3], z_parts[4]], axis=1),
        precision=lax.Precision.HIGHEST,
    )
    north_sums = jnp.dot(north_gather, z_parts[2], precision=lax.Precision.HIGHEST)

    def column(index):
        return paired[:, index * half_z : (index + 1) * half_z]

    slot_sums = jnp.stack([column(0), column(1), north_sums, column(2), column(3)])
    slot_sums = slot_sums.reshape(5, width_x + 1, half_y, half_z)
    coarse = slot_sums[:, 1:]
    edge_sums = slot_sums[:, 0]
    slot_range = jnp.arange(width_x)
    last_slot = (slot_range == count_live - 1).astype(jnp.float32)
    tail_pick = (slot_range[None, :] == count_live - NCS + jnp.arange(NCS)[:, None]).astype(jnp.float32)
    tail_planes = jnp.einsum("ks,qsjl->qkjl", tail_pick, coarse, precision=lax.Precision.HIGHEST)
    head_planes = jnp.concatenate([coarse[:, :NCS], edge_sums[:, None]], axis=1)
    tail_planes, head_planes = lax.optimization_barrier((tail_planes, head_planes))
    from_prev = passed_along(tail_planes, "slab", 1)
    from_next = passed_along(head_planes, "slab", -1)
    coarse = coarse + from_next[:, NCS][:, None] * last_slot[None, :, None, None]
    prev_last = (jnp.arange(NCS) == NCS - 1).astype(jnp.float32)
    from_prev = from_prev + edge_sums[:, None] * prev_last[None, :, None, None]
    x_ext = jnp.concatenate([from_prev, coarse, jnp.zeros_like(tail_planes)], axis=1)
    wide_range = jnp.arange(width_x + 2 * NCS)[:, None]
    place = (wide_range == NCS + count_live + jnp.arange(NCS)[None, :]).astype(jnp.float32)
    x_ext = x_ext + jnp.einsum("tk,qkjl->qtjl", place, from_next[:, :NCS], precision=lax.Precision.HIGHEST)
    coarse_rim = NCS
    rim_y = NCS + 1
    coef_ext = padded(x_ext, ((("pencil", "sub"), 2),), rim_y)
    coarse_corr = jnp.zeros((width_x + 2 * NCS, half_y + 2 * rim_y, half_z), jnp.float32)
    for sweep_index in range(NCS):
        out_rim = NCS - 1 - sweep_index
        start_at = coarse_rim - out_rim
        start_y = start_at
        size_x = width_x + 2 * out_rim
        size_y = half_y + 2 * (out_rim + 1)

        def region(offset_x, offset_y):
            return coef_ext[
                :,
                start_at + offset_x : start_at + offset_x + size_x,
                start_y + offset_y : start_y + offset_y + size_y,
            ]

        here_coef = region(0, 0)
        coarse_rhs = here_coef[0]
        coarse_east = here_coef[1]
        coarse_north = here_coef[2]
        coarse_above = here_coef[3]
        coarse_bound = here_coef[4]
        coarse_west = region(-1, 0)[1]
        coarse_south = region(0, -1)[2]
        zero_plane = jnp.zeros_like(coarse_above[:, :, :1])
        coarse_below = jnp.concatenate([zero_plane, coarse_above[:, :, :-1]], axis=2)
        diag_coarse = (
            coarse_east
            + coarse_west
            + coarse_north
            + coarse_south
            + coarse_above
            + coarse_below
            + coarse_bound
        )
        safe_coarse = jnp.where(diag_coarse > 0, diag_coarse, 1.0)
        coarse_center = coarse_corr[1:-1, 1:-1]
        above_vals = jnp.concatenate([coarse_center[:, :, 1:], zero_plane], axis=2)
        below_vals = jnp.concatenate([zero_plane, coarse_center[:, :, :-1]], axis=2)
        beside_all = coarse_east * coarse_corr[2:, 1:-1] + coarse_west * coarse_corr[:-2, 1:-1]
        beside_all = (
            beside_all
            + coarse_north * coarse_corr[1:-1, 2:]
            + coarse_south * coarse_corr[1:-1, :-2]
        )
        beside_all = beside_all + coarse_above * above_vals + coarse_below * below_vals
        coarse_corr = (
            coarse_center
            + OMEGA * (coarse_rhs - (diag_coarse * coarse_center - beside_all)) / safe_coarse
        )
    last_corr = jnp.sum(last_slot[:, None, None] * coarse_corr, axis=0)
    corr_wide = jnp.concatenate([jnp.zeros_like(last_corr)[None], coarse_corr], axis=0)
    corr_core = corr_wide[:, 1 : 1 + half_y]
    corr_z = jnp.dot(
        corr_core.reshape((width_x + 1) * half_y, half_z), pair_z.T, precision=lax.Precision.HIGHEST
    )
    correction = jnp.dot(spread_map, corr_z, precision=lax.Precision.HIGHEST)
    correction = correction.reshape(width_x, width_y, depth_cells)
    owner_rows = (slot_ids[:, None] + 1 == jnp.arange(width_x + 1)[None, :]).astype(jnp.float32)

    def rim_rows(coarse_row):
        row_z = jnp.dot(corr_wide[:, coarse_row], pair_z.T, precision=lax.Precision.HIGHEST)
        row_fine = jnp.dot(owner_rows, row_z, precision=lax.Precision.HIGHEST)
        return jnp.broadcast_to(row_fine[:, None], (width_x, NU, depth_cells))

    correction = jnp.concatenate([rim_rows(0), correction, rim_rows(half_y + 1)], axis=1)
    base = smooth_rows + correction
    last_z = jnp.dot(last_corr, pair_z.T, precision=lax.Precision.HIGHEST)
    fine_y = np.arange(width_y + 2 * NU) - NU
    rows_ext = jnp.asarray((fine_y[:, None] // 2 + 1 == np.arange(half_y + 2)[None, :]).astype(np.float32))
    last_fine = jnp.dot(rows_ext, last_z, precision=lax.Precision.HIGHEST)
    up_block = jnp.concatenate([base[width_x - NU :], last_fine[None]], axis=0)
    below_prev = passed_along(up_block, "slab", 1)
    above_next = passed_along(base[:NU], "slab", -1)
    from_owner = (slot_ids == -1).astype(jnp.float32)
    own = base + from_owner[:, None, None] * below_prev[NU][None]
    next_ids = ext_ids[width_x + 1 :]
    next_in = ext_pos[width_x + 1 :] < plane_count
    to_owner = ((next_ids == local_ids[-1]) & next_in).astype(jnp.float32)
    high_halo = above_next + to_owner[:, None, None] * last_fine[None]
    post_ext = jnp.concatenate([below_prev[:NU], own, high_halo], axis=0)
    return sweeps(post_ext, source_ext, faces_ext, NU, width_x)


def solution(mesh):
    in_specs = (
        P(("real", "slab"), ("pencil", "sub"), None),
        P(("real", "slab"), ("pencil", "sub"), None),
        P(("real", "slab"), ("pencil", "sub"), None),
        P("real"),
    )
    out_specs = P(("real", "slab"), ("pencil", "sub"), None)
    return jax.shard_map(body, mesh=mesh, in_specs=in_specs, out_specs=out_specs, check_vma=False)
```

```python
import numpy as np
import jax
import jax.numpy as jnp
from jax import lax
from jax.sharding import PartitionSpec as P

NU = 2
NCS = 4


OMEGA = 0.8


def padded(array, sides, width):
    for axis, dim in sides:
        count, length = (lax.axis_size(axis), array.shape[dim])
        up = [(i, (i + 1) % count) for i in range(count - 1)]
        down = [(j, i) for i, j in up]
        last = lax.slice_in_dim(array, length - width, length, axis=dim)
        leading = lax.slice_in_dim(array, 0, width, axis=dim)
        before = lax.ppermute(last, axis, up)
        after = lax.ppermute(leading, axis, down)
        array = jnp.concatenate([before, array, after], axis=dim)
    return array


def passed_along(array, axis, by):
    count = lax.axis_size(axis)
    pairs = [(i, i + by) for i in range(count) if 0 <= i + by < count]
    return lax.ppermute(array, axis, pairs)


def harmonic(lower_k, upper_k, inside):
    denom_sum = jnp.where(inside, lower_k + upper_k, 1.0)
    return jnp.where(inside, 2.0 * lower_k * upper_k / denom_sum, 0.0)


def geometry(perm_ext, glob_x, glob_y, inside_x, inside_y, total_x, total_y):
    count_z = perm_ext.shape[2]
    both_x = (inside_x[:-1] & inside_x[1:])[:, None, None] & inside_y[None, :, None]
    both_y = (inside_y[:-1] & inside_y[1:])[None, :, None] & inside_x[:, None, None]
    plane_in = inside_x[:, None, None] & inside_y[None, :, None]
    face_x = harmonic(perm_ext[:-1], perm_ext[1:], both_x)
    face_y = harmonic(perm_ext[:, :-1], perm_ext[:, 1:], both_y)
    face_z = harmonic(perm_ext[:, :, :-1], perm_ext[:, :, 1:], plane_in)
    cell_perm = perm_ext[1:-1, 1:-1]
    face_west = face_x[:-1, 1:-1]
    face_east = face_x[1:, 1:-1]
    face_south = face_y[1:-1, :-1]
    face_north = face_y[1:-1, 1:]
    zero_plane = jnp.zeros_like(cell_perm[:, :, :1])
    face_below = jnp.concatenate([zero_plane, face_z[1:-1, 1:-1]], axis=2)
    face_above = jnp.concatenate([face_z[1:-1, 1:-1], zero_plane], axis=2)
    cell_x = glob_x[1:-1]
    cell_y = glob_y[1:-1]
    index_z = jnp.arange(count_z)
    ends_x = (cell_x == 0).astype(jnp.float32) + (cell_x == total_x - 1).astype(jnp.float32)
    ends_y = (cell_y == 0).astype(jnp.float32) + (cell_y == total_y - 1).astype(jnp.float32)
    ends_z = (index_z == 0).astype(jnp.float32) + (index_z == count_z - 1).astype(jnp.float32)
    edges = ends_x[:, None, None] + ends_y[None, :, None] + ends_z[None, None, :]
    boundary = 2.0 * cell_perm * edges
    diagonal = face_west + face_east + face_south + face_north + face_below + face_above + boundary
    cell_in = plane_in[1:-1, 1:-1]
    safe_diag = jnp.where(cell_in, diagonal, 1.0)
    return (
        face_west,
        face_east,
        face_south,
        face_north,
        face_below,
        face_above,
        boundary,
        safe_diag,
    )


def apply_fine(ext_field, faces_now):
    face_west, face_east, face_south, face_north, face_below, face_above, boundary, safe_diag = (
        faces_now
    )
    center = ext_field[1:-1, 1:-1]
    zero_plane = jnp.zeros_like(center[:, :, :1])
    below_vals = jnp.concatenate([zero_plane, center[:, :, :-1]], axis=2)
    above_vals = jnp.concatenate([center[:, :, 1:], zero_plane], axis=2)
    beside_all = face_west * ext_field[:-2, 1:-1] + face_east * ext_field[2:, 1:-1]
    beside_all = beside_all + face_south * ext_field[1:-1, :-2] + face_north * ext_field[1:-1, 2:]
    beside_all = beside_all + face_below * below_vals + face_above * above_vals
    return (center, safe_diag * center - beside_all)


def crop(array, rim):
    if rim == 0:
        return array
    return array[rim : array.shape[0] - rim, rim : array.shape[1] - rim]


def sweeps(field_ext, source_ext, faces_ext, count, width):
    def rim_of(array):
        return (array.shape[0] - width) // 2

    for sweep_index in range(count):
        out_rim = rim_of(field_ext) - 1
        faces_now = tuple(crop(member, rim_of(member) - out_rim) for member in faces_ext)
        center, product = apply_fine(field_ext, faces_now)
        source_now = crop(source_ext, rim_of(source_ext) - out_rim)
        field_ext = center + OMEGA * (source_now - product) / faces_now[7]
    return field_ext


def body(permeability, source, pressure, aggregate):
    width_x, width_y, depth_cells = permeability.shape
    slab_index = lax.axis_index("slab")
    slab_count = lax.axis_size("slab")
    row_index = lax.axis_index(("pencil", "sub"))
    row_count = lax.axis_size(("pencil", "sub"))
    total_x = width_x * slab_count
    total_y = width_y * row_count
    sides = (("slab", 0), (("pencil", "sub"), 1))
    stacked_sides = (("slab", 1), (("pencil", "sub"), 2))
    fine_rim = 2 * NU
    ext_x = padded(jnp.stack([permeability, source, pressure]), (("slab", 1),), fine_rim)
    ext_x, aggregate = lax.optimization_barrier((ext_x, aggregate))
    ext_all = padded(ext_x, ((("pencil", "sub"), 2),), fine_rim)
    perm_ext = ext_all[0]
    source_ext = crop(ext_all[1], 1)
    glob_x = slab_index * width_x - fine_rim + jnp.arange(width_x + 2 * fine_rim)
    glob_y = row_index * width_y - fine_rim + jnp.arange(width_y + 2 * fine_rim)
    inside_x = (glob_x >= 0) & (glob_x < total_x)
    inside_y = (glob_y >= 0) & (glob_y < total_y)
    faces_ext = geometry(perm_ext, glob_x, glob_y, inside_x, inside_y, total_x, total_y)
    smooth_ext = sweeps(ext_all[2], source_ext, faces_ext, NU, width_x)
    faces_zero = tuple(crop(member, fine_rim - 1) for member in faces_ext)
    smooth_rows = smooth_ext[NU : NU + width_x]
    center, product = apply_fine(crop(smooth_ext, NU - 1), faces_zero)
    residual = source - product
    half_y = width_y // 2
    half_z = depth_cells // 2

    plane_count = aggregate.shape[0]
    ext_pos = slab_index * width_x - 1 + jnp.arange(width_x + 1 + NU)
    pick_ids = ext_pos[:, None] == jnp.arange(plane_count)[None, :]
    ext_ids = jnp.sum(jnp.where(pick_ids, aggregate.astype(jnp.float32)[None, :], 0.0), axis=1)
    local_ids = ext_ids[1 : width_x + 1]
    straddles = (slab_index > 0) & (ext_ids[0] == local_ids[0])
    first_id = local_ids[0] + straddles.astype(jnp.float32)
    count_live = local_ids[-1] - first_id + 1
    slot_ids = local_ids - first_id
    has_next = ext_pos[2 : width_x + 2] < plane_count
    crossing = ((local_ids != ext_ids[2 : width_x + 2]) & has_next).astype(jnp.float32)
    face_east = faces_zero[1]
    face_north = faces_zero[3]
    face_above = faces_zero[5]
    boundary = faces_zero[6]
    index_z = np.arange(depth_cells)[:, None]
    coarse_z = np.arange(half_z)[None, :]
    pair_z = jnp.asarray((index_z // 2 == coarse_z).astype(np.float32))
    odd_z = jnp.asarray((index_z == 2 * coarse_z + 1).astype(np.float32))
    cells = width_x * width_y

    def z_sum(block_in, pick_z):
        flat = block_in.reshape(cells, depth_cells)
        return jnp.dot(flat, pick_z, precision=lax.Precision.HIGH)

    z_parts = jnp.stack(
        [
            z_sum(residual, pair_z),
            z_sum(face_east * crossing[:, None, None], pair_z),
            z_sum(face_north, pair_z),
            z_sum(face_above, odd_z),
            z_sum(boundary, pair_z),
        ]
    )
    index_y = np.arange(width_y)[:, None]
    coarse_y = np.arange(half_y)[None, :]
    pair_y = jnp.asarray((index_y // 2 == coarse_y).astype(np.float32))
    row_y = np.tile(np.arange(width_y), width_x)
    col_slot = np.repeat(np.arange(width_x + 1), half_y)
    col_y = np.tile(np.arange(half_y), width_x + 1)
    row_slot = jnp.repeat(slot_ids + 1, width_y)
    same_slot = row_slot[:, None] == jnp.asarray(col_slot.astype(np.float32))[None, :]
    pair_rows = row_y[:, None] // 2 == col_y[None, :]
    odd_rows = row_y[:, None] == 2 * col_y[None, :] + 1
    spread_map = (same_slot & pair_rows).astype(jnp.float32)
    gather_map = (same_slot.T & pair_rows.T).astype(jnp.float32)
    north_gather = (same_slot.T & odd_rows.T).astype(jnp.float32)
    paired = jnp.dot(
        gather_map,
        jnp.concatenate([z_parts[0], z_parts[1], z_parts[3], z_parts[4]], axis=1),
        precision=lax.Precision.HIGHEST,
    )
    north_sums = jnp.dot(north_gather, z_parts[2], precision=lax.Precision.HIGHEST)

    def column(index):
        return paired[:, index * half_z : (index + 1) * half_z]

    slot_sums = jnp.stack([column(0), column(1), north_sums, column(2), column(3)])
    slot_sums = slot_sums.reshape(5, width_x + 1, half_y, half_z)
    coarse = slot_sums[:, 1:]
    edge_sums = slot_sums[:, 0]
    slot_range = jnp.arange(width_x)
    last_slot = (slot_range == count_live - 1).astype(jnp.float32)
    tail_pick = (slot_range[None, :] == count_live - NCS + jnp.arange(NCS)[:, None]).astype(jnp.float32)
    tail_planes = jnp.einsum("ks,qsjl->qkjl", tail_pick, coarse, precision=lax.Precision.HIGHEST)
    head_planes = jnp.concatenate([coarse[:, :NCS], edge_sums[:, None]], axis=1)
    tail_planes, head_planes = lax.optimization_barrier((tail_planes, head_planes))
    from_prev = passed_along(tail_planes, "slab", 1)
    from_next = passed_along(head_planes, "slab", -1)
    coarse = coarse + from_next[:, NCS][:, None] * last_slot[None, :, None, None]
    prev_last = (jnp.arange(NCS) == NCS - 1).astype(jnp.float32)
    from_prev = from_prev + edge_sums[:, None] * prev_last[None, :, None, None]
    x_ext = jnp.concatenate([from_prev, coarse, jnp.zeros_like(tail_planes)], axis=1)
    wide_range = jnp.arange(width_x + 2 * NCS)[:, None]
    place = (wide_range == NCS + count_live + jnp.arange(NCS)[None, :]).astype(jnp.float32)
    x_ext = x_ext + jnp.einsum("tk,qkjl->qtjl", place, from_next[:, :NCS], precision=lax.Precision.HIGHEST)
    coarse_rim = NCS
    rim_y = NCS + 1
    coef_ext = padded(x_ext, ((("pencil", "sub"), 2),), rim_y)
    coarse_corr = jnp.zeros((width_x + 2 * NCS, half_y + 2 * rim_y, half_z), jnp.float32)
    for sweep_index in range(NCS):
        out_rim = NCS - 1 - sweep_index
        start_at = coarse_rim - out_rim
        start_y = start_at
        size_x = width_x + 2 * out_rim
        size_y = half_y + 2 * (out_rim + 1)

        def region(offset_x, offset_y):
            return coef_ext[
                :,
                start_at + offset_x : start_at + offset_x + size_x,
                start_y + offset_y : start_y + offset_y + size_y,
            ]

        here_coef = region(0, 0)
        coarse_rhs = here_coef[0]
        coarse_east = here_coef[1]
        coarse_north = here_coef[2]
        coarse_above = here_coef[3]
        coarse_bound = here_coef[4]
        coarse_west = region(-1, 0)[1]
        coarse_south = region(0, -1)[2]
        zero_plane = jnp.zeros_like(coarse_above[:, :, :1])
        coarse_below = jnp.concatenate([zero_plane, coarse_above[:, :, :-1]], axis=2)
        diag_coarse = (
            coarse_east
            + coarse_west
            + coarse_north
            + coarse_south
            + coarse_above
            + coarse_below
            + coarse_bound
        )
        safe_coarse = jnp.where(diag_coarse > 0, diag_coarse, 1.0)
        coarse_center = coarse_corr[1:-1, 1:-1]
        above_vals = jnp.concatenate([coarse_center[:, :, 1:], zero_plane], axis=2)
        below_vals = jnp.concatenate([zero_plane, coarse_center[:, :, :-1]], axis=2)
        beside_all = coarse_east * coarse_corr[2:, 1:-1] + coarse_west * coarse_corr[:-2, 1:-1]
        beside_all = (
            beside_all
            + coarse_north * coarse_corr[1:-1, 2:]
            + coarse_south * coarse_corr[1:-1, :-2]
        )
        beside_all = beside_all + coarse_above * above_vals + coarse_below * below_vals
        coarse_corr = (
            coarse_center
            + OMEGA * (coarse_rhs - (diag_coarse * coarse_center - beside_all)) / safe_coarse
        )
    last_corr = jnp.sum(last_slot[:, None, None] * coarse_corr, axis=0)
    corr_wide = jnp.concatenate([jnp.zeros_like(last_corr)[None], coarse_corr], axis=0)
    corr_core = corr_wide[:, 1 : 1 + half_y]
    corr_z = jnp.dot(
        corr_core.reshape((width_x + 1) * half_y, half_z), pair_z.T, precision=lax.Precision.HIGHEST
    )
    correction = jnp.dot(spread_map, corr_z, precision=lax.Precision.HIGHEST)
    correction = correction.reshape(width_x, width_y, depth_cells)
    owner_rows = (slot_ids[:, None] + 1 == jnp.arange(width_x + 1)[None, :]).astype(jnp.float32)

    def rim_rows(coarse_row):
        row_z = jnp.dot(corr_wide[:, coarse_row], pair_z.T, precision=lax.Precision.HIGHEST)
        row_fine = jnp.dot(owner_rows, row_z, precision=lax.Precision.HIGHEST)
        return jnp.broadcast_to(row_fine[:, None], (width_x, NU, depth_cells))

    correction = jnp.concatenate([rim_rows(0), correction, rim_rows(half_y + 1)], axis=1)
    base = smooth_rows + correction
    last_z = jnp.dot(last_corr, pair_z.T, precision=lax.Precision.HIGHEST)
    fine_y = np.arange(width_y + 2 * NU) - NU
    rows_ext = jnp.asarray((fine_y[:, None] // 2 + 1 == np.arange(half_y + 2)[None, :]).astype(np.float32))
    last_fine = jnp.dot(rows_ext, last_z, precision=lax.Precision.HIGHEST)
    up_block = jnp.concatenate([base[width_x - NU :], last_fine[None]], axis=0)
    below_prev = passed_along(up_block, "slab", 1)
    above_next = passed_along(base[:NU], "slab", -1)
    from_owner = (slot_ids == -1).astype(jnp.float32)
    own = base + from_owner[:, None, None] * below_prev[NU][None]
    next_ids = ext_ids[width_x + 1 :]
    next_in = ext_pos[width_x + 1 :] < plane_count
    to_owner = ((next_ids == local_ids[-1]) & next_in).astype(jnp.float32)
    high_halo = above_next + to_owner[:, None, None] * last_fine[None]
    post_ext = jnp.concatenate([below_prev[:NU], own, high_halo], axis=0)
    return sweeps(post_ext, source_ext, faces_ext, NU, width_x)


def solution(mesh):
    in_specs = (
        P(("real", "slab"), ("pencil", "sub"), None),
        P(("real", "slab"), ("pencil", "sub"), None),
        P(("real", "slab"), ("pencil", "sub"), None),
        P("real"),
    )
    out_specs = P(("real", "slab"), ("pencil", "sub"), None)
    return jax.shard_map(body, mesh=mesh, in_specs=in_specs, out_specs=out_specs, check_vma=False)
```

```python
import numpy as np
import jax
import jax.numpy as jnp
from jax import lax
from jax.sharding import PartitionSpec as P

NU = 2
NCS = 4


OMEGA = 0.8


def padded(array, sides, width):
    for axis, dim in sides:
        count, length = (lax.axis_size(axis), array.shape[dim])
        up = [(i, (i + 1) % count) for i in range(count - 1)]
        down = [(j, i) for i, j in up]
        last = lax.slice_in_dim(array, length - width, length, axis=dim)
        leading = lax.slice_in_dim(array, 0, width, axis=dim)
        before = lax.ppermute(last, axis, up)
        after = lax.ppermute(leading, axis, down)
        array = jnp.concatenate([before, array, after], axis=dim)
    return array


def passed_along(array, axis, by):
    count = lax.axis_size(axis)
    pairs = [(i, i + by) for i in range(count) if 0 <= i + by < count]
    return lax.ppermute(array, axis, pairs)


def harmonic(lower_k, upper_k, inside):
    denom_sum = jnp.where(inside, lower_k + upper_k, 1.0)
    return jnp.where(inside, 2.0 * lower_k * upper_k / denom_sum, 0.0)


def geometry(perm_ext, glob_x, glob_y, inside_x, inside_y, total_x, total_y):
    count_z = perm_ext.shape[2]
    both_x = (inside_x[:-1] & inside_x[1:])[:, None, None] & inside_y[None, :, None]
    both_y = (inside_y[:-1] & inside_y[1:])[None, :, None] & inside_x[:, None, None]
    plane_in = inside_x[:, None, None] & inside_y[None, :, None]
    face_x = harmonic(perm_ext[:-1], perm_ext[1:], both_x)
    face_y = harmonic(perm_ext[:, :-1], perm_ext[:, 1:], both_y)
    face_z = harmonic(perm_ext[:, :, :-1], perm_ext[:, :, 1:], plane_in)
    cell_perm = perm_ext[1:-1, 1:-1]
    face_west = face_x[:-1, 1:-1]
    face_east = face_x[1:, 1:-1]
    face_south = face_y[1:-1, :-1]
    face_north = face_y[1:-1, 1:]
    zero_plane = jnp.zeros_like(cell_perm[:, :, :1])
    face_below = jnp.concatenate([zero_plane, face_z[1:-1, 1:-1]], axis=2)
    face_above = jnp.concatenate([face_z[1:-1, 1:-1], zero_plane], axis=2)
    cell_x = glob_x[1:-1]
    cell_y = glob_y[1:-1]
    index_z = jnp.arange(count_z)
    ends_x = (cell_x == 0).astype(jnp.float32) + (cell_x == total_x - 1).astype(jnp.float32)
    ends_y = (cell_y == 0).astype(jnp.float32) + (cell_y == total_y - 1).astype(jnp.float32)
    ends_z = (index_z == 0).astype(jnp.float32) + (index_z == count_z - 1).astype(jnp.float32)
    edges = ends_x[:, None, None] + ends_y[None, :, None] + ends_z[None, None, :]
    boundary = 2.0 * cell_perm * edges
    diagonal = face_west + face_east + face_south + face_north + face_below + face_above + boundary
    cell_in = plane_in[1:-1, 1:-1]
    safe_diag = jnp.where(cell_in, diagonal, 1.0)
    return (
        face_west,
        face_east,
        face_south,
        face_north,
        face_below,
        face_above,
        boundary,
        safe_diag,
    )


def apply_fine(ext_field, faces_now):
    face_west, face_east, face_south, face_north, face_below, face_above, boundary, safe_diag = (
        faces_now
    )
    center = ext_field[1:-1, 1:-1]
    zero_plane = jnp.zeros_like(center[:, :, :1])
    below_vals = jnp.concatenate([zero_plane, center[:, :, :-1]], axis=2)
    above_vals = jnp.concatenate([center[:, :, 1:], zero_plane], axis=2)
    beside_all = face_west * ext_field[:-2, 1:-1] + face_east * ext_field[2:, 1:-1]
    beside_all = beside_all + face_south * ext_field[1:-1, :-2] + face_north * ext_field[1:-1, 2:]
    beside_all = beside_all + face_below * below_vals + face_above * above_vals
    return (center, safe_diag * center - beside_all)


def crop(array, rim):
    if rim == 0:
        return array
    return array[rim : array.shape[0] - rim, rim : array.shape[1] - rim]


def sweeps(field_ext, source_ext, faces_ext, count, width):
    def rim_of(array):
        return (array.shape[0] - width) // 2

    for sweep_index in range(count):
        out_rim = rim_of(field_ext) - 1
        faces_now = tuple(crop(member, rim_of(member) - out_rim) for member in faces_ext)
        center, product = apply_fine(field_ext, faces_now)
        source_now = crop(source_ext, rim_of(source_ext) - out_rim)
        field_ext = center + OMEGA * (source_now - product) / faces_now[7]
    return field_ext


def body(permeability, source, pressure, aggregate):
    width_x, width_y, depth_cells = permeability.shape
    slab_index = lax.axis_index("slab")
    slab_count = lax.axis_size("slab")
    row_index = lax.axis_index(("pencil", "sub"))
    row_count = lax.axis_size(("pencil", "sub"))
    total_x = width_x * slab_count
    total_y = width_y * row_count
    sides = (("slab", 0), (("pencil", "sub"), 1))
    stacked_sides = (("slab", 1), (("pencil", "sub"), 2))
    fine_rim = 2 * NU
    ext_x = padded(jnp.stack([permeability, source, pressure]), (("slab", 1),), fine_rim)
    ext_x, aggregate = lax.optimization_barrier((ext_x, aggregate))
    ext_all = padded(ext_x, ((("pencil", "sub"), 2),), fine_rim)
    perm_ext = ext_all[0]
    source_ext = crop(ext_all[1], 1)
    glob_x = slab_index * width_x - fine_rim + jnp.arange(width_x + 2 * fine_rim)
    glob_y = row_index * width_y - fine_rim + jnp.arange(width_y + 2 * fine_rim)
    inside_x = (glob_x >= 0) & (glob_x < total_x)
    inside_y = (glob_y >= 0) & (glob_y < total_y)
    faces_ext = geometry(perm_ext, glob_x, glob_y, inside_x, inside_y, total_x, total_y)
    smooth_ext = sweeps(ext_all[2], source_ext, faces_ext, NU, width_x)
    faces_zero = tuple(crop(member, fine_rim - 1) for member in faces_ext)
    smooth_rows = smooth_ext[NU : NU + width_x]
    center, product = apply_fine(crop(smooth_ext, NU - 1), faces_zero)
    residual = source - product
    half_y = width_y // 2
    half_z = depth_cells // 2

    plane_count = aggregate.shape[0]
    ext_pos = slab_index * width_x - 1 + jnp.arange(width_x + 1 + NU)
    pick_ids = ext_pos[:, None] == jnp.arange(plane_count)[None, :]
    ext_ids = jnp.sum(jnp.where(pick_ids, aggregate.astype(jnp.float32)[None, :], 0.0), axis=1)
    local_ids = ext_ids[1 : width_x + 1]
    straddles = (slab_index > 0) & (ext_ids[0] == local_ids[0])
    first_id = local_ids[0] + straddles.astype(jnp.float32)
    count_live = local_ids[-1] - first_id + 1
    slot_ids = local_ids - first_id
    has_next = ext_pos[2 : width_x + 2] < plane_count
    crossing = ((local_ids != ext_ids[2 : width_x + 2]) & has_next).astype(jnp.float32)
    face_east = faces_zero[1]
    face_north = faces_zero[3]
    face_above = faces_zero[5]
    boundary = faces_zero[6]
    index_z = np.arange(depth_cells)[:, None]
    coarse_z = np.arange(half_z)[None, :]
    pair_z = jnp.asarray((index_z // 2 == coarse_z).astype(np.float32))
    odd_z = jnp.asarray((index_z == 2 * coarse_z + 1).astype(np.float32))
    cells = width_x * width_y

    def z_sum(block_in, pick_z):
        flat = block_in.reshape(cells, depth_cells)
        return jnp.dot(flat, pick_z, precision=lax.Precision.HIGHEST)

    z_parts = jnp.stack(
        [
            z_sum(residual, pair_z),
            z_sum(face_east * crossing[:, None, None], pair_z),
            z_sum(face_north, pair_z),
            z_sum(face_above, odd_z),
            z_sum(boundary, pair_z),
        ]
    )
    index_y = np.arange(width_y)[:, None]
    coarse_y = np.arange(half_y)[None, :]
    pair_y = jnp.asarray((index_y // 2 == coarse_y).astype(np.float32))
    row_y = np.tile(np.arange(width_y), width_x)
    col_slot = np.repeat(np.arange(width_x + 1), half_y)
    col_y = np.tile(np.arange(half_y), width_x + 1)
    row_slot = jnp.repeat(slot_ids + 1, width_y)
    same_slot = row_slot[:, None] == jnp.asarray(col_slot.astype(np.float32))[None, :]
    pair_rows = row_y[:, None] // 2 == col_y[None, :]
    odd_rows = row_y[:, None] == 2 * col_y[None, :] + 1
    spread_map = (same_slot & pair_rows).astype(jnp.float32)
    gather_map = (same_slot.T & pair_rows.T).astype(jnp.float32)
    north_gather = (same_slot.T & odd_rows.T).astype(jnp.float32)
    paired = jnp.dot(
        gather_map,
        jnp.concatenate([z_parts[0], z_parts[1], z_parts[3], z_parts[4]], axis=1),
        precision=lax.Precision.HIGHEST,
    )
    north_sums = jnp.dot(north_gather, z_parts[2], precision=lax.Precision.HIGHEST)

    def column(index):
        return paired[:, index * half_z : (index + 1) * half_z]

    slot_sums = jnp.stack([column(0), column(1), north_sums, column(2), column(3)])
    slot_sums = slot_sums.reshape(5, width_x + 1, half_y, half_z)
    coarse = slot_sums[:, 1:]
    edge_sums = slot_sums[:, 0]
    slot_range = jnp.arange(width_x)
    last_slot = (slot_range == count_live - 1).astype(jnp.float32)
    tail_pick = (slot_range[None, :] == count_live - NCS + jnp.arange(NCS)[:, None]).astype(jnp.float32)
    tail_planes = jnp.einsum("ks,qsjl->qkjl", tail_pick, coarse, precision=lax.Precision.HIGHEST)
    head_planes = jnp.concatenate([coarse[:, :NCS], edge_sums[:, None]], axis=1)
    tail_planes, head_planes = lax.optimization_barrier((tail_planes, head_planes))
    from_prev = passed_along(tail_planes, "slab", 1)
    from_next = passed_along(head_planes, "slab", -1)
    coarse = coarse + from_next[:, NCS][:, None] * last_slot[None, :, None, None]
    prev_last = (jnp.arange(NCS) == NCS - 1).astype(jnp.float32)
    from_prev = from_prev + edge_sums[:, None] * prev_last[None, :, None, None]
    x_ext = jnp.concatenate([from_prev, coarse, jnp.zeros_like(tail_planes)], axis=1)
    wide_range = jnp.arange(width_x + 2 * NCS)[:, None]
    place = (wide_range == NCS + count_live + jnp.arange(NCS)[None, :]).astype(jnp.float32)
    x_ext = x_ext + jnp.einsum("tk,qkjl->qtjl", place, from_next[:, :NCS], precision=lax.Precision.HIGHEST)
    coarse_rim = NCS
    rim_y = NCS + 1
    coef_ext = padded(x_ext, ((("pencil", "sub"), 2),), rim_y)
    coarse_corr = jnp.zeros((width_x + 2 * NCS, half_y + 2 * rim_y, half_z), jnp.float32)
    for sweep_index in range(NCS):
        out_rim = NCS - 1 - sweep_index
        start_at = coarse_rim - out_rim
        start_y = start_at
        size_x = width_x + 2 * out_rim
        size_y = half_y + 2 * (out_rim + 1)

        def region(offset_x, offset_y):
            return coef_ext[
                :,
                start_at + offset_x : start_at + offset_x + size_x,
                start_y + offset_y : start_y + offset_y + size_y,
            ]

        here_coef = region(0, 0)
        coarse_rhs = here_coef[0]
        coarse_east = here_coef[1]
        coarse_north = here_coef[2]
        coarse_above = here_coef[3]
        coarse_bound = here_coef[4]
        coarse_west = region(-1, 0)[1]
        coarse_south = region(0, -1)[2]
        zero_plane = jnp.zeros_like(coarse_above[:, :, :1])
        coarse_below = jnp.concatenate([zero_plane, coarse_above[:, :, :-1]], axis=2)
        diag_coarse = (
            coarse_east
            + coarse_west
            + coarse_north
            + coarse_south
            + coarse_above
            + coarse_below
            + coarse_bound
        )
        safe_coarse = jnp.where(diag_coarse > 0, diag_coarse, 1.0)
        coarse_center = coarse_corr[1:-1, 1:-1]
        above_vals = jnp.concatenate([coarse_center[:, :, 1:], zero_plane], axis=2)
        below_vals = jnp.concatenate([zero_plane, coarse_center[:, :, :-1]], axis=2)
        beside_all = coarse_east * coarse_corr[2:, 1:-1] + coarse_west * coarse_corr[:-2, 1:-1]
        beside_all = (
            beside_all
            + coarse_north * coarse_corr[1:-1, 2:]
            + coarse_south * coarse_corr[1:-1, :-2]
        )
        beside_all = beside_all + coarse_above * above_vals + coarse_below * below_vals
        coarse_corr = (
            coarse_center
            + OMEGA * (coarse_rhs - (diag_coarse * coarse_center - beside_all)) / safe_coarse
        )
    last_corr = jnp.sum(last_slot[:, None, None] * coarse_corr, axis=0)
    corr_wide = jnp.concatenate([jnp.zeros_like(last_corr)[None], coarse_corr], axis=0)
    corr_core = corr_wide[:, 1 : 1 + half_y]
    corr_z = jnp.dot(
        corr_core.reshape((width_x + 1) * half_y, half_z), pair_z.T, precision=lax.Precision.HIGHEST
    )
    correction = jnp.dot(spread_map, corr_z, precision=lax.Precision.HIGHEST)
    correction = correction.reshape(width_x, width_y, depth_cells)
    owner_rows = (slot_ids[:, None] + 1 == jnp.arange(width_x + 1)[None, :]).astype(jnp.float32)

    def rim_rows(coarse_row):
        row_z = jnp.dot(corr_wide[:, coarse_row], pair_z.T, precision=lax.Precision.HIGHEST)
        row_fine = jnp.dot(owner_rows, row_z, precision=lax.Precision.HIGHEST)
        return jnp.broadcast_to(row_fine[:, None], (width_x, NU, depth_cells))

    correction = jnp.concatenate([rim_rows(0), correction, rim_rows(half_y + 1)], axis=1)
    base = smooth_rows + correction
    last_z = jnp.dot(last_corr, pair_z.T, precision=lax.Precision.HIGHEST)
    fine_y = np.arange(width_y + 2 * NU) - NU
    rows_ext = jnp.asarray((fine_y[:, None] // 2 + 1 == np.arange(half_y + 2)[None, :]).astype(np.float32))
    last_fine = jnp.dot(rows_ext, last_z, precision=lax.Precision.HIGHEST)
    up_block = jnp.concatenate([base[width_x - NU :], last_fine[None]], axis=0)
    below_prev = passed_along(up_block, "slab", 1)
    above_next = passed_along(base[:NU], "slab", -1)
    from_owner = (slot_ids == -1).astype(jnp.float32)
    own = base + from_owner[:, None, None] * below_prev[NU][None]
    next_ids = ext_ids[width_x + 1 :]
    next_in = ext_pos[width_x + 1 :] < plane_count
    to_owner = ((next_ids == local_ids[-1]) & next_in).astype(jnp.float32)
    high_halo = above_next + to_owner[:, None, None] * last_fine[None]
    post_ext = jnp.concatenate([below_prev[:NU], own, high_halo], axis=0)
    face_rim = fine_rim - 1

    def piece(field, low, high, rim):
        window = (slice(low + face_rim, high + face_rim), slice(face_rim - rim, face_rim + width_y + rim))
        faces_now = tuple(member[window] for member in faces_ext)
        center, product = apply_fine(field, faces_now)
        return center + OMEGA * (source_ext[window] - product) / faces_now[7]

    settled = 3
    first_mid = piece(base[settled:], settled + 1, width_x - 1, 1)
    second_mid = piece(first_mid, settled + 2, width_x - 2, 0)
    first_low = piece(post_ext[: settled + 4], -1, settled + 1, 1)
    first_high = piece(post_ext[width_x:], width_x - 1, width_x + 1, 1)
    second_low = piece(jnp.concatenate([first_low, first_mid[:2]], axis=0), 0, settled + 2, 0)
    second_high = piece(jnp.concatenate([first_mid[-2:], first_high], axis=0), width_x - 2, width_x, 0)
    return jnp.concatenate([second_low, second_mid, second_high], axis=0)


def solution(mesh):
    in_specs = (
        P(("real", "slab"), ("pencil", "sub"), None),
        P(("real", "slab"), ("pencil", "sub"), None),
        P(("real", "slab"), ("pencil", "sub"), None),
        P("real"),
    )
    out_specs = P(("real", "slab"), ("pencil", "sub"), None)
    return jax.shard_map(body, mesh=mesh, in_specs=in_specs, out_specs=out_specs, check_vma=False)
```

```python
import numpy as np
import jax
import jax.numpy as jnp
from jax import lax
from jax.sharding import PartitionSpec as P

NU = 2
NCS = 4


OMEGA = 0.8


def padded(array, sides, width):
    for axis, dim in sides:
        count, length = (lax.axis_size(axis), array.shape[dim])
        up = [(i, (i + 1) % count) for i in range(count - 1)]
        down = [(j, i) for i, j in up]
        last = lax.slice_in_dim(array, length - width, length, axis=dim)
        leading = lax.slice_in_dim(array, 0, width, axis=dim)
        before = lax.ppermute(last, axis, up)
        after = lax.ppermute(leading, axis, down)
        array = jnp.concatenate([before, array, after], axis=dim)
    return array


def passed_along(array, axis, by):
    count = lax.axis_size(axis)
    pairs = [(i, i + by) for i in range(count) if 0 <= i + by < count]
    return lax.ppermute(array, axis, pairs)


def harmonic(lower_k, upper_k, inside):
    denom_sum = jnp.where(inside, lower_k + upper_k, 1.0)
    return jnp.where(inside, 2.0 * lower_k * upper_k / denom_sum, 0.0)


def geometry(perm_ext, glob_x, glob_y, inside_x, inside_y, total_x, total_y):
    count_z = perm_ext.shape[2]
    both_x = (inside_x[:-1] & inside_x[1:])[:, None, None] & inside_y[None, :, None]
    both_y = (inside_y[:-1] & inside_y[1:])[None, :, None] & inside_x[:, None, None]
    plane_in = inside_x[:, None, None] & inside_y[None, :, None]
    face_x = harmonic(perm_ext[:-1], perm_ext[1:], both_x)
    face_y = harmonic(perm_ext[:, :-1], perm_ext[:, 1:], both_y)
    face_z = harmonic(perm_ext[:, :, :-1], perm_ext[:, :, 1:], plane_in)
    cell_perm = perm_ext[1:-1, 1:-1]
    face_west = face_x[:-1, 1:-1]
    face_east = face_x[1:, 1:-1]
    face_south = face_y[1:-1, :-1]
    face_north = face_y[1:-1, 1:]
    zero_plane = jnp.zeros_like(cell_perm[:, :, :1])
    face_below = jnp.concatenate([zero_plane, face_z[1:-1, 1:-1]], axis=2)
    face_above = jnp.concatenate([face_z[1:-1, 1:-1], zero_plane], axis=2)
    cell_x = glob_x[1:-1]
    cell_y = glob_y[1:-1]
    index_z = jnp.arange(count_z)
    ends_x = (cell_x == 0).astype(jnp.float32) + (cell_x == total_x - 1).astype(jnp.float32)
    ends_y = (cell_y == 0).astype(jnp.float32) + (cell_y == total_y - 1).astype(jnp.float32)
    ends_z = (index_z == 0).astype(jnp.float32) + (index_z == count_z - 1).astype(jnp.float32)
    edges = ends_x[:, None, None] + ends_y[None, :, None] + ends_z[None, None, :]
    boundary = 2.0 * cell_perm * edges
    diagonal = face_west + face_east + face_south + face_north + face_below + face_above + boundary
    cell_in = plane_in[1:-1, 1:-1]
    safe_diag = jnp.where(cell_in, diagonal, 1.0)
    return (
        face_west,
        face_east,
        face_south,
        face_north,
        face_below,
        face_above,
        boundary,
        safe_diag,
    )


def apply_fine(ext_field, faces_now):
    face_west, face_east, face_south, face_north, face_below, face_above, boundary, safe_diag = (
        faces_now
    )
    center = ext_field[1:-1, 1:-1]
    zero_plane = jnp.zeros_like(center[:, :, :1])
    below_vals = jnp.concatenate([zero_plane, center[:, :, :-1]], axis=2)
    above_vals = jnp.concatenate([center[:, :, 1:], zero_plane], axis=2)
    beside_all = face_west * ext_field[:-2, 1:-1] + face_east * ext_field[2:, 1:-1]
    beside_all = beside_all + face_south * ext_field[1:-1, :-2] + face_north * ext_field[1:-1, 2:]
    beside_all = beside_all + face_below * below_vals + face_above * above_vals
    return (center, safe_diag * center - beside_all)


def crop(array, rim):
    if rim == 0:
        return array
    return array[rim : array.shape[0] - rim, rim : array.shape[1] - rim]


def sweeps(field_ext, source_ext, faces_ext, count, width):
    def rim_of(array):
        return (array.shape[0] - width) // 2

    for sweep_index in range(count):
        out_rim = rim_of(field_ext) - 1
        faces_now = tuple(crop(member, rim_of(member) - out_rim) for member in faces_ext)
        center, product = apply_fine(field_ext, faces_now)
        source_now = crop(source_ext, rim_of(source_ext) - out_rim)
        field_ext = center + OMEGA * (source_now - product) / faces_now[7]
    return field_ext


def body(permeability, source, pressure, aggregate):
    width_x, width_y, depth_cells = permeability.shape
    slab_index = lax.axis_index("slab")
    slab_count = lax.axis_size("slab")
    row_index = lax.axis_index(("pencil", "sub"))
    row_count = lax.axis_size(("pencil", "sub"))
    total_x = width_x * slab_count
    total_y = width_y * row_count
    sides = (("slab", 0), (("pencil", "sub"), 1))
    stacked_sides = (("slab", 1), (("pencil", "sub"), 2))
    fine_rim = 2 * NU
    ext_x = padded(jnp.stack([permeability, source, pressure]), (("slab", 1),), fine_rim)
    ext_x, aggregate = lax.optimization_barrier((ext_x, aggregate))
    ext_all = padded(ext_x, ((("pencil", "sub"), 2),), fine_rim)
    perm_ext = ext_all[0]
    source_ext = crop(ext_all[1], 1)
    glob_x = slab_index * width_x - fine_rim + jnp.arange(width_x + 2 * fine_rim)
    glob_y = row_index * width_y - fine_rim + jnp.arange(width_y + 2 * fine_rim)
    inside_x = (glob_x >= 0) & (glob_x < total_x)
    inside_y = (glob_y >= 0) & (glob_y < total_y)
    faces_ext = geometry(perm_ext, glob_x, glob_y, inside_x, inside_y, total_x, total_y)
    smooth_ext = sweeps(ext_all[2], source_ext, faces_ext, NU, width_x)
    faces_zero = tuple(crop(member, fine_rim - 1) for member in faces_ext)
    smooth_rows = smooth_ext[NU : NU + width_x]
    center, product = apply_fine(crop(smooth_ext, NU - 1), faces_zero)
    residual = source - product
    half_y = width_y // 2
    half_z = depth_cells // 2

    plane_count = aggregate.shape[0]
    ext_pos = slab_index * width_x - 1 + jnp.arange(width_x + 1 + NU)
    pick_ids = ext_pos[:, None] == jnp.arange(plane_count)[None, :]
    ext_ids = jnp.sum(jnp.where(pick_ids, aggregate.astype(jnp.float32)[None, :], 0.0), axis=1)
    local_ids = ext_ids[1 : width_x + 1]
    straddles = (slab_index > 0) & (ext_ids[0] == local_ids[0])
    first_id = local_ids[0] + straddles.astype(jnp.float32)
    count_live = local_ids[-1] - first_id + 1
    slot_ids = local_ids - first_id
    has_next = ext_pos[2 : width_x + 2] < plane_count
    crossing = ((local_ids != ext_ids[2 : width_x + 2]) & has_next).astype(jnp.float32)
    face_east = faces_zero[1]
    face_north = faces_zero[3]
    face_above = faces_zero[5]
    boundary = faces_zero[6]
    index_z = np.arange(depth_cells)[:, None]
    coarse_z = np.arange(half_z)[None, :]
    pair_z = jnp.asarray((index_z // 2 == coarse_z).astype(np.float32))
    odd_z = jnp.asarray((index_z == 2 * coarse_z + 1).astype(np.float32))
    cells = width_x * width_y

    def z_sum(block_in, pick_z):
        flat = block_in.reshape(cells, depth_cells)
        return jnp.dot(flat, pick_z, precision=lax.Precision.HIGH)

    z_parts = jnp.stack(
        [
            z_sum(residual, pair_z),
            z_sum(face_east * crossing[:, None, None], pair_z),
            z_sum(face_north, pair_z),
            z_sum(face_above, odd_z),
            z_sum(boundary, pair_z),
        ]
    )
    index_y = np.arange(width_y)[:, None]
    coarse_y = np.arange(half_y)[None, :]
    pair_y = jnp.asarray((index_y // 2 == coarse_y).astype(np.float32))
    row_y = np.tile(np.arange(width_y), width_x)
    col_slot = np.repeat(np.arange(width_x + 1), half_y)
    col_y = np.tile(np.arange(half_y), width_x + 1)
    row_slot = jnp.repeat(slot_ids + 1, width_y)
    same_slot = row_slot[:, None] == jnp.asarray(col_slot.astype(np.float32))[None, :]
    pair_rows = row_y[:, None] // 2 == col_y[None, :]
    odd_rows = row_y[:, None] == 2 * col_y[None, :] + 1
    spread_map = (same_slot & pair_rows).astype(jnp.float32)
    gather_map = (same_slot.T & pair_rows.T).astype(jnp.float32)
    north_gather = (same_slot.T & odd_rows.T).astype(jnp.float32)
    paired = jnp.dot(
        gather_map,
        jnp.concatenate([z_parts[0], z_parts[1], z_parts[3], z_parts[4]], axis=1),
        precision=lax.Precision.HIGH,
    )
    north_sums = jnp.dot(north_gather, z_parts[2], precision=lax.Precision.HIGH)

    def column(index):
        return paired[:, index * half_z : (index + 1) * half_z]

    slot_sums = jnp.stack([column(0), column(1), north_sums, column(2), column(3)])
    slot_sums = slot_sums.reshape(5, width_x + 1, half_y, half_z)
    coarse = slot_sums[:, 1:]
    edge_sums = slot_sums[:, 0]
    slot_range = jnp.arange(width_x)
    last_slot = (slot_range == count_live - 1).astype(jnp.float32)
    tail_pick = (slot_range[None, :] == count_live - NCS + jnp.arange(NCS)[:, None]).astype(jnp.float32)
    tail_planes = jnp.einsum("ks,qsjl->qkjl", tail_pick, coarse, precision=lax.Precision.HIGHEST)
    head_planes = jnp.concatenate([coarse[:, :NCS], edge_sums[:, None]], axis=1)
    tail_planes, head_planes = lax.optimization_barrier((tail_planes, head_planes))
    from_prev = passed_along(tail_planes, "slab", 1)
    from_next = passed_along(head_planes, "slab", -1)
    coarse = coarse + from_next[:, NCS][:, None] * last_slot[None, :, None, None]
    prev_last = (jnp.arange(NCS) == NCS - 1).astype(jnp.float32)
    from_prev = from_prev + edge_sums[:, None] * prev_last[None, :, None, None]
    x_ext = jnp.concatenate([from_prev, coarse, jnp.zeros_like(tail_planes)], axis=1)
    wide_range = jnp.arange(width_x + 2 * NCS)[:, None]
    place = (wide_range == NCS + count_live + jnp.arange(NCS)[None, :]).astype(jnp.float32)
    x_ext = x_ext + jnp.einsum("tk,qkjl->qtjl", place, from_next[:, :NCS], precision=lax.Precision.HIGHEST)
    coarse_rim = NCS
    rim_y = NCS + 1
    coef_ext = padded(x_ext, ((("pencil", "sub"), 2),), rim_y)
    coarse_corr = jnp.zeros((width_x + 2 * NCS, half_y + 2 * rim_y, half_z), jnp.float32)
    for sweep_index in range(NCS):
        out_rim = NCS - 1 - sweep_index
        start_at = coarse_rim - out_rim
        start_y = start_at
        size_x = width_x + 2 * out_rim
        size_y = half_y + 2 * (out_rim + 1)

        def region(offset_x, offset_y):
            return coef_ext[
                :,
                start_at + offset_x : start_at + offset_x + size_x,
                start_y + offset_y : start_y + offset_y + size_y,
            ]

        here_coef = region(0, 0)
        coarse_rhs = here_coef[0]
        coarse_east = here_coef[1]
        coarse_north = here_coef[2]
        coarse_above = here_coef[3]
        coarse_bound = here_coef[4]
        coarse_west = region(-1, 0)[1]
        coarse_south = region(0, -1)[2]
        zero_plane = jnp.zeros_like(coarse_above[:, :, :1])
        coarse_below = jnp.concatenate([zero_plane, coarse_above[:, :, :-1]], axis=2)
        diag_coarse = (
            coarse_east
            + coarse_west
            + coarse_north
            + coarse_south
            + coarse_above
            + coarse_below
            + coarse_bound
        )
        safe_coarse = jnp.where(diag_coarse > 0, diag_coarse, 1.0)
        coarse_center = coarse_corr[1:-1, 1:-1]
        above_vals = jnp.concatenate([coarse_center[:, :, 1:], zero_plane], axis=2)
        below_vals = jnp.concatenate([zero_plane, coarse_center[:, :, :-1]], axis=2)
        beside_all = coarse_east * coarse_corr[2:, 1:-1] + coarse_west * coarse_corr[:-2, 1:-1]
        beside_all = (
            beside_all
            + coarse_north * coarse_corr[1:-1, 2:]
            + coarse_south * coarse_corr[1:-1, :-2]
        )
        beside_all = beside_all + coarse_above * above_vals + coarse_below * below_vals
        coarse_corr = (
            coarse_center
            + OMEGA * (coarse_rhs - (diag_coarse * coarse_center - beside_all)) / safe_coarse
        )
    last_corr = jnp.sum(last_slot[:, None, None] * coarse_corr, axis=0)
    corr_wide = jnp.concatenate([jnp.zeros_like(last_corr)[None], coarse_corr], axis=0)
    corr_core = corr_wide[:, 1 : 1 + half_y]
    corr_z = jnp.dot(
        corr_core.reshape((width_x + 1) * half_y, half_z), pair_z.T, precision=lax.Precision.HIGH
    )
    correction = jnp.dot(spread_map, corr_z, precision=lax.Precision.HIGH)
    correction = correction.reshape(width_x, width_y, depth_cells)
    owner_rows = (slot_ids[:, None] + 1 == jnp.arange(width_x + 1)[None, :]).astype(jnp.float32)

    def rim_rows(coarse_row):
        row_z = jnp.dot(corr_wide[:, coarse_row], pair_z.T, precision=lax.Precision.HIGHEST)
        row_fine = jnp.dot(owner_rows, row_z, precision=lax.Precision.HIGHEST)
        return jnp.broadcast_to(row_fine[:, None], (width_x, NU, depth_cells))

    correction = jnp.concatenate([rim_rows(0), correction, rim_rows(half_y + 1)], axis=1)
    base = smooth_rows + correction
    last_z = jnp.dot(last_corr, pair_z.T, precision=lax.Precision.HIGHEST)
    fine_y = np.arange(width_y + 2 * NU) - NU
    rows_ext = jnp.asarray((fine_y[:, None] // 2 + 1 == np.arange(half_y + 2)[None, :]).astype(np.float32))
    last_fine = jnp.dot(rows_ext, last_z, precision=lax.Precision.HIGHEST)
    up_block = jnp.concatenate([base[width_x - NU :], last_fine[None]], axis=0)
    below_prev = passed_along(up_block, "slab", 1)
    above_next = passed_along(base[:NU], "slab", -1)
    from_owner = (slot_ids == -1).astype(jnp.float32)
    own = base + from_owner[:, None, None] * below_prev[NU][None]
    next_ids = ext_ids[width_x + 1 :]
    next_in = ext_pos[width_x + 1 :] < plane_count
    to_owner = ((next_ids == local_ids[-1]) & next_in).astype(jnp.float32)
    high_halo = above_next + to_owner[:, None, None] * last_fine[None]
    post_ext = jnp.concatenate([below_prev[:NU], own, high_halo], axis=0)
    return sweeps(post_ext, source_ext, faces_ext, NU, width_x)


def solution(mesh):
    in_specs = (
        P(("real", "slab"), ("pencil", "sub"), None),
        P(("real", "slab"), ("pencil", "sub"), None),
        P(("real", "slab"), ("pencil", "sub"), None),
        P("real"),
    )
    out_specs = P(("real", "slab"), ("pencil", "sub"), None)
    return jax.shard_map(body, mesh=mesh, in_specs=in_specs, out_specs=out_specs, check_vma=False)
```

```python
import numpy as np
import jax
import jax.numpy as jnp
from jax import lax
from jax.sharding import PartitionSpec as P

NU = 2
NCS = 4


OMEGA = 0.8


def padded(array, sides, width):
    for axis, dim in sides:
        count, length = (lax.axis_size(axis), array.shape[dim])
        up = [(i, (i + 1) % count) for i in range(count - 1)]
        down = [(j, i) for i, j in up]
        last = lax.slice_in_dim(array, length - width, length, axis=dim)
        leading = lax.slice_in_dim(array, 0, width, axis=dim)
        before = lax.ppermute(last, axis, up)
        after = lax.ppermute(leading, axis, down)
        array = jnp.concatenate([before, array, after], axis=dim)
    return array


def passed_along(array, axis, by):
    count = lax.axis_size(axis)
    pairs = [(i, i + by) for i in range(count) if 0 <= i + by < count]
    return lax.ppermute(array, axis, pairs)


def harmonic(lower_k, upper_k, inside):
    denom_sum = jnp.where(inside, lower_k + upper_k, 1.0)
    return jnp.where(inside, 2.0 * lower_k * upper_k / denom_sum, 0.0)


def geometry(perm_ext, glob_x, glob_y, inside_x, inside_y, total_x, total_y):
    count_z = perm_ext.shape[2]
    both_x = (inside_x[:-1] & inside_x[1:])[:, None, None] & inside_y[None, :, None]
    both_y = (inside_y[:-1] & inside_y[1:])[None, :, None] & inside_x[:, None, None]
    plane_in = inside_x[:, None, None] & inside_y[None, :, None]
    face_x = harmonic(perm_ext[:-1], perm_ext[1:], both_x)
    face_y = harmonic(perm_ext[:, :-1], perm_ext[:, 1:], both_y)
    face_z = harmonic(perm_ext[:, :, :-1], perm_ext[:, :, 1:], plane_in)
    cell_perm = perm_ext[1:-1, 1:-1]
    face_west = face_x[:-1, 1:-1]
    face_east = face_x[1:, 1:-1]
    face_south = face_y[1:-1, :-1]
    face_north = face_y[1:-1, 1:]
    zero_plane = jnp.zeros_like(cell_perm[:, :, :1])
    face_below = jnp.concatenate([zero_plane, face_z[1:-1, 1:-1]], axis=2)
    face_above = jnp.concatenate([face_z[1:-1, 1:-1], zero_plane], axis=2)
    cell_x = glob_x[1:-1]
    cell_y = glob_y[1:-1]
    index_z = jnp.arange(count_z)
    ends_x = (cell_x == 0).astype(jnp.float32) + (cell_x == total_x - 1).astype(jnp.float32)
    ends_y = (cell_y == 0).astype(jnp.float32) + (cell_y == total_y - 1).astype(jnp.float32)
    ends_z = (index_z == 0).astype(jnp.float32) + (index_z == count_z - 1).astype(jnp.float32)
    edges = ends_x[:, None, None] + ends_y[None, :, None] + ends_z[None, None, :]
    boundary = 2.0 * cell_perm * edges
    diagonal = face_west + face_east + face_south + face_north + face_below + face_above + boundary
    cell_in = plane_in[1:-1, 1:-1]
    safe_diag = jnp.where(cell_in, diagonal, 1.0)
    return (
        face_west,
        face_east,
        face_south,
        face_north,
        face_below,
        face_above,
        boundary,
        safe_diag,
    )


def apply_fine(ext_field, faces_now):
    face_west, face_east, face_south, face_north, face_below, face_above, boundary, safe_diag = (
        faces_now
    )
    center = ext_field[1:-1, 1:-1]
    zero_plane = jnp.zeros_like(center[:, :, :1])
    below_vals = jnp.concatenate([zero_plane, center[:, :, :-1]], axis=2)
    above_vals = jnp.concatenate([center[:, :, 1:], zero_plane], axis=2)
    beside_all = face_west * ext_field[:-2, 1:-1] + face_east * ext_field[2:, 1:-1]
    beside_all = beside_all + face_south * ext_field[1:-1, :-2] + face_north * ext_field[1:-1, 2:]
    beside_all = beside_all + face_below * below_vals + face_above * above_vals
    return (center, safe_diag * center - beside_all)


def crop(array, rim):
    if rim == 0:
        return array
    return array[rim : array.shape[0] - rim, rim : array.shape[1] - rim]


def sweeps(field_ext, source_ext, faces_ext, count, width):
    def rim_of(array):
        return (array.shape[0] - width) // 2

    for sweep_index in range(count):
        out_rim = rim_of(field_ext) - 1
        faces_now = tuple(crop(member, rim_of(member) - out_rim) for member in faces_ext)
        center, product = apply_fine(field_ext, faces_now)
        source_now = crop(source_ext, rim_of(source_ext) - out_rim)
        field_ext = center + OMEGA * (source_now - product) / faces_now[7]
    return field_ext


def body(permeability, source, pressure, aggregate):
    width_x, width_y, depth_cells = permeability.shape
    slab_index = lax.axis_index("slab")
    slab_count = lax.axis_size("slab")
    row_index = lax.axis_index(("pencil", "sub"))
    row_count = lax.axis_size(("pencil", "sub"))
    total_x = width_x * slab_count
    total_y = width_y * row_count
    sides = (("slab", 0), (("pencil", "sub"), 1))
    stacked_sides = (("slab", 1), (("pencil", "sub"), 2))
    fine_rim = 2 * NU
    ext_x = padded(jnp.stack([permeability, source, pressure]), (("slab", 1),), fine_rim)
    ext_all = padded(ext_x, ((("pencil", "sub"), 2),), fine_rim)
    perm_ext = ext_all[0]
    source_ext = crop(ext_all[1], 1)
    glob_x = slab_index * width_x - fine_rim + jnp.arange(width_x + 2 * fine_rim)
    glob_y = row_index * width_y - fine_rim + jnp.arange(width_y + 2 * fine_rim)
    inside_x = (glob_x >= 0) & (glob_x < total_x)
    inside_y = (glob_y >= 0) & (glob_y < total_y)
    faces_ext = geometry(perm_ext, glob_x, glob_y, inside_x, inside_y, total_x, total_y)
    smooth_ext = sweeps(ext_all[2], source_ext, faces_ext, NU, width_x)
    faces_zero = tuple(crop(member, fine_rim - 1) for member in faces_ext)
    smooth_rows = smooth_ext[NU : NU + width_x]
    center, product = apply_fine(crop(smooth_ext, NU - 1), faces_zero)
    residual = source - product
    half_y = width_y // 2
    half_z = depth_cells // 2

    plane_count = aggregate.shape[0]
    ext_pos = slab_index * width_x - 1 + jnp.arange(width_x + 1 + NU)
    pick_ids = ext_pos[:, None] == jnp.arange(plane_count)[None, :]
    ext_ids = jnp.sum(jnp.where(pick_ids, aggregate.astype(jnp.float32)[None, :], 0.0), axis=1)
    local_ids = ext_ids[1 : width_x + 1]
    straddles = (slab_index > 0) & (ext_ids[0] == local_ids[0])
    first_id = local_ids[0] + straddles.astype(jnp.float32)
    count_live = local_ids[-1] - first_id + 1
    slot_ids = local_ids - first_id
    has_next = ext_pos[2 : width_x + 2] < plane_count
    crossing = ((local_ids != ext_ids[2 : width_x + 2]) & has_next).astype(jnp.float32)
    face_east = faces_zero[1]
    face_north = faces_zero[3]
    face_above = faces_zero[5]
    boundary = faces_zero[6]
    index_z = np.arange(depth_cells)[:, None]
    coarse_z = np.arange(half_z)[None, :]
    pair_z = jnp.asarray((index_z // 2 == coarse_z).astype(np.float32))
    odd_z = jnp.asarray((index_z == 2 * coarse_z + 1).astype(np.float32))
    cells = width_x * width_y

    def z_sum(block_in, pick_z):
        flat = block_in.reshape(cells, depth_cells)
        return jnp.dot(flat, pick_z, precision=lax.Precision.HIGH)

    z_parts = jnp.stack(
        [
            z_sum(residual, pair_z),
            z_sum(face_east * crossing[:, None, None], pair_z),
            z_sum(face_north, pair_z),
            z_sum(face_above, odd_z),
            z_sum(boundary, pair_z),
        ]
    )
    index_y = np.arange(width_y)[:, None]
    coarse_y = np.arange(half_y)[None, :]
    pair_y = jnp.asarray((index_y // 2 == coarse_y).astype(np.float32))
    row_y = np.tile(np.arange(width_y), width_x)
    col_slot = np.repeat(np.arange(width_x + 1), half_y)
    col_y = np.tile(np.arange(half_y), width_x + 1)
    row_slot = jnp.repeat(slot_ids + 1, width_y)
    same_slot = row_slot[:, None] == jnp.asarray(col_slot.astype(np.float32))[None, :]
    pair_rows = row_y[:, None] // 2 == col_y[None, :]
    odd_rows = row_y[:, None] == 2 * col_y[None, :] + 1
    spread_map = (same_slot & pair_rows).astype(jnp.float32)
    gather_map = (same_slot.T & pair_rows.T).astype(jnp.float32)
    north_gather = (same_slot.T & odd_rows.T).astype(jnp.float32)
    paired = jnp.dot(
        gather_map,
        jnp.concatenate([z_parts[0], z_parts[1], z_parts[3], z_parts[4]], axis=1),
        precision=lax.Precision.HIGH,
    )
    north_sums = jnp.dot(north_gather, z_parts[2], precision=lax.Precision.HIGH)

    def column(index):
        return paired[:, index * half_z : (index + 1) * half_z]

    slot_sums = jnp.stack([column(0), column(1), north_sums, column(2), column(3)])
    slot_sums = slot_sums.reshape(5, width_x + 1, half_y, half_z)
    coarse = slot_sums[:, 1:]
    edge_sums = slot_sums[:, 0]
    slot_range = jnp.arange(width_x)
    last_slot = (slot_range == count_live - 1).astype(jnp.float32)
    tail_pick = (slot_range[None, :] == count_live - NCS + jnp.arange(NCS)[:, None]).astype(jnp.float32)
    tail_planes = jnp.einsum("ks,qsjl->qkjl", tail_pick, coarse, precision=lax.Precision.HIGHEST)
    head_planes = jnp.concatenate([coarse[:, :NCS], edge_sums[:, None]], axis=1)
    tail_planes, head_planes = lax.optimization_barrier((tail_planes, head_planes))
    from_prev = passed_along(tail_planes, "slab", 1)
    from_next = passed_along(head_planes, "slab", -1)
    coarse = coarse + from_next[:, NCS][:, None] * last_slot[None, :, None, None]
    prev_last = (jnp.arange(NCS) == NCS - 1).astype(jnp.float32)
    from_prev = from_prev + edge_sums[:, None] * prev_last[None, :, None, None]
    x_ext = jnp.concatenate([from_prev, coarse, jnp.zeros_like(tail_planes)], axis=1)
    wide_range = jnp.arange(width_x + 2 * NCS)[:, None]
    place = (wide_range == NCS + count_live + jnp.arange(NCS)[None, :]).astype(jnp.float32)
    x_ext = x_ext + jnp.einsum("tk,qkjl->qtjl", place, from_next[:, :NCS], precision=lax.Precision.HIGHEST)
    coarse_rim = NCS
    rim_y = NCS + 1
    coef_ext = padded(x_ext, ((("pencil", "sub"), 2),), rim_y)
    coarse_corr = jnp.zeros((width_x + 2 * NCS, half_y + 2 * rim_y, half_z), jnp.float32)
    for sweep_index in range(NCS):
        out_rim = NCS - 1 - sweep_index
        start_at = coarse_rim - out_rim
        start_y = start_at
        size_x = width_x + 2 * out_rim
        size_y = half_y + 2 * (out_rim + 1)

        def region(offset_x, offset_y):
            return coef_ext[
                :,
                start_at + offset_x : start_at + offset_x + size_x,
                start_y + offset_y : start_y + offset_y + size_y,
            ]

        here_coef = region(0, 0)
        coarse_rhs = here_coef[0]
        coarse_east = here_coef[1]
        coarse_north = here_coef[2]
        coarse_above = here_coef[3]
        coarse_bound = here_coef[4]
        coarse_west = region(-1, 0)[1]
        coarse_south = region(0, -1)[2]
        zero_plane = jnp.zeros_like(coarse_above[:, :, :1])
        coarse_below = jnp.concatenate([zero_plane, coarse_above[:, :, :-1]], axis=2)
        diag_coarse = (
            coarse_east
            + coarse_west
            + coarse_north
            + coarse_south
            + coarse_above
            + coarse_below
            + coarse_bound
        )
        safe_coarse = jnp.where(diag_coarse > 0, diag_coarse, 1.0)
        coarse_center = coarse_corr[1:-1, 1:-1]
        above_vals = jnp.concatenate([coarse_center[:, :, 1:], zero_plane], axis=2)
        below_vals = jnp.concatenate([zero_plane, coarse_center[:, :, :-1]], axis=2)
        beside_all = coarse_east * coarse_corr[2:, 1:-1] + coarse_west * coarse_corr[:-2, 1:-1]
        beside_all = (
            beside_all
            + coarse_north * coarse_corr[1:-1, 2:]
            + coarse_south * coarse_corr[1:-1, :-2]
        )
        beside_all = beside_all + coarse_above * above_vals + coarse_below * below_vals
        coarse_corr = (
            coarse_center
            + OMEGA * (coarse_rhs - (diag_coarse * coarse_center - beside_all)) / safe_coarse
        )
    last_corr = jnp.sum(last_slot[:, None, None] * coarse_corr, axis=0)
    corr_wide = jnp.concatenate([jnp.zeros_like(last_corr)[None], coarse_corr], axis=0)
    corr_core = corr_wide[:, 1 : 1 + half_y]
    corr_z = jnp.dot(
        corr_core.reshape((width_x + 1) * half_y, half_z), pair_z.T, precision=lax.Precision.HIGH
    )
    correction = jnp.dot(spread_map, corr_z, precision=lax.Precision.HIGH)
    correction = correction.reshape(width_x, width_y, depth_cells)
    owner_rows = (slot_ids[:, None] + 1 == jnp.arange(width_x + 1)[None, :]).astype(jnp.float32)

    def rim_rows(coarse_row):
        row_z = jnp.dot(corr_wide[:, coarse_row], pair_z.T, precision=lax.Precision.HIGHEST)
        row_fine = jnp.dot(owner_rows, row_z, precision=lax.Precision.HIGHEST)
        return jnp.broadcast_to(row_fine[:, None], (width_x, NU, depth_cells))

    correction = jnp.concatenate([rim_rows(0), correction, rim_rows(half_y + 1)], axis=1)
    base = smooth_rows + correction
    last_z = jnp.dot(last_corr, pair_z.T, precision=lax.Precision.HIGHEST)
    fine_y = np.arange(width_y + 2 * NU) - NU
    rows_ext = jnp.asarray((fine_y[:, None] // 2 + 1 == np.arange(half_y + 2)[None, :]).astype(np.float32))
    last_fine = jnp.dot(rows_ext, last_z, precision=lax.Precision.HIGHEST)
    up_block = jnp.concatenate([base[width_x - NU :], last_fine[None]], axis=0)
    below_prev = passed_along(up_block, "slab", 1)
    above_next = passed_along(base[:NU], "slab", -1)
    from_owner = (slot_ids == -1).astype(jnp.float32)
    own = base + from_owner[:, None, None] * below_prev[NU][None]
    next_ids = ext_ids[width_x + 1 :]
    next_in = ext_pos[width_x + 1 :] < plane_count
    to_owner = ((next_ids == local_ids[-1]) & next_in).astype(jnp.float32)
    high_halo = above_next + to_owner[:, None, None] * last_fine[None]
    post_ext = jnp.concatenate([below_prev[:NU], own, high_halo], axis=0)
    return sweeps(post_ext, source_ext, faces_ext, NU, width_x)


def solution(mesh):
    in_specs = (
        P(("real", "slab"), ("pencil", "sub"), None),
        P(("real", "slab"), ("pencil", "sub"), None),
        P(("real", "slab"), ("pencil", "sub"), None),
        P("real"),
    )
    out_specs = P(("real", "slab"), ("pencil", "sub"), None)
    return jax.shard_map(body, mesh=mesh, in_specs=in_specs, out_specs=out_specs, check_vma=False)
```

```python
import numpy as np
import jax
import jax.numpy as jnp
from jax import lax
from jax.sharding import PartitionSpec as P

NU = 2
NCS = 4


OMEGA = 0.8


def padded(array, sides, width):
    for axis, dim in sides:
        count, length = (lax.axis_size(axis), array.shape[dim])
        up = [(i, (i + 1) % count) for i in range(count - 1)]
        down = [(j, i) for i, j in up]
        last = lax.slice_in_dim(array, length - width, length, axis=dim)
        leading = lax.slice_in_dim(array, 0, width, axis=dim)
        before = lax.ppermute(last, axis, up)
        after = lax.ppermute(leading, axis, down)
        array = jnp.concatenate([before, array, after], axis=dim)
    return array


def passed_along(array, axis, by):
    count = lax.axis_size(axis)
    pairs = [(i, i + by) for i in range(count) if 0 <= i + by < count]
    return lax.ppermute(array, axis, pairs)


def harmonic(lower_k, upper_k, inside):
    denom_sum = jnp.where(inside, lower_k + upper_k, 1.0)
    return jnp.where(inside, 2.0 * lower_k * upper_k / denom_sum, 0.0)


def geometry(perm_ext, glob_x, glob_y, inside_x, inside_y, total_x, total_y):
    count_z = perm_ext.shape[2]
    both_x = (inside_x[:-1] & inside_x[1:])[:, None, None] & inside_y[None, :, None]
    both_y = (inside_y[:-1] & inside_y[1:])[None, :, None] & inside_x[:, None, None]
    plane_in = inside_x[:, None, None] & inside_y[None, :, None]
    face_x = harmonic(perm_ext[:-1], perm_ext[1:], both_x)
    face_y = harmonic(perm_ext[:, :-1], perm_ext[:, 1:], both_y)
    face_z = harmonic(perm_ext[:, :, :-1], perm_ext[:, :, 1:], plane_in)
    cell_perm = perm_ext[1:-1, 1:-1]
    face_west = face_x[:-1, 1:-1]
    face_east = face_x[1:, 1:-1]
    face_south = face_y[1:-1, :-1]
    face_north = face_y[1:-1, 1:]
    zero_plane = jnp.zeros_like(cell_perm[:, :, :1])
    face_below = jnp.concatenate([zero_plane, face_z[1:-1, 1:-1]], axis=2)
    face_above = jnp.concatenate([face_z[1:-1, 1:-1], zero_plane], axis=2)
    cell_x = glob_x[1:-1]
    cell_y = glob_y[1:-1]
    index_z = jnp.arange(count_z)
    ends_x = (cell_x == 0).astype(jnp.float32) + (cell_x == total_x - 1).astype(jnp.float32)
    ends_y = (cell_y == 0).astype(jnp.float32) + (cell_y == total_y - 1).astype(jnp.float32)
    ends_z = (index_z == 0).astype(jnp.float32) + (index_z == count_z - 1).astype(jnp.float32)
    edges = ends_x[:, None, None] + ends_y[None, :, None] + ends_z[None, None, :]
    boundary = 2.0 * cell_perm * edges
    diagonal = face_west + face_east + face_south + face_north + face_below + face_above + boundary
    cell_in = plane_in[1:-1, 1:-1]
    safe_diag = jnp.where(cell_in, diagonal, 1.0)
    return (
        face_west,
        face_east,
        face_south,
        face_north,
        face_below,
        face_above,
        boundary,
        safe_diag,
    )


def apply_fine(ext_field, faces_now):
    face_west, face_east, face_south, face_north, face_below, face_above, boundary, safe_diag = (
        faces_now
    )
    center = ext_field[1:-1, 1:-1]
    zero_plane = jnp.zeros_like(center[:, :, :1])
    below_vals = jnp.concatenate([zero_plane, center[:, :, :-1]], axis=2)
    above_vals = jnp.concatenate([center[:, :, 1:], zero_plane], axis=2)
    beside_all = face_west * ext_field[:-2, 1:-1] + face_east * ext_field[2:, 1:-1]
    beside_all = beside_all + face_south * ext_field[1:-1, :-2] + face_north * ext_field[1:-1, 2:]
    beside_all = beside_all + face_below * below_vals + face_above * above_vals
    return (center, safe_diag * center - beside_all)


def crop(array, rim):
    if rim == 0:
        return array
    return array[rim : array.shape[0] - rim, rim : array.shape[1] - rim]


def sweeps(field_ext, source_ext, faces_ext, count, width):
    def rim_of(array):
        return (array.shape[0] - width) // 2

    for sweep_index in range(count):
        out_rim = rim_of(field_ext) - 1
        faces_now = tuple(crop(member, rim_of(member) - out_rim) for member in faces_ext)
        center, product = apply_fine(field_ext, faces_now)
        source_now = crop(source_ext, rim_of(source_ext) - out_rim)
        field_ext = center + OMEGA * (source_now - product) / faces_now[7]
    return field_ext


def body(permeability, source, pressure, aggregate):
    width_x, width_y, depth_cells = permeability.shape
    slab_index = lax.axis_index("slab")
    slab_count = lax.axis_size("slab")
    row_index = lax.axis_index(("pencil", "sub"))
    row_count = lax.axis_size(("pencil", "sub"))
    total_x = width_x * slab_count
    total_y = width_y * row_count
    sides = (("slab", 0), (("pencil", "sub"), 1))
    stacked_sides = (("slab", 1), (("pencil", "sub"), 2))
    fine_rim = 2 * NU
    ext_x = padded(jnp.stack([permeability, source, pressure]), (("slab", 1),), fine_rim)
    ext_x, aggregate = lax.optimization_barrier((ext_x, aggregate))
    ext_all = padded(ext_x, ((("pencil", "sub"), 2),), fine_rim)
    perm_ext = ext_all[0]
    source_ext = crop(ext_all[1], 1)
    glob_x = slab_index * width_x - fine_rim + jnp.arange(width_x + 2 * fine_rim)
    glob_y = row_index * width_y - fine_rim + jnp.arange(width_y + 2 * fine_rim)
    inside_x = (glob_x >= 0) & (glob_x < total_x)
    inside_y = (glob_y >= 0) & (glob_y < total_y)
    faces_ext = geometry(perm_ext, glob_x, glob_y, inside_x, inside_y, total_x, total_y)
    smooth_ext = sweeps(ext_all[2], source_ext, faces_ext, NU, width_x)
    faces_zero = tuple(crop(member, fine_rim - 1) for member in faces_ext)
    smooth_rows = smooth_ext[NU : NU + width_x]
    center, product = apply_fine(crop(smooth_ext, NU - 1), faces_zero)
    residual = source - product
    half_y = width_y // 2
    half_z = depth_cells // 2

    plane_count = aggregate.shape[0]
    ext_pos = slab_index * width_x - 1 + jnp.arange(width_x + 1 + NU)
    pick_ids = ext_pos[:, None] == jnp.arange(plane_count)[None, :]
    ext_ids = jnp.sum(jnp.where(pick_ids, aggregate.astype(jnp.float32)[None, :], 0.0), axis=1)
    local_ids = ext_ids[1 : width_x + 1]
    straddles = (slab_index > 0) & (ext_ids[0] == local_ids[0])
    first_id = local_ids[0] + straddles.astype(jnp.float32)
    count_live = local_ids[-1] - first_id + 1
    slot_ids = local_ids - first_id
    has_next = ext_pos[2 : width_x + 2] < plane_count
    crossing = ((local_ids != ext_ids[2 : width_x + 2]) & has_next).astype(jnp.float32)
    face_east = faces_zero[1]
    face_north = faces_zero[3]
    face_above = faces_zero[5]
    boundary = faces_zero[6]
    index_z = np.arange(depth_cells)[:, None]
    coarse_z = np.arange(half_z)[None, :]
    pair_z = jnp.asarray((index_z // 2 == coarse_z).astype(np.float32))
    odd_z = jnp.asarray((index_z == 2 * coarse_z + 1).astype(np.float32))
    cells = width_x * width_y

    def z_sum(block_in, pick_z):
        flat = block_in.reshape(cells, depth_cells)
        return jnp.dot(flat, pick_z, precision=lax.Precision.HIGH)

    z_parts = jnp.stack(
        [
            z_sum(residual, pair_z),
            z_sum(face_east * crossing[:, None, None], pair_z),
            z_sum(face_north, pair_z),
            z_sum(face_above, odd_z),
            z_sum(boundary, pair_z),
        ]
    )
    index_y = np.arange(width_y)[:, None]
    coarse_y = np.arange(half_y)[None, :]
    pair_y = jnp.asarray((index_y // 2 == coarse_y).astype(np.float32))
    row_y = np.tile(np.arange(width_y), width_x)
    col_slot = np.repeat(np.arange(width_x + 1), half_y)
    col_y = np.tile(np.arange(half_y), width_x + 1)
    row_slot = jnp.repeat(slot_ids + 1, width_y)
    same_slot = row_slot[:, None] == jnp.asarray(col_slot.astype(np.float32))[None, :]
    pair_rows = row_y[:, None] // 2 == col_y[None, :]
    odd_rows = row_y[:, None] == 2 * col_y[None, :] + 1
    spread_map = (same_slot & pair_rows).astype(jnp.float32)
    gather_map = (same_slot.T & pair_rows.T).astype(jnp.float32)
    north_gather = (same_slot.T & odd_rows.T).astype(jnp.float32)
    paired = jnp.dot(
        gather_map,
        jnp.concatenate([z_parts[0], z_parts[1], z_parts[3], z_parts[4]], axis=1),
        precision=lax.Precision.HIGH,
    )
    north_sums = jnp.dot(north_gather, z_parts[2], precision=lax.Precision.HIGH)

    def column(index):
        return paired[:, index * half_z : (index + 1) * half_z]

    slot_sums = jnp.stack([column(0), column(1), north_sums, column(2), column(3)])
    slot_sums = slot_sums.reshape(5, width_x + 1, half_y, half_z)
    coarse = slot_sums[:, 1:]
    edge_sums = slot_sums[:, 0]
    slot_range = jnp.arange(width_x)
    last_slot = (slot_range == count_live - 1).astype(jnp.float32)
    tail_pick = (slot_range[None, :] == count_live - NCS + jnp.arange(NCS)[:, None]).astype(jnp.float32)
    tail_planes = jnp.einsum("ks,qsjl->qkjl", tail_pick, coarse, precision=lax.Precision.HIGHEST)
    head_planes = jnp.concatenate([coarse[:, :NCS], edge_sums[:, None]], axis=1)
    tail_wide = jnp.concatenate([tail_planes, jnp.zeros_like(edge_sums[:, None])], axis=1)
    slab_range = jnp.arange(slab_count)
    to_next = (slab_range == slab_index + 1).astype(jnp.float32)[:, None, None, None, None]
    to_prev = (slab_range == slab_index - 1).astype(jnp.float32)[:, None, None, None, None]
    outgoing = to_next * tail_wide[None] + to_prev * head_planes[None]
    incoming = lax.all_to_all(outgoing, "slab", 0, 0, tiled=False)
    from_prev = jnp.sum(to_prev * incoming, axis=0)[:, :NCS]
    from_next = jnp.sum(to_next * incoming, axis=0)
    coarse = coarse + from_next[:, NCS][:, None] * last_slot[None, :, None, None]
    prev_last = (jnp.arange(NCS) == NCS - 1).astype(jnp.float32)
    from_prev = from_prev + edge_sums[:, None] * prev_last[None, :, None, None]
    x_ext = jnp.concatenate([from_prev, coarse, jnp.zeros_like(tail_planes)], axis=1)
    wide_range = jnp.arange(width_x + 2 * NCS)[:, None]
    place = (wide_range == NCS + count_live + jnp.arange(NCS)[None, :]).astype(jnp.float32)
    x_ext = x_ext + jnp.einsum("tk,qkjl->qtjl", place, from_next[:, :NCS], precision=lax.Precision.HIGHEST)
    coarse_rim = NCS
    rim_y = NCS + 1
    coef_ext = padded(x_ext, ((("pencil", "sub"), 2),), rim_y)
    coarse_corr = jnp.zeros((width_x + 2 * NCS, half_y + 2 * rim_y, half_z), jnp.float32)
    for sweep_index in range(NCS):
        out_rim = NCS - 1 - sweep_index
        start_at = coarse_rim - out_rim
        start_y = start_at
        size_x = width_x + 2 * out_rim
        size_y = half_y + 2 * (out_rim + 1)

        def region(offset_x, offset_y):
            return coef_ext[
                :,
                start_at + offset_x : start_at + offset_x + size_x,
                start_y + offset_y : start_y + offset_y + size_y,
            ]

        here_coef = region(0, 0)
        coarse_rhs = here_coef[0]
        coarse_east = here_coef[1]
        coarse_north = here_coef[2]
        coarse_above = here_coef[3]
        coarse_bound = here_coef[4]
        coarse_west = region(-1, 0)[1]
        coarse_south = region(0, -1)[2]
        zero_plane = jnp.zeros_like(coarse_above[:, :, :1])
        coarse_below = jnp.concatenate([zero_plane, coarse_above[:, :, :-1]], axis=2)
        diag_coarse = (
            coarse_east
            + coarse_west
            + coarse_north
            + coarse_south
            + coarse_above
            + coarse_below
            + coarse_bound
        )
        safe_coarse = jnp.where(diag_coarse > 0, diag_coarse, 1.0)
        coarse_center = coarse_corr[1:-1, 1:-1]
        above_vals = jnp.concatenate([coarse_center[:, :, 1:], zero_plane], axis=2)
        below_vals = jnp.concatenate([zero_plane, coarse_center[:, :, :-1]], axis=2)
        beside_all = coarse_east * coarse_corr[2:, 1:-1] + coarse_west * coarse_corr[:-2, 1:-1]
        beside_all = (
            beside_all
            + coarse_north * coarse_corr[1:-1, 2:]
            + coarse_south * coarse_corr[1:-1, :-2]
        )
        beside_all = beside_all + coarse_above * above_vals + coarse_below * below_vals
        coarse_corr = (
            coarse_center
            + OMEGA * (coarse_rhs - (diag_coarse * coarse_center - beside_all)) / safe_coarse
        )
    last_corr = jnp.sum(last_slot[:, None, None] * coarse_corr, axis=0)
    corr_wide = jnp.concatenate([jnp.zeros_like(last_corr)[None], coarse_corr], axis=0)
    corr_core = corr_wide[:, 1 : 1 + half_y]
    corr_z = jnp.dot(
        corr_core.reshape((width_x + 1) * half_y, half_z), pair_z.T, precision=lax.Precision.HIGH
    )
    correction = jnp.dot(spread_map, corr_z, precision=lax.Precision.HIGH)
    correction = correction.reshape(width_x, width_y, depth_cells)
    owner_rows = (slot_ids[:, None] + 1 == jnp.arange(width_x + 1)[None, :]).astype(jnp.float32)

    def rim_rows(coarse_row):
        row_z = jnp.dot(corr_wide[:, coarse_row], pair_z.T, precision=lax.Precision.HIGHEST)
        row_fine = jnp.dot(owner_rows, row_z, precision=lax.Precision.HIGHEST)
        return jnp.broadcast_to(row_fine[:, None], (width_x, NU, depth_cells))

    correction = jnp.concatenate([rim_rows(0), correction, rim_rows(half_y + 1)], axis=1)
    base = smooth_rows + correction
    last_z = jnp.dot(last_corr, pair_z.T, precision=lax.Precision.HIGHEST)
    fine_y = np.arange(width_y + 2 * NU) - NU
    rows_ext = jnp.asarray((fine_y[:, None] // 2 + 1 == np.arange(half_y + 2)[None, :]).astype(np.float32))
    last_fine = jnp.dot(rows_ext, last_z, precision=lax.Precision.HIGHEST)
    up_block = jnp.concatenate([base[width_x - NU :], last_fine[None]], axis=0)
    below_prev = passed_along(up_block, "slab", 1)
    above_next = passed_along(base[:NU], "slab", -1)
    from_owner = (slot_ids == -1).astype(jnp.float32)
    own = base + from_owner[:, None, None] * below_prev[NU][None]
    next_ids = ext_ids[width_x + 1 :]
    next_in = ext_pos[width_x + 1 :] < plane_count
    to_owner = ((next_ids == local_ids[-1]) & next_in).astype(jnp.float32)
    high_halo = above_next + to_owner[:, None, None] * last_fine[None]
    post_ext = jnp.concatenate([below_prev[:NU], own, high_halo], axis=0)
    return sweeps(post_ext, source_ext, faces_ext, NU, width_x)


def solution(mesh):
    in_specs = (
        P(("real", "slab"), ("pencil", "sub"), None),
        P(("real", "slab"), ("pencil", "sub"), None),
        P(("real", "slab"), ("pencil", "sub"), None),
        P("real"),
    )
    out_specs = P(("real", "slab"), ("pencil", "sub"), None)
    return jax.shard_map(body, mesh=mesh, in_specs=in_specs, out_specs=out_specs, check_vma=False)
```

```python
import numpy as np
import jax
import jax.numpy as jnp
from jax import lax
from jax.sharding import PartitionSpec as P

NU = 2
NCS = 4


OMEGA = 0.8


def padded(array, sides, width):
    for axis, dim in sides:
        count, length = (lax.axis_size(axis), array.shape[dim])
        up = [(i, (i + 1) % count) for i in range(count - 1)]
        down = [(j, i) for i, j in up]
        last = lax.slice_in_dim(array, length - width, length, axis=dim)
        leading = lax.slice_in_dim(array, 0, width, axis=dim)
        before = lax.ppermute(last, axis, up)
        after = lax.ppermute(leading, axis, down)
        array = jnp.concatenate([before, array, after], axis=dim)
    return array


def passed_along(array, axis, by):
    count = lax.axis_size(axis)
    pairs = [(i, i + by) for i in range(count) if 0 <= i + by < count]
    return lax.ppermute(array, axis, pairs)


def harmonic(lower_k, upper_k, inside):
    denom_sum = jnp.where(inside, lower_k + upper_k, 1.0)
    return jnp.where(inside, 2.0 * lower_k * upper_k / denom_sum, 0.0)


def geometry(perm_ext, glob_x, glob_y, inside_x, inside_y, total_x, total_y):
    count_z = perm_ext.shape[2]
    both_x = (inside_x[:-1] & inside_x[1:])[:, None, None] & inside_y[None, :, None]
    both_y = (inside_y[:-1] & inside_y[1:])[None, :, None] & inside_x[:, None, None]
    plane_in = inside_x[:, None, None] & inside_y[None, :, None]
    face_x = harmonic(perm_ext[:-1], perm_ext[1:], both_x)
    face_y = harmonic(perm_ext[:, :-1], perm_ext[:, 1:], both_y)
    face_z = harmonic(perm_ext[:, :, :-1], perm_ext[:, :, 1:], plane_in)
    cell_perm = perm_ext[1:-1, 1:-1]
    face_west = face_x[:-1, 1:-1]
    face_east = face_x[1:, 1:-1]
    face_south = face_y[1:-1, :-1]
    face_north = face_y[1:-1, 1:]
    zero_plane = jnp.zeros_like(cell_perm[:, :, :1])
    face_below = jnp.concatenate([zero_plane, face_z[1:-1, 1:-1]], axis=2)
    face_above = jnp.concatenate([face_z[1:-1, 1:-1], zero_plane], axis=2)
    cell_x = glob_x[1:-1]
    cell_y = glob_y[1:-1]
    index_z = jnp.arange(count_z)
    ends_x = (cell_x == 0).astype(jnp.float32) + (cell_x == total_x - 1).astype(jnp.float32)
    ends_y = (cell_y == 0).astype(jnp.float32) + (cell_y == total_y - 1).astype(jnp.float32)
    ends_z = (index_z == 0).astype(jnp.float32) + (index_z == count_z - 1).astype(jnp.float32)
    edges = ends_x[:, None, None] + ends_y[None, :, None] + ends_z[None, None, :]
    boundary = 2.0 * cell_perm * edges
    diagonal = face_west + face_east + face_south + face_north + face_below + face_above + boundary
    cell_in = plane_in[1:-1, 1:-1]
    safe_diag = jnp.where(cell_in, diagonal, 1.0)
    return (
        face_west,
        face_east,
        face_south,
        face_north,
        face_below,
        face_above,
        boundary,
        safe_diag,
    )


def apply_fine(ext_field, faces_now):
    face_west, face_east, face_south, face_north, face_below, face_above, boundary, safe_diag = (
        faces_now
    )
    center = ext_field[1:-1, 1:-1]
    zero_plane = jnp.zeros_like(center[:, :, :1])
    below_vals = jnp.concatenate([zero_plane, center[:, :, :-1]], axis=2)
    above_vals = jnp.concatenate([center[:, :, 1:], zero_plane], axis=2)
    beside_all = face_west * ext_field[:-2, 1:-1] + face_east * ext_field[2:, 1:-1]
    beside_all = beside_all + face_south * ext_field[1:-1, :-2] + face_north * ext_field[1:-1, 2:]
    beside_all = beside_all + face_below * below_vals + face_above * above_vals
    return (center, safe_diag * center - beside_all)


def crop(array, rim):
    if rim == 0:
        return array
    return array[rim : array.shape[0] - rim, rim : array.shape[1] - rim]


def sweeps(field_ext, source_ext, faces_ext, count, width):
    def rim_of(array):
        return (array.shape[0] - width) // 2

    for sweep_index in range(count):
        out_rim = rim_of(field_ext) - 1
        faces_now = tuple(crop(member, rim_of(member) - out_rim) for member in faces_ext)
        center, product = apply_fine(field_ext, faces_now)
        source_now = crop(source_ext, rim_of(source_ext) - out_rim)
        field_ext = center + OMEGA * (source_now - product) / faces_now[7]
    return field_ext


def body(permeability, source, pressure, aggregate):
    width_x, width_y, depth_cells = permeability.shape
    slab_index = lax.axis_index("slab")
    slab_count = lax.axis_size("slab")
    row_index = lax.axis_index(("pencil", "sub"))
    row_count = lax.axis_size(("pencil", "sub"))
    total_x = width_x * slab_count
    total_y = width_y * row_count
    sides = (("slab", 0), (("pencil", "sub"), 1))
    stacked_sides = (("slab", 1), (("pencil", "sub"), 2))
    fine_rim = 2 * NU
    ext_x = padded(jnp.stack([permeability, source, pressure]), (("slab", 1),), fine_rim)
    ext_x, aggregate = lax.optimization_barrier((ext_x, aggregate))
    ext_all = padded(ext_x, ((("pencil", "sub"), 2),), fine_rim)
    perm_ext = ext_all[0]
    source_ext = crop(ext_all[1], 1)
    glob_x = slab_index * width_x - fine_rim + jnp.arange(width_x + 2 * fine_rim)
    glob_y = row_index * width_y - fine_rim + jnp.arange(width_y + 2 * fine_rim)
    inside_x = (glob_x >= 0) & (glob_x < total_x)
    inside_y = (glob_y >= 0) & (glob_y < total_y)
    faces_ext = geometry(perm_ext, glob_x, glob_y, inside_x, inside_y, total_x, total_y)
    smooth_ext = sweeps(ext_all[2], source_ext, faces_ext, NU, width_x)
    faces_zero = tuple(crop(member, fine_rim - 1) for member in faces_ext)
    smooth_rows = smooth_ext[NU : NU + width_x]
    center, product = apply_fine(crop(smooth_ext, NU - 1), faces_zero)
    residual = source - product
    half_y = width_y // 2
    half_z = depth_cells // 2

    plane_count = aggregate.shape[0]
    ext_pos = slab_index * width_x - 1 + jnp.arange(width_x + 1 + NU)
    pick_ids = ext_pos[:, None] == jnp.arange(plane_count)[None, :]
    ext_ids = jnp.sum(jnp.where(pick_ids, aggregate.astype(jnp.float32)[None, :], 0.0), axis=1)
    local_ids = ext_ids[1 : width_x + 1]
    straddles = (slab_index > 0) & (ext_ids[0] == local_ids[0])
    first_id = local_ids[0] + straddles.astype(jnp.float32)
    count_live = local_ids[-1] - first_id + 1
    slot_ids = local_ids - first_id
    has_next = ext_pos[2 : width_x + 2] < plane_count
    crossing = ((local_ids != ext_ids[2 : width_x + 2]) & has_next).astype(jnp.float32)
    face_east = faces_zero[1]
    face_north = faces_zero[3]
    face_above = faces_zero[5]
    boundary = faces_zero[6]
    index_z = np.arange(depth_cells)[:, None]
    coarse_z = np.arange(half_z)[None, :]
    pair_z = jnp.asarray((index_z // 2 == coarse_z).astype(np.float32))
    odd_z = jnp.asarray((index_z == 2 * coarse_z + 1).astype(np.float32))
    cells = width_x * width_y

    def z_sum(block_in, pick_z):
        flat = block_in.reshape(cells, depth_cells)
        return jnp.dot(flat, pick_z, precision=lax.Precision.HIGH)

    z_parts = jnp.stack(
        [
            z_sum(residual, pair_z),
            z_sum(face_east * crossing[:, None, None], pair_z),
            z_sum(face_north, pair_z),
            z_sum(face_above, odd_z),
            z_sum(boundary, pair_z),
        ]
    )
    index_y = np.arange(width_y)[:, None]
    coarse_y = np.arange(half_y)[None, :]
    pair_y = jnp.asarray((index_y // 2 == coarse_y).astype(np.float32))
    row_y = np.tile(np.arange(width_y), width_x)
    col_slot = np.repeat(np.arange(width_x + 1), half_y)
    col_y = np.tile(np.arange(half_y), width_x + 1)
    row_slot = jnp.repeat(slot_ids + 1, width_y)
    same_slot = row_slot[:, None] == jnp.asarray(col_slot.astype(np.float32))[None, :]
    pair_rows = row_y[:, None] // 2 == col_y[None, :]
    odd_rows = row_y[:, None] == 2 * col_y[None, :] + 1
    spread_map = (same_slot & pair_rows).astype(jnp.float32)
    gather_map = (same_slot.T & pair_rows.T).astype(jnp.float32)
    north_gather = (same_slot.T & odd_rows.T).astype(jnp.float32)
    paired = jnp.dot(
        gather_map,
        jnp.concatenate([z_parts[0], z_parts[1], z_parts[3], z_parts[4]], axis=1),
        precision=lax.Precision.HIGH,
    )
    north_sums = jnp.dot(north_gather, z_parts[2], precision=lax.Precision.HIGH)

    def column(index):
        return paired[:, index * half_z : (index + 1) * half_z]

    slot_sums = jnp.stack([column(0), column(1), north_sums, column(2), column(3)])
    slot_sums = slot_sums.reshape(5, width_x + 1, half_y, half_z)
    coarse = slot_sums[:, 1:]
    edge_sums = slot_sums[:, 0]
    slot_range = jnp.arange(width_x)
    last_slot = (slot_range == count_live - 1).astype(jnp.float32)
    tail_pick = (slot_range[None, :] == count_live - NCS + jnp.arange(NCS)[:, None]).astype(jnp.float32)
    tail_planes = jnp.einsum("ks,qsjl->qkjl", tail_pick, coarse, precision=lax.Precision.HIGHEST)
    head_planes = jnp.concatenate([coarse[:, :NCS], edge_sums[:, None]], axis=1)
    tail_planes, head_planes = lax.optimization_barrier((tail_planes, head_planes))
    from_prev = passed_along(tail_planes, "slab", 1)
    from_next = passed_along(head_planes, "slab", -1)
    coarse = coarse + from_next[:, NCS][:, None] * last_slot[None, :, None, None]
    prev_last = (jnp.arange(NCS) == NCS - 1).astype(jnp.float32)
    from_prev = from_prev + edge_sums[:, None] * prev_last[None, :, None, None]
    x_ext = jnp.concatenate([from_prev, coarse, jnp.zeros_like(tail_planes)], axis=1)
    wide_range = jnp.arange(width_x + 2 * NCS)[:, None]
    place = (wide_range == NCS + count_live + jnp.arange(NCS)[None, :]).astype(jnp.float32)
    x_ext = x_ext + jnp.einsum("tk,qkjl->qtjl", place, from_next[:, :NCS], precision=lax.Precision.HIGHEST)
    coarse_rim = NCS
    rim_y = NCS + 1
    coef_ext = padded(x_ext, ((("pencil", "sub"), 2),), rim_y)
    coarse_corr = jnp.zeros((width_x + 2 * NCS, half_y + 2 * rim_y, half_z), jnp.float32)
    for sweep_index in range(NCS):
        out_rim = NCS - 1 - sweep_index
        start_at = coarse_rim - out_rim
        start_y = start_at
        size_x = width_x + 2 * out_rim
        size_y = half_y + 2 * (out_rim + 1)

        def region(offset_x, offset_y):
            return coef_ext[
                :,
                start_at + offset_x : start_at + offset_x + size_x,
                start_y + offset_y : start_y + offset_y + size_y,
            ]

        here_coef = region(0, 0)
        coarse_rhs = here_coef[0]
        coarse_east = here_coef[1]
        coarse_north = here_coef[2]
        coarse_above = here_coef[3]
        coarse_bound = here_coef[4]
        coarse_west = region(-1, 0)[1]
        coarse_south = region(0, -1)[2]
        zero_plane = jnp.zeros_like(coarse_above[:, :, :1])
        coarse_below = jnp.concatenate([zero_plane, coarse_above[:, :, :-1]], axis=2)
        diag_coarse = (
            coarse_east
            + coarse_west
            + coarse_north
            + coarse_south
            + coarse_above
            + coarse_below
            + coarse_bound
        )
        safe_coarse = jnp.where(diag_coarse > 0, diag_coarse, 1.0)
        coarse_center = coarse_corr[1:-1, 1:-1]
        above_vals = jnp.concatenate([coarse_center[:, :, 1:], zero_plane], axis=2)
        below_vals = jnp.concatenate([zero_plane, coarse_center[:, :, :-1]], axis=2)
        beside_all = coarse_east * coarse_corr[2:, 1:-1] + coarse_west * coarse_corr[:-2, 1:-1]
        beside_all = (
            beside_all
            + coarse_north * coarse_corr[1:-1, 2:]
            + coarse_south * coarse_corr[1:-1, :-2]
        )
        beside_all = beside_all + coarse_above * above_vals + coarse_below * below_vals
        coarse_corr = (
            coarse_center
            + OMEGA * (coarse_rhs - (diag_coarse * coarse_center - beside_all)) / safe_coarse
        )
    last_corr = jnp.sum(last_slot[:, None, None] * coarse_corr, axis=0)
    corr_wide = jnp.concatenate([jnp.zeros_like(last_corr)[None], coarse_corr], axis=0)
    corr_core = corr_wide[:, 1 : 1 + half_y]
    corr_z = jnp.dot(
        corr_core.reshape((width_x + 1) * half_y, half_z), pair_z.T, precision=lax.Precision.HIGH
    )
    correction = jnp.dot(spread_map, corr_z, precision=lax.Precision.HIGH)
    correction = correction.reshape(width_x, width_y, depth_cells)
    owner_rows = (slot_ids[:, None] + 1 == jnp.arange(width_x + 1)[None, :]).astype(jnp.float32)

    def rim_rows(coarse_row):
        row_z = jnp.dot(corr_wide[:, coarse_row], pair_z.T, precision=lax.Precision.HIGH)
        row_fine = jnp.dot(owner_rows, row_z, precision=lax.Precision.HIGH)
        return jnp.broadcast_to(row_fine[:, None], (width_x, NU, depth_cells))

    correction = jnp.concatenate([rim_rows(0), correction, rim_rows(half_y + 1)], axis=1)
    base = smooth_rows + correction
    last_z = jnp.dot(last_corr, pair_z.T, precision=lax.Precision.HIGH)
    fine_y = np.arange(width_y + 2 * NU) - NU
    rows_ext = jnp.asarray((fine_y[:, None] // 2 + 1 == np.arange(half_y + 2)[None, :]).astype(np.float32))
    last_fine = jnp.dot(rows_ext, last_z, precision=lax.Precision.HIGH)
    up_block = jnp.concatenate([base[width_x - NU :], last_fine[None]], axis=0)
    below_prev = passed_along(up_block, "slab", 1)
    above_next = passed_along(base[:NU], "slab", -1)
    from_owner = (slot_ids == -1).astype(jnp.float32)
    own = base + from_owner[:, None, None] * below_prev[NU][None]
    next_ids = ext_ids[width_x + 1 :]
    next_in = ext_pos[width_x + 1 :] < plane_count
    to_owner = ((next_ids == local_ids[-1]) & next_in).astype(jnp.float32)
    high_halo = above_next + to_owner[:, None, None] * last_fine[None]
    post_ext = jnp.concatenate([below_prev[:NU], own, high_halo], axis=0)
    return sweeps(post_ext, source_ext, faces_ext, NU, width_x)


def solution(mesh):
    in_specs = (
        P(("real", "slab"), ("pencil", "sub"), None),
        P(("real", "slab"), ("pencil", "sub"), None),
        P(("real", "slab"), ("pencil", "sub"), None),
        P("real"),
    )
    out_specs = P(("real", "slab"), ("pencil", "sub"), None)
    return jax.shard_map(body, mesh=mesh, in_specs=in_specs, out_specs=out_specs, check_vma=False)
```

```python
import numpy as np
import jax
import jax.numpy as jnp
from jax import lax
from jax.sharding import PartitionSpec as P

NU = 2
NCS = 4


OMEGA = 0.8


def padded(array, sides, width):
    for axis, dim in sides:
        count, length = (lax.axis_size(axis), array.shape[dim])
        up = [(i, (i + 1) % count) for i in range(count - 1)]
        down = [(j, i) for i, j in up]
        last = lax.slice_in_dim(array, length - width, length, axis=dim)
        leading = lax.slice_in_dim(array, 0, width, axis=dim)
        before = lax.ppermute(last, axis, up)
        after = lax.ppermute(leading, axis, down)
        array = jnp.concatenate([before, array, after], axis=dim)
    return array


def passed_along(array, axis, by):
    count = lax.axis_size(axis)
    pairs = [(i, i + by) for i in range(count) if 0 <= i + by < count]
    return lax.ppermute(array, axis, pairs)


def harmonic(lower_k, upper_k, inside):
    denom_sum = jnp.where(inside, lower_k + upper_k, 1.0)
    return jnp.where(inside, 2.0 * lower_k * upper_k / denom_sum, 0.0)


def geometry(perm_ext, glob_x, glob_y, inside_x, inside_y, total_x, total_y):
    count_z = perm_ext.shape[2]
    both_x = (inside_x[:-1] & inside_x[1:])[:, None, None] & inside_y[None, :, None]
    both_y = (inside_y[:-1] & inside_y[1:])[None, :, None] & inside_x[:, None, None]
    plane_in = inside_x[:, None, None] & inside_y[None, :, None]
    face_x = harmonic(perm_ext[:-1], perm_ext[1:], both_x)
    face_y = harmonic(perm_ext[:, :-1], perm_ext[:, 1:], both_y)
    face_z = harmonic(perm_ext[:, :, :-1], perm_ext[:, :, 1:], plane_in)
    cell_perm = perm_ext[1:-1, 1:-1]
    face_west = face_x[:-1, 1:-1]
    face_east = face_x[1:, 1:-1]
    face_south = face_y[1:-1, :-1]
    face_north = face_y[1:-1, 1:]
    zero_plane = jnp.zeros_like(cell_perm[:, :, :1])
    face_below = jnp.concatenate([zero_plane, face_z[1:-1, 1:-1]], axis=2)
    face_above = jnp.concatenate([face_z[1:-1, 1:-1], zero_plane], axis=2)
    cell_x = glob_x[1:-1]
    cell_y = glob_y[1:-1]
    index_z = jnp.arange(count_z)
    ends_x = (cell_x == 0).astype(jnp.float32) + (cell_x == total_x - 1).astype(jnp.float32)
    ends_y = (cell_y == 0).astype(jnp.float32) + (cell_y == total_y - 1).astype(jnp.float32)
    ends_z = (index_z == 0).astype(jnp.float32) + (index_z == count_z - 1).astype(jnp.float32)
    edges = ends_x[:, None, None] + ends_y[None, :, None] + ends_z[None, None, :]
    boundary = 2.0 * cell_perm * edges
    diagonal = face_west + face_east + face_south + face_north + face_below + face_above + boundary
    cell_in = plane_in[1:-1, 1:-1]
    safe_diag = jnp.where(cell_in, diagonal, 1.0)
    return (
        face_west,
        face_east,
        face_south,
        face_north,
        face_below,
        face_above,
        boundary,
        safe_diag,
    )


def apply_fine(ext_field, faces_now):
    face_west, face_east, face_south, face_north, face_below, face_above, boundary, safe_diag = (
        faces_now
    )
    center = ext_field[1:-1, 1:-1]
    zero_plane = jnp.zeros_like(center[:, :, :1])
    below_vals = jnp.concatenate([zero_plane, center[:, :, :-1]], axis=2)
    above_vals = jnp.concatenate([center[:, :, 1:], zero_plane], axis=2)
    beside_all = face_west * ext_field[:-2, 1:-1] + face_east * ext_field[2:, 1:-1]
    beside_all = beside_all + face_south * ext_field[1:-1, :-2] + face_north * ext_field[1:-1, 2:]
    beside_all = beside_all + face_below * below_vals + face_above * above_vals
    return (center, safe_diag * center - beside_all)


def crop(array, rim):
    if rim == 0:
        return array
    return array[rim : array.shape[0] - rim, rim : array.shape[1] - rim]


def sweeps(field_ext, source_ext, faces_ext, count, width):
    def rim_of(array):
        return (array.shape[0] - width) // 2

    for sweep_index in range(count):
        out_rim = rim_of(field_ext) - 1
        faces_now = tuple(crop(member, rim_of(member) - out_rim) for member in faces_ext)
        center, product = apply_fine(field_ext, faces_now)
        source_now = crop(source_ext, rim_of(source_ext) - out_rim)
        field_ext = center + OMEGA * (source_now - product) / faces_now[7]
    return field_ext


def body(permeability, source, pressure, aggregate):
    width_x, width_y, depth_cells = permeability.shape
    slab_index = lax.axis_index("slab")
    slab_count = lax.axis_size("slab")
    row_index = lax.axis_index(("pencil", "sub"))
    row_count = lax.axis_size(("pencil", "sub"))
    total_x = width_x * slab_count
    total_y = width_y * row_count
    sides = (("slab", 0), (("pencil", "sub"), 1))
    stacked_sides = (("slab", 1), (("pencil", "sub"), 2))
    fine_rim = 2 * NU
    ext_x = padded(jnp.stack([permeability, source, pressure]), (("slab", 1),), fine_rim)
    ext_x, aggregate = lax.optimization_barrier((ext_x, aggregate))
    ext_all = padded(ext_x, ((("pencil", "sub"), 2),), fine_rim)
    perm_ext = ext_all[0]
    source_ext = crop(ext_all[1], 1)
    glob_x = slab_index * width_x - fine_rim + jnp.arange(width_x + 2 * fine_rim)
    glob_y = row_index * width_y - fine_rim + jnp.arange(width_y + 2 * fine_rim)
    inside_x = (glob_x >= 0) & (glob_x < total_x)
    inside_y = (glob_y >= 0) & (glob_y < total_y)
    faces_ext = geometry(perm_ext, glob_x, glob_y, inside_x, inside_y, total_x, total_y)
    smooth_ext = sweeps(ext_all[2], source_ext, faces_ext, NU, width_x)
    faces_zero = tuple(crop(member, fine_rim - 1) for member in faces_ext)
    smooth_rows = smooth_ext[NU : NU + width_x]
    center, product = apply_fine(crop(smooth_ext, NU - 1), faces_zero)
    residual = source - product
    half_y = width_y // 2
    half_z = depth_cells // 2

    plane_count = aggregate.shape[0]
    ext_pos = slab_index * width_x - 1 + jnp.arange(width_x + 1 + NU)
    pick_ids = ext_pos[:, None] == jnp.arange(plane_count)[None, :]
    ext_ids = jnp.sum(jnp.where(pick_ids, aggregate.astype(jnp.float32)[None, :], 0.0), axis=1)
    local_ids = ext_ids[1 : width_x + 1]
    straddles = (slab_index > 0) & (ext_ids[0] == local_ids[0])
    first_id = local_ids[0] + straddles.astype(jnp.float32)
    count_live = local_ids[-1] - first_id + 1
    slot_ids = local_ids - first_id
    has_next = ext_pos[2 : width_x + 2] < plane_count
    crossing = ((local_ids != ext_ids[2 : width_x + 2]) & has_next).astype(jnp.float32)
    face_east = faces_zero[1]
    face_north = faces_zero[3]
    face_above = faces_zero[5]
    boundary = faces_zero[6]
    index_z = np.arange(depth_cells)[:, None]
    coarse_z = np.arange(half_z)[None, :]
    pair_z = jnp.asarray((index_z // 2 == coarse_z).astype(np.float32))
    odd_z = jnp.asarray((index_z == 2 * coarse_z + 1).astype(np.float32))
    cells = width_x * width_y

    def z_sum(block_in, pick_z):
        flat = block_in.reshape(cells, depth_cells)
        return jnp.dot(flat, pick_z, precision=lax.Precision.HIGH)

    z_parts = jnp.stack(
        [
            z_sum(residual, pair_z),
            z_sum(face_east * crossing[:, None, None], pair_z),
            z_sum(face_north, pair_z),
            z_sum(face_above, odd_z),
            z_sum(boundary, pair_z),
        ]
    )
    index_y = np.arange(width_y)[:, None]
    coarse_y = np.arange(half_y)[None, :]
    pair_y = jnp.asarray((index_y // 2 == coarse_y).astype(np.float32))
    row_y = np.tile(np.arange(width_y), width_x)
    col_slot = np.repeat(np.arange(width_x + 1), half_y)
    col_y = np.tile(np.arange(half_y), width_x + 1)
    row_slot = jnp.repeat(slot_ids + 1, width_y)
    same_slot = row_slot[:, None] == jnp.asarray(col_slot.astype(np.float32))[None, :]
    pair_rows = row_y[:, None] // 2 == col_y[None, :]
    odd_rows = row_y[:, None] == 2 * col_y[None, :] + 1
    spread_map = (same_slot & pair_rows).astype(jnp.float32)
    gather_map = (same_slot.T & pair_rows.T).astype(jnp.float32)
    north_gather = (same_slot.T & odd_rows.T).astype(jnp.float32)
    paired = jnp.dot(
        gather_map,
        jnp.concatenate([z_parts[0], z_parts[1], z_parts[3], z_parts[4]], axis=1),
        precision=lax.Precision.HIGH,
    )
    north_sums = jnp.dot(north_gather, z_parts[2], precision=lax.Precision.HIGH)

    def column(index):
        return paired[:, index * half_z : (index + 1) * half_z]

    slot_sums = jnp.stack([column(0), column(1), north_sums, column(2), column(3)])
    slot_sums = slot_sums.reshape(5, width_x + 1, half_y, half_z)
    coarse = slot_sums[:, 1:]
    edge_sums = slot_sums[:, 0]
    slot_range = jnp.arange(width_x)
    last_slot = (slot_range == count_live - 1).astype(jnp.float32)
    tail_pick = (slot_range[None, :] == count_live - NCS + jnp.arange(NCS)[:, None]).astype(jnp.float32)
    tail_planes = jnp.einsum("ks,qsjl->qkjl", tail_pick, coarse, precision=lax.Precision.HIGH)
    head_planes = jnp.concatenate([coarse[:, :NCS], edge_sums[:, None]], axis=1)
    tail_planes, head_planes = lax.optimization_barrier((tail_planes, head_planes))
    from_prev = passed_along(tail_planes, "slab", 1)
    from_next = passed_along(head_planes, "slab", -1)
    coarse = coarse + from_next[:, NCS][:, None] * last_slot[None, :, None, None]
    prev_last = (jnp.arange(NCS) == NCS - 1).astype(jnp.float32)
    from_prev = from_prev + edge_sums[:, None] * prev_last[None, :, None, None]
    x_ext = jnp.concatenate([from_prev, coarse, jnp.zeros_like(tail_planes)], axis=1)
    wide_range = jnp.arange(width_x + 2 * NCS)[:, None]
    place = (wide_range == NCS + count_live + jnp.arange(NCS)[None, :]).astype(jnp.float32)
    x_ext = x_ext + jnp.einsum("tk,qkjl->qtjl", place, from_next[:, :NCS], precision=lax.Precision.HIGH)
    coarse_rim = NCS
    rim_y = NCS + 1
    coef_ext = padded(x_ext, ((("pencil", "sub"), 2),), rim_y)
    coarse_corr = jnp.zeros((width_x + 2 * NCS, half_y + 2 * rim_y, half_z), jnp.float32)
    for sweep_index in range(NCS):
        out_rim = NCS - 1 - sweep_index
        start_at = coarse_rim - out_rim
        start_y = start_at
        size_x = width_x + 2 * out_rim
        size_y = half_y + 2 * (out_rim + 1)

        def region(offset_x, offset_y):
            return coef_ext[
                :,
                start_at + offset_x : start_at + offset_x + size_x,
                start_y + offset_y : start_y + offset_y + size_y,
            ]

        here_coef = region(0, 0)
        coarse_rhs = here_coef[0]
        coarse_east = here_coef[1]
        coarse_north = here_coef[2]
        coarse_above = here_coef[3]
        coarse_bound = here_coef[4]
        coarse_west = region(-1, 0)[1]
        coarse_south = region(0, -1)[2]
        zero_plane = jnp.zeros_like(coarse_above[:, :, :1])
        coarse_below = jnp.concatenate([zero_plane, coarse_above[:, :, :-1]], axis=2)
        diag_coarse = (
            coarse_east
            + coarse_west
            + coarse_north
            + coarse_south
            + coarse_above
            + coarse_below
            + coarse_bound
        )
        safe_coarse = jnp.where(diag_coarse > 0, diag_coarse, 1.0)
        coarse_center = coarse_corr[1:-1, 1:-1]
        above_vals = jnp.concatenate([coarse_center[:, :, 1:], zero_plane], axis=2)
        below_vals = jnp.concatenate([zero_plane, coarse_center[:, :, :-1]], axis=2)
        beside_all = coarse_east * coarse_corr[2:, 1:-1] + coarse_west * coarse_corr[:-2, 1:-1]
        beside_all = (
            beside_all
            + coarse_north * coarse_corr[1:-1, 2:]
            + coarse_south * coarse_corr[1:-1, :-2]
        )
        beside_all = beside_all + coarse_above * above_vals + coarse_below * below_vals
        coarse_corr = (
            coarse_center
            + OMEGA * (coarse_rhs - (diag_coarse * coarse_center - beside_all)) / safe_coarse
        )
    last_corr = jnp.sum(last_slot[:, None, None] * coarse_corr, axis=0)
    corr_wide = jnp.concatenate([jnp.zeros_like(last_corr)[None], coarse_corr], axis=0)
    corr_core = corr_wide[:, 1 : 1 + half_y]
    corr_z = jnp.dot(
        corr_core.reshape((width_x + 1) * half_y, half_z), pair_z.T, precision=lax.Precision.HIGH
    )
    correction = jnp.dot(spread_map, corr_z, precision=lax.Precision.HIGH)
    correction = correction.reshape(width_x, width_y, depth_cells)
    owner_rows = (slot_ids[:, None] + 1 == jnp.arange(width_x + 1)[None, :]).astype(jnp.float32)

    def rim_rows(coarse_row):
        row_z = jnp.dot(corr_wide[:, coarse_row], pair_z.T, precision=lax.Precision.HIGH)
        row_fine = jnp.dot(owner_rows, row_z, precision=lax.Precision.HIGH)
        return jnp.broadcast_to(row_fine[:, None], (width_x, NU, depth_cells))

    correction = jnp.concatenate([rim_rows(0), correction, rim_rows(half_y + 1)], axis=1)
    base = smooth_rows + correction
    last_z = jnp.dot(last_corr, pair_z.T, precision=lax.Precision.HIGH)
    fine_y = np.arange(width_y + 2 * NU) - NU
    rows_ext = jnp.asarray((fine_y[:, None] // 2 + 1 == np.arange(half_y + 2)[None, :]).astype(np.float32))
    last_fine = jnp.dot(rows_ext, last_z, precision=lax.Precision.HIGH)
    up_block = jnp.concatenate([base[width_x - NU :], last_fine[None]], axis=0)
    below_prev = passed_along(up_block, "slab", 1)
    above_next = passed_along(base[:NU], "slab", -1)
    from_owner = (slot_ids == -1).astype(jnp.float32)
    own = base + from_owner[:, None, None] * below_prev[NU][None]
    next_ids = ext_ids[width_x + 1 :]
    next_in = ext_pos[width_x + 1 :] < plane_count
    to_owner = ((next_ids == local_ids[-1]) & next_in).astype(jnp.float32)
    high_halo = above_next + to_owner[:, None, None] * last_fine[None]
    post_ext = jnp.concatenate([below_prev[:NU], own, high_halo], axis=0)
    return sweeps(post_ext, source_ext, faces_ext, NU, width_x)


def solution(mesh):
    in_specs = (
        P(("real", "slab"), ("pencil", "sub"), None),
        P(("real", "slab"), ("pencil", "sub"), None),
        P(("real", "slab"), ("pencil", "sub"), None),
        P("real"),
    )
    out_specs = P(("real", "slab"), ("pencil", "sub"), None)
    return jax.shard_map(body, mesh=mesh, in_specs=in_specs, out_specs=out_specs, check_vma=False)
```

```python
import numpy as np
import jax
import jax.numpy as jnp
from jax import lax
from jax.sharding import PartitionSpec as P

NU = 2
NCS = 4


OMEGA = 0.8


def padded(array, sides, width):
    for axis, dim in sides:
        count, length = (lax.axis_size(axis), array.shape[dim])
        up = [(i, (i + 1) % count) for i in range(count - 1)]
        down = [(j, i) for i, j in up]
        last = lax.slice_in_dim(array, length - width, length, axis=dim)
        leading = lax.slice_in_dim(array, 0, width, axis=dim)
        before = lax.ppermute(last, axis, up)
        after = lax.ppermute(leading, axis, down)
        array = jnp.concatenate([before, array, after], axis=dim)
    return array


def passed_along(array, axis, by):
    count = lax.axis_size(axis)
    pairs = [(i, i + by) for i in range(count) if 0 <= i + by < count]
    return lax.ppermute(array, axis, pairs)


def harmonic(lower_k, upper_k, inside):
    denom_sum = jnp.where(inside, lower_k + upper_k, 1.0)
    return jnp.where(inside, 2.0 * lower_k * upper_k / denom_sum, 0.0)


def geometry(perm_ext, glob_x, glob_y, inside_x, inside_y, total_x, total_y):
    count_z = perm_ext.shape[2]
    both_x = (inside_x[:-1] & inside_x[1:])[:, None, None] & inside_y[None, :, None]
    both_y = (inside_y[:-1] & inside_y[1:])[None, :, None] & inside_x[:, None, None]
    plane_in = inside_x[:, None, None] & inside_y[None, :, None]
    face_x = harmonic(perm_ext[:-1], perm_ext[1:], both_x)
    face_y = harmonic(perm_ext[:, :-1], perm_ext[:, 1:], both_y)
    face_z = harmonic(perm_ext[:, :, :-1], perm_ext[:, :, 1:], plane_in)
    cell_perm = perm_ext[1:-1, 1:-1]
    face_west = face_x[:-1, 1:-1]
    face_east = face_x[1:, 1:-1]
    face_south = face_y[1:-1, :-1]
    face_north = face_y[1:-1, 1:]
    zero_plane = jnp.zeros_like(cell_perm[:, :, :1])
    face_below = jnp.concatenate([zero_plane, face_z[1:-1, 1:-1]], axis=2)
    face_above = jnp.concatenate([face_z[1:-1, 1:-1], zero_plane], axis=2)
    cell_x = glob_x[1:-1]
    cell_y = glob_y[1:-1]
    index_z = jnp.arange(count_z)
    ends_x = (cell_x == 0).astype(jnp.float32) + (cell_x == total_x - 1).astype(jnp.float32)
    ends_y = (cell_y == 0).astype(jnp.float32) + (cell_y == total_y - 1).astype(jnp.float32)
    ends_z = (index_z == 0).astype(jnp.float32) + (index_z == count_z - 1).astype(jnp.float32)
    edges = ends_x[:, None, None] + ends_y[None, :, None] + ends_z[None, None, :]
    boundary = 2.0 * cell_perm * edges
    diagonal = face_west + face_east + face_south + face_north + face_below + face_above + boundary
    cell_in = plane_in[1:-1, 1:-1]
    safe_diag = jnp.where(cell_in, diagonal, 1.0)
    return (
        face_west,
        face_east,
        face_south,
        face_north,
        face_below,
        face_above,
        boundary,
        safe_diag,
    )


def apply_fine(ext_field, faces_now):
    face_west, face_east, face_south, face_north, face_below, face_above, boundary, safe_diag = (
        faces_now
    )
    center = ext_field[1:-1, 1:-1]
    zero_plane = jnp.zeros_like(center[:, :, :1])
    below_vals = jnp.concatenate([zero_plane, center[:, :, :-1]], axis=2)
    above_vals = jnp.concatenate([center[:, :, 1:], zero_plane], axis=2)
    beside_all = face_west * ext_field[:-2, 1:-1] + face_east * ext_field[2:, 1:-1]
    beside_all = beside_all + face_south * ext_field[1:-1, :-2] + face_north * ext_field[1:-1, 2:]
    beside_all = beside_all + face_below * below_vals + face_above * above_vals
    return (center, safe_diag * center - beside_all)


def crop(array, rim, rim_y=None):
    rim_y = rim if rim_y is None else rim_y
    return array[rim : array.shape[0] - rim, rim_y : array.shape[1] - rim_y]


def sweeps(field_ext, source_ext, faces_ext, count, width):
    def rims(array):
        return (array.shape[0] - width) // 2, (array.shape[1] - width) // 2

    def cut(array, out_x, out_y):
        rim_x, rim_y = rims(array)
        return crop(array, rim_x - out_x, rim_y - out_y)

    for sweep_index in range(count):
        out_x, out_y = (rim - 1 for rim in rims(field_ext))
        faces_now = tuple(cut(member, out_x, out_y) for member in faces_ext)
        center, product = apply_fine(field_ext, faces_now)
        source_now = cut(source_ext, out_x, out_y)
        field_ext = center + OMEGA * (source_now - product) / faces_now[7]
    return field_ext


def body(permeability, source, pressure, aggregate):
    width_x, width_y, depth_cells = permeability.shape
    slab_index = lax.axis_index("slab")
    slab_count = lax.axis_size("slab")
    row_index = lax.axis_index(("pencil", "sub"))
    row_count = lax.axis_size(("pencil", "sub"))
    total_x = width_x * slab_count
    total_y = width_y * row_count
    sides = (("slab", 0), (("pencil", "sub"), 1))
    stacked_sides = (("slab", 1), (("pencil", "sub"), 2))
    fine_rim = 2 * NU
    rim_x = NU + 1
    ext_x = padded(jnp.stack([permeability, source, pressure]), (("slab", 1),), rim_x)
    ext_x, aggregate = lax.optimization_barrier((ext_x, aggregate))
    ext_all = padded(ext_x, ((("pencil", "sub"), 2),), fine_rim)
    perm_ext = ext_all[0]
    source_ext = crop(ext_all[1], 1)
    glob_x = slab_index * width_x - rim_x + jnp.arange(width_x + 2 * rim_x)
    glob_y = row_index * width_y - fine_rim + jnp.arange(width_y + 2 * fine_rim)
    inside_x = (glob_x >= 0) & (glob_x < total_x)
    inside_y = (glob_y >= 0) & (glob_y < total_y)
    faces_ext = geometry(perm_ext, glob_x, glob_y, inside_x, inside_y, total_x, total_y)
    smooth_ext = sweeps(ext_all[2], source_ext, faces_ext, NU, width_x)
    faces_zero = tuple(crop(member, rim_x - 1, fine_rim - 1) for member in faces_ext)
    smooth_rows = smooth_ext[1 : 1 + width_x]
    center, product = apply_fine(crop(smooth_ext, 0, NU - 1), faces_zero)
    residual = source - product
    half_y = width_y // 2
    half_z = depth_cells // 2

    plane_count = aggregate.shape[0]
    ext_pos = slab_index * width_x - 1 + jnp.arange(width_x + 1 + NU)
    pick_ids = ext_pos[:, None] == jnp.arange(plane_count)[None, :]
    ext_ids = jnp.sum(jnp.where(pick_ids, aggregate.astype(jnp.float32)[None, :], 0.0), axis=1)
    local_ids = ext_ids[1 : width_x + 1]
    straddles = (slab_index > 0) & (ext_ids[0] == local_ids[0])
    first_id = local_ids[0] + straddles.astype(jnp.float32)
    count_live = local_ids[-1] - first_id + 1
    slot_ids = local_ids - first_id
    has_next = ext_pos[2 : width_x + 2] < plane_count
    crossing = ((local_ids != ext_ids[2 : width_x + 2]) & has_next).astype(jnp.float32)
    face_east = faces_zero[1]
    face_north = faces_zero[3]
    face_above = faces_zero[5]
    boundary = faces_zero[6]
    index_z = np.arange(depth_cells)[:, None]
    coarse_z = np.arange(half_z)[None, :]
    pair_z = jnp.asarray((index_z // 2 == coarse_z).astype(np.float32))
    odd_z = jnp.asarray((index_z == 2 * coarse_z + 1).astype(np.float32))
    cells = width_x * width_y

    def z_sum(block_in, pick_z):
        flat = block_in.reshape(cells, depth_cells)
        return jnp.dot(flat, pick_z, precision=lax.Precision.HIGH)

    z_parts = jnp.stack(
        [
            z_sum(residual, pair_z),
            z_sum(face_east * crossing[:, None, None], pair_z),
            z_sum(face_north, pair_z),
            z_sum(face_above, odd_z),
            z_sum(boundary, pair_z),
        ]
    )
    index_y = np.arange(width_y)[:, None]
    coarse_y = np.arange(half_y)[None, :]
    pair_y = jnp.asarray((index_y // 2 == coarse_y).astype(np.float32))
    row_y = np.tile(np.arange(width_y), width_x)
    col_slot = np.repeat(np.arange(width_x + 1), half_y)
    col_y = np.tile(np.arange(half_y), width_x + 1)
    row_slot = jnp.repeat(slot_ids + 1, width_y)
    same_slot = row_slot[:, None] == jnp.asarray(col_slot.astype(np.float32))[None, :]
    pair_rows = row_y[:, None] // 2 == col_y[None, :]
    odd_rows = row_y[:, None] == 2 * col_y[None, :] + 1
    spread_map = (same_slot & pair_rows).astype(jnp.float32)
    gather_map = (same_slot.T & pair_rows.T).astype(jnp.float32)
    north_gather = (same_slot.T & odd_rows.T).astype(jnp.float32)
    paired = jnp.dot(
        gather_map,
        jnp.concatenate([z_parts[0], z_parts[1], z_parts[3], z_parts[4]], axis=1),
        precision=lax.Precision.HIGH,
    )
    north_sums = jnp.dot(north_gather, z_parts[2], precision=lax.Precision.HIGH)

    def column(index):
        return paired[:, index * half_z : (index + 1) * half_z]

    slot_sums = jnp.stack([column(0), column(1), north_sums, column(2), column(3)])
    slot_sums = slot_sums.reshape(5, width_x + 1, half_y, half_z)
    coarse = slot_sums[:, 1:]
    edge_sums = slot_sums[:, 0]
    slot_range = jnp.arange(width_x)
    last_slot = (slot_range == count_live - 1).astype(jnp.float32)
    tail_pick = (slot_range[None, :] == count_live - NCS + jnp.arange(NCS)[:, None]).astype(jnp.float32)
    tail_planes = jnp.einsum("ks,qsjl->qkjl", tail_pick, coarse, precision=lax.Precision.HIGH)
    head_planes = jnp.concatenate([coarse[:, :NCS], edge_sums[:, None]], axis=1)
    tail_planes, head_planes = lax.optimization_barrier((tail_planes, head_planes))
    from_prev = passed_along(tail_planes, "slab", 1)
    from_next = passed_along(head_planes, "slab", -1)
    coarse = coarse + from_next[:, NCS][:, None] * last_slot[None, :, None, None]
    prev_last = (jnp.arange(NCS) == NCS - 1).astype(jnp.float32)
    from_prev = from_prev + edge_sums[:, None] * prev_last[None, :, None, None]
    x_ext = jnp.concatenate([from_prev, coarse, jnp.zeros_like(tail_planes)], axis=1)
    wide_range = jnp.arange(width_x + 2 * NCS)[:, None]
    place = (wide_range == NCS + count_live + jnp.arange(NCS)[None, :]).astype(jnp.float32)
    x_ext = x_ext + jnp.einsum("tk,qkjl->qtjl", place, from_next[:, :NCS], precision=lax.Precision.HIGH)
    coarse_rim = NCS
    rim_y = NCS + 1
    coef_ext = padded(x_ext, ((("pencil", "sub"), 2),), rim_y)
    coarse_corr = jnp.zeros((width_x + 2 * NCS, half_y + 2 * rim_y, half_z), jnp.float32)
    for sweep_index in range(NCS):
        out_rim = NCS - 1 - sweep_index
        start_at = coarse_rim - out_rim
        start_y = start_at
        size_x = width_x + 2 * out_rim
        size_y = half_y + 2 * (out_rim + 1)

        def region(offset_x, offset_y):
            return coef_ext[
                :,
                start_at + offset_x : start_at + offset_x + size_x,
                start_y + offset_y : start_y + offset_y + size_y,
            ]

        here_coef = region(0, 0)
        coarse_rhs = here_coef[0]
        coarse_east = here_coef[1]
        coarse_north = here_coef[2]
        coarse_above = here_coef[3]
        coarse_bound = here_coef[4]
        coarse_west = region(-1, 0)[1]
        coarse_south = region(0, -1)[2]
        zero_plane = jnp.zeros_like(coarse_above[:, :, :1])
        coarse_below = jnp.concatenate([zero_plane, coarse_above[:, :, :-1]], axis=2)
        diag_coarse = (
            coarse_east
            + coarse_west
            + coarse_north
            + coarse_south
            + coarse_above
            + coarse_below
            + coarse_bound
        )
        safe_coarse = jnp.where(diag_coarse > 0, diag_coarse, 1.0)
        coarse_center = coarse_corr[1:-1, 1:-1]
        above_vals = jnp.concatenate([coarse_center[:, :, 1:], zero_plane], axis=2)
        below_vals = jnp.concatenate([zero_plane, coarse_center[:, :, :-1]], axis=2)
        beside_all = coarse_east * coarse_corr[2:, 1:-1] + coarse_west * coarse_corr[:-2, 1:-1]
        beside_all = (
            beside_all
            + coarse_north * coarse_corr[1:-1, 2:]
            + coarse_south * coarse_corr[1:-1, :-2]
        )
        beside_all = beside_all + coarse_above * above_vals + coarse_below * below_vals
        coarse_corr = (
            coarse_center
            + OMEGA * (coarse_rhs - (diag_coarse * coarse_center - beside_all)) / safe_coarse
        )
    last_corr = jnp.sum(last_slot[:, None, None] * coarse_corr, axis=0)
    corr_wide = jnp.concatenate([jnp.zeros_like(last_corr)[None], coarse_corr], axis=0)
    corr_core = corr_wide[:, 1 : 1 + half_y]
    corr_z = jnp.dot(
        corr_core.reshape((width_x + 1) * half_y, half_z), pair_z.T, precision=lax.Precision.HIGH
    )
    correction = jnp.dot(spread_map, corr_z, precision=lax.Precision.HIGH)
    correction = correction.reshape(width_x, width_y, depth_cells)
    owner_rows = (slot_ids[:, None] + 1 == jnp.arange(width_x + 1)[None, :]).astype(jnp.float32)

    def rim_rows(coarse_row):
        row_z = jnp.dot(corr_wide[:, coarse_row], pair_z.T, precision=lax.Precision.HIGH)
        row_fine = jnp.dot(owner_rows, row_z, precision=lax.Precision.HIGH)
        return jnp.broadcast_to(row_fine[:, None], (width_x, NU, depth_cells))

    correction = jnp.concatenate([rim_rows(0), correction, rim_rows(half_y + 1)], axis=1)
    base = smooth_rows + correction
    last_z = jnp.dot(last_corr, pair_z.T, precision=lax.Precision.HIGH)
    fine_y = np.arange(width_y + 2 * NU) - NU
    rows_ext = jnp.asarray((fine_y[:, None] // 2 + 1 == np.arange(half_y + 2)[None, :]).astype(np.float32))
    last_fine = jnp.dot(rows_ext, last_z, precision=lax.Precision.HIGH)
    up_block = jnp.concatenate([base[width_x - NU :], last_fine[None]], axis=0)
    below_prev = passed_along(up_block, "slab", 1)
    above_next = passed_along(base[:NU], "slab", -1)
    from_owner = (slot_ids == -1).astype(jnp.float32)
    own = base + from_owner[:, None, None] * below_prev[NU][None]
    next_ids = ext_ids[width_x + 1 :]
    next_in = ext_pos[width_x + 1 :] < plane_count
    to_owner = ((next_ids == local_ids[-1]) & next_in).astype(jnp.float32)
    high_halo = above_next + to_owner[:, None, None] * last_fine[None]
    post_ext = jnp.concatenate([below_prev[:NU], own, high_halo], axis=0)
    return sweeps(post_ext, source_ext, faces_ext, NU, width_x)


def solution(mesh):
    in_specs = (
        P(("real", "slab"), ("pencil", "sub"), None),
        P(("real", "slab"), ("pencil", "sub"), None),
        P(("real", "slab"), ("pencil", "sub"), None),
        P("real"),
    )
    out_specs = P(("real", "slab"), ("pencil", "sub"), None)
    return jax.shard_map(body, mesh=mesh, in_specs=in_specs, out_specs=out_specs, check_vma=False)
```

```python
import numpy as np
import jax
import jax.numpy as jnp
from jax import lax
from jax.sharding import PartitionSpec as P

NU = 2
NCS = 4


OMEGA = 0.8


def padded(array, sides, width):
    for axis, dim in sides:
        count, length = (lax.axis_size(axis), array.shape[dim])
        up = [(i, (i + 1) % count) for i in range(count - 1)]
        down = [(j, i) for i, j in up]
        last = lax.slice_in_dim(array, length - width, length, axis=dim)
        leading = lax.slice_in_dim(array, 0, width, axis=dim)
        before = lax.ppermute(last, axis, up)
        after = lax.ppermute(leading, axis, down)
        array = jnp.concatenate([before, array, after], axis=dim)
    return array


def passed_along(array, axis, by):
    count = lax.axis_size(axis)
    pairs = [(i, i + by) for i in range(count) if 0 <= i + by < count]
    return lax.ppermute(array, axis, pairs)


def harmonic(lower_k, upper_k, inside):
    denom_sum = jnp.where(inside, lower_k + upper_k, 1.0)
    return jnp.where(inside, 2.0 * lower_k * upper_k / denom_sum, 0.0)


def geometry(perm_ext, glob_x, glob_y, inside_x, inside_y, total_x, total_y):
    count_z = perm_ext.shape[2]
    both_x = (inside_x[:-1] & inside_x[1:])[:, None, None] & inside_y[None, :, None]
    both_y = (inside_y[:-1] & inside_y[1:])[None, :, None] & inside_x[:, None, None]
    plane_in = inside_x[:, None, None] & inside_y[None, :, None]
    face_x = harmonic(perm_ext[:-1], perm_ext[1:], both_x)
    face_y = harmonic(perm_ext[:, :-1], perm_ext[:, 1:], both_y)
    face_z = harmonic(perm_ext[:, :, :-1], perm_ext[:, :, 1:], plane_in)
    cell_perm = perm_ext[1:-1, 1:-1]
    face_west = face_x[:-1, 1:-1]
    face_east = face_x[1:, 1:-1]
    face_south = face_y[1:-1, :-1]
    face_north = face_y[1:-1, 1:]
    zero_plane = jnp.zeros_like(cell_perm[:, :, :1])
    face_below = jnp.concatenate([zero_plane, face_z[1:-1, 1:-1]], axis=2)
    face_above = jnp.concatenate([face_z[1:-1, 1:-1], zero_plane], axis=2)
    cell_x = glob_x[1:-1]
    cell_y = glob_y[1:-1]
    index_z = jnp.arange(count_z)
    ends_x = (cell_x == 0).astype(jnp.float32) + (cell_x == total_x - 1).astype(jnp.float32)
    ends_y = (cell_y == 0).astype(jnp.float32) + (cell_y == total_y - 1).astype(jnp.float32)
    ends_z = (index_z == 0).astype(jnp.float32) + (index_z == count_z - 1).astype(jnp.float32)
    edges = ends_x[:, None, None] + ends_y[None, :, None] + ends_z[None, None, :]
    boundary = 2.0 * cell_perm * edges
    diagonal = face_west + face_east + face_south + face_north + face_below + face_above + boundary
    cell_in = plane_in[1:-1, 1:-1]
    safe_diag = jnp.where(cell_in, diagonal, 1.0)
    return (
        face_west,
        face_east,
        face_south,
        face_north,
        face_below,
        face_above,
        boundary,
        safe_diag,
    )


def apply_fine(ext_field, faces_now):
    face_west, face_east, face_south, face_north, face_below, face_above, boundary, safe_diag = (
        faces_now
    )
    center = ext_field[1:-1, 1:-1]
    zero_plane = jnp.zeros_like(center[:, :, :1])
    below_vals = jnp.concatenate([zero_plane, center[:, :, :-1]], axis=2)
    above_vals = jnp.concatenate([center[:, :, 1:], zero_plane], axis=2)
    beside_all = face_west * ext_field[:-2, 1:-1] + face_east * ext_field[2:, 1:-1]
    beside_all = beside_all + face_south * ext_field[1:-1, :-2] + face_north * ext_field[1:-1, 2:]
    beside_all = beside_all + face_below * below_vals + face_above * above_vals
    return (center, safe_diag * center - beside_all)


def crop(array, rim, rim_y=None):
    rim_y = rim if rim_y is None else rim_y
    return array[rim : array.shape[0] - rim, rim_y : array.shape[1] - rim_y]


def sweeps(field_ext, source_ext, faces_ext, count, width):
    def rims(array):
        return (array.shape[0] - width) // 2, (array.shape[1] - width) // 2

    def cut(array, out_x, out_y):
        rim_x, rim_y = rims(array)
        return crop(array, rim_x - out_x, rim_y - out_y)

    for sweep_index in range(count):
        out_x, out_y = (rim - 1 for rim in rims(field_ext))
        faces_now = tuple(cut(member, out_x, out_y) for member in faces_ext)
        center, product = apply_fine(field_ext, faces_now)
        source_now = cut(source_ext, out_x, out_y)
        field_ext = center + OMEGA * (source_now - product) / faces_now[7]
    return field_ext


def body(permeability, source, pressure, aggregate):
    width_x, width_y, depth_cells = permeability.shape
    slab_index = lax.axis_index("slab")
    slab_count = lax.axis_size("slab")
    row_index = lax.axis_index(("pencil", "sub"))
    row_count = lax.axis_size(("pencil", "sub"))
    total_x = width_x * slab_count
    total_y = width_y * row_count
    sides = (("slab", 0), (("pencil", "sub"), 1))
    stacked_sides = (("slab", 1), (("pencil", "sub"), 2))
    fine_rim = 2 * NU
    rim_x = NU + 1
    ext_x = padded(jnp.stack([permeability, source, pressure]), (("slab", 1),), rim_x)
    ext_x, aggregate = lax.optimization_barrier((ext_x, aggregate))
    ext_all = padded(ext_x, ((("pencil", "sub"), 2),), fine_rim)
    perm_ext = ext_all[0]
    source_ext = crop(ext_all[1], 1)
    glob_x = slab_index * width_x - rim_x + jnp.arange(width_x + 2 * rim_x)
    glob_y = row_index * width_y - fine_rim + jnp.arange(width_y + 2 * fine_rim)
    inside_x = (glob_x >= 0) & (glob_x < total_x)
    inside_y = (glob_y >= 0) & (glob_y < total_y)
    faces_ext = geometry(perm_ext, glob_x, glob_y, inside_x, inside_y, total_x, total_y)
    smooth_ext = sweeps(ext_all[2], source_ext, faces_ext, NU, width_x)
    faces_zero = tuple(crop(member, rim_x - 1, fine_rim - 1) for member in faces_ext)
    smooth_rows = smooth_ext[1 : 1 + width_x]
    center, product = apply_fine(crop(smooth_ext, 0, NU - 1), faces_zero)
    residual = source - product
    half_y = width_y // 2
    half_z = depth_cells // 2

    plane_count = aggregate.shape[0]
    ext_pos = slab_index * width_x - 1 + jnp.arange(width_x + 1 + NU)
    pick_ids = ext_pos[:, None] == jnp.arange(plane_count)[None, :]
    ext_ids = jnp.sum(jnp.where(pick_ids, aggregate.astype(jnp.float32)[None, :], 0.0), axis=1)
    local_ids = ext_ids[1 : width_x + 1]
    straddles = (slab_index > 0) & (ext_ids[0] == local_ids[0])
    first_id = local_ids[0] + straddles.astype(jnp.float32)
    count_live = local_ids[-1] - first_id + 1
    slot_ids = local_ids - first_id
    has_next = ext_pos[2 : width_x + 2] < plane_count
    crossing = ((local_ids != ext_ids[2 : width_x + 2]) & has_next).astype(jnp.float32)
    face_east = faces_zero[1]
    face_north = faces_zero[3]
    face_above = faces_zero[5]
    boundary = faces_zero[6]
    index_z = np.arange(depth_cells)[:, None]
    coarse_z = np.arange(half_z)[None, :]
    pair_z = jnp.asarray((index_z // 2 == coarse_z).astype(np.float32))
    odd_z = jnp.asarray((index_z == 2 * coarse_z + 1).astype(np.float32))
    cells = width_x * width_y

    def z_sum(block_in, pick_z):
        flat = block_in.reshape(cells, depth_cells)
        return jnp.dot(flat, pick_z, precision=lax.Precision.HIGH)

    z_parts = jnp.stack(
        [
            z_sum(residual, pair_z),
            z_sum(face_east * crossing[:, None, None], pair_z),
            z_sum(face_north, pair_z),
            z_sum(face_above, odd_z),
            z_sum(boundary, pair_z),
        ]
    )
    index_y = np.arange(width_y)[:, None]
    coarse_y = np.arange(half_y)[None, :]
    pair_y = jnp.asarray((index_y // 2 == coarse_y).astype(np.float32))
    row_y = np.tile(np.arange(width_y), width_x)
    col_slot = np.repeat(np.arange(width_x + 1), half_y)
    col_y = np.tile(np.arange(half_y), width_x + 1)
    row_slot = jnp.repeat(slot_ids + 1, width_y)
    same_slot = row_slot[:, None] == jnp.asarray(col_slot.astype(np.float32))[None, :]
    pair_rows = row_y[:, None] // 2 == col_y[None, :]
    odd_rows = row_y[:, None] == 2 * col_y[None, :] + 1
    spread_map = (same_slot & pair_rows).astype(jnp.float32)
    gather_map = (same_slot.T & pair_rows.T).astype(jnp.float32)
    north_gather = (same_slot.T & odd_rows.T).astype(jnp.float32)
    paired = jnp.dot(
        gather_map,
        jnp.concatenate([z_parts[0], z_parts[1], z_parts[3], z_parts[4]], axis=1),
        precision=lax.Precision.HIGH,
    )
    north_sums = jnp.dot(north_gather, z_parts[2], precision=lax.Precision.HIGH)

    def column(index):
        return paired[:, index * half_z : (index + 1) * half_z]

    slot_sums = jnp.stack([column(0), column(1), north_sums, column(2), column(3)])
    slot_sums = slot_sums.reshape(5, width_x + 1, half_y, half_z)
    coarse = slot_sums[:, 1:]
    edge_sums = slot_sums[:, 0]
    slot_range = jnp.arange(width_x)
    last_slot = (slot_range == count_live - 1).astype(jnp.float32)
    tail_pick = (slot_range[None, :] == count_live - NCS + jnp.arange(NCS)[:, None]).astype(jnp.float32)
    tail_planes = jnp.einsum("ks,qsjl->qkjl", tail_pick, coarse, precision=lax.Precision.HIGH)
    head_planes = jnp.concatenate([coarse[:, :NCS], edge_sums[:, None]], axis=1)
    tail_planes, head_planes = lax.optimization_barrier((tail_planes, head_planes))
    from_prev = passed_along(tail_planes, "slab", 1)
    from_next = passed_along(head_planes, "slab", -1)
    coarse = coarse + from_next[:, NCS][:, None] * last_slot[None, :, None, None]
    prev_last = (jnp.arange(NCS) == NCS - 1).astype(jnp.float32)
    from_prev = from_prev + edge_sums[:, None] * prev_last[None, :, None, None]
    x_ext = jnp.concatenate([from_prev, coarse, jnp.zeros_like(tail_planes)], axis=1)
    wide_range = jnp.arange(width_x + 2 * NCS)[:, None]
    place = (wide_range == NCS + count_live + jnp.arange(NCS)[None, :]).astype(jnp.float32)
    x_ext = x_ext + jnp.einsum("tk,qkjl->qtjl", place, from_next[:, :NCS], precision=lax.Precision.HIGH)
    coarse_rim = NCS
    rim_y = NCS + 1
    rows_axis = ("pencil", "sub")
    from_below = passed_along(x_ext[:, :, half_y - rim_y :], rows_axis, 1)
    from_above = passed_along(x_ext[:, :, : rim_y - 1], rows_axis, -1)
    coef_ext = jnp.concatenate([from_below, x_ext, from_above], axis=2)
    coarse_corr = jnp.zeros((width_x + 2 * NCS, half_y + 2 * rim_y, half_z), jnp.float32)
    for sweep_index in range(NCS):
        out_rim = NCS - 1 - sweep_index
        start_at = coarse_rim - out_rim
        start_y = start_at
        size_x = width_x + 2 * out_rim
        size_y = half_y + 2 * (out_rim + 1)

        def region(offset_x, offset_y):
            return coef_ext[
                :,
                start_at + offset_x : start_at + offset_x + size_x,
                start_y + offset_y : start_y + offset_y + size_y,
            ]

        here_coef = region(0, 0)
        coarse_rhs = here_coef[0]
        coarse_east = here_coef[1]
        coarse_north = here_coef[2]
        coarse_above = here_coef[3]
        coarse_bound = here_coef[4]
        coarse_west = region(-1, 0)[1]
        coarse_south = region(0, -1)[2]
        zero_plane = jnp.zeros_like(coarse_above[:, :, :1])
        coarse_below = jnp.concatenate([zero_plane, coarse_above[:, :, :-1]], axis=2)
        diag_coarse = (
            coarse_east
            + coarse_west
            + coarse_north
            + coarse_south
            + coarse_above
            + coarse_below
            + coarse_bound
        )
        safe_coarse = jnp.where(diag_coarse > 0, diag_coarse, 1.0)
        coarse_center = coarse_corr[1:-1, 1:-1]
        above_vals = jnp.concatenate([coarse_center[:, :, 1:], zero_plane], axis=2)
        below_vals = jnp.concatenate([zero_plane, coarse_center[:, :, :-1]], axis=2)
        beside_all = coarse_east * coarse_corr[2:, 1:-1] + coarse_west * coarse_corr[:-2, 1:-1]
        beside_all = (
            beside_all
            + coarse_north * coarse_corr[1:-1, 2:]
            + coarse_south * coarse_corr[1:-1, :-2]
        )
        beside_all = beside_all + coarse_above * above_vals + coarse_below * below_vals
        coarse_corr = (
            coarse_center
            + OMEGA * (coarse_rhs - (diag_coarse * coarse_center - beside_all)) / safe_coarse
        )
    last_corr = jnp.sum(last_slot[:, None, None] * coarse_corr, axis=0)
    corr_wide = jnp.concatenate([jnp.zeros_like(last_corr)[None], coarse_corr], axis=0)
    corr_core = corr_wide[:, 1 : 1 + half_y]
    corr_z = jnp.dot(
        corr_core.reshape((width_x + 1) * half_y, half_z), pair_z.T, precision=lax.Precision.HIGH
    )
    correction = jnp.dot(spread_map, corr_z, precision=lax.Precision.HIGH)
    correction = correction.reshape(width_x, width_y, depth_cells)
    owner_rows = (slot_ids[:, None] + 1 == jnp.arange(width_x + 1)[None, :]).astype(jnp.float32)

    def rim_rows(coarse_row):
        row_z = jnp.dot(corr_wide[:, coarse_row], pair_z.T, precision=lax.Precision.HIGH)
        row_fine = jnp.dot(owner_rows, row_z, precision=lax.Precision.HIGH)
        return jnp.broadcast_to(row_fine[:, None], (width_x, NU, depth_cells))

    correction = jnp.concatenate([rim_rows(0), correction, rim_rows(half_y + 1)], axis=1)
    base = smooth_rows + correction
    last_z = jnp.dot(last_corr, pair_z.T, precision=lax.Precision.HIGH)
    fine_y = np.arange(width_y + 2 * NU) - NU
    rows_ext = jnp.asarray((fine_y[:, None] // 2 + 1 == np.arange(half_y + 2)[None, :]).astype(np.float32))
    last_fine = jnp.dot(rows_ext, last_z, precision=lax.Precision.HIGH)
    up_block = jnp.concatenate([base[width_x - NU :], last_fine[None]], axis=0)
    below_prev = passed_along(up_block, "slab", 1)
    above_next = passed_along(base[:NU], "slab", -1)
    from_owner = (slot_ids == -1).astype(jnp.float32)
    own = base + from_owner[:, None, None] * below_prev[NU][None]
    next_ids = ext_ids[width_x + 1 :]
    next_in = ext_pos[width_x + 1 :] < plane_count
    to_owner = ((next_ids == local_ids[-1]) & next_in).astype(jnp.float32)
    high_halo = above_next + to_owner[:, None, None] * last_fine[None]
    post_ext = jnp.concatenate([below_prev[:NU], own, high_halo], axis=0)
    return sweeps(post_ext, source_ext, faces_ext, NU, width_x)


def solution(mesh):
    in_specs = (
        P(("real", "slab"), ("pencil", "sub"), None),
        P(("real", "slab"), ("pencil", "sub"), None),
        P(("real", "slab"), ("pencil", "sub"), None),
        P("real"),
    )
    out_specs = P(("real", "slab"), ("pencil", "sub"), None)
    return jax.shard_map(body, mesh=mesh, in_specs=in_specs, out_specs=out_specs, check_vma=False)
```

```python
import numpy as np
import jax
import jax.numpy as jnp
from jax import lax
from jax.sharding import PartitionSpec as P

NU = 2
NCS = 4


OMEGA = 0.8


def padded(array, sides, width):
    for axis, dim in sides:
        count, length = (lax.axis_size(axis), array.shape[dim])
        up = [(i, (i + 1) % count) for i in range(count - 1)]
        down = [(j, i) for i, j in up]
        last = lax.slice_in_dim(array, length - width, length, axis=dim)
        leading = lax.slice_in_dim(array, 0, width, axis=dim)
        before = lax.ppermute(last, axis, up)
        after = lax.ppermute(leading, axis, down)
        array = jnp.concatenate([before, array, after], axis=dim)
    return array


def passed_along(array, axis, by):
    count = lax.axis_size(axis)
    pairs = [(i, i + by) for i in range(count) if 0 <= i + by < count]
    return lax.ppermute(array, axis, pairs)


def harmonic(lower_k, upper_k, inside):
    denom_sum = jnp.where(inside, lower_k + upper_k, 1.0)
    return jnp.where(inside, 2.0 * lower_k * upper_k / denom_sum, 0.0)


def geometry(perm_ext, glob_x, glob_y, inside_x, inside_y, total_x, total_y):
    count_z = perm_ext.shape[2]
    both_x = (inside_x[:-1] & inside_x[1:])[:, None, None] & inside_y[None, :, None]
    both_y = (inside_y[:-1] & inside_y[1:])[None, :, None] & inside_x[:, None, None]
    plane_in = inside_x[:, None, None] & inside_y[None, :, None]
    face_x = harmonic(perm_ext[:-1], perm_ext[1:], both_x)
    face_y = harmonic(perm_ext[:, :-1], perm_ext[:, 1:], both_y)
    face_z = harmonic(perm_ext[:, :, :-1], perm_ext[:, :, 1:], plane_in)
    cell_perm = perm_ext[1:-1, 1:-1]
    face_west = face_x[:-1, 1:-1]
    face_east = face_x[1:, 1:-1]
    face_south = face_y[1:-1, :-1]
    face_north = face_y[1:-1, 1:]
    zero_plane = jnp.zeros_like(cell_perm[:, :, :1])
    face_below = jnp.concatenate([zero_plane, face_z[1:-1, 1:-1]], axis=2)
    face_above = jnp.concatenate([face_z[1:-1, 1:-1], zero_plane], axis=2)
    cell_x = glob_x[1:-1]
    cell_y = glob_y[1:-1]
    index_z = jnp.arange(count_z)
    ends_x = (cell_x == 0).astype(jnp.float32) + (cell_x == total_x - 1).astype(jnp.float32)
    ends_y = (cell_y == 0).astype(jnp.float32) + (cell_y == total_y - 1).astype(jnp.float32)
    ends_z = (index_z == 0).astype(jnp.float32) + (index_z == count_z - 1).astype(jnp.float32)
    edges = ends_x[:, None, None] + ends_y[None, :, None] + ends_z[None, None, :]
    boundary = 2.0 * cell_perm * edges
    diagonal = face_west + face_east + face_south + face_north + face_below + face_above + boundary
    cell_in = plane_in[1:-1, 1:-1]
    safe_diag = jnp.where(cell_in, diagonal, 1.0)
    return (
        face_west,
        face_east,
        face_south,
        face_north,
        face_below,
        face_above,
        boundary,
        safe_diag,
    )


def apply_fine(ext_field, faces_now):
    face_west, face_east, face_south, face_north, face_below, face_above, boundary, safe_diag = (
        faces_now
    )
    center = ext_field[1:-1, 1:-1]
    zero_plane = jnp.zeros_like(center[:, :, :1])
    below_vals = jnp.concatenate([zero_plane, center[:, :, :-1]], axis=2)
    above_vals = jnp.concatenate([center[:, :, 1:], zero_plane], axis=2)
    beside_all = face_west * ext_field[:-2, 1:-1] + face_east * ext_field[2:, 1:-1]
    beside_all = beside_all + face_south * ext_field[1:-1, :-2] + face_north * ext_field[1:-1, 2:]
    beside_all = beside_all + face_below * below_vals + face_above * above_vals
    return (center, safe_diag * center - beside_all)


def crop(array, rim, rim_y=None):
    rim_y = rim if rim_y is None else rim_y
    return array[rim : array.shape[0] - rim, rim_y : array.shape[1] - rim_y]


def sweeps(field_ext, source_ext, faces_ext, count, width):
    def rims(array):
        return (array.shape[0] - width) // 2, (array.shape[1] - width) // 2

    def cut(array, out_x, out_y):
        rim_x, rim_y = rims(array)
        return crop(array, rim_x - out_x, rim_y - out_y)

    for sweep_index in range(count):
        out_x, out_y = (rim - 1 for rim in rims(field_ext))
        faces_now = tuple(cut(member, out_x, out_y) for member in faces_ext)
        center, product = apply_fine(field_ext, faces_now)
        source_now = cut(source_ext, out_x, out_y)
        field_ext = center + OMEGA * (source_now - product) / faces_now[7]
    return field_ext


def body(permeability, source, pressure, aggregate):
    width_x, width_y, depth_cells = permeability.shape
    slab_index = lax.axis_index("slab")
    slab_count = lax.axis_size("slab")
    row_index = lax.axis_index(("pencil", "sub"))
    row_count = lax.axis_size(("pencil", "sub"))
    total_x = width_x * slab_count
    total_y = width_y * row_count
    sides = (("slab", 0), (("pencil", "sub"), 1))
    stacked_sides = (("slab", 1), (("pencil", "sub"), 2))
    fine_rim = 2 * NU
    rim_x = NU + 1
    ext_x = padded(jnp.stack([permeability, source, pressure]), (("slab", 1),), rim_x)
    ext_x, aggregate = lax.optimization_barrier((ext_x, aggregate))
    ext_all = padded(ext_x, ((("pencil", "sub"), 2),), fine_rim)
    perm_ext = ext_all[0]
    source_ext = crop(ext_all[1], 1)
    glob_x = slab_index * width_x - rim_x + jnp.arange(width_x + 2 * rim_x)
    glob_y = row_index * width_y - fine_rim + jnp.arange(width_y + 2 * fine_rim)
    inside_x = (glob_x >= 0) & (glob_x < total_x)
    inside_y = (glob_y >= 0) & (glob_y < total_y)
    faces_ext = geometry(perm_ext, glob_x, glob_y, inside_x, inside_y, total_x, total_y)
    smooth_ext = sweeps(ext_all[2], source_ext, faces_ext, NU, width_x)
    faces_zero = tuple(crop(member, rim_x - 1, fine_rim - 1) for member in faces_ext)
    smooth_rows = smooth_ext[1 : 1 + width_x]
    center, product = apply_fine(crop(smooth_ext, 0, NU - 1), faces_zero)
    residual = source - product
    half_y = width_y // 2
    half_z = depth_cells // 2

    plane_count = aggregate.shape[0]
    ext_pos = slab_index * width_x - 1 + jnp.arange(width_x + 1 + NU)
    pick_ids = ext_pos[:, None] == jnp.arange(plane_count)[None, :]
    ext_ids = jnp.sum(jnp.where(pick_ids, aggregate.astype(jnp.float32)[None, :], 0.0), axis=1)
    local_ids = ext_ids[1 : width_x + 1]
    straddles = (slab_index > 0) & (ext_ids[0] == local_ids[0])
    first_id = local_ids[0] + straddles.astype(jnp.float32)
    count_live = local_ids[-1] - first_id + 1
    slot_ids = local_ids - first_id
    has_next = ext_pos[2 : width_x + 2] < plane_count
    crossing = ((local_ids != ext_ids[2 : width_x + 2]) & has_next).astype(jnp.float32)
    face_east = faces_zero[1]
    face_north = faces_zero[3]
    face_above = faces_zero[5]
    boundary = faces_zero[6]
    index_z = np.arange(depth_cells)[:, None]
    coarse_z = np.arange(half_z)[None, :]
    pair_z = jnp.asarray((index_z // 2 == coarse_z).astype(np.float32))
    odd_z = jnp.asarray((index_z == 2 * coarse_z + 1).astype(np.float32))
    cells = width_x * width_y

    def z_sum(block_in, pick_z):
        flat = block_in.reshape(cells, depth_cells)
        return jnp.dot(flat, pick_z, precision=lax.Precision.HIGH)

    z_parts = jnp.stack(
        [
            z_sum(residual, pair_z),
            z_sum(face_east * crossing[:, None, None], pair_z),
            z_sum(face_north, pair_z),
            z_sum(face_above, odd_z),
            z_sum(boundary, pair_z),
        ]
    )
    index_y = np.arange(width_y)[:, None]
    coarse_y = np.arange(half_y)[None, :]
    pair_y = jnp.asarray((index_y // 2 == coarse_y).astype(np.float32))
    row_y = np.tile(np.arange(width_y), width_x)
    col_slot = np.repeat(np.arange(width_x + 1), half_y)
    col_y = np.tile(np.arange(half_y), width_x + 1)
    row_slot = jnp.repeat(slot_ids + 1, width_y)
    same_slot = row_slot[:, None] == jnp.asarray(col_slot.astype(np.float32))[None, :]
    pair_rows = row_y[:, None] // 2 == col_y[None, :]
    odd_rows = row_y[:, None] == 2 * col_y[None, :] + 1
    spread_map = (same_slot & pair_rows).astype(jnp.float32)
    gather_map = (same_slot.T & pair_rows.T).astype(jnp.float32)
    north_gather = (same_slot.T & odd_rows.T).astype(jnp.float32)
    paired = jnp.dot(
        gather_map,
        jnp.concatenate([z_parts[0], z_parts[1], z_parts[3], z_parts[4]], axis=1),
        precision=lax.Precision.HIGH,
    )
    north_sums = jnp.dot(north_gather, z_parts[2], precision=lax.Precision.HIGH)

    def column(index):
        return paired[:, index * half_z : (index + 1) * half_z]

    slot_sums = jnp.stack([column(0), column(1), north_sums, column(2), column(3)])
    slot_sums = slot_sums.reshape(5, width_x + 1, half_y, half_z)
    coarse = slot_sums[:, 1:]
    edge_sums = slot_sums[:, 0]
    slot_range = jnp.arange(width_x)
    last_slot = (slot_range == count_live - 1).astype(jnp.float32)
    tail_pick = (slot_range[None, :] == count_live - NCS + jnp.arange(NCS)[:, None]).astype(jnp.float32)
    tail_planes = jnp.einsum("ks,qsjl->qkjl", tail_pick, coarse, precision=lax.Precision.HIGH)
    ahead = NCS - 1
    head_planes = jnp.concatenate([coarse[:, :ahead], edge_sums[:, None]], axis=1)
    tail_planes, head_planes = lax.optimization_barrier((tail_planes, head_planes))
    from_prev = passed_along(tail_planes, "slab", 1)
    from_next = passed_along(head_planes, "slab", -1)
    coarse = coarse + from_next[:, ahead][:, None] * last_slot[None, :, None, None]
    prev_last = (jnp.arange(NCS) == NCS - 1).astype(jnp.float32)
    from_prev = from_prev + edge_sums[:, None] * prev_last[None, :, None, None]
    x_ext = jnp.concatenate([from_prev, coarse, jnp.zeros_like(tail_planes)], axis=1)
    wide_range = jnp.arange(width_x + 2 * NCS)[:, None]
    place = (wide_range == NCS + count_live + jnp.arange(ahead)[None, :]).astype(jnp.float32)
    x_ext = x_ext + jnp.einsum("tk,qkjl->qtjl", place, from_next[:, :ahead], precision=lax.Precision.HIGH)
    coarse_rim = NCS
    rim_y = NCS + 1
    rows_axis = ("pencil", "sub")
    from_below = passed_along(x_ext[:, :, half_y - rim_y :], rows_axis, 1)
    from_above = passed_along(x_ext[:, :, : rim_y - 1], rows_axis, -1)
    coef_ext = jnp.concatenate([from_below, x_ext, from_above], axis=2)
    coarse_corr = jnp.zeros((width_x + 2 * NCS, half_y + 2 * rim_y, half_z), jnp.float32)
    for sweep_index in range(NCS):
        out_rim = NCS - 1 - sweep_index
        start_at = coarse_rim - out_rim
        start_y = start_at
        size_x = width_x + 2 * out_rim
        size_y = half_y + 2 * (out_rim + 1)

        def region(offset_x, offset_y):
            return coef_ext[
                :,
                start_at + offset_x : start_at + offset_x + size_x,
                start_y + offset_y : start_y + offset_y + size_y,
            ]

        here_coef = region(0, 0)
        coarse_rhs = here_coef[0]
        coarse_east = here_coef[1]
        coarse_north = here_coef[2]
        coarse_above = here_coef[3]
        coarse_bound = here_coef[4]
        coarse_west = region(-1, 0)[1]
        coarse_south = region(0, -1)[2]
        zero_plane = jnp.zeros_like(coarse_above[:, :, :1])
        coarse_below = jnp.concatenate([zero_plane, coarse_above[:, :, :-1]], axis=2)
        diag_coarse = (
            coarse_east
            + coarse_west
            + coarse_north
            + coarse_south
            + coarse_above
            + coarse_below
            + coarse_bound
        )
        safe_coarse = jnp.where(diag_coarse > 0, diag_coarse, 1.0)
        coarse_center = coarse_corr[1:-1, 1:-1]
        above_vals = jnp.concatenate([coarse_center[:, :, 1:], zero_plane], axis=2)
        below_vals = jnp.concatenate([zero_plane, coarse_center[:, :, :-1]], axis=2)
        beside_all = coarse_east * coarse_corr[2:, 1:-1] + coarse_west * coarse_corr[:-2, 1:-1]
        beside_all = (
            beside_all
            + coarse_north * coarse_corr[1:-1, 2:]
            + coarse_south * coarse_corr[1:-1, :-2]
        )
        beside_all = beside_all + coarse_above * above_vals + coarse_below * below_vals
        coarse_corr = (
            coarse_center
            + OMEGA * (coarse_rhs - (diag_coarse * coarse_center - beside_all)) / safe_coarse
        )
    last_corr = jnp.sum(last_slot[:, None, None] * coarse_corr, axis=0)
    corr_wide = jnp.concatenate([jnp.zeros_like(last_corr)[None], coarse_corr], axis=0)
    corr_core = corr_wide[:, 1 : 1 + half_y]
    corr_z = jnp.dot(
        corr_core.reshape((width_x + 1) * half_y, half_z), pair_z.T, precision=lax.Precision.HIGH
    )
    correction = jnp.dot(spread_map, corr_z, precision=lax.Precision.HIGH)
    correction = correction.reshape(width_x, width_y, depth_cells)
    owner_rows = (slot_ids[:, None] + 1 == jnp.arange(width_x + 1)[None, :]).astype(jnp.float32)

    def rim_rows(coarse_row):
        row_z = jnp.dot(corr_wide[:, coarse_row], pair_z.T, precision=lax.Precision.HIGH)
        row_fine = jnp.dot(owner_rows, row_z, precision=lax.Precision.HIGH)
        return jnp.broadcast_to(row_fine[:, None], (width_x, NU, depth_cells))

    correction = jnp.concatenate([rim_rows(0), correction, rim_rows(half_y + 1)], axis=1)
    base = smooth_rows + correction
    last_z = jnp.dot(last_corr, pair_z.T, precision=lax.Precision.HIGH)
    fine_y = np.arange(width_y + 2 * NU) - NU
    rows_ext = jnp.asarray((fine_y[:, None] // 2 + 1 == np.arange(half_y + 2)[None, :]).astype(np.float32))
    last_fine = jnp.dot(rows_ext, last_z, precision=lax.Precision.HIGH)
    up_block = jnp.concatenate([base[width_x - NU :], last_fine[None]], axis=0)
    below_prev = passed_along(up_block, "slab", 1)
    above_next = passed_along(base[:NU], "slab", -1)
    from_owner = (slot_ids == -1).astype(jnp.float32)
    own = base + from_owner[:, None, None] * below_prev[NU][None]
    next_ids = ext_ids[width_x + 1 :]
    next_in = ext_pos[width_x + 1 :] < plane_count
    to_owner = ((next_ids == local_ids[-1]) & next_in).astype(jnp.float32)
    high_halo = above_next + to_owner[:, None, None] * last_fine[None]
    post_ext = jnp.concatenate([below_prev[:NU], own, high_halo], axis=0)
    return sweeps(post_ext, source_ext, faces_ext, NU, width_x)


def solution(mesh):
    in_specs = (
        P(("real", "slab"), ("pencil", "sub"), None),
        P(("real", "slab"), ("pencil", "sub"), None),
        P(("real", "slab"), ("pencil", "sub"), None),
        P("real"),
    )
    out_specs = P(("real", "slab"), ("pencil", "sub"), None)
    return jax.shard_map(body, mesh=mesh, in_specs=in_specs, out_specs=out_specs, check_vma=False)
```

```python
import numpy as np
import jax
import jax.numpy as jnp
from jax import lax
from jax.sharding import PartitionSpec as P

NU = 2
NCS = 4


OMEGA = 0.8


def padded(array, sides, width):
    for axis, dim in sides:
        count, length = (lax.axis_size(axis), array.shape[dim])
        up = [(i, (i + 1) % count) for i in range(count - 1)]
        down = [(j, i) for i, j in up]
        last = lax.slice_in_dim(array, length - width, length, axis=dim)
        leading = lax.slice_in_dim(array, 0, width, axis=dim)
        before = lax.ppermute(last, axis, up)
        after = lax.ppermute(leading, axis, down)
        array = jnp.concatenate([before, array, after], axis=dim)
    return array


def passed_along(array, axis, by):
    count = lax.axis_size(axis)
    pairs = [(i, i + by) for i in range(count) if 0 <= i + by < count]
    return lax.ppermute(array, axis, pairs)


def harmonic(lower_k, upper_k, inside):
    denom_sum = jnp.where(inside, lower_k + upper_k, 1.0)
    return jnp.where(inside, 2.0 * lower_k * upper_k / denom_sum, 0.0)


def geometry(perm_ext, glob_x, glob_y, inside_x, inside_y, total_x, total_y):
    count_z = perm_ext.shape[2]
    both_x = (inside_x[:-1] & inside_x[1:])[:, None, None] & inside_y[None, :, None]
    both_y = (inside_y[:-1] & inside_y[1:])[None, :, None] & inside_x[:, None, None]
    plane_in = inside_x[:, None, None] & inside_y[None, :, None]
    face_x = harmonic(perm_ext[:-1], perm_ext[1:], both_x)
    face_y = harmonic(perm_ext[:, :-1], perm_ext[:, 1:], both_y)
    face_z = harmonic(perm_ext[:, :, :-1], perm_ext[:, :, 1:], plane_in)
    cell_perm = perm_ext[1:-1, 1:-1]
    face_west = face_x[:-1, 1:-1]
    face_east = face_x[1:, 1:-1]
    face_south = face_y[1:-1, :-1]
    face_north = face_y[1:-1, 1:]
    zero_plane = jnp.zeros_like(cell_perm[:, :, :1])
    face_below = jnp.concatenate([zero_plane, face_z[1:-1, 1:-1]], axis=2)
    face_above = jnp.concatenate([face_z[1:-1, 1:-1], zero_plane], axis=2)
    cell_x = glob_x[1:-1]
    cell_y = glob_y[1:-1]
    index_z = jnp.arange(count_z)
    ends_x = (cell_x == 0).astype(jnp.float32) + (cell_x == total_x - 1).astype(jnp.float32)
    ends_y = (cell_y == 0).astype(jnp.float32) + (cell_y == total_y - 1).astype(jnp.float32)
    ends_z = (index_z == 0).astype(jnp.float32) + (index_z == count_z - 1).astype(jnp.float32)
    edges = ends_x[:, None, None] + ends_y[None, :, None] + ends_z[None, None, :]
    boundary = 2.0 * cell_perm * edges
    diagonal = face_west + face_east + face_south + face_north + face_below + face_above + boundary
    cell_in = plane_in[1:-1, 1:-1]
    safe_diag = jnp.where(cell_in, diagonal, 1.0)
    return (
        face_west,
        face_east,
        face_south,
        face_north,
        face_below,
        face_above,
        boundary,
        safe_diag,
    )


def apply_fine(ext_field, faces_now):
    face_west, face_east, face_south, face_north, face_below, face_above, boundary, safe_diag = (
        faces_now
    )
    center = ext_field[1:-1, 1:-1]
    zero_plane = jnp.zeros_like(center[:, :, :1])
    below_vals = jnp.concatenate([zero_plane, center[:, :, :-1]], axis=2)
    above_vals = jnp.concatenate([center[:, :, 1:], zero_plane], axis=2)
    beside_all = face_west * ext_field[:-2, 1:-1] + face_east * ext_field[2:, 1:-1]
    beside_all = beside_all + face_south * ext_field[1:-1, :-2] + face_north * ext_field[1:-1, 2:]
    beside_all = beside_all + face_below * below_vals + face_above * above_vals
    return (center, safe_diag * center - beside_all)


def crop(array, rim, rim_y=None):
    rim_y = rim if rim_y is None else rim_y
    return array[rim : array.shape[0] - rim, rim_y : array.shape[1] - rim_y]


def sweeps(field_ext, source_ext, faces_ext, count, width):
    def rims(array):
        return (array.shape[0] - width) // 2, (array.shape[1] - width) // 2

    def cut(array, out_x, out_y):
        rim_x, rim_y = rims(array)
        return crop(array, rim_x - out_x, rim_y - out_y)

    for sweep_index in range(count):
        out_x, out_y = (rim - 1 for rim in rims(field_ext))
        faces_now = tuple(cut(member, out_x, out_y) for member in faces_ext)
        center, product = apply_fine(field_ext, faces_now)
        source_now = cut(source_ext, out_x, out_y)
        field_ext = center + OMEGA * (source_now - product) / faces_now[7]
    return field_ext


def body(permeability, source, pressure, aggregate):
    width_x, width_y, depth_cells = permeability.shape
    slab_index = lax.axis_index("slab")
    slab_count = lax.axis_size("slab")
    row_index = lax.axis_index(("pencil", "sub"))
    row_count = lax.axis_size(("pencil", "sub"))
    total_x = width_x * slab_count
    total_y = width_y * row_count
    sides = (("slab", 0), (("pencil", "sub"), 1))
    stacked_sides = (("slab", 1), (("pencil", "sub"), 2))
    fine_rim = 2 * NU
    rim_x = NU + 1
    ext_x = padded(jnp.stack([permeability, source, pressure]), (("slab", 1),), rim_x)
    ext_x, aggregate = lax.optimization_barrier((ext_x, aggregate))
    ext_all = padded(ext_x, ((("pencil", "sub"), 2),), fine_rim)
    perm_ext = ext_all[0]
    source_ext = crop(ext_all[1], 1)
    glob_x = slab_index * width_x - rim_x + jnp.arange(width_x + 2 * rim_x)
    glob_y = row_index * width_y - fine_rim + jnp.arange(width_y + 2 * fine_rim)
    inside_x = (glob_x >= 0) & (glob_x < total_x)
    inside_y = (glob_y >= 0) & (glob_y < total_y)
    faces_ext = geometry(perm_ext, glob_x, glob_y, inside_x, inside_y, total_x, total_y)
    smooth_ext = sweeps(ext_all[2], source_ext, faces_ext, NU, width_x)
    faces_zero = tuple(crop(member, rim_x - 1, fine_rim - 1) for member in faces_ext)
    smooth_rows = smooth_ext[1 : 1 + width_x]
    center, product = apply_fine(crop(smooth_ext, 0, NU - 1), faces_zero)
    residual = source - product
    half_y = width_y // 2
    half_z = depth_cells // 2

    plane_count = aggregate.shape[0]
    ext_pos = slab_index * width_x - 1 + jnp.arange(width_x + 1 + NU)
    pick_ids = ext_pos[:, None] == jnp.arange(plane_count)[None, :]
    ext_ids = jnp.sum(jnp.where(pick_ids, aggregate.astype(jnp.float32)[None, :], 0.0), axis=1)
    local_ids = ext_ids[1 : width_x + 1]
    straddles = (slab_index > 0) & (ext_ids[0] == local_ids[0])
    first_id = local_ids[0] + straddles.astype(jnp.float32)
    count_live = local_ids[-1] - first_id + 1
    slot_ids = local_ids - first_id
    has_next = ext_pos[2 : width_x + 2] < plane_count
    crossing = ((local_ids != ext_ids[2 : width_x + 2]) & has_next).astype(jnp.float32)
    face_east = faces_zero[1]
    face_north = faces_zero[3]
    face_above = faces_zero[5]
    boundary = faces_zero[6]
    index_z = np.arange(depth_cells)[:, None]
    coarse_z = np.arange(half_z)[None, :]
    pair_z = jnp.asarray((index_z // 2 == coarse_z).astype(np.float32))
    odd_z = jnp.asarray((index_z == 2 * coarse_z + 1).astype(np.float32))
    cells = width_x * width_y

    def z_sum(block_in, pick_z):
        flat = block_in.reshape(cells, depth_cells)
        return jnp.dot(flat, pick_z, precision=lax.Precision.HIGH)

    z_parts = jnp.stack(
        [
            z_sum(residual, pair_z),
            z_sum(face_east * crossing[:, None, None], pair_z),
            z_sum(face_north, pair_z),
            z_sum(face_above, odd_z),
            z_sum(boundary, pair_z),
        ]
    )
    index_y = np.arange(width_y)[:, None]
    coarse_y = np.arange(half_y)[None, :]
    pair_y = jnp.asarray((index_y // 2 == coarse_y).astype(np.float32))
    row_y = np.tile(np.arange(width_y), width_x)
    col_slot = np.repeat(np.arange(width_x + 1), half_y)
    col_y = np.tile(np.arange(half_y), width_x + 1)
    row_slot = jnp.repeat(slot_ids + 1, width_y)
    same_slot = row_slot[:, None] == jnp.asarray(col_slot.astype(np.float32))[None, :]
    pair_rows = row_y[:, None] // 2 == col_y[None, :]
    odd_rows = row_y[:, None] == 2 * col_y[None, :] + 1
    spread_map = (same_slot & pair_rows).astype(jnp.float32)
    gather_map = (same_slot.T & pair_rows.T).astype(jnp.float32)
    north_gather = (same_slot.T & odd_rows.T).astype(jnp.float32)
    paired = jnp.dot(
        gather_map,
        jnp.concatenate([z_parts[0], z_parts[1], z_parts[3], z_parts[4]], axis=1),
        precision=lax.Precision.HIGH,
    )
    north_sums = jnp.dot(north_gather, z_parts[2], precision=lax.Precision.HIGH)

    def column(index):
        return paired[:, index * half_z : (index + 1) * half_z]

    slot_sums = jnp.stack([column(0), column(1), north_sums, column(2), column(3)])
    slot_sums = slot_sums.reshape(5, width_x + 1, half_y, half_z)
    coarse = slot_sums[:, 1:]
    edge_sums = slot_sums[:, 0]
    slot_range = jnp.arange(width_x)
    last_slot = (slot_range == count_live - 1).astype(jnp.float32)
    tail_pick = (slot_range[None, :] == count_live - NCS + jnp.arange(NCS)[:, None]).astype(jnp.float32)
    tail_planes = jnp.einsum("ks,qsjl->qkjl", tail_pick, coarse, precision=lax.Precision.HIGH)
    ahead = NCS - 1
    head_planes = jnp.concatenate([coarse[:, :ahead], edge_sums[:, None]], axis=1)
    tail_planes, head_planes = lax.optimization_barrier((tail_planes, head_planes))
    from_prev = passed_along(tail_planes, "slab", 1)
    from_next = passed_along(head_planes, "slab", -1)
    coarse = coarse + from_next[:, ahead][:, None] * last_slot[None, :, None, None]
    prev_last = (jnp.arange(NCS) == NCS - 1).astype(jnp.float32)
    from_prev = from_prev + edge_sums[:, None] * prev_last[None, :, None, None]
    x_ext = jnp.concatenate([from_prev, coarse, jnp.zeros_like(tail_planes)], axis=1)
    wide_range = jnp.arange(width_x + 2 * NCS)[:, None]
    place = (wide_range == NCS + count_live + jnp.arange(ahead)[None, :]).astype(jnp.float32)
    x_ext = x_ext + jnp.einsum("tk,qkjl->qtjl", place, from_next[:, :ahead], precision=lax.Precision.HIGH)
    coarse_rim = NCS
    rim_y = NCS + 1
    rows_axis = ("pencil", "sub")
    from_below = passed_along(x_ext[:, :, half_y - rim_y :], rows_axis, 1)
    from_above = passed_along(x_ext[:, :, : rim_y - 1], rows_axis, -1)
    coef_ext = jnp.concatenate([from_below, x_ext, from_above], axis=2)
    coarse_corr = jnp.zeros((width_x + 2 * NCS, half_y + 2 * rim_y, half_z), jnp.float32)
    for sweep_index in range(NCS):
        out_rim = NCS - 1 - sweep_index
        start_at = coarse_rim - out_rim
        start_y = start_at
        size_x = width_x + 2 * out_rim
        size_y = half_y + 2 * (out_rim + 1)

        def region(offset_x, offset_y):
            return coef_ext[
                :,
                start_at + offset_x : start_at + offset_x + size_x,
                start_y + offset_y : start_y + offset_y + size_y,
            ]

        here_coef = region(0, 0)
        coarse_rhs = here_coef[0]
        coarse_east = here_coef[1]
        coarse_north = here_coef[2]
        coarse_above = here_coef[3]
        coarse_bound = here_coef[4]
        coarse_west = region(-1, 0)[1]
        coarse_south = region(0, -1)[2]
        zero_plane = jnp.zeros_like(coarse_above[:, :, :1])
        coarse_below = jnp.concatenate([zero_plane, coarse_above[:, :, :-1]], axis=2)
        diag_coarse = (
            coarse_east
            + coarse_west
            + coarse_north
            + coarse_south
            + coarse_above
            + coarse_below
            + coarse_bound
        )
        safe_coarse = jnp.where(diag_coarse > 0, diag_coarse, 1.0)
        coarse_center = coarse_corr[1:-1, 1:-1]
        above_vals = jnp.concatenate([coarse_center[:, :, 1:], zero_plane], axis=2)
        below_vals = jnp.concatenate([zero_plane, coarse_center[:, :, :-1]], axis=2)
        beside_all = coarse_east * coarse_corr[2:, 1:-1] + coarse_west * coarse_corr[:-2, 1:-1]
        beside_all = (
            beside_all
            + coarse_north * coarse_corr[1:-1, 2:]
            + coarse_south * coarse_corr[1:-1, :-2]
        )
        beside_all = beside_all + coarse_above * above_vals + coarse_below * below_vals
        coarse_corr = (
            coarse_center
            + OMEGA * (coarse_rhs - (diag_coarse * coarse_center - beside_all)) / safe_coarse
        )
    last_corr = jnp.sum(last_slot[:, None, None] * coarse_corr, axis=0)
    corr_wide = jnp.concatenate([jnp.zeros_like(last_corr)[None], coarse_corr], axis=0)
    corr_core = corr_wide[:, 1 : 1 + half_y]
    corr_z = jnp.dot(
        corr_core.reshape((width_x + 1) * half_y, half_z), pair_z.T, precision=lax.Precision.HIGH
    )
    correction = jnp.dot(spread_map, corr_z, precision=lax.Precision.HIGH)
    correction = correction.reshape(width_x, width_y, depth_cells)
    owner_rows = (slot_ids[:, None] + 1 == jnp.arange(width_x + 1)[None, :]).astype(jnp.float32)

    def rim_rows(coarse_row):
        row_z = jnp.dot(corr_wide[:, coarse_row], pair_z.T, precision=lax.Precision.HIGH)
        row_fine = jnp.dot(owner_rows, row_z, precision=lax.Precision.HIGH)
        return jnp.broadcast_to(row_fine[:, None], (width_x, NU, depth_cells))

    correction = jnp.concatenate([rim_rows(0), correction, rim_rows(half_y + 1)], axis=1)
    base = smooth_rows + correction
    last_z = jnp.dot(last_corr, pair_z.T, precision=lax.Precision.HIGH)
    fine_y = np.arange(width_y + 2 * NU) - NU
    rows_ext = jnp.asarray((fine_y[:, None] // 2 + 1 == np.arange(half_y + 2)[None, :]).astype(np.float32))
    last_fine = jnp.dot(rows_ext, last_z, precision=lax.Precision.HIGH)
    up_block = jnp.concatenate([base[width_x - NU :], last_fine[None]], axis=0)
    below_prev = passed_along(up_block, "slab", 1)
    above_next = passed_along(jnp.concatenate([base[:NU], last_fine[None]], axis=0), "slab", -1)[:NU]
    from_owner = (slot_ids == -1).astype(jnp.float32)
    own = base + from_owner[:, None, None] * below_prev[NU][None]
    next_ids = ext_ids[width_x + 1 :]
    next_in = ext_pos[width_x + 1 :] < plane_count
    to_owner = ((next_ids == local_ids[-1]) & next_in).astype(jnp.float32)
    high_halo = above_next + to_owner[:, None, None] * last_fine[None]
    post_ext = jnp.concatenate([below_prev[:NU], own, high_halo], axis=0)
    return sweeps(post_ext, source_ext, faces_ext, NU, width_x)


def solution(mesh):
    in_specs = (
        P(("real", "slab"), ("pencil", "sub"), None),
        P(("real", "slab"), ("pencil", "sub"), None),
        P(("real", "slab"), ("pencil", "sub"), None),
        P("real"),
    )
    out_specs = P(("real", "slab"), ("pencil", "sub"), None)
    return jax.shard_map(body, mesh=mesh, in_specs=in_specs, out_specs=out_specs, check_vma=False)
```

```python
import numpy as np
import jax
import jax.numpy as jnp
from jax import lax
from jax.sharding import PartitionSpec as P

NU = 2
NCS = 4


OMEGA = 0.8


def padded(array, sides, width):
    for axis, dim in sides:
        count, length = (lax.axis_size(axis), array.shape[dim])
        up = [(i, (i + 1) % count) for i in range(count - 1)]
        down = [(j, i) for i, j in up]
        last = lax.slice_in_dim(array, length - width, length, axis=dim)
        leading = lax.slice_in_dim(array, 0, width, axis=dim)
        before = lax.ppermute(last, axis, up)
        after = lax.ppermute(leading, axis, down)
        array = jnp.concatenate([before, array, after], axis=dim)
    return array


def passed_along(array, axis, by):
    count = lax.axis_size(axis)
    pairs = [(i, i + by) for i in range(count) if 0 <= i + by < count]
    return lax.ppermute(array, axis, pairs)


def harmonic(lower_k, upper_k, inside):
    denom_sum = jnp.where(inside, lower_k + upper_k, 1.0)
    return jnp.where(inside, 2.0 * lower_k * upper_k / denom_sum, 0.0)


def geometry(perm_ext, glob_x, glob_y, inside_x, inside_y, total_x, total_y):
    count_z = perm_ext.shape[2]
    both_x = (inside_x[:-1] & inside_x[1:])[:, None, None] & inside_y[None, :, None]
    both_y = (inside_y[:-1] & inside_y[1:])[None, :, None] & inside_x[:, None, None]
    plane_in = inside_x[:, None, None] & inside_y[None, :, None]
    face_x = harmonic(perm_ext[:-1], perm_ext[1:], both_x)
    face_y = harmonic(perm_ext[:, :-1], perm_ext[:, 1:], both_y)
    face_z = harmonic(perm_ext[:, :, :-1], perm_ext[:, :, 1:], plane_in)
    cell_perm = perm_ext[1:-1, 1:-1]
    face_west = face_x[:-1, 1:-1]
    face_east = face_x[1:, 1:-1]
    face_south = face_y[1:-1, :-1]
    face_north = face_y[1:-1, 1:]
    zero_plane = jnp.zeros_like(cell_perm[:, :, :1])
    face_below = jnp.concatenate([zero_plane, face_z[1:-1, 1:-1]], axis=2)
    face_above = jnp.concatenate([face_z[1:-1, 1:-1], zero_plane], axis=2)
    cell_x = glob_x[1:-1]
    cell_y = glob_y[1:-1]
    index_z = jnp.arange(count_z)
    ends_x = (cell_x == 0).astype(jnp.float32) + (cell_x == total_x - 1).astype(jnp.float32)
    ends_y = (cell_y == 0).astype(jnp.float32) + (cell_y == total_y - 1).astype(jnp.float32)
    ends_z = (index_z == 0).astype(jnp.float32) + (index_z == count_z - 1).astype(jnp.float32)
    edges = ends_x[:, None, None] + ends_y[None, :, None] + ends_z[None, None, :]
    boundary = 2.0 * cell_perm * edges
    diagonal = face_west + face_east + face_south + face_north + face_below + face_above + boundary
    cell_in = plane_in[1:-1, 1:-1]
    safe_diag = jnp.where(cell_in, diagonal, 1.0)
    return (
        face_west,
        face_east,
        face_south,
        face_north,
        face_below,
        face_above,
        boundary,
        safe_diag,
    )


def apply_fine(ext_field, faces_now):
    face_west, face_east, face_south, face_north, face_below, face_above, boundary, safe_diag = (
        faces_now
    )
    center = ext_field[1:-1, 1:-1]
    zero_plane = jnp.zeros_like(center[:, :, :1])
    below_vals = jnp.concatenate([zero_plane, center[:, :, :-1]], axis=2)
    above_vals = jnp.concatenate([center[:, :, 1:], zero_plane], axis=2)
    beside_all = face_west * ext_field[:-2, 1:-1] + face_east * ext_field[2:, 1:-1]
    beside_all = beside_all + face_south * ext_field[1:-1, :-2] + face_north * ext_field[1:-1, 2:]
    beside_all = beside_all + face_below * below_vals + face_above * above_vals
    return (center, safe_diag * center - beside_all)


def crop(array, rim, rim_y=None):
    rim_y = rim if rim_y is None else rim_y
    return array[rim : array.shape[0] - rim, rim_y : array.shape[1] - rim_y]


def sweeps(field_ext, source_ext, faces_ext, count, width):
    def rims(array):
        return (array.shape[0] - width) // 2, (array.shape[1] - width) // 2

    def cut(array, out_x, out_y):
        rim_x, rim_y = rims(array)
        return crop(array, rim_x - out_x, rim_y - out_y)

    for sweep_index in range(count):
        out_x, out_y = (rim - 1 for rim in rims(field_ext))
        faces_now = tuple(cut(member, out_x, out_y) for member in faces_ext)
        center, product = apply_fine(field_ext, faces_now)
        source_now = cut(source_ext, out_x, out_y)
        field_ext = center + OMEGA * (source_now - product) / faces_now[7]
    return field_ext


def body(permeability, source, pressure, aggregate):
    width_x, width_y, depth_cells = permeability.shape
    slab_index = lax.axis_index("slab")
    slab_count = lax.axis_size("slab")
    row_index = lax.axis_index(("pencil", "sub"))
    row_count = lax.axis_size(("pencil", "sub"))
    total_x = width_x * slab_count
    total_y = width_y * row_count
    sides = (("slab", 0), (("pencil", "sub"), 1))
    stacked_sides = (("slab", 1), (("pencil", "sub"), 2))
    fine_rim = 2 * NU
    rim_x = NU + 1
    ext_x = padded(jnp.stack([permeability, source, pressure]), (("slab", 1),), rim_x)
    ext_all = padded(ext_x, ((("pencil", "sub"), 2),), fine_rim)
    perm_ext = ext_all[0]
    source_ext = crop(ext_all[1], 1)
    glob_x = slab_index * width_x - rim_x + jnp.arange(width_x + 2 * rim_x)
    glob_y = row_index * width_y - fine_rim + jnp.arange(width_y + 2 * fine_rim)
    inside_x = (glob_x >= 0) & (glob_x < total_x)
    inside_y = (glob_y >= 0) & (glob_y < total_y)
    faces_ext = geometry(perm_ext, glob_x, glob_y, inside_x, inside_y, total_x, total_y)
    smooth_ext = sweeps(ext_all[2], source_ext, faces_ext, NU, width_x)
    faces_zero = tuple(crop(member, rim_x - 1, fine_rim - 1) for member in faces_ext)
    smooth_rows = smooth_ext[1 : 1 + width_x]
    center, product = apply_fine(crop(smooth_ext, 0, NU - 1), faces_zero)
    residual = source - product
    half_y = width_y // 2
    half_z = depth_cells // 2

    plane_count = aggregate.shape[0]
    ext_pos = slab_index * width_x - 1 + jnp.arange(width_x + 1 + NU)
    pick_ids = ext_pos[:, None] == jnp.arange(plane_count)[None, :]
    ext_ids = jnp.sum(jnp.where(pick_ids, aggregate.astype(jnp.float32)[None, :], 0.0), axis=1)
    local_ids = ext_ids[1 : width_x + 1]
    straddles = (slab_index > 0) & (ext_ids[0] == local_ids[0])
    first_id = local_ids[0] + straddles.astype(jnp.float32)
    count_live = local_ids[-1] - first_id + 1
    slot_ids = local_ids - first_id
    has_next = ext_pos[2 : width_x + 2] < plane_count
    crossing = ((local_ids != ext_ids[2 : width_x + 2]) & has_next).astype(jnp.float32)
    face_east = faces_zero[1]
    face_north = faces_zero[3]
    face_above = faces_zero[5]
    boundary = faces_zero[6]
    index_z = np.arange(depth_cells)[:, None]
    coarse_z = np.arange(half_z)[None, :]
    pair_z = jnp.asarray((index_z // 2 == coarse_z).astype(np.float32))
    odd_z = jnp.asarray((index_z == 2 * coarse_z + 1).astype(np.float32))
    cells = width_x * width_y

    def z_sum(block_in, pick_z):
        flat = block_in.reshape(cells, depth_cells)
        return jnp.dot(flat, pick_z, precision=lax.Precision.HIGH)

    z_parts = jnp.stack(
        [
            z_sum(residual, pair_z),
            z_sum(face_east * crossing[:, None, None], pair_z),
            z_sum(face_north, pair_z),
            z_sum(face_above, odd_z),
            z_sum(boundary, pair_z),
        ]
    )
    index_y = np.arange(width_y)[:, None]
    coarse_y = np.arange(half_y)[None, :]
    pair_y = jnp.asarray((index_y // 2 == coarse_y).astype(np.float32))
    row_y = np.tile(np.arange(width_y), width_x)
    col_slot = np.repeat(np.arange(width_x + 1), half_y)
    col_y = np.tile(np.arange(half_y), width_x + 1)
    row_slot = jnp.repeat(slot_ids + 1, width_y)
    same_slot = row_slot[:, None] == jnp.asarray(col_slot.astype(np.float32))[None, :]
    pair_rows = row_y[:, None] // 2 == col_y[None, :]
    odd_rows = row_y[:, None] == 2 * col_y[None, :] + 1
    spread_map = (same_slot & pair_rows).astype(jnp.float32)
    gather_map = (same_slot.T & pair_rows.T).astype(jnp.float32)
    north_gather = (same_slot.T & odd_rows.T).astype(jnp.float32)
    paired = jnp.dot(
        gather_map,
        jnp.concatenate([z_parts[0], z_parts[1], z_parts[3], z_parts[4]], axis=1),
        precision=lax.Precision.HIGH,
    )
    north_sums = jnp.dot(north_gather, z_parts[2], precision=lax.Precision.HIGH)

    def column(index):
        return paired[:, index * half_z : (index + 1) * half_z]

    slot_sums = jnp.stack([column(0), column(1), north_sums, column(2), column(3)])
    slot_sums = slot_sums.reshape(5, width_x + 1, half_y, half_z)
    coarse = slot_sums[:, 1:]
    edge_sums = slot_sums[:, 0]
    slot_range = jnp.arange(width_x)
    last_slot = (slot_range == count_live - 1).astype(jnp.float32)
    tail_pick = (slot_range[None, :] == count_live - NCS + jnp.arange(NCS)[:, None]).astype(jnp.float32)
    tail_planes = jnp.einsum("ks,qsjl->qkjl", tail_pick, coarse, precision=lax.Precision.HIGH)
    ahead = NCS - 1
    head_planes = jnp.concatenate([coarse[:, :ahead], edge_sums[:, None]], axis=1)
    tail_planes, head_planes = lax.optimization_barrier((tail_planes, head_planes))
    from_prev = passed_along(tail_planes, "slab", 1)
    from_next = passed_along(head_planes, "slab", -1)
    coarse = coarse + from_next[:, ahead][:, None] * last_slot[None, :, None, None]
    prev_last = (jnp.arange(NCS) == NCS - 1).astype(jnp.float32)
    from_prev = from_prev + edge_sums[:, None] * prev_last[None, :, None, None]
    x_ext = jnp.concatenate([from_prev, coarse, jnp.zeros_like(tail_planes)], axis=1)
    wide_range = jnp.arange(width_x + 2 * NCS)[:, None]
    place = (wide_range == NCS + count_live + jnp.arange(ahead)[None, :]).astype(jnp.float32)
    x_ext = x_ext + jnp.einsum("tk,qkjl->qtjl", place, from_next[:, :ahead], precision=lax.Precision.HIGH)
    coarse_rim = NCS
    rim_y = NCS + 1
    rows_axis = ("pencil", "sub")
    from_below = passed_along(x_ext[:, :, half_y - rim_y :], rows_axis, 1)
    from_above = passed_along(x_ext[:, :, : rim_y - 1], rows_axis, -1)
    coef_ext = jnp.concatenate([from_below, x_ext, from_above], axis=2)
    coarse_corr = jnp.zeros((width_x + 2 * NCS, half_y + 2 * rim_y, half_z), jnp.float32)
    for sweep_index in range(NCS):
        out_rim = NCS - 1 - sweep_index
        start_at = coarse_rim - out_rim
        start_y = start_at
        size_x = width_x + 2 * out_rim
        size_y = half_y + 2 * (out_rim + 1)

        def region(offset_x, offset_y):
            return coef_ext[
                :,
                start_at + offset_x : start_at + offset_x + size_x,
                start_y + offset_y : start_y + offset_y + size_y,
            ]

        here_coef = region(0, 0)
        coarse_rhs = here_coef[0]
        coarse_east = here_coef[1]
        coarse_north = here_coef[2]
        coarse_above = here_coef[3]
        coarse_bound = here_coef[4]
        coarse_west = region(-1, 0)[1]
        coarse_south = region(0, -1)[2]
        zero_plane = jnp.zeros_like(coarse_above[:, :, :1])
        coarse_below = jnp.concatenate([zero_plane, coarse_above[:, :, :-1]], axis=2)
        diag_coarse = (
            coarse_east
            + coarse_west
            + coarse_north
            + coarse_south
            + coarse_above
            + coarse_below
            + coarse_bound
        )
        safe_coarse = jnp.where(diag_coarse > 0, diag_coarse, 1.0)
        coarse_center = coarse_corr[1:-1, 1:-1]
        above_vals = jnp.concatenate([coarse_center[:, :, 1:], zero_plane], axis=2)
        below_vals = jnp.concatenate([zero_plane, coarse_center[:, :, :-1]], axis=2)
        beside_all = coarse_east * coarse_corr[2:, 1:-1] + coarse_west * coarse_corr[:-2, 1:-1]
        beside_all = (
            beside_all
            + coarse_north * coarse_corr[1:-1, 2:]
            + coarse_south * coarse_corr[1:-1, :-2]
        )
        beside_all = beside_all + coarse_above * above_vals + coarse_below * below_vals
        coarse_corr = (
            coarse_center
            + OMEGA * (coarse_rhs - (diag_coarse * coarse_center - beside_all)) / safe_coarse
        )
    last_corr = jnp.sum(last_slot[:, None, None] * coarse_corr, axis=0)
    corr_wide = jnp.concatenate([jnp.zeros_like(last_corr)[None], coarse_corr], axis=0)
    corr_core = corr_wide[:, 1 : 1 + half_y]
    corr_z = jnp.dot(
        corr_core.reshape((width_x + 1) * half_y, half_z), pair_z.T, precision=lax.Precision.HIGH
    )
    correction = jnp.dot(spread_map, corr_z, precision=lax.Precision.HIGH)
    correction = correction.reshape(width_x, width_y, depth_cells)
    owner_rows = (slot_ids[:, None] + 1 == jnp.arange(width_x + 1)[None, :]).astype(jnp.float32)

    def rim_rows(coarse_row):
        row_z = jnp.dot(corr_wide[:, coarse_row], pair_z.T, precision=lax.Precision.HIGH)
        row_fine = jnp.dot(owner_rows, row_z, precision=lax.Precision.HIGH)
        return jnp.broadcast_to(row_fine[:, None], (width_x, NU, depth_cells))

    correction = jnp.concatenate([rim_rows(0), correction, rim_rows(half_y + 1)], axis=1)
    base = smooth_rows + correction
    last_z = jnp.dot(last_corr, pair_z.T, precision=lax.Precision.HIGH)
    fine_y = np.arange(width_y + 2 * NU) - NU
    rows_ext = jnp.asarray((fine_y[:, None] // 2 + 1 == np.arange(half_y + 2)[None, :]).astype(np.float32))
    last_fine = jnp.dot(rows_ext, last_z, precision=lax.Precision.HIGH)
    up_block = jnp.concatenate([base[width_x - NU :], last_fine[None]], axis=0)
    below_prev = passed_along(up_block, "slab", 1)
    above_next = passed_along(base[:NU], "slab", -1)
    from_owner = (slot_ids == -1).astype(jnp.float32)
    own = base + from_owner[:, None, None] * below_prev[NU][None]
    next_ids = ext_ids[width_x + 1 :]
    next_in = ext_pos[width_x + 1 :] < plane_count
    to_owner = ((next_ids == local_ids[-1]) & next_in).astype(jnp.float32)
    high_halo = above_next + to_owner[:, None, None] * last_fine[None]
    post_ext = jnp.concatenate([below_prev[:NU], own, high_halo], axis=0)
    return sweeps(post_ext, source_ext, faces_ext, NU, width_x)


def solution(mesh):
    in_specs = (
        P(("real", "slab"), ("pencil", "sub"), None),
        P(("real", "slab"), ("pencil", "sub"), None),
        P(("real", "slab"), ("pencil", "sub"), None),
        P("real"),
    )
    out_specs = P(("real", "slab"), ("pencil", "sub"), None)
    return jax.shard_map(body, mesh=mesh, in_specs=in_specs, out_specs=out_specs, check_vma=False)
```

```python
import numpy as np
import jax
import jax.numpy as jnp
from jax import lax
from jax.sharding import PartitionSpec as P

NU = 2
NCS = 4


OMEGA = 0.8


def padded(array, sides, width):
    for axis, dim in sides:
        count, length = (lax.axis_size(axis), array.shape[dim])
        up = [(i, (i + 1) % count) for i in range(count - 1)]
        down = [(j, i) for i, j in up]
        last = lax.slice_in_dim(array, length - width, length, axis=dim)
        leading = lax.slice_in_dim(array, 0, width, axis=dim)
        before = lax.ppermute(last, axis, up)
        after = lax.ppermute(leading, axis, down)
        array = jnp.concatenate([before, array, after], axis=dim)
    return array


def passed_along(array, axis, by):
    count = lax.axis_size(axis)
    pairs = [(i, i + by) for i in range(count) if 0 <= i + by < count]
    return lax.ppermute(array, axis, pairs)


def harmonic(lower_k, upper_k, inside):
    denom_sum = jnp.where(inside, lower_k + upper_k, 1.0)
    return jnp.where(inside, 2.0 * lower_k * upper_k / denom_sum, 0.0)


def geometry(perm_ext, glob_x, glob_y, inside_x, inside_y, total_x, total_y):
    count_z = perm_ext.shape[2]
    both_x = (inside_x[:-1] & inside_x[1:])[:, None, None] & inside_y[None, :, None]
    both_y = (inside_y[:-1] & inside_y[1:])[None, :, None] & inside_x[:, None, None]
    plane_in = inside_x[:, None, None] & inside_y[None, :, None]
    face_x = harmonic(perm_ext[:-1], perm_ext[1:], both_x)
    face_y = harmonic(perm_ext[:, :-1], perm_ext[:, 1:], both_y)
    face_z = harmonic(perm_ext[:, :, :-1], perm_ext[:, :, 1:], plane_in)
    cell_perm = perm_ext[1:-1, 1:-1]
    face_west = face_x[:-1, 1:-1]
    face_east = face_x[1:, 1:-1]
    face_south = face_y[1:-1, :-1]
    face_north = face_y[1:-1, 1:]
    zero_plane = jnp.zeros_like(cell_perm[:, :, :1])
    face_below = jnp.concatenate([zero_plane, face_z[1:-1, 1:-1]], axis=2)
    face_above = jnp.concatenate([face_z[1:-1, 1:-1], zero_plane], axis=2)
    cell_x = glob_x[1:-1]
    cell_y = glob_y[1:-1]
    index_z = jnp.arange(count_z)
    ends_x = (cell_x == 0).astype(jnp.float32) + (cell_x == total_x - 1).astype(jnp.float32)
    ends_y = (cell_y == 0).astype(jnp.float32) + (cell_y == total_y - 1).astype(jnp.float32)
    ends_z = (index_z == 0).astype(jnp.float32) + (index_z == count_z - 1).astype(jnp.float32)
    edges = ends_x[:, None, None] + ends_y[None, :, None] + ends_z[None, None, :]
    boundary = 2.0 * cell_perm * edges
    diagonal = face_west + face_east + face_south + face_north + face_below + face_above + boundary
    cell_in = plane_in[1:-1, 1:-1]
    safe_diag = jnp.where(cell_in, diagonal, 1.0)
    return (
        face_west,
        face_east,
        face_south,
        face_north,
        face_below,
        face_above,
        boundary,
        safe_diag,
    )


def apply_fine(ext_field, faces_now):
    face_west, face_east, face_south, face_north, face_below, face_above, boundary, safe_diag = (
        faces_now
    )
    center = ext_field[1:-1, 1:-1]
    zero_plane = jnp.zeros_like(center[:, :, :1])
    below_vals = jnp.concatenate([zero_plane, center[:, :, :-1]], axis=2)
    above_vals = jnp.concatenate([center[:, :, 1:], zero_plane], axis=2)
    beside_all = face_west * ext_field[:-2, 1:-1] + face_east * ext_field[2:, 1:-1]
    beside_all = beside_all + face_south * ext_field[1:-1, :-2] + face_north * ext_field[1:-1, 2:]
    beside_all = beside_all + face_below * below_vals + face_above * above_vals
    return (center, safe_diag * center - beside_all)


def crop(array, rim, rim_y=None):
    rim_y = rim if rim_y is None else rim_y
    return array[rim : array.shape[0] - rim, rim_y : array.shape[1] - rim_y]


def sweeps(field_ext, source_ext, faces_ext, count, width):
    def rims(array):
        return (array.shape[0] - width) // 2, (array.shape[1] - width) // 2

    def cut(array, out_x, out_y):
        rim_x, rim_y = rims(array)
        return crop(array, rim_x - out_x, rim_y - out_y)

    for sweep_index in range(count):
        out_x, out_y = (rim - 1 for rim in rims(field_ext))
        faces_now = tuple(cut(member, out_x, out_y) for member in faces_ext)
        center, product = apply_fine(field_ext, faces_now)
        source_now = cut(source_ext, out_x, out_y)
        field_ext = center + OMEGA * (source_now - product) / faces_now[7]
    return field_ext


def body(permeability, source, pressure, aggregate):
    width_x, width_y, depth_cells = permeability.shape
    slab_index = lax.axis_index("slab")
    slab_count = lax.axis_size("slab")
    row_index = lax.axis_index(("pencil", "sub"))
    row_count = lax.axis_size(("pencil", "sub"))
    total_x = width_x * slab_count
    total_y = width_y * row_count
    sides = (("slab", 0), (("pencil", "sub"), 1))
    stacked_sides = (("slab", 1), (("pencil", "sub"), 2))
    fine_rim = 2 * NU
    rim_x = NU + 1
    ext_x = padded(jnp.stack([permeability, source, pressure]), (("slab", 1),), rim_x)
    ext_x, aggregate = lax.optimization_barrier((ext_x, aggregate))
    ext_all = padded(ext_x, ((("pencil", "sub"), 2),), fine_rim)
    perm_ext = ext_all[0]
    source_ext = crop(ext_all[1], 1)
    glob_x = slab_index * width_x - rim_x + jnp.arange(width_x + 2 * rim_x)
    glob_y = row_index * width_y - fine_rim + jnp.arange(width_y + 2 * fine_rim)
    inside_x = (glob_x >= 0) & (glob_x < total_x)
    inside_y = (glob_y >= 0) & (glob_y < total_y)
    faces_ext = geometry(perm_ext, glob_x, glob_y, inside_x, inside_y, total_x, total_y)
    smooth_ext = sweeps(ext_all[2], source_ext, faces_ext, NU, width_x)
    faces_zero = tuple(crop(member, rim_x - 1, fine_rim - 1) for member in faces_ext)
    smooth_rows = smooth_ext[1 : 1 + width_x]
    center, product = apply_fine(crop(smooth_ext, 0, NU - 1), faces_zero)
    residual = source - product
    half_y = width_y // 2
    half_z = depth_cells // 2

    plane_count = aggregate.shape[0]
    ext_pos = slab_index * width_x - 1 + jnp.arange(width_x + 1 + NU)
    pick_ids = ext_pos[:, None] == jnp.arange(plane_count)[None, :]
    ext_ids = jnp.sum(jnp.where(pick_ids, aggregate.astype(jnp.float32)[None, :], 0.0), axis=1)
    local_ids = ext_ids[1 : width_x + 1]
    straddles = (slab_index > 0) & (ext_ids[0] == local_ids[0])
    first_id = local_ids[0] + straddles.astype(jnp.float32)
    count_live = local_ids[-1] - first_id + 1
    slot_ids = local_ids - first_id
    has_next = ext_pos[2 : width_x + 2] < plane_count
    crossing = ((local_ids != ext_ids[2 : width_x + 2]) & has_next).astype(jnp.float32)
    face_east = faces_zero[1]
    face_north = faces_zero[3]
    face_above = faces_zero[5]
    boundary = faces_zero[6]
    index_z = np.arange(depth_cells)[:, None]
    coarse_z = np.arange(half_z)[None, :]
    pair_z = jnp.asarray((index_z // 2 == coarse_z).astype(np.float32))
    odd_z = jnp.asarray((index_z == 2 * coarse_z + 1).astype(np.float32))
    cells = width_x * width_y

    def z_sum(block_in, pick_z):
        flat = block_in.reshape(cells, depth_cells)
        return jnp.dot(flat, pick_z, precision=lax.Precision.HIGH)

    z_parts = jnp.stack(
        [
            z_sum(residual, pair_z),
            z_sum(face_east * crossing[:, None, None], pair_z),
            z_sum(face_north, pair_z),
            z_sum(face_above, odd_z),
            z_sum(boundary, pair_z),
        ]
    )
    index_y = np.arange(width_y)[:, None]
    coarse_y = np.arange(half_y)[None, :]
    pair_y = jnp.asarray((index_y // 2 == coarse_y).astype(np.float32))
    row_y = np.tile(np.arange(width_y), width_x)
    col_slot = np.repeat(np.arange(width_x + 1), half_y)
    col_y = np.tile(np.arange(half_y), width_x + 1)
    row_slot = jnp.repeat(slot_ids + 1, width_y)
    same_slot = row_slot[:, None] == jnp.asarray(col_slot.astype(np.float32))[None, :]
    pair_rows = row_y[:, None] // 2 == col_y[None, :]
    odd_rows = row_y[:, None] == 2 * col_y[None, :] + 1
    spread_map = (same_slot & pair_rows).astype(jnp.float32)
    gather_map = (same_slot.T & pair_rows.T).astype(jnp.float32)
    north_gather = (same_slot.T & odd_rows.T).astype(jnp.float32)
    paired = jnp.dot(
        gather_map,
        jnp.concatenate([z_parts[0], z_parts[1], z_parts[3], z_parts[4]], axis=1),
        precision=lax.Precision.HIGH,
    )
    north_sums = jnp.dot(north_gather, z_parts[2], precision=lax.Precision.HIGH)

    def column(index):
        return paired[:, index * half_z : (index + 1) * half_z]

    slot_sums = jnp.stack([column(0), column(1), north_sums, column(2), column(3)])
    slot_sums = slot_sums.reshape(5, width_x + 1, half_y, half_z)
    coarse = slot_sums[:, 1:]
    edge_sums = slot_sums[:, 0]
    slot_range = jnp.arange(width_x)
    last_slot = (slot_range == count_live - 1).astype(jnp.float32)
    tail_pick = (slot_range[None, :] == count_live - NCS + jnp.arange(NCS)[:, None]).astype(jnp.float32)
    tail_planes = jnp.einsum("ks,qsjl->qkjl", tail_pick, coarse, precision=lax.Precision.HIGH)
    ahead = NCS - 1
    head_planes = jnp.concatenate([coarse[:, :ahead], edge_sums[:, None]], axis=1)
    tail_planes, head_planes = lax.optimization_barrier((tail_planes, head_planes))
    from_prev = passed_along(tail_planes, "slab", 1)
    from_next = passed_along(head_planes, "slab", -1)
    coarse = coarse + from_next[:, ahead][:, None] * last_slot[None, :, None, None]
    prev_last = (jnp.arange(NCS) == NCS - 1).astype(jnp.float32)
    from_prev = from_prev + edge_sums[:, None] * prev_last[None, :, None, None]
    x_ext = jnp.concatenate([from_prev, coarse, jnp.zeros_like(tail_planes[:, :ahead])], axis=1)
    wide_range = jnp.arange(width_x + NCS + ahead)[:, None]
    place = (wide_range == NCS + count_live + jnp.arange(ahead)[None, :]).astype(jnp.float32)
    x_ext = x_ext + jnp.einsum("tk,qkjl->qtjl", place, from_next[:, :ahead], precision=lax.Precision.HIGH)
    coarse_rim = NCS
    rim_y = NCS + 1
    rows_axis = ("pencil", "sub")
    from_below = passed_along(x_ext[:, :, half_y - rim_y :], rows_axis, 1)
    from_above = passed_along(x_ext[:, :, : rim_y - 1], rows_axis, -1)
    coef_ext = jnp.concatenate([from_below, x_ext, from_above], axis=2)
    coarse_corr = jnp.zeros((width_x + 2 * NCS, half_y + 2 * rim_y, half_z), jnp.float32)
    for sweep_index in range(NCS):
        out_rim = NCS - 1 - sweep_index
        start_at = coarse_rim - out_rim
        start_y = start_at
        size_x = width_x + 2 * out_rim
        size_y = half_y + 2 * (out_rim + 1)

        def region(offset_x, offset_y):
            return coef_ext[
                :,
                start_at + offset_x : start_at + offset_x + size_x,
                start_y + offset_y : start_y + offset_y + size_y,
            ]

        here_coef = region(0, 0)
        coarse_rhs = here_coef[0]
        coarse_east = here_coef[1]
        coarse_north = here_coef[2]
        coarse_above = here_coef[3]
        coarse_bound = here_coef[4]
        coarse_west = region(-1, 0)[1]
        coarse_south = region(0, -1)[2]
        zero_plane = jnp.zeros_like(coarse_above[:, :, :1])
        coarse_below = jnp.concatenate([zero_plane, coarse_above[:, :, :-1]], axis=2)
        diag_coarse = (
            coarse_east
            + coarse_west
            + coarse_north
            + coarse_south
            + coarse_above
            + coarse_below
            + coarse_bound
        )
        safe_coarse = jnp.where(diag_coarse > 0, diag_coarse, 1.0)
        coarse_center = coarse_corr[1:-1, 1:-1]
        above_vals = jnp.concatenate([coarse_center[:, :, 1:], zero_plane], axis=2)
        below_vals = jnp.concatenate([zero_plane, coarse_center[:, :, :-1]], axis=2)
        beside_all = coarse_east * coarse_corr[2:, 1:-1] + coarse_west * coarse_corr[:-2, 1:-1]
        beside_all = (
            beside_all
            + coarse_north * coarse_corr[1:-1, 2:]
            + coarse_south * coarse_corr[1:-1, :-2]
        )
        beside_all = beside_all + coarse_above * above_vals + coarse_below * below_vals
        coarse_corr = (
            coarse_center
            + OMEGA * (coarse_rhs - (diag_coarse * coarse_center - beside_all)) / safe_coarse
        )
    last_corr = jnp.sum(last_slot[:, None, None] * coarse_corr, axis=0)
    corr_wide = jnp.concatenate([jnp.zeros_like(last_corr)[None], coarse_corr], axis=0)
    corr_core = corr_wide[:, 1 : 1 + half_y]
    corr_z = jnp.dot(
        corr_core.reshape((width_x + 1) * half_y, half_z), pair_z.T, precision=lax.Precision.HIGH
    )
    correction = jnp.dot(spread_map, corr_z, precision=lax.Precision.HIGH)
    correction = correction.reshape(width_x, width_y, depth_cells)
    owner_rows = (slot_ids[:, None] + 1 == jnp.arange(width_x + 1)[None, :]).astype(jnp.float32)

    def rim_rows(coarse_row):
        row_z = jnp.dot(corr_wide[:, coarse_row], pair_z.T, precision=lax.Precision.HIGH)
        row_fine = jnp.dot(owner_rows, row_z, precision=lax.Precision.HIGH)
        return jnp.broadcast_to(row_fine[:, None], (width_x, NU, depth_cells))

    correction = jnp.concatenate([rim_rows(0), correction, rim_rows(half_y + 1)], axis=1)
    base = smooth_rows + correction
    last_z = jnp.dot(last_corr, pair_z.T, precision=lax.Precision.HIGH)
    fine_y = np.arange(width_y + 2 * NU) - NU
    rows_ext = jnp.asarray((fine_y[:, None] // 2 + 1 == np.arange(half_y + 2)[None, :]).astype(np.float32))
    last_fine = jnp.dot(rows_ext, last_z, precision=lax.Precision.HIGH)
    up_block = jnp.concatenate([base[width_x - NU :], last_fine[None]], axis=0)
    below_prev = passed_along(up_block, "slab", 1)
    above_next = passed_along(base[:NU], "slab", -1)
    from_owner = (slot_ids == -1).astype(jnp.float32)
    own = base + from_owner[:, None, None] * below_prev[NU][None]
    next_ids = ext_ids[width_x + 1 :]
    next_in = ext_pos[width_x + 1 :] < plane_count
    to_owner = ((next_ids == local_ids[-1]) & next_in).astype(jnp.float32)
    high_halo = above_next + to_owner[:, None, None] * last_fine[None]
    post_ext = jnp.concatenate([below_prev[:NU], own, high_halo], axis=0)
    return sweeps(post_ext, source_ext, faces_ext, NU, width_x)


def solution(mesh):
    in_specs = (
        P(("real", "slab"), ("pencil", "sub"), None),
        P(("real", "slab"), ("pencil", "sub"), None),
        P(("real", "slab"), ("pencil", "sub"), None),
        P("real"),
    )
    out_specs = P(("real", "slab"), ("pencil", "sub"), None)
    return jax.shard_map(body, mesh=mesh, in_specs=in_specs, out_specs=out_specs, check_vma=False)
```
